32 devices in a mesh: groups: 2 (over x), seq: 16 (over z, y, core).
Axes of the slice: x: 2, y: 2, z: 4, core: 2. Of those that a mesh axis runs over, the one named last changes fastest.
Arguments:
- fine_qkv: bfloat16 [16384, 3, 1024], P(('groups', 'seq')), parts along dimension 0, may hold values from -64 to 64
- clip_ids: int32 [4096], P('groups'), parts along dimension 0, may hold values from 0 to 1, never falling along the last dimension, each value on 1 to 1792 neighbouring positions
- w_coarse: bfloat16 [1024, 3, 1024], replicated, may hold values from -16 to 16
- w_out: bfloat16 [1024, 1024], replicated, may hold values from -0.25 to 0.25
Outputs:
- mixed: bfloat16 [16384, 1024], P(('groups', 'seq')), parts along dimension 0
The draws below stay inside these ranges and needn't reach their ends.
There are 2 independent parts, one for each index of `groups`. The reference program is written for one: setup_inputs(seed, part) draws one part's arguments, and reference() takes and returns one part's arrays. A program takes and returns all parts, laid end to end along the dimension named above; an argument that names none is the same for every part. Nothing has to cross between parts.
Inputs may be any that keep to these rules, and one draw needn't show every extreme that they name: clip_ids never falls along the positions; each clip covers 1 to 1792 positions, one exactly 1792.
All inputs are finite; a program needn't handle non-finite values.
Results may differ from the reference program's by a relative error of at most 0.018.
The reference program's roundings to bfloat16 on the way count: a program that leaves them out, or rounds other values in their place, can miss the bound.
Values may be sent and summed in bfloat16 or wider, within the bound.
No kernel may reach another device: no remote copies, remote signals or barrier semaphores. Data moves between devices by JAX's collectives and lax.ppermute only.
A program may use at most 128 MiB of HBM per device.

```python
import math
import jax
import jax.numpy as jnp
import numpy as np
from jax import lax

FHEADS = 16
CHEADS = 8
TOK_DEV = 512
POOL = 4
QUARTERS = 4
FREACH = 2
CREACH = 3
FD = 1024
CW = 1024
SEQ_LEN = 8192
CROWS = 128
COARSE = 2048
CLIPS = 2
CLIP_MOST = 1792


def draw_fine_qkv(key, part):
    base_key = jax.random.fold_in(key, 0)
    base_draw = jax.random.normal(base_key, (SEQ_LEN, 3, FD), jnp.float32)
    spread_by = jnp.array([1.22, 1.22, 4.0], jnp.float32)
    drawn = base_draw * spread_by[None, :, None]
    return drawn.astype(jnp.bfloat16)


def draw_w_coarse(key, part):
    first_key, second_key, third_key = jax.random.split(key, 3)
    spread_qk = 4.8 / jnp.sqrt(jnp.float32(FD))
    spread_v = 8.0 / jnp.sqrt(jnp.float32(FD))
    query_part = jax.random.normal(first_key, (FD, CW), jnp.float32) * spread_qk
    key_part = jax.random.normal(second_key, (FD, CW), jnp.float32) * spread_qk
    value_part = jax.random.normal(third_key, (FD, CW), jnp.float32) * spread_v
    return jnp.stack([query_part, key_part, value_part], axis=1).astype(jnp.bfloat16)


def profile(amount, total, reach, slope):
    portions = [(1 << 20) // math.isqrt(rank ** slope) + 1 for rank in range(2, amount + 1)]
    spare, counts = total - reach - (amount - 1), [1] * (amount - 1)
    while spare > 0:
        free = [i for i in range(amount - 1) if counts[i] < reach]
        mass, remaining = sum([portions[i] for i in free]), spare
        for i in free:
            addition = min(reach - counts[i], max(1, remaining * portions[i] // mass), spare)
            counts[i] = counts[i] + addition
            spare = spare - addition
    return np.array([reach] + counts)


def ragged_sizes(rng, count, total, most, skew):
    if count == 2:
        one = jax.random.randint(rng, (), max(1, total - most), min(most, total - 1) + 1)
        return jnp.stack([one, total - one])
    lengths = jnp.asarray(profile(count, total, most, skew), jnp.int32)
    pairs = (count - 1) // 2
    source_of, receiver = lengths[1:1 + 2 * pairs:2], lengths[2:2 + 2 * pairs:2]
    margin = jnp.minimum(source_of - 1, most - receiver)
    passed = jax.random.randint(jax.random.fold_in(rng, 1), (pairs,), 0, 1 << 20) % (margin + 1)
    lengths = lengths.at[1:1 + 2 * pairs:2].set(source_of - passed).at[2:2 + 2 * pairs:2].set(receiver + passed)
    return lengths[jax.random.permutation(jax.random.fold_in(rng, 2), count)]


def bell_draw(stream_key, shape, scale, limit, kind=jnp.bfloat16):
    values = jax.random.normal(stream_key, shape, jnp.float32) * scale
    return jnp.minimum(jnp.maximum(values, -limit), limit).astype(kind)


def setup_inputs(seed: int = 0, part: int = 0) -> dict:
    streams_of = jax.random.split(jax.random.key(seed), 5)
    part_splits = jax.random.split(jax.random.fold_in(streams_of[4], part), 5)
    return {
        "fine_qkv": draw_fine_qkv(jax.random.fold_in(jax.random.fold_in(streams_of[4], part), 71), part),
        "clip_ids": jnp.searchsorted(jnp.cumsum(ragged_sizes(part_splits[1], CLIPS, COARSE, CLIP_MOST, 0)), jnp.arange(COARSE), side="right").astype(jnp.int32),
        "w_coarse": draw_w_coarse(jax.random.fold_in(streams_of[4], 71), part),
        "w_out": bell_draw(streams_of[3], (CW, FD), (CW // 2) ** -0.5, 0.25),
    }


def attend(queries, key_rows, value_rows, allowed, heads):
    row_count = queries.shape[0]
    feat_width = queries.shape[1]
    head_dim = feat_width // heads
    score_scale = 1.0 / math.sqrt(head_dim)
    query_heads = queries.astype(jnp.float32).reshape(row_count, heads, head_dim)
    key_heads = key_rows.astype(jnp.float32).reshape(key_rows.shape[0], heads, head_dim)
    value_heads = value_rows.astype(jnp.float32).reshape(value_rows.shape[0], heads, head_dim)
    scores = jnp.einsum('rhd,khd->hrk', query_heads, key_heads) * score_scale
    masked = jnp.where(allowed[None], scores, -1e+30)
    row_top = lax.optimization_barrier(jnp.max(masked, axis=2, keepdims=True))
    weights = jnp.where(allowed[None], jnp.exp(masked - row_top), 0.0)
    row_total = lax.optimization_barrier(jnp.sum(weights, axis=2))
    rounded = lax.optimization_barrier(weights.astype(jnp.bfloat16)).astype(jnp.float32)
    summed = jnp.einsum('hrk,khd->rhd', rounded, value_heads)
    return (summed / jnp.transpose(row_total)[:, :, None]).reshape(row_count, feat_width).astype(jnp.bfloat16)

def reference(fine_qkv, clip_ids, w_coarse, w_out):
    seq_len = fine_qkv.shape[0]
    feat_width = fine_qkv.shape[2]
    coarse_len = clip_ids.shape[0]
    fine_pad = FREACH * TOK_DEV
    queries = fine_qkv[:, 0]
    key_rows = jnp.concatenate([jnp.zeros((fine_pad, feat_width), jnp.bfloat16), fine_qkv[:, 1]], axis=0)
    value_rows = jnp.concatenate([jnp.zeros((fine_pad, feat_width), jnp.bfloat16), fine_qkv[:, 2]], axis=0)
    token_clip = jnp.repeat(clip_ids, POOL)
    clip_front = jnp.concatenate([jnp.full((fine_pad,), -1, jnp.int32), token_clip])

    def fine_block(block_index):
        block_start = (block_index * TOK_DEV).astype(jnp.int32)
        block_queries = lax.dynamic_slice_in_dim(queries, block_start, TOK_DEV, 0)
        block_keys = lax.dynamic_slice_in_dim(key_rows, block_start, (FREACH + 1) * TOK_DEV, 0)
        block_values = lax.dynamic_slice_in_dim(value_rows, block_start, (FREACH + 1) * TOK_DEV, 0)
        query_clip = lax.dynamic_slice_in_dim(token_clip, block_start, TOK_DEV, 0)
        key_clip = lax.dynamic_slice_in_dim(clip_front, block_start, (FREACH + 1) * TOK_DEV, 0)
        query_pos = jnp.arange(TOK_DEV, dtype=jnp.int32) + fine_pad
        key_pos = jnp.arange((FREACH + 1) * TOK_DEV, dtype=jnp.int32)
        allowed = (key_pos[None, :] <= query_pos[:, None]) & (key_clip[None, :] == query_clip[:, None])
        return attend(block_queries, block_keys, block_values, allowed, FHEADS)
    fine_out = lax.map(fine_block, jnp.arange(seq_len // TOK_DEV, dtype=jnp.int32)).reshape(seq_len, feat_width)
    pooled = lax.optimization_barrier(jnp.mean(fine_out.astype(jnp.float32).reshape(coarse_len, POOL, feat_width), axis=1)).astype(jnp.bfloat16)
    projected = [jnp.dot(pooled, w_coarse[:, member, :], preferred_element_type=jnp.float32).astype(jnp.bfloat16) for member in range(3)]
    coarse_width = w_coarse.shape[2]
    group_rows = QUARTERS * CROWS
    coarse_pad = CREACH * group_rows
    coarse_keys = jnp.concatenate([jnp.zeros((coarse_pad, coarse_width), jnp.bfloat16), projected[1]], axis=0)
    coarse_values = jnp.concatenate([jnp.zeros((coarse_pad, coarse_width), jnp.bfloat16), projected[2]], axis=0)
    clip_back = jnp.concatenate([jnp.full((coarse_pad,), -1, jnp.int32), clip_ids])

    def coarse_block(block_index):
        block_start = (block_index * group_rows).astype(jnp.int32)
        block_queries = lax.dynamic_slice_in_dim(projected[0], block_start, group_rows, 0)
        block_keys = lax.dynamic_slice_in_dim(coarse_keys, block_start, (CREACH + 1) * group_rows, 0)
        block_values = lax.dynamic_slice_in_dim(coarse_values, block_start, (CREACH + 1) * group_rows, 0)
        query_clip = lax.dynamic_slice_in_dim(clip_ids, block_start, group_rows, 0)
        key_clip = lax.dynamic_slice_in_dim(clip_back, block_start, (CREACH + 1) * group_rows, 0)
        query_pos = jnp.arange(group_rows, dtype=jnp.int32) + coarse_pad
        key_pos = jnp.arange((CREACH + 1) * group_rows, dtype=jnp.int32)
        allowed = (key_pos[None, :] <= query_pos[:, None]) & (key_clip[None, :] == query_clip[:, None])
        return attend(block_queries, block_keys, block_values, allowed, CHEADS)
    coarse_att = lax.map(coarse_block, jnp.arange(coarse_len // group_rows, dtype=jnp.int32)).reshape(coarse_len, coarse_width)
    coarse_up = jnp.dot(coarse_att, w_out, preferred_element_type=jnp.float32).astype(jnp.bfloat16)
    previous = jnp.concatenate([jnp.zeros((1, feat_width), jnp.bfloat16), coarse_up[:-1]], axis=0)
    prev_clip = jnp.concatenate([jnp.full((1,), -1, jnp.int32), clip_ids[:-1]])
    joined = prev_clip == clip_ids
    lifted = jnp.where(joined[:, None], previous.astype(jnp.float32), 0.0)
    mixed_rows = fine_out.astype(jnp.float32).reshape(coarse_len, POOL, feat_width) + lifted[:, None, :]
    return mixed_rows.reshape(seq_len, feat_width).astype(jnp.bfloat16)
```

```python
import functools
import math

import jax
import jax.numpy as jnp
from jax import lax
from jax.experimental import pallas as pl
from jax.experimental.pallas import tpu as pltpu
from jax.sharding import PartitionSpec as P

FHEADS = 16
CHEADS = 8
POOL = 4
QUARTERS = 4
FREACH = 2
CREACH = 3
FINE_TILE = 256


def passed_along(value, axis, steps):
    count = lax.axis_size(axis)
    first, last = (max(0, -steps), min(count, count - steps))
    return lax.ppermute(value, axis, [(source, source + steps) for source in range(first, last)])


def within_group(value, axis, shift):
    count = lax.axis_size(axis)
    pairs = []
    for source in range(count):
        base = source - source % QUARTERS
        pairs.append((source, base + (source % QUARTERS + shift) % QUARTERS))
    return lax.ppermute(value, axis, pairs)


def fine_kernel(qclip_ref, kclip0_ref, kclip1_ref, kclip2_ref, q_ref,
                k0_ref, v0_ref, k1_ref, v1_ref, k2_ref, v2_ref, out_ref, *, scale):
    tile = q_ref.shape[0]
    width = q_ref.shape[1]
    half = width // 2
    q = q_ref[...]
    lane = lax.broadcasted_iota(jnp.int32, (1, width), 1)
    low = lane < half
    zero = jnp.zeros_like(q)
    head_q = (jnp.where(low, q, zero), jnp.where(low, zero, q))
    qclip = qclip_ref[...]
    keys = (k0_ref, k1_ref, k2_ref)
    values = (v0_ref, v1_ref, v2_ref)
    clips = (kclip0_ref, kclip1_ref, kclip2_ref)
    seg = k0_ref.shape[0]
    qpos = pl.program_id(1) * tile + lax.broadcasted_iota(jnp.int32, (tile, seg), 0)
    kpos = lax.broadcasted_iota(jnp.int32, (tile, seg), 1)
    masks = []
    for j in range(3):
        allowed = clips[j][...] == qclip
        if j == 2:
            allowed = allowed & (kpos <= qpos)
        masks.append(allowed)
    results = []
    for h in range(2):
        scores = []
        for j in range(3):
            s = lax.dot_general(head_q[h], keys[j][...], (((1,), (1,)), ((), ())),
                                preferred_element_type=jnp.float32) * scale
            scores.append(jnp.where(masks[j], s, -1e30))
        top = jnp.max(scores[0], axis=1, keepdims=True)
        for j in range(1, 3):
            top = jnp.maximum(top, jnp.max(scores[j], axis=1, keepdims=True))
        total = None
        summed = None
        for j in range(3):
            w = jnp.where(masks[j], jnp.exp(scores[j] - top), 0.0)
            part = jnp.sum(w, axis=1, keepdims=True)
            pv = jnp.dot(w.astype(jnp.bfloat16), values[j][...], preferred_element_type=jnp.float32)
            total = part if total is None else total + part
            summed = pv if summed is None else summed + pv
        results.append(summed / total)
    out_ref[...] = jnp.where(low, results[0], results[1]).astype(out_ref.dtype)


def fine_attention(qkv_flat, prev0, prev1, qclip, kclip, heads):
    tok, width3 = qkv_flat.shape
    width = width3 // 3
    head_dim = width // heads
    pair = 2 * head_dim
    pairs = width // pair
    tile = min(FINE_TILE, tok)
    nq = tok // tile
    kernel = functools.partial(fine_kernel, scale=1.0 / math.sqrt(head_dim))
    qspec = pl.BlockSpec((tile, pair), lambda h, i: (i, h))
    own_k = pl.BlockSpec((tok, pair), lambda h, i: (0, pairs + h))
    own_v = pl.BlockSpec((tok, pair), lambda h, i: (0, 2 * pairs + h))
    prev_k = pl.BlockSpec((tok, pair), lambda h, i: (0, h))
    prev_v = pl.BlockSpec((tok, pair), lambda h, i: (0, pairs + h))
    return pl.pallas_call(
        kernel,
        grid=(pairs, nq),
        in_specs=[
            pl.BlockSpec((tile, 1), lambda h, i: (i, 0)),
            pl.BlockSpec((1, tok), lambda h, i: (0, 0)),
            pl.BlockSpec((1, tok), lambda h, i: (0, 1)),
            pl.BlockSpec((1, tok), lambda h, i: (0, 2)),
            qspec, prev_k, prev_v, prev_k, prev_v, own_k, own_v,
        ],
        out_specs=pl.BlockSpec((tile, pair), lambda h, i: (i, h)),
        out_shape=jax.ShapeDtypeStruct((tok, width), jnp.bfloat16),
    )(qclip, kclip, kclip, kclip, qkv_flat, prev0, prev0, prev1, prev1, qkv_flat, qkv_flat)


def attend(queries, key_rows, value_rows, allowed, heads, head_groups):
    row_count = queries.shape[0]
    feat_width = queries.shape[1]
    head_dim = feat_width // heads
    per_group = heads // head_groups
    score_scale = 1.0 / math.sqrt(head_dim)

    def split_heads(source_rows):
        return source_rows.reshape(
            source_rows.shape[0], head_groups, per_group, head_dim
        ).transpose(1, 0, 2, 3)

    def one_group(operands):
        group_queries, group_keys, group_values = operands
        scores = (
            jnp.einsum(
                "rhd,khd->hrk", group_queries, group_keys, preferred_element_type=jnp.float32
            )
            * score_scale
        )
        masked = jnp.where(allowed[None], scores, -1e30)
        row_top = jnp.max(masked, axis=2, keepdims=True)
        weights = jnp.where(allowed[None], jnp.exp(masked - row_top), 0.0)
        row_total = jnp.sum(weights, axis=2)
        summed = jnp.einsum(
            "hrk,khd->rhd",
            weights.astype(jnp.bfloat16),
            group_values,
            preferred_element_type=jnp.float32,
        )
        return summed / jnp.transpose(row_total)[:, :, None]

    results = lax.map(
        one_group, (split_heads(queries), split_heads(key_rows), split_heads(value_rows))
    )
    return results.transpose(1, 0, 2, 3).reshape(row_count, feat_width).astype(jnp.bfloat16)


def body(fine_qkv, clip_ids, w_coarse, w_out):
    tok_count = fine_qkv.shape[0]
    feat_width = fine_qkv.shape[2]
    coarse_rows = tok_count // POOL
    group_rows = QUARTERS * coarse_rows
    position = lax.axis_index("seq")
    quarter = position % QUARTERS
    cycle_place = position // QUARTERS
    qkv_flat = fine_qkv.reshape(tok_count, 3 * feat_width)
    own_pairs = qkv_flat[:, feat_width:]
    prev1 = passed_along(own_pairs, "seq", 1)
    prev0 = passed_along(own_pairs, "seq", 2)
    clip_front = jnp.concatenate([jnp.full((FREACH * coarse_rows,), -1, jnp.int32), clip_ids])
    key_clip = jnp.repeat(
        lax.dynamic_slice_in_dim(clip_front, position * coarse_rows, (FREACH + 1) * coarse_rows, 0),
        POOL,
    )
    own_clip = lax.dynamic_slice_in_dim(clip_ids, position * coarse_rows, coarse_rows, 0)
    query_clip = jnp.repeat(own_clip, POOL)
    fine_out = fine_attention(
        qkv_flat, prev0, prev1, query_clip.reshape(tok_count, 1),
        key_clip.reshape(1, (FREACH + 1) * tok_count), FHEADS,
    )
    pooled = jnp.mean(
        fine_out.astype(jnp.float32).reshape(coarse_rows, POOL, feat_width), axis=1
    ).astype(jnp.bfloat16)
    received = [pooled] + [within_group(pooled, "seq", shift) for shift in range(1, QUARTERS)]
    from_next = jnp.stack([received[0]] + received[:0:-1], axis=0)
    gathered = jnp.roll(from_next, quarter, axis=0).reshape(group_rows, feat_width)
    quarter_width = w_coarse.shape[2] // QUARTERS
    quarter_weight = lax.dynamic_slice_in_dim(w_coarse, quarter * quarter_width, quarter_width, 2)
    projected = jnp.dot(
        gathered,
        quarter_weight.reshape(feat_width, 3 * quarter_width),
        preferred_element_type=jnp.float32,
    )
    projected = projected.astype(jnp.bfloat16).reshape(group_rows, 3, quarter_width)
    coarse_queries = projected[:, 0]
    coarse_pairs = projected[:, 1:3]
    earlier = [passed_along(coarse_pairs, "seq", QUARTERS * hop) for hop in range(CREACH, 0, -1)]
    coarse_window = jnp.concatenate(earlier + [coarse_pairs], axis=0)
    clip_back = jnp.concatenate([jnp.full((CREACH * group_rows,), -1, jnp.int32), clip_ids])
    coarse_key_clip = lax.dynamic_slice_in_dim(
        clip_back, cycle_place * group_rows, (CREACH + 1) * group_rows, 0
    )
    coarse_query_clip = lax.dynamic_slice_in_dim(clip_ids, cycle_place * group_rows, group_rows, 0)
    coarse_qpos = jnp.arange(group_rows, dtype=jnp.int32) + CREACH * group_rows
    coarse_kpos = jnp.arange((CREACH + 1) * group_rows, dtype=jnp.int32)
    coarse_allowed = (coarse_kpos[None, :] <= coarse_qpos[:, None]) & (
        coarse_key_clip[None, :] == coarse_query_clip[:, None]
    )
    coarse_att = attend(
        coarse_queries,
        coarse_window[:, 0],
        coarse_window[:, 1],
        coarse_allowed,
        CHEADS // QUARTERS,
        1,
    )
    row_weight = lax.dynamic_slice_in_dim(w_out, quarter * quarter_width, quarter_width, 0)
    stacked = jnp.dot(coarse_att, row_weight, preferred_element_type=jnp.float32).reshape(
        QUARTERS, coarse_rows, feat_width
    )
    summed_up = lax.dynamic_index_in_dim(stacked, quarter, 0, False)
    for shift in range(1, QUARTERS):
        outgoing = lax.dynamic_index_in_dim(stacked, (quarter + shift) % QUARTERS, 0, False)
        summed_up = summed_up + within_group(outgoing, "seq", shift)
    coarse_up = summed_up.astype(jnp.bfloat16)
    carried = passed_along(coarse_up[-1:], "seq", 1)
    previous = jnp.concatenate([carried, coarse_up[:-1]], axis=0)
    clip_before = jnp.concatenate([jnp.full((1,), -1, jnp.int32), clip_ids])
    prev_clip = lax.dynamic_slice_in_dim(clip_before, position * coarse_rows, coarse_rows, 0)
    joined = prev_clip == own_clip
    lifted = jnp.where(joined[:, None], previous.astype(jnp.float32), 0.0)
    mixed_rows = (
        fine_out.astype(jnp.float32).reshape(coarse_rows, POOL, feat_width) + lifted[:, None, :]
    )
    return mixed_rows.reshape(tok_count, feat_width).astype(jnp.bfloat16)


def solution(mesh):
    return jax.shard_map(
        body,
        mesh=mesh,
        in_specs=(P(("groups", "seq"), None, None), P("groups"), P(), P()),
        out_specs=P(("groups", "seq"), None),
        check_vma=False,
    )
```

```python
import functools
import math

import jax
import jax.numpy as jnp
from jax import lax
from jax.experimental import pallas as pl
from jax.experimental.pallas import tpu as pltpu
from jax.sharding import PartitionSpec as P

FHEADS = 16
CHEADS = 8
POOL = 4
QUARTERS = 4
FREACH = 2
CREACH = 3
FINE_TILE = 256


def passed_along(value, axis, steps):
    count = lax.axis_size(axis)
    first, last = (max(0, -steps), min(count, count - steps))
    return lax.ppermute(value, axis, [(source, source + steps) for source in range(first, last)])


def within_group(value, axis, shift):
    count = lax.axis_size(axis)
    pairs = []
    for source in range(count):
        base = source - source % QUARTERS
        pairs.append((source, base + (source % QUARTERS + shift) % QUARTERS))
    return lax.ppermute(value, axis, pairs)


def fine_kernel(qclip_ref, kclip0_ref, kclip1_ref, kclip2_ref, q_ref,
                k0_ref, v0_ref, k1_ref, v1_ref, k1b_ref, v1b_ref, k2_ref, v2_ref,
                out_ref, pool_ref, *, scale):
    tile = q_ref.shape[0]
    width = q_ref.shape[1]
    half = width // 2
    q = q_ref[...] * jnp.asarray(scale, q_ref.dtype)
    lane = lax.broadcasted_iota(jnp.int32, (1, width), 1)
    low = lane < half
    zero = jnp.zeros_like(q)
    head_q = (jnp.where(low, q, zero), jnp.where(low, zero, q))
    qclip = qclip_ref[...]
    keys = (k0_ref[...], k1_ref[...] + k1b_ref[...], k2_ref[...])
    values = (v0_ref[...], v1_ref[...] + v1b_ref[...], v2_ref[...])
    clips = (kclip0_ref, kclip1_ref, kclip2_ref)
    seg = k0_ref.shape[0]
    qpos = pl.program_id(1) * tile + lax.broadcasted_iota(jnp.int32, (tile, seg), 0)
    kpos = lax.broadcasted_iota(jnp.int32, (tile, seg), 1)
    masks = []
    for j in range(3):
        allowed = clips[j][...] == qclip
        if j == 2:
            allowed = allowed & (kpos <= qpos)
        masks.append(allowed)
    results = []
    for h in range(2):
        scores = []
        for j in range(3):
            s = lax.dot_general(head_q[h], keys[j], (((1,), (1,)), ((), ())),
                                preferred_element_type=jnp.float32)
            scores.append(jnp.where(masks[j], s, -1e30))
        top = jnp.max(scores[0], axis=1, keepdims=True)
        for j in range(1, 3):
            top = jnp.maximum(top, jnp.max(scores[j], axis=1, keepdims=True))
        total = None
        summed = None
        for j in range(3):
            w = jnp.exp(scores[j] - top)
            part = jnp.sum(w, axis=1, keepdims=True)
            pv = jnp.dot(w.astype(jnp.bfloat16), values[j], preferred_element_type=jnp.float32)
            total = part if total is None else total + part
            summed = pv if summed is None else summed + pv
        results.append(summed / total)
    out = jnp.where(low, results[0], results[1]).astype(out_ref.dtype)
    out_ref[...] = out
    rows = tile // POOL
    pool_row = lax.broadcasted_iota(jnp.int32, (rows, tile), 0)
    pool_col = lax.broadcasted_iota(jnp.int32, (rows, tile), 1)
    pool_mat = jnp.where(pool_col // POOL == pool_row, 1.0 / POOL, 0.0).astype(jnp.bfloat16)
    pool_ref[...] = jnp.dot(pool_mat, out, preferred_element_type=jnp.float32).astype(pool_ref.dtype)


def fine_attention(planes, prev0, prev1a, prev1b, qclip, kclip, heads):
    _, tok, width = planes.shape
    head_dim = width // heads
    pair = 2 * head_dim
    pairs = width // pair
    tile = min(FINE_TILE, tok)
    nq = tok // tile
    kernel = functools.partial(fine_kernel, scale=1.0 / math.sqrt(head_dim))

    def plane_spec(plane):
        return pl.BlockSpec((None, tok, pair), lambda h, i: (plane, 0, h))

    return pl.pallas_call(
        kernel,
        grid=(pairs, nq),
        in_specs=[
            pl.BlockSpec((tile, 1), lambda h, i: (i, 0)),
            pl.BlockSpec((1, tok), lambda h, i: (0, 0)),
            pl.BlockSpec((1, tok), lambda h, i: (0, 1)),
            pl.BlockSpec((1, tok), lambda h, i: (0, 2)),
            pl.BlockSpec((None, tile, pair), lambda h, i: (0, i, h)),
            plane_spec(0), plane_spec(1),
            plane_spec(0), plane_spec(1),
            plane_spec(0), plane_spec(1),
            plane_spec(1), plane_spec(2),
        ],
        out_specs=[
            pl.BlockSpec((tile, pair), lambda h, i: (i, h)),
            pl.BlockSpec((tile // POOL, pair), lambda h, i: (i, h)),
        ],
        out_shape=[
            jax.ShapeDtypeStruct((tok, width), jnp.bfloat16),
            jax.ShapeDtypeStruct((tok // POOL, width), jnp.bfloat16),
        ],
    )(qclip, kclip, kclip, kclip, planes, prev0, prev0, prev1a, prev1a, prev1b, prev1b,
      planes, planes)


def mix_kernel(fine_ref, lift_ref, out_ref):
    tile = fine_ref.shape[0]
    rows = lift_ref.shape[0]
    spread_row = lax.broadcasted_iota(jnp.int32, (tile, rows), 0)
    spread_col = lax.broadcasted_iota(jnp.int32, (tile, rows), 1)
    spread = jnp.where(spread_row // POOL == spread_col, 1.0, 0.0).astype(jnp.bfloat16)
    lifted = jnp.dot(spread, lift_ref[...], preferred_element_type=jnp.float32)
    out_ref[...] = (fine_ref[...].astype(jnp.float32) + lifted).astype(out_ref.dtype)


def mix(fine_out, lifted):
    tok, width = fine_out.shape
    tile = min(FINE_TILE, tok)
    return pl.pallas_call(
        mix_kernel,
        grid=(tok // tile,),
        in_specs=[
            pl.BlockSpec((tile, width), lambda i: (i, 0)),
            pl.BlockSpec((tile // POOL, width), lambda i: (i, 0)),
        ],
        out_specs=pl.BlockSpec((tile, width), lambda i: (i, 0)),
        out_shape=jax.ShapeDtypeStruct((tok, width), fine_out.dtype),
    )(fine_out, lifted)


def pair_swap(value, axis, from_odd):
    count = lax.axis_size(axis)
    start = 1 if from_odd else 0
    step = -1 if from_odd else 1
    return lax.ppermute(value, axis, [(source, source + step) for source in range(start, count, 2)])


def attend(queries, key_rows, value_rows, allowed, heads, head_groups):
    row_count = queries.shape[0]
    feat_width = queries.shape[1]
    head_dim = feat_width // heads
    per_group = heads // head_groups
    score_scale = 1.0 / math.sqrt(head_dim)

    def split_heads(source_rows):
        return source_rows.reshape(
            source_rows.shape[0], head_groups, per_group, head_dim
        ).transpose(1, 0, 2, 3)

    def one_group(operands):
        group_queries, group_keys, group_values = operands
        scores = (
            jnp.einsum(
                "rhd,khd->hrk", group_queries, group_keys, preferred_element_type=jnp.float32
            )
            * score_scale
        )
        masked = jnp.where(allowed[None], scores, -1e30)
        row_top = jnp.max(masked, axis=2, keepdims=True)
        weights = jnp.where(allowed[None], jnp.exp(masked - row_top), 0.0)
        row_total = jnp.sum(weights, axis=2)
        summed = jnp.einsum(
            "hrk,khd->rhd",
            weights.astype(jnp.bfloat16),
            group_values,
            preferred_element_type=jnp.float32,
        )
        return summed / jnp.transpose(row_total)[:, :, None]

    results = lax.map(
        one_group, (split_heads(queries), split_heads(key_rows), split_heads(value_rows))
    )
    return results.transpose(1, 0, 2, 3).reshape(row_count, feat_width).astype(jnp.bfloat16)


def body(fine_qkv, clip_ids, w_coarse, w_out):
    tok_count = fine_qkv.shape[0]
    feat_width = fine_qkv.shape[2]
    coarse_rows = tok_count // POOL
    group_rows = QUARTERS * coarse_rows
    position = lax.axis_index("seq")
    quarter = position % QUARTERS
    cycle_place = position // QUARTERS
    planes = jnp.transpose(fine_qkv, (1, 0, 2))
    own_pairs = planes[1:]
    prev0 = passed_along(own_pairs, "seq", 2)
    prev1a = pair_swap(own_pairs, "seq", False)
    prev1b = pair_swap(prev0, "seq", True)
    clip_front = jnp.concatenate([jnp.full((FREACH * coarse_rows,), -1, jnp.int32), clip_ids])
    key_clip = jnp.repeat(
        lax.dynamic_slice_in_dim(clip_front, position * coarse_rows, (FREACH + 1) * coarse_rows, 0),
        POOL,
    )
    own_clip = lax.dynamic_slice_in_dim(clip_ids, position * coarse_rows, coarse_rows, 0)
    query_clip = jnp.repeat(own_clip, POOL)
    fine_out, pooled = fine_attention(
        planes, prev0, prev1a, prev1b, query_clip.reshape(tok_count, 1),
        key_clip.reshape(1, (FREACH + 1) * tok_count), FHEADS,
    )
    received = [pooled] + [within_group(pooled, "seq", shift) for shift in range(1, QUARTERS)]
    from_next = jnp.stack([received[0]] + received[:0:-1], axis=0)
    gathered = jnp.roll(from_next, quarter, axis=0).reshape(group_rows, feat_width)
    quarter_width = w_coarse.shape[2] // QUARTERS
    quarter_weight = lax.dynamic_slice_in_dim(w_coarse, quarter * quarter_width, quarter_width, 2)
    projected = jnp.dot(
        gathered,
        quarter_weight.reshape(feat_width, 3 * quarter_width),
        preferred_element_type=jnp.float32,
    )
    projected = projected.astype(jnp.bfloat16).reshape(group_rows, 3, quarter_width)
    coarse_queries = projected[:, 0]
    coarse_pairs = projected[:, 1:3]
    earlier = [passed_along(coarse_pairs, "seq", QUARTERS * hop) for hop in range(CREACH, 0, -1)]
    coarse_window = jnp.concatenate(earlier + [coarse_pairs], axis=0)
    clip_back = jnp.concatenate([jnp.full((CREACH * group_rows,), -1, jnp.int32), clip_ids])
    coarse_key_clip = lax.dynamic_slice_in_dim(
        clip_back, cycle_place * group_rows, (CREACH + 1) * group_rows, 0
    )
    coarse_query_clip = lax.dynamic_slice_in_dim(clip_ids, cycle_place * group_rows, group_rows, 0)
    coarse_qpos = jnp.arange(group_rows, dtype=jnp.int32) + CREACH * group_rows
    coarse_kpos = jnp.arange((CREACH + 1) * group_rows, dtype=jnp.int32)
    coarse_allowed = (coarse_kpos[None, :] <= coarse_qpos[:, None]) & (
        coarse_key_clip[None, :] == coarse_query_clip[:, None]
    )
    coarse_att = attend(
        coarse_queries,
        coarse_window[:, 0],
        coarse_window[:, 1],
        coarse_allowed,
        CHEADS // QUARTERS,
        1,
    )
    row_weight = lax.dynamic_slice_in_dim(w_out, quarter * quarter_width, quarter_width, 0)
    stacked = jnp.dot(coarse_att, row_weight, preferred_element_type=jnp.float32).reshape(
        QUARTERS, coarse_rows, feat_width
    )
    summed_up = lax.dynamic_index_in_dim(stacked, quarter, 0, False)
    for shift in range(1, QUARTERS):
        outgoing = lax.dynamic_index_in_dim(stacked, (quarter + shift) % QUARTERS, 0, False)
        summed_up = summed_up + within_group(outgoing, "seq", shift)
    coarse_up = summed_up.astype(jnp.bfloat16)
    carried = passed_along(coarse_up[-1:], "seq", 1)
    previous = jnp.concatenate([carried, coarse_up[:-1]], axis=0)
    clip_before = jnp.concatenate([jnp.full((1,), -1, jnp.int32), clip_ids])
    prev_clip = lax.dynamic_slice_in_dim(clip_before, position * coarse_rows, coarse_rows, 0)
    joined = prev_clip == own_clip
    lifted = jnp.where(joined[:, None], previous, jnp.zeros_like(previous))
    return mix(fine_out, lifted)


def solution(mesh):
    return jax.shard_map(
        body,
        mesh=mesh,
        in_specs=(P(("groups", "seq"), None, None), P("groups"), P(), P()),
        out_specs=P(("groups", "seq"), None),
        check_vma=False,
    )
```

```python
import functools
import math

import jax
import jax.numpy as jnp
from jax import lax
from jax.experimental import pallas as pl
from jax.experimental.pallas import tpu as pltpu
from jax.sharding import PartitionSpec as P

FHEADS = 16
CHEADS = 8
POOL = 4
QUARTERS = 4
FREACH = 2
CREACH = 3
FINE_TILE = 256


def passed_along(value, axis, steps):
    count = lax.axis_size(axis)
    first, last = (max(0, -steps), min(count, count - steps))
    return lax.ppermute(value, axis, [(source, source + steps) for source in range(first, last)])


def within_group(value, axis, shift):
    count = lax.axis_size(axis)
    pairs = []
    for source in range(count):
        base = source - source % QUARTERS
        pairs.append((source, base + (source % QUARTERS + shift) % QUARTERS))
    return lax.ppermute(value, axis, pairs)


def fine_kernel(qclip_ref, kclip0_ref, kclip1_ref, kclip2_ref, q_ref,
                k0_ref, v0_ref, k1_ref, v1_ref, k1b_ref, v1b_ref, k2_ref, v2_ref,
                out_ref, pool_ref, *, scale):
    tile = q_ref.shape[0]
    width = q_ref.shape[1]
    half = width // 2
    q = q_ref[...] * jnp.asarray(scale, q_ref.dtype)
    lane = lax.broadcasted_iota(jnp.int32, (1, width), 1)
    low = lane < half
    zero = jnp.zeros_like(q)
    head_q = (jnp.where(low, q, zero), jnp.where(low, zero, q))
    qclip = qclip_ref[...]
    keys = (k0_ref[...], k1_ref[...] + k1b_ref[...], k2_ref[...])
    values = (v0_ref[...], v1_ref[...] + v1b_ref[...], v2_ref[...])
    clips = (kclip0_ref, kclip1_ref, kclip2_ref)
    seg = k0_ref.shape[0]
    qpos = pl.program_id(1) * tile + lax.broadcasted_iota(jnp.int32, (tile, seg), 0)
    kpos = lax.broadcasted_iota(jnp.int32, (tile, seg), 1)
    masks = []
    for j in range(3):
        allowed = clips[j][...] == qclip
        if j == 2:
            allowed = allowed & (kpos <= qpos)
        masks.append(allowed)
    results = []
    for h in range(2):
        scores = []
        for j in range(3):
            s = lax.dot_general(head_q[h], keys[j], (((1,), (1,)), ((), ())),
                                preferred_element_type=jnp.float32)
            scores.append(jnp.where(masks[j], s, -1e30))
        top = jnp.max(scores[0], axis=1, keepdims=True)
        for j in range(1, 3):
            top = jnp.maximum(top, jnp.max(scores[j], axis=1, keepdims=True))
        total = None
        summed = None
        for j in range(3):
            w = jnp.exp(scores[j] - top)
            part = jnp.sum(w, axis=1, keepdims=True)
            pv = jnp.dot(w.astype(jnp.bfloat16), values[j], preferred_element_type=jnp.float32)
            total = part if total is None else total + part
            summed = pv if summed is None else summed + pv
        results.append(summed / total)
    out = jnp.where(low, results[0], results[1]).astype(out_ref.dtype)
    out_ref[...] = out
    rows = tile // POOL
    pool_row = lax.broadcasted_iota(jnp.int32, (rows, tile), 0)
    pool_col = lax.broadcasted_iota(jnp.int32, (rows, tile), 1)
    pool_mat = jnp.where(pool_col // POOL == pool_row, 1.0 / POOL, 0.0).astype(jnp.bfloat16)
    pool_ref[...] = jnp.dot(pool_mat, out, preferred_element_type=jnp.float32).astype(pool_ref.dtype)


def fine_attention(planes, prev0, prev1a, prev1b, qclip, kclip, heads):
    _, tok, width = planes.shape
    head_dim = width // heads
    pair = 2 * head_dim
    pairs = width // pair
    tile = min(FINE_TILE, tok)
    nq = tok // tile
    kernel = functools.partial(fine_kernel, scale=1.0 / math.sqrt(head_dim))

    def plane_spec(plane):
        return pl.BlockSpec((None, tok, pair), lambda h, i: (plane, 0, h))

    return pl.pallas_call(
        kernel,
        grid=(pairs, nq),
        in_specs=[
            pl.BlockSpec((tile, 1), lambda h, i: (i, 0)),
            pl.BlockSpec((1, tok), lambda h, i: (0, 0)),
            pl.BlockSpec((1, tok), lambda h, i: (0, 1)),
            pl.BlockSpec((1, tok), lambda h, i: (0, 2)),
            pl.BlockSpec((None, tile, pair), lambda h, i: (0, i, h)),
            plane_spec(0), plane_spec(1),
            plane_spec(0), plane_spec(1),
            plane_spec(0), plane_spec(1),
            plane_spec(1), plane_spec(2),
        ],
        out_specs=[
            pl.BlockSpec((tile, pair), lambda h, i: (i, h)),
            pl.BlockSpec((tile // POOL, pair), lambda h, i: (i, h)),
        ],
        out_shape=[
            jax.ShapeDtypeStruct((tok, width), jnp.bfloat16),
            jax.ShapeDtypeStruct((tok // POOL, width), jnp.bfloat16),
        ],
    )(qclip, kclip, kclip, kclip, planes, prev0, prev0, prev1a, prev1a, prev1b, prev1b,
      planes, planes)


def mix_kernel(fine_ref, lift_ref, out_ref):
    tile = fine_ref.shape[0]
    rows = lift_ref.shape[0]
    spread_row = lax.broadcasted_iota(jnp.int32, (tile, rows), 0)
    spread_col = lax.broadcasted_iota(jnp.int32, (tile, rows), 1)
    spread = jnp.where(spread_row // POOL == spread_col, 1.0, 0.0).astype(jnp.bfloat16)
    lifted = jnp.dot(spread, lift_ref[...], preferred_element_type=jnp.float32)
    out_ref[...] = (fine_ref[...].astype(jnp.float32) + lifted).astype(out_ref.dtype)


def mix(fine_out, lifted):
    tok, width = fine_out.shape
    tile = min(FINE_TILE, tok)
    return pl.pallas_call(
        mix_kernel,
        grid=(tok // tile,),
        in_specs=[
            pl.BlockSpec((tile, width), lambda i: (i, 0)),
            pl.BlockSpec((tile // POOL, width), lambda i: (i, 0)),
        ],
        out_specs=pl.BlockSpec((tile, width), lambda i: (i, 0)),
        out_shape=jax.ShapeDtypeStruct((tok, width), fine_out.dtype),
    )(fine_out, lifted)


def pair_swap(value, axis, from_odd):
    count = lax.axis_size(axis)
    start = 1 if from_odd else 0
    step = -1 if from_odd else 1
    return lax.ppermute(value, axis, [(source, source + step) for source in range(start, count, 2)])


def coarse_kernel(qclip_ref, kc0_ref, kc1_ref, kc2_ref, kc3_ref, q_ref,
                  k0_ref, v0_ref, k1_ref, v1_ref, k2_ref, v2_ref, k3_ref, v3_ref,
                  out_ref, *, scale):
    tile = q_ref.shape[0]
    seg = k0_ref.shape[0]
    q = q_ref[...]
    qclip = qclip_ref[...]
    keys = (k0_ref, k1_ref, k2_ref, k3_ref)
    values = (v0_ref, v1_ref, v2_ref, v3_ref)
    clips = (kc0_ref, kc1_ref, kc2_ref, kc3_ref)
    qpos = pl.program_id(1) * tile + lax.broadcasted_iota(jnp.int32, (tile, seg), 0)
    kpos = lax.broadcasted_iota(jnp.int32, (tile, seg), 1)
    last = len(keys) - 1
    scores = []
    masks = []
    for j in range(len(keys)):
        allowed = clips[j][...] == qclip
        if j == last:
            allowed = allowed & (kpos <= qpos)
        s = lax.dot_general(q, keys[j][...], (((1,), (1,)), ((), ())),
                            preferred_element_type=jnp.float32) * scale
        scores.append(jnp.where(allowed, s, -1e30))
    top = jnp.max(scores[0], axis=1, keepdims=True)
    for j in range(1, len(keys)):
        top = jnp.maximum(top, jnp.max(scores[j], axis=1, keepdims=True))
    total = None
    summed = None
    for j in range(len(keys)):
        w = jnp.exp(scores[j] - top)
        part = jnp.sum(w, axis=1, keepdims=True)
        pv = jnp.dot(w.astype(jnp.bfloat16), values[j][...], preferred_element_type=jnp.float32)
        total = part if total is None else total + part
        summed = pv if summed is None else summed + pv
    out_ref[...] = (summed / total).astype(out_ref.dtype)


def coarse_attention(queries, windows, qclip, kclip, heads):
    rows, width = queries.shape
    head_dim = width // heads
    tile = min(FINE_TILE, rows)
    seg = windows[0].shape[1]
    kernel = functools.partial(coarse_kernel, scale=1.0 / math.sqrt(head_dim))
    clip_specs = [pl.BlockSpec((1, seg), functools.partial(lambda j, h, i: (0, j), j))
                  for j in range(len(windows))]
    kv_specs = []
    kv_args = []
    for window in windows:
        kv_specs.append(pl.BlockSpec((None, seg, head_dim), lambda h, i: (0, 0, h)))
        kv_specs.append(pl.BlockSpec((None, seg, head_dim), lambda h, i: (1, 0, h)))
        kv_args += [window, window]
    return pl.pallas_call(
        kernel,
        grid=(heads, rows // tile),
        in_specs=[pl.BlockSpec((tile, 1), lambda h, i: (i, 0))] + clip_specs
        + [pl.BlockSpec((tile, head_dim), lambda h, i: (i, h))] + kv_specs,
        out_specs=pl.BlockSpec((tile, head_dim), lambda h, i: (i, h)),
        out_shape=jax.ShapeDtypeStruct((rows, width), jnp.bfloat16),
    )(qclip, *([kclip] * len(windows)), queries, *kv_args)


def group_order(parts, quarter):
    ordered = jnp.stack([parts[0]] + parts[:0:-1], axis=0)
    return jnp.roll(ordered, quarter, axis=0)


def attend(queries, key_rows, value_rows, allowed, heads, head_groups):
    row_count = queries.shape[0]
    feat_width = queries.shape[1]
    head_dim = feat_width // heads
    per_group = heads // head_groups
    score_scale = 1.0 / math.sqrt(head_dim)

    def split_heads(source_rows):
        return source_rows.reshape(
            source_rows.shape[0], head_groups, per_group, head_dim
        ).transpose(1, 0, 2, 3)

    def one_group(operands):
        group_queries, group_keys, group_values = operands
        scores = (
            jnp.einsum(
                "rhd,khd->hrk", group_queries, group_keys, preferred_element_type=jnp.float32
            )
            * score_scale
        )
        masked = jnp.where(allowed[None], scores, -1e30)
        row_top = jnp.max(masked, axis=2, keepdims=True)
        weights = jnp.where(allowed[None], jnp.exp(masked - row_top), 0.0)
        row_total = jnp.sum(weights, axis=2)
        summed = jnp.einsum(
            "hrk,khd->rhd",
            weights.astype(jnp.bfloat16),
            group_values,
            preferred_element_type=jnp.float32,
        )
        return summed / jnp.transpose(row_total)[:, :, None]

    results = lax.map(
        one_group, (split_heads(queries), split_heads(key_rows), split_heads(value_rows))
    )
    return results.transpose(1, 0, 2, 3).reshape(row_count, feat_width).astype(jnp.bfloat16)


def body(fine_qkv, clip_ids, w_coarse, w_out):
    tok_count = fine_qkv.shape[0]
    feat_width = fine_qkv.shape[2]
    coarse_rows = tok_count // POOL
    group_rows = QUARTERS * coarse_rows
    position = lax.axis_index("seq")
    quarter = position % QUARTERS
    cycle_place = position // QUARTERS
    planes = jnp.transpose(fine_qkv, (1, 0, 2))
    own_pairs = planes[1:]
    prev0 = passed_along(own_pairs, "seq", 2)
    prev1a = pair_swap(own_pairs, "seq", False)
    prev1b = pair_swap(prev0, "seq", True)
    clip_front = jnp.concatenate([jnp.full((FREACH * coarse_rows,), -1, jnp.int32), clip_ids])
    key_clip = jnp.repeat(
        lax.dynamic_slice_in_dim(clip_front, position * coarse_rows, (FREACH + 1) * coarse_rows, 0),
        POOL,
    )
    own_clip = lax.dynamic_slice_in_dim(clip_ids, position * coarse_rows, coarse_rows, 0)
    query_clip = jnp.repeat(own_clip, POOL)
    fine_out, pooled = fine_attention(
        planes, prev0, prev1a, prev1b, query_clip.reshape(tok_count, 1),
        key_clip.reshape(1, (FREACH + 1) * tok_count), FHEADS,
    )
    quarter_width = w_coarse.shape[2] // QUARTERS
    wplanes = jnp.transpose(w_coarse, (1, 0, 2))
    projected = jnp.einsum(
        "rd,mdc->mrc", pooled, wplanes, preferred_element_type=jnp.float32
    ).astype(jnp.bfloat16)
    pieces = []
    for shift in range(QUARTERS):
        piece = lax.dynamic_slice_in_dim(
            projected, ((quarter + shift) % QUARTERS) * quarter_width, quarter_width, 2
        )
        pieces.append(piece if shift == 0 else within_group(piece, "seq", shift))
    grouped = group_order(pieces, quarter)
    grouped = jnp.transpose(grouped, (1, 0, 2, 3)).reshape(3, group_rows, quarter_width)
    coarse_queries = grouped[0]
    coarse_pairs = grouped[1:]
    earlier = [passed_along(coarse_pairs, "seq", QUARTERS * hop) for hop in range(CREACH, 0, -1)]
    clip_back = jnp.concatenate([jnp.full((CREACH * group_rows,), -1, jnp.int32), clip_ids])
    coarse_key_clip = lax.dynamic_slice_in_dim(
        clip_back, cycle_place * group_rows, (CREACH + 1) * group_rows, 0
    )
    coarse_query_clip = lax.dynamic_slice_in_dim(clip_ids, cycle_place * group_rows, group_rows, 0)
    coarse_att = coarse_attention(
        coarse_queries, earlier + [coarse_pairs], coarse_query_clip.reshape(group_rows, 1),
        coarse_key_clip.reshape(1, (CREACH + 1) * group_rows), CHEADS // QUARTERS,
    )
    shares = []
    for shift in range(QUARTERS):
        share = lax.dynamic_slice_in_dim(
            coarse_att, ((quarter + shift) % QUARTERS) * coarse_rows, coarse_rows, 0
        )
        shares.append(share if shift == 0 else within_group(share, "seq", shift))
    att_rows = jnp.transpose(group_order(shares, quarter), (1, 0, 2)).reshape(
        coarse_rows, QUARTERS * quarter_width
    )
    coarse_up = jnp.dot(att_rows, w_out, preferred_element_type=jnp.float32).astype(jnp.bfloat16)
    carried = passed_along(coarse_up[-1:], "seq", 1)
    previous = jnp.concatenate([carried, coarse_up[:-1]], axis=0)
    clip_before = jnp.concatenate([jnp.full((1,), -1, jnp.int32), clip_ids])
    prev_clip = lax.dynamic_slice_in_dim(clip_before, position * coarse_rows, coarse_rows, 0)
    joined = prev_clip == own_clip
    lifted = jnp.where(joined[:, None], previous, jnp.zeros_like(previous))
    return mix(fine_out, lifted)


def solution(mesh):
    return jax.shard_map(
        body,
        mesh=mesh,
        in_specs=(P(("groups", "seq"), None, None), P("groups"), P(), P()),
        out_specs=P(("groups", "seq"), None),
        check_vma=False,
    )
```

```python
import functools
import math

import jax
import jax.numpy as jnp
from jax import lax
from jax.experimental import pallas as pl
from jax.experimental.pallas import tpu as pltpu
from jax.sharding import PartitionSpec as P

FHEADS = 16
CHEADS = 8
POOL = 4
QUARTERS = 4
FREACH = 2
CREACH = 3
FINE_TILE = 256


def passed_along(value, axis, steps):
    count = lax.axis_size(axis)
    first, last = (max(0, -steps), min(count, count - steps))
    return lax.ppermute(value, axis, [(source, source + steps) for source in range(first, last)])


def within_group(value, axis, shift):
    count = lax.axis_size(axis)
    pairs = []
    for source in range(count):
        base = source - source % QUARTERS
        pairs.append((source, base + (source % QUARTERS + shift) % QUARTERS))
    return lax.ppermute(value, axis, pairs)


def fine_kernel(qclip_ref, kclip0_ref, kclip1_ref, kclip2_ref, q_ref,
                k0_ref, v0_ref, k1_ref, v1_ref, k1b_ref, v1b_ref, k2_ref, v2_ref,
                out_ref, pool_ref, *, scale):
    tile = q_ref.shape[0]
    width = q_ref.shape[1]
    half = width // 2
    q = q_ref[...] * jnp.asarray(scale, q_ref.dtype)
    lane = lax.broadcasted_iota(jnp.int32, (1, width), 1)
    low = lane < half
    zero = jnp.zeros_like(q)
    head_q = (jnp.where(low, q, zero), jnp.where(low, zero, q))
    qclip = qclip_ref[...]
    keys = (k0_ref[...], k1_ref[...] + k1b_ref[...], k2_ref[...])
    values = (v0_ref[...], v1_ref[...] + v1b_ref[...], v2_ref[...])
    clips = (kclip0_ref, kclip1_ref, kclip2_ref)
    seg = k0_ref.shape[0]
    qpos = pl.program_id(1) * tile + lax.broadcasted_iota(jnp.int32, (tile, seg), 0)
    kpos = lax.broadcasted_iota(jnp.int32, (tile, seg), 1)
    masks = []
    for j in range(3):
        allowed = clips[j][...] == qclip
        if j == 2:
            allowed = allowed & (kpos <= qpos)
        masks.append(allowed)
    results = []
    for h in range(2):
        scores = []
        for j in range(3):
            s = lax.dot_general(head_q[h], keys[j], (((1,), (1,)), ((), ())),
                                preferred_element_type=jnp.float32)
            scores.append(jnp.where(masks[j], s, -1e30))
        top = jnp.max(scores[0], axis=1, keepdims=True)
        for j in range(1, 3):
            top = jnp.maximum(top, jnp.max(scores[j], axis=1, keepdims=True))
        total = None
        summed = None
        for j in range(3):
            w = jnp.exp(scores[j] - top)
            part = jnp.sum(w, axis=1, keepdims=True)
            pv = jnp.dot(w.astype(jnp.bfloat16), values[j], preferred_element_type=jnp.float32)
            total = part if total is None else total + part
            summed = pv if summed is None else summed + pv
        results.append(summed / total)
    out = jnp.where(low, results[0], results[1]).astype(out_ref.dtype)
    out_ref[...] = out
    rows = tile // POOL
    pool_row = lax.broadcasted_iota(jnp.int32, (rows, tile), 0)
    pool_col = lax.broadcasted_iota(jnp.int32, (rows, tile), 1)
    pool_mat = jnp.where(pool_col // POOL == pool_row, 1.0 / POOL, 0.0).astype(jnp.bfloat16)
    pool_ref[...] = jnp.dot(pool_mat, out, preferred_element_type=jnp.float32).astype(pool_ref.dtype)


def fine_attention(planes, prev0, prev1a, prev1b, qclip, kclip, heads):
    _, tok, width = planes.shape
    head_dim = width // heads
    pair = 2 * head_dim
    pairs = width // pair
    tile = min(FINE_TILE, tok)
    nq = tok // tile
    kernel = functools.partial(fine_kernel, scale=1.0 / math.sqrt(head_dim))

    def plane_spec(plane):
        return pl.BlockSpec((None, tok, pair), lambda h, i: (plane, 0, h))

    return pl.pallas_call(
        kernel,
        grid=(pairs, nq),
        in_specs=[
            pl.BlockSpec((tile, 1), lambda h, i: (i, 0)),
            pl.BlockSpec((1, tok), lambda h, i: (0, 0)),
            pl.BlockSpec((1, tok), lambda h, i: (0, 1)),
            pl.BlockSpec((1, tok), lambda h, i: (0, 2)),
            pl.BlockSpec((None, tile, pair), lambda h, i: (0, i, h)),
            plane_spec(0), plane_spec(1),
            plane_spec(0), plane_spec(1),
            plane_spec(0), plane_spec(1),
            plane_spec(1), plane_spec(2),
        ],
        out_specs=[
            pl.BlockSpec((tile, pair), lambda h, i: (i, h)),
            pl.BlockSpec((tile // POOL, pair), lambda h, i: (i, h)),
        ],
        out_shape=[
            jax.ShapeDtypeStruct((tok, width), jnp.bfloat16),
            jax.ShapeDtypeStruct((tok // POOL, width), jnp.bfloat16),
        ],
    )(qclip, kclip, kclip, kclip, planes, prev0, prev0, prev1a, prev1a, prev1b, prev1b,
      planes, planes)


def mix_kernel(fine_ref, lift_ref, out_ref):
    tile = fine_ref.shape[0]
    rows = lift_ref.shape[0]
    spread_row = lax.broadcasted_iota(jnp.int32, (tile, rows), 0)
    spread_col = lax.broadcasted_iota(jnp.int32, (tile, rows), 1)
    spread = jnp.where(spread_row // POOL == spread_col, 1.0, 0.0).astype(jnp.bfloat16)
    lifted = jnp.dot(spread, lift_ref[...], preferred_element_type=jnp.float32)
    out_ref[...] = (fine_ref[...].astype(jnp.float32) + lifted).astype(out_ref.dtype)


def mix(fine_out, lifted):
    tok, width = fine_out.shape
    tile = min(FINE_TILE, tok)
    return pl.pallas_call(
        mix_kernel,
        grid=(tok // tile,),
        in_specs=[
            pl.BlockSpec((tile, width), lambda i: (i, 0)),
            pl.BlockSpec((tile // POOL, width), lambda i: (i, 0)),
        ],
        out_specs=pl.BlockSpec((tile, width), lambda i: (i, 0)),
        out_shape=jax.ShapeDtypeStruct((tok, width), fine_out.dtype),
    )(fine_out, lifted)


def pair_swap(value, axis, from_odd):
    count = lax.axis_size(axis)
    start = 1 if from_odd else 0
    step = -1 if from_odd else 1
    return lax.ppermute(value, axis, [(source, source + step) for source in range(start, count, 2)])


def coarse_kernel(qclip_ref, kc0_ref, kc1_ref, kc2_ref, kc3_ref, q_ref,
                  k0_ref, v0_ref, k1_ref, v1_ref, k2_ref, v2_ref, k3_ref, v3_ref,
                  out_ref, *, scale):
    tile = q_ref.shape[0]
    seg = k0_ref.shape[0]
    q = q_ref[...]
    qclip = qclip_ref[...]
    keys = (k0_ref, k1_ref, k2_ref, k3_ref)
    values = (v0_ref, v1_ref, v2_ref, v3_ref)
    clips = (kc0_ref, kc1_ref, kc2_ref, kc3_ref)
    qpos = pl.program_id(1) * tile + lax.broadcasted_iota(jnp.int32, (tile, seg), 0)
    kpos = lax.broadcasted_iota(jnp.int32, (tile, seg), 1)
    last = len(keys) - 1
    scores = []
    masks = []
    for j in range(len(keys)):
        allowed = clips[j][...] == qclip
        if j == last:
            allowed = allowed & (kpos <= qpos)
        s = lax.dot_general(q, keys[j][...], (((1,), (1,)), ((), ())),
                            preferred_element_type=jnp.float32) * scale
        scores.append(jnp.where(allowed, s, -1e30))
    top = jnp.max(scores[0], axis=1, keepdims=True)
    for j in range(1, len(keys)):
        top = jnp.maximum(top, jnp.max(scores[j], axis=1, keepdims=True))
    total = None
    summed = None
    for j in range(len(keys)):
        w = jnp.exp(scores[j] - top)
        part = jnp.sum(w, axis=1, keepdims=True)
        pv = jnp.dot(w.astype(jnp.bfloat16), values[j][...], preferred_element_type=jnp.float32)
        total = part if total is None else total + part
        summed = pv if summed is None else summed + pv
    out_ref[...] = (summed / total).astype(out_ref.dtype)


def coarse_attention(queries, windows, qclip, kclip, heads):
    rows, width = queries.shape
    head_dim = width // heads
    tile = min(FINE_TILE, rows)
    seg = windows[0].shape[1]
    kernel = functools.partial(coarse_kernel, scale=1.0 / math.sqrt(head_dim))
    clip_specs = [pl.BlockSpec((1, seg), functools.partial(lambda j, h, i: (0, j), j))
                  for j in range(len(windows))]
    kv_specs = []
    kv_args = []
    for window in windows:
        kv_specs.append(pl.BlockSpec((None, seg, head_dim), lambda h, i: (0, 0, h)))
        kv_specs.append(pl.BlockSpec((None, seg, head_dim), lambda h, i: (1, 0, h)))
        kv_args += [window, window]
    return pl.pallas_call(
        kernel,
        grid=(heads, rows // tile),
        in_specs=[pl.BlockSpec((tile, 1), lambda h, i: (i, 0))] + clip_specs
        + [pl.BlockSpec((tile, head_dim), lambda h, i: (i, h))] + kv_specs,
        out_specs=pl.BlockSpec((tile, head_dim), lambda h, i: (i, h)),
        out_shape=jax.ShapeDtypeStruct((rows, width), jnp.bfloat16),
    )(qclip, *([kclip] * len(windows)), queries, *kv_args)


def group_order(parts, quarter):
    ordered = jnp.stack([parts[0]] + parts[:0:-1], axis=0)
    return jnp.roll(ordered, quarter, axis=0)


def attend(queries, key_rows, value_rows, allowed, heads, head_groups):
    row_count = queries.shape[0]
    feat_width = queries.shape[1]
    head_dim = feat_width // heads
    per_group = heads // head_groups
    score_scale = 1.0 / math.sqrt(head_dim)

    def split_heads(source_rows):
        return source_rows.reshape(
            source_rows.shape[0], head_groups, per_group, head_dim
        ).transpose(1, 0, 2, 3)

    def one_group(operands):
        group_queries, group_keys, group_values = operands
        scores = (
            jnp.einsum(
                "rhd,khd->hrk", group_queries, group_keys, preferred_element_type=jnp.float32
            )
            * score_scale
        )
        masked = jnp.where(allowed[None], scores, -1e30)
        row_top = jnp.max(masked, axis=2, keepdims=True)
        weights = jnp.where(allowed[None], jnp.exp(masked - row_top), 0.0)
        row_total = jnp.sum(weights, axis=2)
        summed = jnp.einsum(
            "hrk,khd->rhd",
            weights.astype(jnp.bfloat16),
            group_values,
            preferred_element_type=jnp.float32,
        )
        return summed / jnp.transpose(row_total)[:, :, None]

    results = lax.map(
        one_group, (split_heads(queries), split_heads(key_rows), split_heads(value_rows))
    )
    return results.transpose(1, 0, 2, 3).reshape(row_count, feat_width).astype(jnp.bfloat16)


def body(fine_qkv, clip_ids, w_coarse, w_out):
    tok_count = fine_qkv.shape[0]
    feat_width = fine_qkv.shape[2]
    coarse_rows = tok_count // POOL
    group_rows = QUARTERS * coarse_rows
    position = lax.axis_index("seq")
    quarter = position % QUARTERS
    cycle_place = position // QUARTERS
    planes = jnp.transpose(fine_qkv, (1, 0, 2))
    own_pairs = planes[1:]
    prev0 = passed_along(own_pairs, "seq", 2)
    prev1a = pair_swap(own_pairs, "seq", False)
    prev1b = pair_swap(prev0, "seq", True)
    clip_front = jnp.concatenate([jnp.full((FREACH * coarse_rows,), -1, jnp.int32), clip_ids])
    key_clip = jnp.repeat(
        lax.dynamic_slice_in_dim(clip_front, position * coarse_rows, (FREACH + 1) * coarse_rows, 0),
        POOL,
    )
    own_clip = lax.dynamic_slice_in_dim(clip_ids, position * coarse_rows, coarse_rows, 0)
    query_clip = jnp.repeat(own_clip, POOL)
    fine_out, pooled = fine_attention(
        planes, prev0, prev1a, prev1b, query_clip.reshape(tok_count, 1),
        key_clip.reshape(1, (FREACH + 1) * tok_count), FHEADS,
    )
    quarter_width = w_coarse.shape[2] // QUARTERS
    wplanes = jnp.transpose(w_coarse, (1, 0, 2))
    projected = jnp.einsum(
        "rd,mdc->mrc", pooled, wplanes, preferred_element_type=jnp.float32
    ).astype(jnp.bfloat16)
    pieces = []
    for shift in range(QUARTERS):
        piece = lax.dynamic_slice_in_dim(
            projected, ((quarter + shift) % QUARTERS) * quarter_width, quarter_width, 2
        )
        pieces.append(piece if shift == 0 else within_group(piece, "seq", shift))
    grouped = group_order(pieces, quarter)
    grouped = jnp.transpose(grouped, (1, 0, 2, 3)).reshape(3, group_rows, quarter_width)
    coarse_queries = grouped[0]
    coarse_pairs = grouped[1:]
    one_back = passed_along(coarse_pairs, "seq", QUARTERS)
    two_back = passed_along(coarse_pairs, "seq", 2 * QUARTERS)
    three_back = passed_along(two_back, "seq", QUARTERS)
    earlier = [three_back, two_back, one_back]
    clip_back = jnp.concatenate([jnp.full((CREACH * group_rows,), -1, jnp.int32), clip_ids])
    coarse_key_clip = lax.dynamic_slice_in_dim(
        clip_back, cycle_place * group_rows, (CREACH + 1) * group_rows, 0
    )
    coarse_query_clip = lax.dynamic_slice_in_dim(clip_ids, cycle_place * group_rows, group_rows, 0)
    coarse_att = coarse_attention(
        coarse_queries, earlier + [coarse_pairs], coarse_query_clip.reshape(group_rows, 1),
        coarse_key_clip.reshape(1, (CREACH + 1) * group_rows), CHEADS // QUARTERS,
    )
    shares = []
    for shift in range(QUARTERS):
        share = lax.dynamic_slice_in_dim(
            coarse_att, ((quarter + shift) % QUARTERS) * coarse_rows, coarse_rows, 0
        )
        shares.append(share if shift == 0 else within_group(share, "seq", shift))
    att_rows = jnp.transpose(group_order(shares, quarter), (1, 0, 2)).reshape(
        coarse_rows, QUARTERS * quarter_width
    )
    coarse_up = jnp.dot(att_rows, w_out, preferred_element_type=jnp.float32).astype(jnp.bfloat16)
    carried = passed_along(coarse_up[-1:], "seq", 1)
    previous = jnp.concatenate([carried, coarse_up[:-1]], axis=0)
    clip_before = jnp.concatenate([jnp.full((1,), -1, jnp.int32), clip_ids])
    prev_clip = lax.dynamic_slice_in_dim(clip_before, position * coarse_rows, coarse_rows, 0)
    joined = prev_clip == own_clip
    lifted = jnp.where(joined[:, None], previous, jnp.zeros_like(previous))
    return mix(fine_out, lifted)


def solution(mesh):
    return jax.shard_map(
        body,
        mesh=mesh,
        in_specs=(P(("groups", "seq"), None, None), P("groups"), P(), P()),
        out_specs=P(("groups", "seq"), None),
        check_vma=False,
    )
```

```python
import functools
import math

import jax
import jax.numpy as jnp
from jax import lax
from jax.experimental import pallas as pl
from jax.experimental.pallas import tpu as pltpu
from jax.sharding import PartitionSpec as P

FHEADS = 16
CHEADS = 8
POOL = 4
QUARTERS = 4
FREACH = 2
CREACH = 3
FINE_TILE = 256


def passed_along(value, axis, steps):
    count = lax.axis_size(axis)
    first, last = (max(0, -steps), min(count, count - steps))
    return lax.ppermute(value, axis, [(source, source + steps) for source in range(first, last)])


def within_group(value, axis, shift):
    count = lax.axis_size(axis)
    pairs = []
    for source in range(count):
        base = source - source % QUARTERS
        pairs.append((source, base + (source % QUARTERS + shift) % QUARTERS))
    return lax.ppermute(value, axis, pairs)


def fine_kernel(qclip_ref, kclip0_ref, kclip1_ref, kclip2_ref, q_ref,
                k0_ref, v0_ref, k1_ref, v1_ref, k1b_ref, v1b_ref, k2_ref, v2_ref,
                out_ref, pool_ref, *, scale):
    tile = q_ref.shape[0]
    width = q_ref.shape[1]
    half = width // 2
    q = q_ref[...] * jnp.asarray(scale, q_ref.dtype)
    lane = lax.broadcasted_iota(jnp.int32, (1, width), 1)
    low = lane < half
    zero = jnp.zeros_like(q)
    head_q = (jnp.where(low, q, zero), jnp.where(low, zero, q))
    qclip = qclip_ref[...]
    keys = (k0_ref[...], k1_ref[...] + k1b_ref[...], k2_ref[...])
    values = (v0_ref[...], v1_ref[...] + v1b_ref[...], v2_ref[...])
    clips = (kclip0_ref, kclip1_ref, kclip2_ref)
    seg = k0_ref.shape[0]
    qpos = pl.program_id(1) * tile + lax.broadcasted_iota(jnp.int32, (tile, seg), 0)
    kpos = lax.broadcasted_iota(jnp.int32, (tile, seg), 1)
    masks = []
    for j in range(3):
        allowed = clips[j][...] == qclip
        if j == 2:
            allowed = allowed & (kpos <= qpos)
        masks.append(allowed)
    results = []
    for h in range(2):
        scores = []
        for j in range(3):
            s = lax.dot_general(head_q[h], keys[j], (((1,), (1,)), ((), ())),
                                preferred_element_type=jnp.float32)
            scores.append(jnp.where(masks[j], s, -1e30))
        top = jnp.max(scores[0], axis=1, keepdims=True)
        for j in range(1, 3):
            top = jnp.maximum(top, jnp.max(scores[j], axis=1, keepdims=True))
        total = None
        summed = None
        for j in range(3):
            w = jnp.exp(scores[j] - top)
            part = jnp.sum(w, axis=1, keepdims=True)
            pv = jnp.dot(w.astype(jnp.bfloat16), values[j], preferred_element_type=jnp.float32)
            total = part if total is None else total + part
            summed = pv if summed is None else summed + pv
        results.append(summed / total)
    out = jnp.where(low, results[0], results[1]).astype(out_ref.dtype)
    out_ref[...] = out
    rows = tile // POOL
    pool_row = lax.broadcasted_iota(jnp.int32, (rows, tile), 0)
    pool_col = lax.broadcasted_iota(jnp.int32, (rows, tile), 1)
    pool_mat = jnp.where(pool_col // POOL == pool_row, 1.0 / POOL, 0.0).astype(jnp.bfloat16)
    pool_ref[...] = jnp.dot(pool_mat, out, preferred_element_type=jnp.float32).astype(pool_ref.dtype)


def fine_attention(planes, prev0, prev1a, prev1b, qclip, kclip, heads):
    _, tok, width = planes.shape
    head_dim = width // heads
    pair = 2 * head_dim
    pairs = width // pair
    tile = min(FINE_TILE, tok)
    nq = tok // tile
    kernel = functools.partial(fine_kernel, scale=1.0 / math.sqrt(head_dim))

    def plane_spec(plane):
        return pl.BlockSpec((None, tok, pair), lambda h, i: (plane, 0, h))

    return pl.pallas_call(
        kernel,
        grid=(pairs, nq),
        in_specs=[
            pl.BlockSpec((tile, 1), lambda h, i: (i, 0)),
            pl.BlockSpec((1, tok), lambda h, i: (0, 0)),
            pl.BlockSpec((1, tok), lambda h, i: (0, 1)),
            pl.BlockSpec((1, tok), lambda h, i: (0, 2)),
            pl.BlockSpec((None, tile, pair), lambda h, i: (0, i, h)),
            plane_spec(0), plane_spec(1),
            plane_spec(0), plane_spec(1),
            plane_spec(0), plane_spec(1),
            plane_spec(1), plane_spec(2),
        ],
        out_specs=[
            pl.BlockSpec((tile, pair), lambda h, i: (i, h)),
            pl.BlockSpec((tile // POOL, pair), lambda h, i: (i, h)),
        ],
        out_shape=[
            jax.ShapeDtypeStruct((tok, width), jnp.bfloat16),
            jax.ShapeDtypeStruct((tok // POOL, width), jnp.bfloat16),
        ],
    )(qclip, kclip, kclip, kclip, planes, prev0, prev0, prev1a, prev1a, prev1b, prev1b,
      planes, planes)


def mix_kernel(fine_ref, lift_ref, out_ref):
    tile = fine_ref.shape[0]
    rows = lift_ref.shape[0]
    spread_row = lax.broadcasted_iota(jnp.int32, (tile, rows), 0)
    spread_col = lax.broadcasted_iota(jnp.int32, (tile, rows), 1)
    spread = jnp.where(spread_row // POOL == spread_col, 1.0, 0.0).astype(jnp.bfloat16)
    lifted = jnp.dot(spread, lift_ref[...], preferred_element_type=jnp.float32)
    out_ref[...] = (fine_ref[...].astype(jnp.float32) + lifted).astype(out_ref.dtype)


def mix(fine_out, lifted):
    tok, width = fine_out.shape
    tile = min(FINE_TILE, tok)
    return pl.pallas_call(
        mix_kernel,
        grid=(tok // tile,),
        in_specs=[
            pl.BlockSpec((tile, width), lambda i: (i, 0)),
            pl.BlockSpec((tile // POOL, width), lambda i: (i, 0)),
        ],
        out_specs=pl.BlockSpec((tile, width), lambda i: (i, 0)),
        out_shape=jax.ShapeDtypeStruct((tok, width), fine_out.dtype),
    )(fine_out, lifted)


def pair_swap(value, axis, from_odd):
    count = lax.axis_size(axis)
    start = 1 if from_odd else 0
    step = -1 if from_odd else 1
    return lax.ppermute(value, axis, [(source, source + step) for source in range(start, count, 2)])


def coarse_kernel(qclip_ref, kc0_ref, kc1_ref, kc2_ref, kc3_ref, q_ref,
                  k0_ref, v0_ref, k1_ref, v1_ref, k2_ref, v2_ref, k3_ref, v3_ref,
                  out_ref, *, scale):
    tile = q_ref.shape[0]
    seg = k0_ref.shape[0]
    q = q_ref[...]
    qclip = qclip_ref[...]
    keys = (k0_ref, k1_ref, k2_ref, k3_ref)
    values = (v0_ref, v1_ref, v2_ref, v3_ref)
    clips = (kc0_ref, kc1_ref, kc2_ref, kc3_ref)
    qpos = pl.program_id(1) * tile + lax.broadcasted_iota(jnp.int32, (tile, seg), 0)
    kpos = lax.broadcasted_iota(jnp.int32, (tile, seg), 1)
    last = len(keys) - 1
    scores = []
    masks = []
    for j in range(len(keys)):
        allowed = clips[j][...] == qclip
        if j == last:
            allowed = allowed & (kpos <= qpos)
        s = lax.dot_general(q, keys[j][...], (((1,), (1,)), ((), ())),
                            preferred_element_type=jnp.float32) * scale
        scores.append(jnp.where(allowed, s, -1e30))
    top = jnp.max(scores[0], axis=1, keepdims=True)
    for j in range(1, len(keys)):
        top = jnp.maximum(top, jnp.max(scores[j], axis=1, keepdims=True))
    total = None
    summed = None
    for j in range(len(keys)):
        w = jnp.exp(scores[j] - top)
        part = jnp.sum(w, axis=1, keepdims=True)
        pv = jnp.dot(w.astype(jnp.bfloat16), values[j][...], preferred_element_type=jnp.float32)
        total = part if total is None else total + part
        summed = pv if summed is None else summed + pv
    out_ref[...] = (summed / total).astype(out_ref.dtype)


def coarse_attention(queries, windows, qclip, kclip, heads):
    rows, width = queries.shape
    head_dim = width // heads
    tile = min(FINE_TILE, rows)
    seg = windows[0].shape[1]
    kernel = functools.partial(coarse_kernel, scale=1.0 / math.sqrt(head_dim))
    clip_specs = [pl.BlockSpec((1, seg), functools.partial(lambda j, h, i: (0, j), j))
                  for j in range(len(windows))]
    kv_specs = []
    kv_args = []
    for window in windows:
        kv_specs.append(pl.BlockSpec((None, seg, head_dim), lambda h, i: (0, 0, h)))
        kv_specs.append(pl.BlockSpec((None, seg, head_dim), lambda h, i: (1, 0, h)))
        kv_args += [window, window]
    return pl.pallas_call(
        kernel,
        grid=(heads, rows // tile),
        in_specs=[pl.BlockSpec((tile, 1), lambda h, i: (i, 0))] + clip_specs
        + [pl.BlockSpec((tile, head_dim), lambda h, i: (i, h))] + kv_specs,
        out_specs=pl.BlockSpec((tile, head_dim), lambda h, i: (i, h)),
        out_shape=jax.ShapeDtypeStruct((rows, width), jnp.bfloat16),
    )(qclip, *([kclip] * len(windows)), queries, *kv_args)


def group_order(parts, quarter):
    ordered = jnp.stack([parts[0]] + parts[:0:-1], axis=0)
    return jnp.roll(ordered, quarter, axis=0)


def attend(queries, key_rows, value_rows, allowed, heads, head_groups):
    row_count = queries.shape[0]
    feat_width = queries.shape[1]
    head_dim = feat_width // heads
    per_group = heads // head_groups
    score_scale = 1.0 / math.sqrt(head_dim)

    def split_heads(source_rows):
        return source_rows.reshape(
            source_rows.shape[0], head_groups, per_group, head_dim
        ).transpose(1, 0, 2, 3)

    def one_group(operands):
        group_queries, group_keys, group_values = operands
        scores = (
            jnp.einsum(
                "rhd,khd->hrk", group_queries, group_keys, preferred_element_type=jnp.float32
            )
            * score_scale
        )
        masked = jnp.where(allowed[None], scores, -1e30)
        row_top = jnp.max(masked, axis=2, keepdims=True)
        weights = jnp.where(allowed[None], jnp.exp(masked - row_top), 0.0)
        row_total = jnp.sum(weights, axis=2)
        summed = jnp.einsum(
            "hrk,khd->rhd",
            weights.astype(jnp.bfloat16),
            group_values,
            preferred_element_type=jnp.float32,
        )
        return summed / jnp.transpose(row_total)[:, :, None]

    results = lax.map(
        one_group, (split_heads(queries), split_heads(key_rows), split_heads(value_rows))
    )
    return results.transpose(1, 0, 2, 3).reshape(row_count, feat_width).astype(jnp.bfloat16)


def body(fine_qkv, clip_ids, w_coarse, w_out):
    tok_count = fine_qkv.shape[0]
    feat_width = fine_qkv.shape[2]
    coarse_rows = tok_count // POOL
    group_rows = QUARTERS * coarse_rows
    position = lax.axis_index("seq")
    quarter = position % QUARTERS
    cycle_place = position // QUARTERS
    planes = jnp.transpose(fine_qkv, (1, 0, 2))
    own_pairs = planes[1:]
    prev0 = passed_along(own_pairs, "seq", 2)
    prev1a = pair_swap(own_pairs, "seq", False)
    prev1b = pair_swap(prev0, "seq", True)
    clip_front = jnp.concatenate([jnp.full((FREACH * coarse_rows,), -1, jnp.int32), clip_ids])
    key_clip = jnp.repeat(
        lax.dynamic_slice_in_dim(clip_front, position * coarse_rows, (FREACH + 1) * coarse_rows, 0),
        POOL,
    )
    own_clip = lax.dynamic_slice_in_dim(clip_ids, position * coarse_rows, coarse_rows, 0)
    query_clip = jnp.repeat(own_clip, POOL)
    fine_out, pooled = fine_attention(
        planes, prev0, prev1a, prev1b, query_clip.reshape(tok_count, 1),
        key_clip.reshape(1, (FREACH + 1) * tok_count), FHEADS,
    )
    quarter_width = w_coarse.shape[2] // QUARTERS
    wplanes = jnp.transpose(w_coarse, (1, 0, 2))
    projected = jnp.einsum(
        "rd,mdc->mrc", pooled, wplanes, preferred_element_type=jnp.float32
    ).astype(jnp.bfloat16)
    pieces = []
    for shift in range(QUARTERS):
        piece = lax.dynamic_slice_in_dim(
            projected, ((quarter + shift) % QUARTERS) * quarter_width, quarter_width, 2
        )
        pieces.append(piece if shift == 0 else within_group(piece, "seq", shift))
    grouped = group_order(pieces, quarter)
    grouped = jnp.transpose(grouped, (1, 0, 2, 3)).reshape(3, group_rows, quarter_width)
    coarse_queries = grouped[0]
    coarse_pairs = grouped[1:]
    one_back = passed_along(coarse_pairs, "seq", QUARTERS)
    two_back = passed_along(coarse_pairs, "seq", 2 * QUARTERS)
    three_back = passed_along(two_back, "seq", QUARTERS)
    earlier = [three_back, two_back, one_back]
    clip_back = jnp.concatenate([jnp.full((CREACH * group_rows,), -1, jnp.int32), clip_ids])
    coarse_key_clip = lax.dynamic_slice_in_dim(
        clip_back, cycle_place * group_rows, (CREACH + 1) * group_rows, 0
    )
    coarse_query_clip = lax.dynamic_slice_in_dim(clip_ids, cycle_place * group_rows, group_rows, 0)
    coarse_att = coarse_attention(
        coarse_queries, earlier + [coarse_pairs], coarse_query_clip.reshape(group_rows, 1),
        coarse_key_clip.reshape(1, (CREACH + 1) * group_rows), CHEADS // QUARTERS,
    )
    att_pad = jnp.concatenate([jnp.zeros_like(coarse_att[:1]), coarse_att], axis=0)
    shares = []
    for shift in range(QUARTERS):
        share = lax.dynamic_slice_in_dim(
            att_pad, ((quarter + shift) % QUARTERS) * coarse_rows, coarse_rows, 0
        )
        shares.append(share if shift == 0 else within_group(share, "seq", shift))
    att_rows = jnp.transpose(group_order(shares, quarter), (1, 0, 2)).reshape(
        coarse_rows, QUARTERS * quarter_width
    )
    count = lax.axis_size("seq")
    group_last = coarse_att[-1:]
    cross = []
    for source_quarter in range(QUARTERS):
        pairs = [
            (source, source + QUARTERS - source_quarter)
            for source in range(source_quarter, count - QUARTERS + source_quarter, QUARTERS)
        ]
        cross.append(lax.ppermute(group_last, "seq", pairs))
    cross_row = jnp.concatenate(cross, axis=1)
    first_row = jnp.where(quarter == 0, cross_row, att_rows[:1])
    att_rows = jnp.concatenate([first_row, att_rows[1:]], axis=0)
    previous = jnp.dot(att_rows, w_out, preferred_element_type=jnp.float32).astype(jnp.bfloat16)
    clip_before = jnp.concatenate([jnp.full((1,), -1, jnp.int32), clip_ids])
    prev_clip = lax.dynamic_slice_in_dim(clip_before, position * coarse_rows, coarse_rows, 0)
    joined = prev_clip == own_clip
    lifted = jnp.where(joined[:, None], previous, jnp.zeros_like(previous))
    return mix(fine_out, lifted)


def solution(mesh):
    return jax.shard_map(
        body,
        mesh=mesh,
        in_specs=(P(("groups", "seq"), None, None), P("groups"), P(), P()),
        out_specs=P(("groups", "seq"), None),
        check_vma=False,
    )
```

```python
import functools
import math

import jax
import jax.numpy as jnp
from jax import lax
from jax.experimental import pallas as pl
from jax.experimental.pallas import tpu as pltpu
from jax.sharding import PartitionSpec as P

FHEADS = 16
CHEADS = 8
POOL = 4
QUARTERS = 4
FREACH = 2
CREACH = 3
FINE_TILE = 256


def passed_along(value, axis, steps):
    count = lax.axis_size(axis)
    first, last = (max(0, -steps), min(count, count - steps))
    return lax.ppermute(value, axis, [(source, source + steps) for source in range(first, last)])


def within_group(value, axis, shift):
    count = lax.axis_size(axis)
    pairs = []
    for source in range(count):
        base = source - source % QUARTERS
        pairs.append((source, base + (source % QUARTERS + shift) % QUARTERS))
    return lax.ppermute(value, axis, pairs)


def fine_kernel(qclip_ref, kclip0_ref, kclip1_ref, kclip2_ref, q_ref,
                k0_ref, v0_ref, k1_ref, v1_ref, k1b_ref, v1b_ref, k2_ref, v2_ref,
                out_ref, pool_ref, *, scale):
    tile = q_ref.shape[0]
    width = q_ref.shape[1]
    half = width // 2
    q = q_ref[...] * jnp.asarray(scale, q_ref.dtype)
    lane = lax.broadcasted_iota(jnp.int32, (1, width), 1)
    low = lane < half
    zero = jnp.zeros_like(q)
    head_q = (jnp.where(low, q, zero), jnp.where(low, zero, q))
    qclip = qclip_ref[...]
    seg = k0_ref.shape[0]

    def run(step):
        own = (step + 1) * tile
        keys = (k0_ref[...], k1_ref[...] + k1b_ref[...], k2_ref[0:own, :])
        values = (v0_ref[...], v1_ref[...] + v1b_ref[...], v2_ref[0:own, :])
        qpos = step * tile + lax.broadcasted_iota(jnp.int32, (tile, own), 0)
        kpos = lax.broadcasted_iota(jnp.int32, (tile, own), 1)
        masks = (
            kclip0_ref[...] == qclip,
            kclip1_ref[...] == qclip,
            (kclip2_ref[:, 0:own] == qclip) & (kpos <= qpos),
        )
        results = []
        for h in range(2):
            scores = []
            for j in range(3):
                s = lax.dot_general(head_q[h], keys[j], (((1,), (1,)), ((), ())),
                                    preferred_element_type=jnp.float32)
                scores.append(jnp.where(masks[j], s, -1e30))
            top = jnp.max(scores[0], axis=1, keepdims=True)
            for j in range(1, 3):
                top = jnp.maximum(top, jnp.max(scores[j], axis=1, keepdims=True))
            total = None
            summed = None
            for j in range(3):
                w = jnp.exp(scores[j] - top)
                part = jnp.sum(w, axis=1, keepdims=True)
                pv = jnp.dot(w.astype(jnp.bfloat16), values[j], preferred_element_type=jnp.float32)
                total = part if total is None else total + part
                summed = pv if summed is None else summed + pv
            results.append(summed / total)
        out = jnp.where(low, results[0], results[1]).astype(out_ref.dtype)
        out_ref[...] = out
        rows = tile // POOL
        pool_row = lax.broadcasted_iota(jnp.int32, (rows, tile), 0)
        pool_col = lax.broadcasted_iota(jnp.int32, (rows, tile), 1)
        pool_mat = jnp.where(pool_col // POOL == pool_row, 1.0 / POOL, 0.0).astype(jnp.bfloat16)
        pool_ref[...] = jnp.dot(pool_mat, out, preferred_element_type=jnp.float32).astype(
            pool_ref.dtype)

    for step in range(seg // tile):
        pl.when(pl.program_id(1) == step)(functools.partial(run, step))


def fine_attention(planes, prev0, prev1a, prev1b, qclip, kclip, heads):
    _, tok, width = planes.shape
    head_dim = width // heads
    pair = 2 * head_dim
    pairs = width // pair
    tile = min(FINE_TILE, tok)
    nq = tok // tile
    kernel = functools.partial(fine_kernel, scale=1.0 / math.sqrt(head_dim))

    def plane_spec(plane):
        return pl.BlockSpec((None, tok, pair), lambda h, i: (plane, 0, h))

    return pl.pallas_call(
        kernel,
        grid=(pairs, nq),
        in_specs=[
            pl.BlockSpec((tile, 1), lambda h, i: (i, 0)),
            pl.BlockSpec((1, tok), lambda h, i: (0, 0)),
            pl.BlockSpec((1, tok), lambda h, i: (0, 1)),
            pl.BlockSpec((1, tok), lambda h, i: (0, 2)),
            pl.BlockSpec((None, tile, pair), lambda h, i: (0, i, h)),
            plane_spec(0), plane_spec(1),
            plane_spec(0), plane_spec(1),
            plane_spec(0), plane_spec(1),
            plane_spec(1), plane_spec(2),
        ],
        out_specs=[
            pl.BlockSpec((tile, pair), lambda h, i: (i, h)),
            pl.BlockSpec((tile // POOL, pair), lambda h, i: (i, h)),
        ],
        out_shape=[
            jax.ShapeDtypeStruct((tok, width), jnp.bfloat16),
            jax.ShapeDtypeStruct((tok // POOL, width), jnp.bfloat16),
        ],
    )(qclip, kclip, kclip, kclip, planes, prev0, prev0, prev1a, prev1a, prev1b, prev1b,
      planes, planes)


def mix_kernel(fine_ref, lift_ref, out_ref):
    tile = fine_ref.shape[0]
    rows = lift_ref.shape[0]
    spread_row = lax.broadcasted_iota(jnp.int32, (tile, rows), 0)
    spread_col = lax.broadcasted_iota(jnp.int32, (tile, rows), 1)
    spread = jnp.where(spread_row // POOL == spread_col, 1.0, 0.0).astype(jnp.bfloat16)
    lifted = jnp.dot(spread, lift_ref[...], preferred_element_type=jnp.float32)
    out_ref[...] = (fine_ref[...].astype(jnp.float32) + lifted).astype(out_ref.dtype)


def mix(fine_out, lifted):
    tok, width = fine_out.shape
    tile = min(FINE_TILE, tok)
    return pl.pallas_call(
        mix_kernel,
        grid=(tok // tile,),
        in_specs=[
            pl.BlockSpec((tile, width), lambda i: (i, 0)),
            pl.BlockSpec((tile // POOL, width), lambda i: (i, 0)),
        ],
        out_specs=pl.BlockSpec((tile, width), lambda i: (i, 0)),
        out_shape=jax.ShapeDtypeStruct((tok, width), fine_out.dtype),
    )(fine_out, lifted)


def pair_swap(value, axis, from_odd):
    count = lax.axis_size(axis)
    start = 1 if from_odd else 0
    step = -1 if from_odd else 1
    return lax.ppermute(value, axis, [(source, source + step) for source in range(start, count, 2)])


def coarse_kernel(qclip_ref, kc0_ref, kc1_ref, kc2_ref, kc3_ref, q_ref,
                  k0_ref, v0_ref, k1_ref, v1_ref, k2_ref, v2_ref, k3_ref, v3_ref,
                  out_ref, *, scale):
    tile = q_ref.shape[0]
    seg = k0_ref.shape[0]
    q = q_ref[...]
    qclip = qclip_ref[...]
    keys = (k0_ref, k1_ref, k2_ref, k3_ref)
    values = (v0_ref, v1_ref, v2_ref, v3_ref)
    clips = (kc0_ref, kc1_ref, kc2_ref, kc3_ref)
    qpos = pl.program_id(1) * tile + lax.broadcasted_iota(jnp.int32, (tile, seg), 0)
    kpos = lax.broadcasted_iota(jnp.int32, (tile, seg), 1)
    last = len(keys) - 1
    scores = []
    masks = []
    for j in range(len(keys)):
        allowed = clips[j][...] == qclip
        if j == last:
            allowed = allowed & (kpos <= qpos)
        s = lax.dot_general(q, keys[j][...], (((1,), (1,)), ((), ())),
                            preferred_element_type=jnp.float32) * scale
        scores.append(jnp.where(allowed, s, -1e30))
    top = jnp.max(scores[0], axis=1, keepdims=True)
    for j in range(1, len(keys)):
        top = jnp.maximum(top, jnp.max(scores[j], axis=1, keepdims=True))
    total = None
    summed = None
    for j in range(len(keys)):
        w = jnp.exp(scores[j] - top)
        part = jnp.sum(w, axis=1, keepdims=True)
        pv = jnp.dot(w.astype(jnp.bfloat16), values[j][...], preferred_element_type=jnp.float32)
        total = part if total is None else total + part
        summed = pv if summed is None else summed + pv
    out_ref[...] = (summed / total).astype(out_ref.dtype)


def coarse_attention(queries, windows, qclip, kclip, heads):
    rows, width = queries.shape
    head_dim = width // heads
    tile = min(FINE_TILE, rows)
    seg = windows[0].shape[1]
    kernel = functools.partial(coarse_kernel, scale=1.0 / math.sqrt(head_dim))
    clip_specs = [pl.BlockSpec((1, seg), functools.partial(lambda j, h, i: (0, j), j))
                  for j in range(len(windows))]
    kv_specs = []
    kv_args = []
    for window in windows:
        kv_specs.append(pl.BlockSpec((None, seg, head_dim), lambda h, i: (0, 0, h)))
        kv_specs.append(pl.BlockSpec((None, seg, head_dim), lambda h, i: (1, 0, h)))
        kv_args += [window, window]
    return pl.pallas_call(
        kernel,
        grid=(heads, rows // tile),
        in_specs=[pl.BlockSpec((tile, 1), lambda h, i: (i, 0))] + clip_specs
        + [pl.BlockSpec((tile, head_dim), lambda h, i: (i, h))] + kv_specs,
        out_specs=pl.BlockSpec((tile, head_dim), lambda h, i: (i, h)),
        out_shape=jax.ShapeDtypeStruct((rows, width), jnp.bfloat16),
    )(qclip, *([kclip] * len(windows)), queries, *kv_args)


def group_order(parts, quarter):
    ordered = jnp.stack([parts[0]] + parts[:0:-1], axis=0)
    return jnp.roll(ordered, quarter, axis=0)


def attend(queries, key_rows, value_rows, allowed, heads, head_groups):
    row_count = queries.shape[0]
    feat_width = queries.shape[1]
    head_dim = feat_width // heads
    per_group = heads // head_groups
    score_scale = 1.0 / math.sqrt(head_dim)

    def split_heads(source_rows):
        return source_rows.reshape(
            source_rows.shape[0], head_groups, per_group, head_dim
        ).transpose(1, 0, 2, 3)

    def one_group(operands):
        group_queries, group_keys, group_values = operands
        scores = (
            jnp.einsum(
                "rhd,khd->hrk", group_queries, group_keys, preferred_element_type=jnp.float32
            )
            * score_scale
        )
        masked = jnp.where(allowed[None], scores, -1e30)
        row_top = jnp.max(masked, axis=2, keepdims=True)
        weights = jnp.where(allowed[None], jnp.exp(masked - row_top), 0.0)
        row_total = jnp.sum(weights, axis=2)
        summed = jnp.einsum(
            "hrk,khd->rhd",
            weights.astype(jnp.bfloat16),
            group_values,
            preferred_element_type=jnp.float32,
        )
        return summed / jnp.transpose(row_total)[:, :, None]

    results = lax.map(
        one_group, (split_heads(queries), split_heads(key_rows), split_heads(value_rows))
    )
    return results.transpose(1, 0, 2, 3).reshape(row_count, feat_width).astype(jnp.bfloat16)


def body(fine_qkv, clip_ids, w_coarse, w_out):
    tok_count = fine_qkv.shape[0]
    feat_width = fine_qkv.shape[2]
    coarse_rows = tok_count // POOL
    group_rows = QUARTERS * coarse_rows
    position = lax.axis_index("seq")
    quarter = position % QUARTERS
    cycle_place = position // QUARTERS
    planes = jnp.transpose(fine_qkv, (1, 0, 2))
    own_pairs = planes[1:]
    prev0 = passed_along(own_pairs, "seq", 2)
    prev1a = pair_swap(own_pairs, "seq", False)
    prev1b = pair_swap(prev0, "seq", True)
    clip_front = jnp.concatenate([jnp.full((FREACH * coarse_rows,), -1, jnp.int32), clip_ids])
    key_clip = jnp.repeat(
        lax.dynamic_slice_in_dim(clip_front, position * coarse_rows, (FREACH + 1) * coarse_rows, 0),
        POOL,
    )
    own_clip = lax.dynamic_slice_in_dim(clip_ids, position * coarse_rows, coarse_rows, 0)
    query_clip = jnp.repeat(own_clip, POOL)
    fine_out, pooled = fine_attention(
        planes, prev0, prev1a, prev1b, query_clip.reshape(tok_count, 1),
        key_clip.reshape(1, (FREACH + 1) * tok_count), FHEADS,
    )
    quarter_width = w_coarse.shape[2] // QUARTERS
    wplanes = jnp.transpose(w_coarse, (1, 0, 2))
    projected = jnp.einsum(
        "rd,mdc->mrc", pooled, wplanes, preferred_element_type=jnp.float32
    ).astype(jnp.bfloat16)
    pieces = []
    for shift in range(QUARTERS):
        piece = lax.dynamic_slice_in_dim(
            projected, ((quarter + shift) % QUARTERS) * quarter_width, quarter_width, 2
        )
        pieces.append(piece if shift == 0 else within_group(piece, "seq", shift))
    grouped = group_order(pieces, quarter)
    grouped = jnp.transpose(grouped, (1, 0, 2, 3)).reshape(3, group_rows, quarter_width)
    coarse_queries = grouped[0]
    coarse_pairs = grouped[1:]
    one_back = passed_along(coarse_pairs, "seq", QUARTERS)
    two_back = passed_along(coarse_pairs, "seq", 2 * QUARTERS)
    three_back = passed_along(two_back, "seq", QUARTERS)
    earlier = [three_back, two_back, one_back]
    clip_back = jnp.concatenate([jnp.full((CREACH * group_rows,), -1, jnp.int32), clip_ids])
    coarse_key_clip = lax.dynamic_slice_in_dim(
        clip_back, cycle_place * group_rows, (CREACH + 1) * group_rows, 0
    )
    coarse_query_clip = lax.dynamic_slice_in_dim(clip_ids, cycle_place * group_rows, group_rows, 0)
    coarse_att = coarse_attention(
        coarse_queries, earlier + [coarse_pairs], coarse_query_clip.reshape(group_rows, 1),
        coarse_key_clip.reshape(1, (CREACH + 1) * group_rows), CHEADS // QUARTERS,
    )
    shares = []
    for shift in range(QUARTERS):
        share = lax.dynamic_slice_in_dim(
            coarse_att, ((quarter + shift) % QUARTERS) * coarse_rows, coarse_rows, 0
        )
        shares.append(share if shift == 0 else within_group(share, "seq", shift))
    att_rows = jnp.transpose(group_order(shares, quarter), (1, 0, 2)).reshape(
        coarse_rows, QUARTERS * quarter_width
    )
    coarse_up = jnp.dot(att_rows, w_out, preferred_element_type=jnp.float32).astype(jnp.bfloat16)
    carried = passed_along(coarse_up[-1:], "seq", 1)
    previous = jnp.concatenate([carried, coarse_up[:-1]], axis=0)
    clip_before = jnp.concatenate([jnp.full((1,), -1, jnp.int32), clip_ids])
    prev_clip = lax.dynamic_slice_in_dim(clip_before, position * coarse_rows, coarse_rows, 0)
    joined = prev_clip == own_clip
    lifted = jnp.where(joined[:, None], previous, jnp.zeros_like(previous))
    return mix(fine_out, lifted)


def solution(mesh):
    return jax.shard_map(
        body,
        mesh=mesh,
        in_specs=(P(("groups", "seq"), None, None), P("groups"), P(), P()),
        out_specs=P(("groups", "seq"), None),
        check_vma=False,
    )
```

```python
import functools
import math

import jax
import jax.numpy as jnp
from jax import lax
from jax.experimental import pallas as pl
from jax.experimental.pallas import tpu as pltpu
from jax.sharding import PartitionSpec as P

FHEADS = 16
CHEADS = 8
POOL = 4
QUARTERS = 4
FREACH = 2
CREACH = 3
FINE_TILE = 256


def passed_along(value, axis, steps):
    count = lax.axis_size(axis)
    first, last = (max(0, -steps), min(count, count - steps))
    return lax.ppermute(value, axis, [(source, source + steps) for source in range(first, last)])


def within_group(value, axis, shift):
    count = lax.axis_size(axis)
    pairs = []
    for source in range(count):
        base = source - source % QUARTERS
        pairs.append((source, base + (source % QUARTERS + shift) % QUARTERS))
    return lax.ppermute(value, axis, pairs)


def head_queries(q_ref, scale):
    width = q_ref.shape[1]
    q = q_ref[...] * jnp.asarray(scale, q_ref.dtype)
    lane = lax.broadcasted_iota(jnp.int32, (1, width), 1)
    low = lane < width // 2
    zero = jnp.zeros_like(q)
    return (jnp.where(low, q, zero), jnp.where(low, zero, q)), lane, low


def scores_of(query, keys, allowed):
    s = lax.dot_general(query, keys, (((1,), (1,)), ((), ())), preferred_element_type=jnp.float32)
    return jnp.where(allowed, s, -1e30)


def own_kernel(qclip_ref, kclip_ref, q_ref, k_ref, v_ref, o_ref, st_ref, *, scale):
    tile, width = q_ref.shape
    head_q, lane, low = head_queries(q_ref, scale)
    qclip = qclip_ref[...]
    slot = lane // (width // 4)

    def run(step):
        own = (step + 1) * tile
        keys = k_ref[0:own, :]
        values = v_ref[0:own, :]
        qpos = step * tile + lax.broadcasted_iota(jnp.int32, (tile, own), 0)
        kpos = lax.broadcasted_iota(jnp.int32, (tile, own), 1)
        allowed = (kclip_ref[:, 0:own] == qclip) & (kpos <= qpos)
        outs, tops, totals = [], [], []
        for h in range(2):
            s = scores_of(head_q[h], keys, allowed)
            top = jnp.max(s, axis=1, keepdims=True)
            w = jnp.exp(s - top)
            totals.append(jnp.sum(w, axis=1, keepdims=True))
            tops.append(top)
            outs.append(jnp.dot(w.astype(jnp.bfloat16), values, preferred_element_type=jnp.float32))
        o_ref[...] = jnp.where(low, outs[0], outs[1])
        st_ref[...] = jnp.where(
            slot == 0, tops[0], jnp.where(slot == 1, totals[0], jnp.where(slot == 2, tops[1], totals[1]))
        )

    for step in range(k_ref.shape[0] // tile):
        pl.when(pl.program_id(1) == step)(functools.partial(run, step))


def remote_kernel(qclip_ref, kclip0_ref, kclip1_ref, q_ref, k0_ref, v0_ref, k1_ref, v1_ref,
                  k1b_ref, v1b_ref, o_ref, st_ref, out_ref, pool_ref, *, scale):
    tile, width = q_ref.shape
    quarter = width // 4
    head_q, lane, low = head_queries(q_ref, scale)
    qclip = qclip_ref[...]
    keys = (k0_ref[...], k1_ref[...] + k1b_ref[...])
    values = (v0_ref[...], v1_ref[...] + v1b_ref[...])
    masks = (kclip0_ref[...] == qclip, kclip1_ref[...] == qclip)
    st = st_ref[...]
    own_out = o_ref[...]
    results = []
    for h in range(2):
        own_top = st[:, 2 * h * quarter:2 * h * quarter + 1]
        own_total = st[:, (2 * h + 1) * quarter:(2 * h + 1) * quarter + 1]
        scores = [scores_of(head_q[h], keys[j], masks[j]) for j in range(2)]
        top = own_top
        for j in range(2):
            top = jnp.maximum(top, jnp.max(scores[j], axis=1, keepdims=True))
        rescale = jnp.exp(own_top - top)
        total = own_total * rescale
        summed = own_out * rescale
        for j in range(2):
            w = jnp.exp(scores[j] - top)
            total = total + jnp.sum(w, axis=1, keepdims=True)
            summed = summed + jnp.dot(w.astype(jnp.bfloat16), values[j],
                                      preferred_element_type=jnp.float32)
        results.append(summed / total)
    out = jnp.where(low, results[0], results[1]).astype(out_ref.dtype)
    out_ref[...] = out
    rows = tile // POOL
    pool_row = lax.broadcasted_iota(jnp.int32, (rows, tile), 0)
    pool_col = lax.broadcasted_iota(jnp.int32, (rows, tile), 1)
    pool_mat = jnp.where(pool_col // POOL == pool_row, 1.0 / POOL, 0.0).astype(jnp.bfloat16)
    pool_ref[...] = jnp.dot(pool_mat, out, preferred_element_type=jnp.float32).astype(pool_ref.dtype)


def fine_attention(planes, prev0, prev1a, qclip, kclip, heads):
    _, tok, width = planes.shape
    head_dim = width // heads
    pair = 2 * head_dim
    pairs = width // pair
    tile = min(FINE_TILE, tok)
    nq = tok // tile
    scale = 1.0 / math.sqrt(head_dim)

    def plane_spec(plane):
        return pl.BlockSpec((None, tok, pair), lambda h, i: (plane, 0, h))

    qclip_spec = pl.BlockSpec((tile, 1), lambda h, i: (i, 0))
    q_spec = pl.BlockSpec((None, tile, pair), lambda h, i: (0, i, h))
    tile_spec = pl.BlockSpec((tile, pair), lambda h, i: (i, h))
    own_out, own_stats = pl.pallas_call(
        functools.partial(own_kernel, scale=scale),
        grid=(pairs, nq),
        in_specs=[qclip_spec, pl.BlockSpec((1, tok), lambda h, i: (0, 2)), q_spec,
                  plane_spec(1), plane_spec(2)],
        out_specs=[tile_spec, tile_spec],
        out_shape=[jax.ShapeDtypeStruct((tok, width), jnp.float32)] * 2,
    )(qclip, kclip, planes, planes, planes)
    prev0, own_stats = lax.optimization_barrier((prev0, own_stats))
    prev1b = pair_swap(prev0, "seq", True)
    return pl.pallas_call(
        functools.partial(remote_kernel, scale=scale),
        grid=(pairs, nq),
        in_specs=[
            qclip_spec,
            pl.BlockSpec((1, tok), lambda h, i: (0, 0)),
            pl.BlockSpec((1, tok), lambda h, i: (0, 1)),
            q_spec,
            plane_spec(0), plane_spec(1),
            plane_spec(0), plane_spec(1),
            plane_spec(0), plane_spec(1),
            tile_spec, tile_spec,
        ],
        out_specs=[tile_spec, pl.BlockSpec((tile // POOL, pair), lambda h, i: (i, h))],
        out_shape=[
            jax.ShapeDtypeStruct((tok, width), jnp.bfloat16),
            jax.ShapeDtypeStruct((tok // POOL, width), jnp.bfloat16),
        ],
    )(qclip, kclip, kclip, planes, prev0, prev0, prev1a, prev1a, prev1b, prev1b,
      own_out, own_stats)


def mix_kernel(fine_ref, lift_ref, out_ref):
    tile = fine_ref.shape[0]
    rows = lift_ref.shape[0]
    spread_row = lax.broadcasted_iota(jnp.int32, (tile, rows), 0)
    spread_col = lax.broadcasted_iota(jnp.int32, (tile, rows), 1)
    spread = jnp.where(spread_row // POOL == spread_col, 1.0, 0.0).astype(jnp.bfloat16)
    lifted = jnp.dot(spread, lift_ref[...], preferred_element_type=jnp.float32)
    out_ref[...] = (fine_ref[...].astype(jnp.float32) + lifted).astype(out_ref.dtype)


def mix(fine_out, lifted):
    tok, width = fine_out.shape
    tile = min(FINE_TILE, tok)
    return pl.pallas_call(
        mix_kernel,
        grid=(tok // tile,),
        in_specs=[
            pl.BlockSpec((tile, width), lambda i: (i, 0)),
            pl.BlockSpec((tile // POOL, width), lambda i: (i, 0)),
        ],
        out_specs=pl.BlockSpec((tile, width), lambda i: (i, 0)),
        out_shape=jax.ShapeDtypeStruct((tok, width), fine_out.dtype),
    )(fine_out, lifted)


def pair_swap(value, axis, from_odd):
    count = lax.axis_size(axis)
    start = 1 if from_odd else 0
    step = -1 if from_odd else 1
    return lax.ppermute(value, axis, [(source, source + step) for source in range(start, count, 2)])


def coarse_kernel(qclip_ref, kc0_ref, kc1_ref, kc2_ref, kc3_ref, q_ref,
                  k0_ref, v0_ref, k1_ref, v1_ref, k2_ref, v2_ref, k3_ref, v3_ref,
                  out_ref, *, scale):
    tile = q_ref.shape[0]
    seg = k0_ref.shape[0]
    q = q_ref[...]
    qclip = qclip_ref[...]
    keys = (k0_ref, k1_ref, k2_ref, k3_ref)
    values = (v0_ref, v1_ref, v2_ref, v3_ref)
    clips = (kc0_ref, kc1_ref, kc2_ref, kc3_ref)
    qpos = pl.program_id(1) * tile + lax.broadcasted_iota(jnp.int32, (tile, seg), 0)
    kpos = lax.broadcasted_iota(jnp.int32, (tile, seg), 1)
    last = len(keys) - 1
    scores = []
    masks = []
    for j in range(len(keys)):
        allowed = clips[j][...] == qclip
        if j == last:
            allowed = allowed & (kpos <= qpos)
        s = lax.dot_general(q, keys[j][...], (((1,), (1,)), ((), ())),
                            preferred_element_type=jnp.float32) * scale
        scores.append(jnp.where(allowed, s, -1e30))
    top = jnp.max(scores[0], axis=1, keepdims=True)
    for j in range(1, len(keys)):
        top = jnp.maximum(top, jnp.max(scores[j], axis=1, keepdims=True))
    total = None
    summed = None
    for j in range(len(keys)):
        w = jnp.exp(scores[j] - top)
        part = jnp.sum(w, axis=1, keepdims=True)
        pv = jnp.dot(w.astype(jnp.bfloat16), values[j][...], preferred_element_type=jnp.float32)
        total = part if total is None else total + part
        summed = pv if summed is None else summed + pv
    out_ref[...] = (summed / total).astype(out_ref.dtype)


def coarse_attention(queries, windows, qclip, kclip, heads):
    rows, width = queries.shape
    head_dim = width // heads
    tile = min(FINE_TILE, rows)
    seg = windows[0].shape[1]
    kernel = functools.partial(coarse_kernel, scale=1.0 / math.sqrt(head_dim))
    clip_specs = [pl.BlockSpec((1, seg), functools.partial(lambda j, h, i: (0, j), j))
                  for j in range(len(windows))]
    kv_specs = []
    kv_args = []
    for window in windows:
        kv_specs.append(pl.BlockSpec((None, seg, head_dim), lambda h, i: (0, 0, h)))
        kv_specs.append(pl.BlockSpec((None, seg, head_dim), lambda h, i: (1, 0, h)))
        kv_args += [window, window]
    return pl.pallas_call(
        kernel,
        grid=(heads, rows // tile),
        in_specs=[pl.BlockSpec((tile, 1), lambda h, i: (i, 0))] + clip_specs
        + [pl.BlockSpec((tile, head_dim), lambda h, i: (i, h))] + kv_specs,
        out_specs=pl.BlockSpec((tile, head_dim), lambda h, i: (i, h)),
        out_shape=jax.ShapeDtypeStruct((rows, width), jnp.bfloat16),
    )(qclip, *([kclip] * len(windows)), queries, *kv_args)


def group_order(parts, quarter):
    ordered = jnp.stack([parts[0]] + parts[:0:-1], axis=0)
    return jnp.roll(ordered, quarter, axis=0)


def attend(queries, key_rows, value_rows, allowed, heads, head_groups):
    row_count = queries.shape[0]
    feat_width = queries.shape[1]
    head_dim = feat_width // heads
    per_group = heads // head_groups
    score_scale = 1.0 / math.sqrt(head_dim)

    def split_heads(source_rows):
        return source_rows.reshape(
            source_rows.shape[0], head_groups, per_group, head_dim
        ).transpose(1, 0, 2, 3)

    def one_group(operands):
        group_queries, group_keys, group_values = operands
        scores = (
            jnp.einsum(
                "rhd,khd->hrk", group_queries, group_keys, preferred_element_type=jnp.float32
            )
            * score_scale
        )
        masked = jnp.where(allowed[None], scores, -1e30)
        row_top = jnp.max(masked, axis=2, keepdims=True)
        weights = jnp.where(allowed[None], jnp.exp(masked - row_top), 0.0)
        row_total = jnp.sum(weights, axis=2)
        summed = jnp.einsum(
            "hrk,khd->rhd",
            weights.astype(jnp.bfloat16),
            group_values,
            preferred_element_type=jnp.float32,
        )
        return summed / jnp.transpose(row_total)[:, :, None]

    results = lax.map(
        one_group, (split_heads(queries), split_heads(key_rows), split_heads(value_rows))
    )
    return results.transpose(1, 0, 2, 3).reshape(row_count, feat_width).astype(jnp.bfloat16)


def body(fine_qkv, clip_ids, w_coarse, w_out):
    tok_count = fine_qkv.shape[0]
    feat_width = fine_qkv.shape[2]
    coarse_rows = tok_count // POOL
    group_rows = QUARTERS * coarse_rows
    position = lax.axis_index("seq")
    quarter = position % QUARTERS
    cycle_place = position // QUARTERS
    planes = jnp.transpose(fine_qkv, (1, 0, 2))
    own_pairs = planes[1:]
    prev0 = passed_along(own_pairs, "seq", 2)
    prev1a = pair_swap(own_pairs, "seq", False)
    clip_front = jnp.concatenate([jnp.full((FREACH * coarse_rows,), -1, jnp.int32), clip_ids])
    key_clip = jnp.repeat(
        lax.dynamic_slice_in_dim(clip_front, position * coarse_rows, (FREACH + 1) * coarse_rows, 0),
        POOL,
    )
    own_clip = lax.dynamic_slice_in_dim(clip_ids, position * coarse_rows, coarse_rows, 0)
    query_clip = jnp.repeat(own_clip, POOL)
    fine_out, pooled = fine_attention(
        planes, prev0, prev1a, query_clip.reshape(tok_count, 1),
        key_clip.reshape(1, (FREACH + 1) * tok_count), FHEADS,
    )
    quarter_width = w_coarse.shape[2] // QUARTERS
    wplanes = jnp.transpose(w_coarse, (1, 0, 2))
    projected = jnp.einsum(
        "rd,mdc->mrc", pooled, wplanes, preferred_element_type=jnp.float32
    ).astype(jnp.bfloat16)
    pieces = []
    for shift in range(QUARTERS):
        piece = lax.dynamic_slice_in_dim(
            projected, ((quarter + shift) % QUARTERS) * quarter_width, quarter_width, 2
        )
        pieces.append(piece if shift == 0 else within_group(piece, "seq", shift))
    grouped = group_order(pieces, quarter)
    grouped = jnp.transpose(grouped, (1, 0, 2, 3)).reshape(3, group_rows, quarter_width)
    coarse_queries = grouped[0]
    coarse_pairs = grouped[1:]
    one_back = passed_along(coarse_pairs, "seq", QUARTERS)
    two_back = passed_along(coarse_pairs, "seq", 2 * QUARTERS)
    three_back = passed_along(two_back, "seq", QUARTERS)
    earlier = [three_back, two_back, one_back]
    clip_back = jnp.concatenate([jnp.full((CREACH * group_rows,), -1, jnp.int32), clip_ids])
    coarse_key_clip = lax.dynamic_slice_in_dim(
        clip_back, cycle_place * group_rows, (CREACH + 1) * group_rows, 0
    )
    coarse_query_clip = lax.dynamic_slice_in_dim(clip_ids, cycle_place * group_rows, group_rows, 0)
    coarse_att = coarse_attention(
        coarse_queries, earlier + [coarse_pairs], coarse_query_clip.reshape(group_rows, 1),
        coarse_key_clip.reshape(1, (CREACH + 1) * group_rows), CHEADS // QUARTERS,
    )
    shares = []
    for shift in range(QUARTERS):
        share = lax.dynamic_slice_in_dim(
            coarse_att, ((quarter + shift) % QUARTERS) * coarse_rows, coarse_rows, 0
        )
        shares.append(share if shift == 0 else within_group(share, "seq", shift))
    att_rows = jnp.transpose(group_order(shares, quarter), (1, 0, 2)).reshape(
        coarse_rows, QUARTERS * quarter_width
    )
    coarse_up = jnp.dot(att_rows, w_out, preferred_element_type=jnp.float32).astype(jnp.bfloat16)
    carried = passed_along(coarse_up[-1:], "seq", 1)
    previous = jnp.concatenate([carried, coarse_up[:-1]], axis=0)
    clip_before = jnp.concatenate([jnp.full((1,), -1, jnp.int32), clip_ids])
    prev_clip = lax.dynamic_slice_in_dim(clip_before, position * coarse_rows, coarse_rows, 0)
    joined = prev_clip == own_clip
    lifted = jnp.where(joined[:, None], previous, jnp.zeros_like(previous))
    return mix(fine_out, lifted)


def solution(mesh):
    return jax.shard_map(
        body,
        mesh=mesh,
        in_specs=(P(("groups", "seq"), None, None), P("groups"), P(), P()),
        out_specs=P(("groups", "seq"), None),
        check_vma=False,
    )
```

```python
import functools
import math

import jax
import jax.numpy as jnp
from jax import lax
from jax.experimental import pallas as pl
from jax.experimental.pallas import tpu as pltpu
from jax.sharding import PartitionSpec as P

FHEADS = 16
CHEADS = 8
POOL = 4
QUARTERS = 4
FREACH = 2
CREACH = 3
FINE_TILE = 256


def passed_along(value, axis, steps):
    count = lax.axis_size(axis)
    first, last = (max(0, -steps), min(count, count - steps))
    return lax.ppermute(value, axis, [(source, source + steps) for source in range(first, last)])


def within_group(value, axis, shift):
    count = lax.axis_size(axis)
    pairs = []
    for source in range(count):
        base = source - source % QUARTERS
        pairs.append((source, base + (source % QUARTERS + shift) % QUARTERS))
    return lax.ppermute(value, axis, pairs)


def fine_kernel(qclip_ref, kclip0_ref, kclip1_ref, kclip2_ref, q_ref,
                k0_ref, v0_ref, k1_ref, v1_ref, k1b_ref, v1b_ref, k2_ref, v2_ref,
                out_ref, pool_ref, *, scale):
    tile = q_ref.shape[0]
    width = q_ref.shape[1]
    half = width // 2
    q = q_ref[...] * jnp.asarray(scale, q_ref.dtype)
    lane = lax.broadcasted_iota(jnp.int32, (1, width), 1)
    low = lane < half
    zero = jnp.zeros_like(q)
    head_q = (jnp.where(low, q, zero), jnp.where(low, zero, q))
    qclip = qclip_ref[...]
    seg = k0_ref.shape[0]

    def run(step):
        own = (step + 1) * tile
        keys = (k0_ref[...], k1_ref[...] + k1b_ref[...], k2_ref[0:own, :])
        values = (v0_ref[...], v1_ref[...] + v1b_ref[...], v2_ref[0:own, :])
        qpos = step * tile + lax.broadcasted_iota(jnp.int32, (tile, own), 0)
        kpos = lax.broadcasted_iota(jnp.int32, (tile, own), 1)
        masks = (
            kclip0_ref[...] == qclip,
            kclip1_ref[...] == qclip,
            (kclip2_ref[:, 0:own] == qclip) & (kpos <= qpos),
        )
        results = []
        for h in range(2):
            scores = []
            for j in range(3):
                s = lax.dot_general(head_q[h], keys[j], (((1,), (1,)), ((), ())),
                                    preferred_element_type=jnp.float32)
                scores.append(jnp.where(masks[j], s, -1e30))
            top = jnp.max(scores[0], axis=1, keepdims=True)
            for j in range(1, 3):
                top = jnp.maximum(top, jnp.max(scores[j], axis=1, keepdims=True))
            total = None
            summed = None
            for j in range(3):
                w = jnp.exp(scores[j] - top)
                part = jnp.sum(w, axis=1, keepdims=True)
                pv = jnp.dot(w.astype(jnp.bfloat16), values[j], preferred_element_type=jnp.float32)
                total = part if total is None else total + part
                summed = pv if summed is None else summed + pv
            results.append(summed / total)
        out = jnp.where(low, results[0], results[1]).astype(out_ref.dtype)
        out_ref[...] = out
        rows = tile // POOL
        pool_row = lax.broadcasted_iota(jnp.int32, (rows, tile), 0)
        pool_col = lax.broadcasted_iota(jnp.int32, (rows, tile), 1)
        pool_mat = jnp.where(pool_col // POOL == pool_row, 1.0 / POOL, 0.0).astype(jnp.bfloat16)
        pool_ref[...] = jnp.dot(pool_mat, out, preferred_element_type=jnp.float32).astype(
            pool_ref.dtype)

    for step in range(seg // tile):
        pl.when(pl.program_id(1) == step)(functools.partial(run, step))


def fine_attention(planes, prev0, prev1a, prev1b, qclip, kclip, heads):
    _, tok, width = planes.shape
    head_dim = width // heads
    pair = 2 * head_dim
    pairs = width // pair
    tile = min(FINE_TILE, tok)
    nq = tok // tile
    kernel = functools.partial(fine_kernel, scale=1.0 / math.sqrt(head_dim))

    def plane_spec(plane):
        return pl.BlockSpec((None, tok, pair), lambda h, i: (plane, 0, h))

    return pl.pallas_call(
        kernel,
        grid=(pairs, nq),
        in_specs=[
            pl.BlockSpec((tile, 1), lambda h, i: (i, 0)),
            pl.BlockSpec((1, tok), lambda h, i: (0, 0)),
            pl.BlockSpec((1, tok), lambda h, i: (0, 1)),
            pl.BlockSpec((1, tok), lambda h, i: (0, 2)),
            pl.BlockSpec((None, tile, pair), lambda h, i: (0, i, h)),
            plane_spec(0), plane_spec(1),
            plane_spec(0), plane_spec(1),
            plane_spec(0), plane_spec(1),
            plane_spec(1), plane_spec(2),
        ],
        out_specs=[
            pl.BlockSpec((tile, pair), lambda h, i: (i, h)),
            pl.BlockSpec((tile // POOL, pair), lambda h, i: (i, h)),
        ],
        out_shape=[
            jax.ShapeDtypeStruct((tok, width), jnp.bfloat16),
            jax.ShapeDtypeStruct((tok // POOL, width), jnp.bfloat16),
        ],
    )(qclip, kclip, kclip, kclip, planes, prev0, prev0, prev1a, prev1a, prev1b, prev1b,
      planes, planes)


def mix_kernel(fine_ref, lift_ref, out_ref):
    tile = fine_ref.shape[0]
    rows = lift_ref.shape[0]
    spread_row = lax.broadcasted_iota(jnp.int32, (tile, rows), 0)
    spread_col = lax.broadcasted_iota(jnp.int32, (tile, rows), 1)
    spread = jnp.where(spread_row // POOL == spread_col, 1.0, 0.0).astype(jnp.bfloat16)
    lifted = jnp.dot(spread, lift_ref[...], preferred_element_type=jnp.float32)
    out_ref[...] = (fine_ref[...].astype(jnp.float32) + lifted).astype(out_ref.dtype)


def mix(fine_out, lifted):
    tok, width = fine_out.shape
    tile = min(FINE_TILE, tok)
    return pl.pallas_call(
        mix_kernel,
        grid=(tok // tile,),
        in_specs=[
            pl.BlockSpec((tile, width), lambda i: (i, 0)),
            pl.BlockSpec((tile // POOL, width), lambda i: (i, 0)),
        ],
        out_specs=pl.BlockSpec((tile, width), lambda i: (i, 0)),
        out_shape=jax.ShapeDtypeStruct((tok, width), fine_out.dtype),
    )(fine_out, lifted)


def pair_swap(value, axis, from_odd):
    count = lax.axis_size(axis)
    start = 1 if from_odd else 0
    step = -1 if from_odd else 1
    return lax.ppermute(value, axis, [(source, source + step) for source in range(start, count, 2)])


def coarse_kernel(qclip_ref, kc0_ref, kc1_ref, kc2_ref, kc3_ref, q_ref,
                  k0_ref, v0_ref, k1_ref, v1_ref, k2_ref, v2_ref, k3_ref, v3_ref,
                  out_ref, *, scale):
    tile = q_ref.shape[0]
    seg = k0_ref.shape[0]
    q = q_ref[...]
    qclip = qclip_ref[...]
    keys = (k0_ref, k1_ref, k2_ref, k3_ref)
    values = (v0_ref, v1_ref, v2_ref, v3_ref)
    clips = (kc0_ref, kc1_ref, kc2_ref, kc3_ref)
    qpos = pl.program_id(1) * tile + lax.broadcasted_iota(jnp.int32, (tile, seg), 0)
    kpos = lax.broadcasted_iota(jnp.int32, (tile, seg), 1)
    last = len(keys) - 1
    scores = []
    masks = []
    for j in range(len(keys)):
        allowed = clips[j][...] == qclip
        if j == last:
            allowed = allowed & (kpos <= qpos)
        s = lax.dot_general(q, keys[j][...], (((1,), (1,)), ((), ())),
                            preferred_element_type=jnp.float32) * scale
        scores.append(jnp.where(allowed, s, -1e30))
    top = jnp.max(scores[0], axis=1, keepdims=True)
    for j in range(1, len(keys)):
        top = jnp.maximum(top, jnp.max(scores[j], axis=1, keepdims=True))
    total = None
    summed = None
    for j in range(len(keys)):
        w = jnp.exp(scores[j] - top)
        part = jnp.sum(w, axis=1, keepdims=True)
        pv = jnp.dot(w.astype(jnp.bfloat16), values[j][...], preferred_element_type=jnp.float32)
        total = part if total is None else total + part
        summed = pv if summed is None else summed + pv
    out_ref[...] = (summed / total).astype(out_ref.dtype)


def coarse_attention(queries, windows, qclip, kclip, heads):
    rows, width = queries.shape
    head_dim = width // heads
    tile = min(FINE_TILE, rows)
    seg = windows[0].shape[1]
    kernel = functools.partial(coarse_kernel, scale=1.0 / math.sqrt(head_dim))
    clip_specs = [pl.BlockSpec((1, seg), functools.partial(lambda j, h, i: (0, j), j))
                  for j in range(len(windows))]
    kv_specs = []
    kv_args = []
    for window in windows:
        kv_specs.append(pl.BlockSpec((None, seg, head_dim), lambda h, i: (0, 0, h)))
        kv_specs.append(pl.BlockSpec((None, seg, head_dim), lambda h, i: (1, 0, h)))
        kv_args += [window, window]
    return pl.pallas_call(
        kernel,
        grid=(heads, rows // tile),
        in_specs=[pl.BlockSpec((tile, 1), lambda h, i: (i, 0))] + clip_specs
        + [pl.BlockSpec((tile, head_dim), lambda h, i: (i, h))] + kv_specs,
        out_specs=pl.BlockSpec((tile, head_dim), lambda h, i: (i, h)),
        out_shape=jax.ShapeDtypeStruct((rows, width), jnp.bfloat16),
    )(qclip, *([kclip] * len(windows)), queries, *kv_args)


def group_order(parts, quarter):
    ordered = jnp.stack([parts[0]] + parts[:0:-1], axis=0)
    return jnp.roll(ordered, quarter, axis=0)


def attend(queries, key_rows, value_rows, allowed, heads, head_groups):
    row_count = queries.shape[0]
    feat_width = queries.shape[1]
    head_dim = feat_width // heads
    per_group = heads // head_groups
    score_scale = 1.0 / math.sqrt(head_dim)

    def split_heads(source_rows):
        return source_rows.reshape(
            source_rows.shape[0], head_groups, per_group, head_dim
        ).transpose(1, 0, 2, 3)

    def one_group(operands):
        group_queries, group_keys, group_values = operands
        scores = (
            jnp.einsum(
                "rhd,khd->hrk", group_queries, group_keys, preferred_element_type=jnp.float32
            )
            * score_scale
        )
        masked = jnp.where(allowed[None], scores, -1e30)
        row_top = jnp.max(masked, axis=2, keepdims=True)
        weights = jnp.where(allowed[None], jnp.exp(masked - row_top), 0.0)
        row_total = jnp.sum(weights, axis=2)
        summed = jnp.einsum(
            "hrk,khd->rhd",
            weights.astype(jnp.bfloat16),
            group_values,
            preferred_element_type=jnp.float32,
        )
        return summed / jnp.transpose(row_total)[:, :, None]

    results = lax.map(
        one_group, (split_heads(queries), split_heads(key_rows), split_heads(value_rows))
    )
    return results.transpose(1, 0, 2, 3).reshape(row_count, feat_width).astype(jnp.bfloat16)


def body(fine_qkv, clip_ids, w_coarse, w_out):
    tok_count = fine_qkv.shape[0]
    feat_width = fine_qkv.shape[2]
    coarse_rows = tok_count // POOL
    group_rows = QUARTERS * coarse_rows
    position = lax.axis_index("seq")
    quarter = position % QUARTERS
    cycle_place = position // QUARTERS
    planes = jnp.transpose(fine_qkv, (1, 0, 2))
    own_pairs = planes[1:]
    prev0 = passed_along(own_pairs, "seq", 2)
    prev1a = pair_swap(own_pairs, "seq", False)
    prev1b = pair_swap(prev0, "seq", True)
    clip_front = jnp.concatenate([jnp.full((FREACH * coarse_rows,), -1, jnp.int32), clip_ids])
    key_clip = jnp.repeat(
        lax.dynamic_slice_in_dim(clip_front, position * coarse_rows, (FREACH + 1) * coarse_rows, 0),
        POOL,
    )
    own_clip = lax.dynamic_slice_in_dim(clip_ids, position * coarse_rows, coarse_rows, 0)
    query_clip = jnp.repeat(own_clip, POOL)
    fine_out, pooled = fine_attention(
        planes, prev0, prev1a, prev1b, query_clip.reshape(tok_count, 1),
        key_clip.reshape(1, (FREACH + 1) * tok_count), FHEADS,
    )
    quarter_width = w_coarse.shape[2] // QUARTERS
    wplanes = jnp.transpose(w_coarse, (1, 0, 2))
    projected = jnp.einsum(
        "rd,mdc->mrc", pooled, wplanes, preferred_element_type=jnp.float32
    ).astype(jnp.bfloat16)
    pieces = []
    for shift in range(QUARTERS):
        piece = lax.dynamic_slice_in_dim(
            projected, ((quarter + shift) % QUARTERS) * quarter_width, quarter_width, 2
        )
        pieces.append(piece if shift == 0 else within_group(piece, "seq", shift))
    grouped = group_order(pieces, quarter)
    grouped = jnp.transpose(grouped, (1, 0, 2, 3)).reshape(3, group_rows, quarter_width)
    coarse_queries = grouped[0]
    coarse_pairs = grouped[1:]
    one_back = passed_along(coarse_pairs, "seq", QUARTERS)
    two_back = passed_along(coarse_pairs, "seq", 2 * QUARTERS)
    three_back = passed_along(one_back, "seq", 2 * QUARTERS)
    earlier = [three_back, two_back, one_back]
    clip_back = jnp.concatenate([jnp.full((CREACH * group_rows,), -1, jnp.int32), clip_ids])
    coarse_key_clip = lax.dynamic_slice_in_dim(
        clip_back, cycle_place * group_rows, (CREACH + 1) * group_rows, 0
    )
    coarse_query_clip = lax.dynamic_slice_in_dim(clip_ids, cycle_place * group_rows, group_rows, 0)
    coarse_att = coarse_attention(
        coarse_queries, earlier + [coarse_pairs], coarse_query_clip.reshape(group_rows, 1),
        coarse_key_clip.reshape(1, (CREACH + 1) * group_rows), CHEADS // QUARTERS,
    )
    shares = []
    for shift in range(QUARTERS):
        share = lax.dynamic_slice_in_dim(
            coarse_att, ((quarter + shift) % QUARTERS) * coarse_rows, coarse_rows, 0
        )
        shares.append(share if shift == 0 else within_group(share, "seq", shift))
    att_rows = jnp.transpose(group_order(shares, quarter), (1, 0, 2)).reshape(
        coarse_rows, QUARTERS * quarter_width
    )
    coarse_up = jnp.dot(att_rows, w_out, preferred_element_type=jnp.float32).astype(jnp.bfloat16)
    carried = passed_along(coarse_up[-1:], "seq", 1)
    previous = jnp.concatenate([carried, coarse_up[:-1]], axis=0)
    clip_before = jnp.concatenate([jnp.full((1,), -1, jnp.int32), clip_ids])
    prev_clip = lax.dynamic_slice_in_dim(clip_before, position * coarse_rows, coarse_rows, 0)
    joined = prev_clip == own_clip
    lifted = jnp.where(joined[:, None], previous, jnp.zeros_like(previous))
    return mix(fine_out, lifted)


def solution(mesh):
    return jax.shard_map(
        body,
        mesh=mesh,
        in_specs=(P(("groups", "seq"), None, None), P("groups"), P(), P()),
        out_specs=P(("groups", "seq"), None),
        check_vma=False,
    )
```

```python
import functools
import math

import jax
import jax.numpy as jnp
from jax import lax
from jax.experimental import pallas as pl
from jax.experimental.pallas import tpu as pltpu
from jax.sharding import PartitionSpec as P

FHEADS = 16
CHEADS = 8
POOL = 4
QUARTERS = 4
FREACH = 2
CREACH = 3
FINE_TILE = 256


def passed_along(value, axis, steps):
    count = lax.axis_size(axis)
    first, last = (max(0, -steps), min(count, count - steps))
    return lax.ppermute(value, axis, [(source, source + steps) for source in range(first, last)])


def within_group(value, axis, shift):
    count = lax.axis_size(axis)
    pairs = []
    for source in range(count):
        base = source - source % QUARTERS
        pairs.append((source, base + (source % QUARTERS + shift) % QUARTERS))
    return lax.ppermute(value, axis, pairs)


def fine_kernel(qclip_ref, kclip0_ref, kclip1_ref, kclip2_ref, q_ref,
                k0_ref, v0_ref, k1_ref, v1_ref, k1b_ref, v1b_ref, k2_ref, v2_ref,
                out_ref, pool_ref, *, scale):
    tile = q_ref.shape[0]
    width = q_ref.shape[1]
    half = width // 2
    q = q_ref[...] * jnp.asarray(scale, q_ref.dtype)
    lane = lax.broadcasted_iota(jnp.int32, (1, width), 1)
    low = lane < half
    zero = jnp.zeros_like(q)
    head_q = (jnp.where(low, q, zero), jnp.where(low, zero, q))
    qclip = qclip_ref[...]
    seg = k0_ref.shape[0]

    def run(step):
        own = (step + 1) * tile
        keys = (k0_ref[...], k1_ref[...] + k1b_ref[...], k2_ref[0:own, :])
        values = (v0_ref[...], v1_ref[...] + v1b_ref[...], v2_ref[0:own, :])
        qpos = step * tile + lax.broadcasted_iota(jnp.int32, (tile, own), 0)
        kpos = lax.broadcasted_iota(jnp.int32, (tile, own), 1)
        masks = (
            kclip0_ref[...] == qclip,
            kclip1_ref[...] == qclip,
            (kclip2_ref[:, 0:own] == qclip) & (kpos <= qpos),
        )
        results = []
        for h in range(2):
            scores = []
            for j in range(3):
                s = lax.dot_general(head_q[h], keys[j], (((1,), (1,)), ((), ())),
                                    preferred_element_type=jnp.float32)
                scores.append(jnp.where(masks[j], s, -1e30))
            top = jnp.max(scores[0], axis=1, keepdims=True)
            for j in range(1, 3):
                top = jnp.maximum(top, jnp.max(scores[j], axis=1, keepdims=True))
            total = None
            summed = None
            for j in range(3):
                w = jnp.exp(scores[j] - top)
                part = jnp.sum(w, axis=1, keepdims=True)
                pv = jnp.dot(w.astype(jnp.bfloat16), values[j], preferred_element_type=jnp.float32)
                total = part if total is None else total + part
                summed = pv if summed is None else summed + pv
            results.append(summed / total)
        out = jnp.where(low, results[0], results[1]).astype(out_ref.dtype)
        out_ref[...] = out
        rows = tile // POOL
        pool_row = lax.broadcasted_iota(jnp.int32, (rows, tile), 0)
        pool_col = lax.broadcasted_iota(jnp.int32, (rows, tile), 1)
        pool_mat = jnp.where(pool_col // POOL == pool_row, 1.0 / POOL, 0.0).astype(jnp.bfloat16)
        pool_ref[...] = jnp.dot(pool_mat, out, preferred_element_type=jnp.float32).astype(
            pool_ref.dtype)

    for step in range(seg // tile):
        pl.when(pl.program_id(1) == step)(functools.partial(run, step))


def fine_attention(planes, prev0, prev1a, prev1b, qclip, kclip, heads):
    _, tok, width = planes.shape
    head_dim = width // heads
    pair = 2 * head_dim
    pairs = width // pair
    tile = min(FINE_TILE, tok)
    nq = tok // tile
    kernel = functools.partial(fine_kernel, scale=1.0 / math.sqrt(head_dim))

    def plane_spec(plane):
        return pl.BlockSpec((None, tok, pair), lambda h, i: (plane, 0, h))

    return pl.pallas_call(
        kernel,
        grid=(pairs, nq),
        in_specs=[
            pl.BlockSpec((tile, 1), lambda h, i: (i, 0)),
            pl.BlockSpec((1, tok), lambda h, i: (0, 0)),
            pl.BlockSpec((1, tok), lambda h, i: (0, 1)),
            pl.BlockSpec((1, tok), lambda h, i: (0, 2)),
            pl.BlockSpec((None, tile, pair), lambda h, i: (0, i, h)),
            plane_spec(0), plane_spec(1),
            plane_spec(0), plane_spec(1),
            plane_spec(0), plane_spec(1),
            plane_spec(1), plane_spec(2),
        ],
        out_specs=[
            pl.BlockSpec((tile, pair), lambda h, i: (i, h)),
            pl.BlockSpec((tile // POOL, pair), lambda h, i: (i, h)),
        ],
        out_shape=[
            jax.ShapeDtypeStruct((tok, width), jnp.bfloat16),
            jax.ShapeDtypeStruct((tok // POOL, width), jnp.bfloat16),
        ],
    )(qclip, kclip, kclip, kclip, planes, prev0, prev0, prev1a, prev1a, prev1b, prev1b,
      planes, planes)


def mix_kernel(fine_ref, lift_ref, out_ref):
    tile = fine_ref.shape[0]
    rows = lift_ref.shape[0]
    spread_row = lax.broadcasted_iota(jnp.int32, (tile, rows), 0)
    spread_col = lax.broadcasted_iota(jnp.int32, (tile, rows), 1)
    spread = jnp.where(spread_row // POOL == spread_col, 1.0, 0.0).astype(jnp.bfloat16)
    lifted = jnp.dot(spread, lift_ref[...], preferred_element_type=jnp.float32)
    out_ref[...] = (fine_ref[...].astype(jnp.float32) + lifted).astype(out_ref.dtype)


def mix(fine_out, lifted):
    tok, width = fine_out.shape
    tile = min(FINE_TILE, tok)
    return pl.pallas_call(
        mix_kernel,
        grid=(tok // tile,),
        in_specs=[
            pl.BlockSpec((tile, width), lambda i: (i, 0)),
            pl.BlockSpec((tile // POOL, width), lambda i: (i, 0)),
        ],
        out_specs=pl.BlockSpec((tile, width), lambda i: (i, 0)),
        out_shape=jax.ShapeDtypeStruct((tok, width), fine_out.dtype),
    )(fine_out, lifted)


def pair_swap(value, axis, from_odd):
    count = lax.axis_size(axis)
    start = 1 if from_odd else 0
    step = -1 if from_odd else 1
    return lax.ppermute(value, axis, [(source, source + step) for source in range(start, count, 2)])


def coarse_kernel(qclip_ref, kc0_ref, kc1_ref, kc2_ref, kc3_ref, q_ref,
                  k0_ref, v0_ref, k1_ref, v1_ref, k2_ref, v2_ref, k3_ref, v3_ref,
                  out_ref, *, scale):
    tile = q_ref.shape[0]
    seg = k0_ref.shape[0]
    q = q_ref[...]
    qclip = qclip_ref[...]
    keys = (k0_ref, k1_ref, k2_ref, k3_ref)
    values = (v0_ref, v1_ref, v2_ref, v3_ref)
    clips = (kc0_ref, kc1_ref, kc2_ref, kc3_ref)
    qpos = pl.program_id(1) * tile + lax.broadcasted_iota(jnp.int32, (tile, seg), 0)
    kpos = lax.broadcasted_iota(jnp.int32, (tile, seg), 1)
    last = len(keys) - 1
    scores = []
    masks = []
    for j in range(len(keys)):
        allowed = clips[j][...] == qclip
        if j == last:
            allowed = allowed & (kpos <= qpos)
        s = lax.dot_general(q, keys[j][...], (((1,), (1,)), ((), ())),
                            preferred_element_type=jnp.float32) * scale
        scores.append(jnp.where(allowed, s, -1e30))
    top = jnp.max(scores[0], axis=1, keepdims=True)
    for j in range(1, len(keys)):
        top = jnp.maximum(top, jnp.max(scores[j], axis=1, keepdims=True))
    total = None
    summed = None
    for j in range(len(keys)):
        w = jnp.exp(scores[j] - top)
        part = jnp.sum(w, axis=1, keepdims=True)
        pv = jnp.dot(w.astype(jnp.bfloat16), values[j][...], preferred_element_type=jnp.float32)
        total = part if total is None else total + part
        summed = pv if summed is None else summed + pv
    out_ref[...] = (summed / total).astype(out_ref.dtype)


def coarse_attention(queries, windows, qclip, kclip, heads):
    rows, width = queries.shape
    head_dim = width // heads
    tile = min(FINE_TILE, rows)
    seg = windows[0].shape[1]
    kernel = functools.partial(coarse_kernel, scale=1.0 / math.sqrt(head_dim))
    clip_specs = [pl.BlockSpec((1, seg), functools.partial(lambda j, h, i: (0, j), j))
                  for j in range(len(windows))]
    kv_specs = []
    kv_args = []
    for window in windows:
        kv_specs.append(pl.BlockSpec((None, seg, head_dim), lambda h, i: (0, 0, h)))
        kv_specs.append(pl.BlockSpec((None, seg, head_dim), lambda h, i: (1, 0, h)))
        kv_args += [window, window]
    return pl.pallas_call(
        kernel,
        grid=(heads, rows // tile),
        in_specs=[pl.BlockSpec((tile, 1), lambda h, i: (i, 0))] + clip_specs
        + [pl.BlockSpec((tile, head_dim), lambda h, i: (i, h))] + kv_specs,
        out_specs=pl.BlockSpec((tile, head_dim), lambda h, i: (i, h)),
        out_shape=jax.ShapeDtypeStruct((rows, width), jnp.bfloat16),
    )(qclip, *([kclip] * len(windows)), queries, *kv_args)


def group_order(parts, quarter):
    ordered = jnp.stack([parts[0]] + parts[:0:-1], axis=0)
    return jnp.roll(ordered, quarter, axis=0)


def attend(queries, key_rows, value_rows, allowed, heads, head_groups):
    row_count = queries.shape[0]
    feat_width = queries.shape[1]
    head_dim = feat_width // heads
    per_group = heads // head_groups
    score_scale = 1.0 / math.sqrt(head_dim)

    def split_heads(source_rows):
        return source_rows.reshape(
            source_rows.shape[0], head_groups, per_group, head_dim
        ).transpose(1, 0, 2, 3)

    def one_group(operands):
        group_queries, group_keys, group_values = operands
        scores = (
            jnp.einsum(
                "rhd,khd->hrk", group_queries, group_keys, preferred_element_type=jnp.float32
            )
            * score_scale
        )
        masked = jnp.where(allowed[None], scores, -1e30)
        row_top = jnp.max(masked, axis=2, keepdims=True)
        weights = jnp.where(allowed[None], jnp.exp(masked - row_top), 0.0)
        row_total = jnp.sum(weights, axis=2)
        summed = jnp.einsum(
            "hrk,khd->rhd",
            weights.astype(jnp.bfloat16),
            group_values,
            preferred_element_type=jnp.float32,
        )
        return summed / jnp.transpose(row_total)[:, :, None]

    results = lax.map(
        one_group, (split_heads(queries), split_heads(key_rows), split_heads(value_rows))
    )
    return results.transpose(1, 0, 2, 3).reshape(row_count, feat_width).astype(jnp.bfloat16)


def body(fine_qkv, clip_ids, w_coarse, w_out):
    tok_count = fine_qkv.shape[0]
    feat_width = fine_qkv.shape[2]
    coarse_rows = tok_count // POOL
    group_rows = QUARTERS * coarse_rows
    position = lax.axis_index("seq")
    quarter = position % QUARTERS
    cycle_place = position // QUARTERS
    planes = jnp.transpose(fine_qkv, (1, 0, 2))
    own_pairs = planes[1:]
    prev0 = passed_along(own_pairs, "seq", 2)
    prev1a = pair_swap(own_pairs, "seq", False)
    prev1b = pair_swap(prev0, "seq", True)
    clip_front = jnp.concatenate([jnp.full((FREACH * coarse_rows,), -1, jnp.int32), clip_ids])
    key_clip = jnp.repeat(
        lax.dynamic_slice_in_dim(clip_front, position * coarse_rows, (FREACH + 1) * coarse_rows, 0),
        POOL,
    )
    own_clip = lax.dynamic_slice_in_dim(clip_ids, position * coarse_rows, coarse_rows, 0)
    query_clip = jnp.repeat(own_clip, POOL)
    fine_out, pooled = fine_attention(
        planes, prev0, prev1a, prev1b, query_clip.reshape(tok_count, 1),
        key_clip.reshape(1, (FREACH + 1) * tok_count), FHEADS,
    )
    quarter_width = w_coarse.shape[2] // QUARTERS
    wplanes = jnp.transpose(w_coarse, (1, 0, 2))
    projected = jnp.einsum(
        "rd,mdc->mrc", pooled, wplanes, preferred_element_type=jnp.float32
    ).astype(jnp.bfloat16)
    pieces = []
    for shift in range(QUARTERS):
        piece = lax.dynamic_slice_in_dim(
            projected, ((quarter + shift) % QUARTERS) * quarter_width, quarter_width, 2
        )
        pieces.append(piece if shift == 0 else within_group(piece, "seq", shift))
    grouped = group_order(pieces, quarter)
    grouped = jnp.transpose(grouped, (1, 0, 2, 3)).reshape(3, group_rows, quarter_width)
    coarse_queries = grouped[0]
    coarse_pairs = grouped[1:]
    one_back = passed_along(coarse_pairs, "seq", QUARTERS)
    two_back = passed_along(coarse_pairs, "seq", 2 * QUARTERS)
    three_back = passed_along(two_back, "seq", QUARTERS)
    earlier = [three_back, two_back, one_back]
    clip_back = jnp.concatenate([jnp.full((CREACH * group_rows,), -1, jnp.int32), clip_ids])
    coarse_key_clip = lax.dynamic_slice_in_dim(
        clip_back, cycle_place * group_rows, (CREACH + 1) * group_rows, 0
    )
    coarse_query_clip = lax.dynamic_slice_in_dim(clip_ids, cycle_place * group_rows, group_rows, 0)
    coarse_att = coarse_attention(
        coarse_queries, earlier + [coarse_pairs], coarse_query_clip.reshape(group_rows, 1),
        coarse_key_clip.reshape(1, (CREACH + 1) * group_rows), CHEADS // QUARTERS,
    )
    shares = []
    for shift in range(QUARTERS):
        share = lax.dynamic_slice_in_dim(
            coarse_att, ((quarter + shift) % QUARTERS) * coarse_rows, coarse_rows, 0
        )
        shares.append(share if shift == 0 else within_group(share, "seq", shift))
    att_rows = jnp.transpose(group_order(shares, quarter), (1, 0, 2)).reshape(
        coarse_rows, QUARTERS * quarter_width
    )
    coarse_up = jnp.dot(att_rows, w_out, preferred_element_type=jnp.float32).astype(jnp.bfloat16)
    carried = passed_along(coarse_up[-1:], "seq", 1)
    previous = jnp.concatenate([jnp.zeros_like(carried), coarse_up[:-1]], axis=0)
    clip_before = jnp.concatenate([jnp.full((1,), -1, jnp.int32), clip_ids])
    prev_clip = lax.dynamic_slice_in_dim(clip_before, position * coarse_rows, coarse_rows, 0)
    joined = prev_clip == own_clip
    lifted = jnp.where(joined[:, None], previous, jnp.zeros_like(previous))
    mixed = mix(fine_out, lifted)
    head_lift = jnp.where(joined[:1, None], carried, jnp.zeros_like(carried)).astype(jnp.float32)
    head_rows = (fine_out[:POOL].astype(jnp.float32) + head_lift).astype(mixed.dtype)
    return lax.dynamic_update_slice(mixed, head_rows, (0, 0))


def solution(mesh):
    return jax.shard_map(
        body,
        mesh=mesh,
        in_specs=(P(("groups", "seq"), None, None), P("groups"), P(), P()),
        out_specs=P(("groups", "seq"), None),
        check_vma=False,
    )
```

```python
import functools
import math

import jax
import jax.numpy as jnp
from jax import lax
from jax.experimental import pallas as pl
from jax.experimental.pallas import tpu as pltpu
from jax.sharding import PartitionSpec as P

FHEADS = 16
CHEADS = 8
POOL = 4
QUARTERS = 4
FREACH = 2
CREACH = 3
FINE_TILE = 256


def passed_along(value, axis, steps):
    count = lax.axis_size(axis)
    first, last = (max(0, -steps), min(count, count - steps))
    return lax.ppermute(value, axis, [(source, source + steps) for source in range(first, last)])


def within_group(value, axis, shift):
    count = lax.axis_size(axis)
    pairs = []
    for source in range(count):
        base = source - source % QUARTERS
        pairs.append((source, base + (source % QUARTERS + shift) % QUARTERS))
    return lax.ppermute(value, axis, pairs)


def fine_kernel(qclip_ref, kclip0_ref, kclip1_ref, kclip2_ref, q_ref,
                k0_ref, v0_ref, k1_ref, v1_ref, k1b_ref, v1b_ref, k2_ref, v2_ref,
                out_ref, pool_ref, bias_ref, *, scale):
    tile = q_ref.shape[0]
    width = q_ref.shape[1]
    half = width // 2
    seg = k0_ref.shape[0]
    tile_index = pl.program_id(0)

    @pl.when(pl.program_id(1) == 0)
    def _():
        qclip = qclip_ref[...]
        qpos = tile_index * tile + lax.broadcasted_iota(jnp.int32, (tile, seg), 0)
        kpos = lax.broadcasted_iota(jnp.int32, (tile, seg), 1)
        allowed = (
            kclip0_ref[...] == qclip,
            kclip1_ref[...] == qclip,
            (kclip2_ref[...] == qclip) & (kpos <= qpos),
        )
        for j in range(3):
            bias_ref[:, j * seg:(j + 1) * seg] = jnp.where(allowed[j], 0.0, -1e30)

    q = q_ref[...] * jnp.asarray(scale, q_ref.dtype)
    lane = lax.broadcasted_iota(jnp.int32, (1, width), 1)
    low = lane < half
    zero = jnp.zeros_like(q)
    head_q = (jnp.where(low, q, zero), jnp.where(low, zero, q))

    def run(step):
        own = (step + 1) * tile
        keys = (k0_ref[...], k1_ref[...] + k1b_ref[...], k2_ref[0:own, :])
        values = (v0_ref[...], v1_ref[...] + v1b_ref[...], v2_ref[0:own, :])
        spans = ((0, seg), (seg, seg), (2 * seg, own))
        results = []
        for h in range(2):
            scores = []
            for j in range(3):
                s = lax.dot_general(head_q[h], keys[j], (((1,), (1,)), ((), ())),
                                    preferred_element_type=jnp.float32)
                start, length = spans[j]
                scores.append(s + bias_ref[:, start:start + length])
            top = jnp.max(scores[0], axis=1, keepdims=True)
            for j in range(1, 3):
                top = jnp.maximum(top, jnp.max(scores[j], axis=1, keepdims=True))
            total = None
            summed = None
            for j in range(3):
                w = jnp.exp(scores[j] - top)
                part = jnp.sum(w, axis=1, keepdims=True)
                pv = jnp.dot(w.astype(jnp.bfloat16), values[j], preferred_element_type=jnp.float32)
                total = part if total is None else total + part
                summed = pv if summed is None else summed + pv
            results.append(summed / total)
        out = jnp.where(low, results[0], results[1]).astype(out_ref.dtype)
        out_ref[...] = out
        rows = tile // POOL
        pool_row = lax.broadcasted_iota(jnp.int32, (rows, tile), 0)
        pool_col = lax.broadcasted_iota(jnp.int32, (rows, tile), 1)
        pool_mat = jnp.where(pool_col // POOL == pool_row, 1.0 / POOL, 0.0).astype(jnp.bfloat16)
        pool_ref[...] = jnp.dot(pool_mat, out, preferred_element_type=jnp.float32).astype(
            pool_ref.dtype)

    for step in range(seg // tile):
        pl.when(tile_index == step)(functools.partial(run, step))


def fine_attention(planes, prev0, prev1a, prev1b, qclip, kclip, heads):
    _, tok, width = planes.shape
    head_dim = width // heads
    pair = 2 * head_dim
    pairs = width // pair
    tile = min(FINE_TILE, tok)
    nq = tok // tile
    kernel = functools.partial(fine_kernel, scale=1.0 / math.sqrt(head_dim))

    def plane_spec(plane):
        return pl.BlockSpec((None, tok, pair), lambda i, h: (plane, 0, h))

    return pl.pallas_call(
        kernel,
        grid=(nq, pairs),
        in_specs=[
            pl.BlockSpec((tile, 1), lambda i, h: (i, 0)),
            pl.BlockSpec((1, tok), lambda i, h: (0, 0)),
            pl.BlockSpec((1, tok), lambda i, h: (0, 1)),
            pl.BlockSpec((1, tok), lambda i, h: (0, 2)),
            pl.BlockSpec((None, tile, pair), lambda i, h: (0, i, h)),
            plane_spec(0), plane_spec(1),
            plane_spec(0), plane_spec(1),
            plane_spec(0), plane_spec(1),
            plane_spec(1), plane_spec(2),
        ],
        out_specs=[
            pl.BlockSpec((tile, pair), lambda i, h: (i, h)),
            pl.BlockSpec((tile // POOL, pair), lambda i, h: (i, h)),
        ],
        out_shape=[
            jax.ShapeDtypeStruct((tok, width), jnp.bfloat16),
            jax.ShapeDtypeStruct((tok // POOL, width), jnp.bfloat16),
        ],
        scratch_shapes=[pltpu.VMEM((tile, 3 * tok), jnp.float32)],
    )(qclip, kclip, kclip, kclip, planes, prev0, prev0, prev1a, prev1a, prev1b, prev1b,
      planes, planes)


def mix_kernel(fine_ref, lift_ref, out_ref):
    tile = fine_ref.shape[0]
    rows = lift_ref.shape[0]
    spread_row = lax.broadcasted_iota(jnp.int32, (tile, rows), 0)
    spread_col = lax.broadcasted_iota(jnp.int32, (tile, rows), 1)
    spread = jnp.where(spread_row // POOL == spread_col, 1.0, 0.0).astype(jnp.bfloat16)
    lifted = jnp.dot(spread, lift_ref[...], preferred_element_type=jnp.float32)
    out_ref[...] = (fine_ref[...].astype(jnp.float32) + lifted).astype(out_ref.dtype)


def mix(fine_out, lifted):
    tok, width = fine_out.shape
    tile = min(FINE_TILE, tok)
    return pl.pallas_call(
        mix_kernel,
        grid=(tok // tile,),
        in_specs=[
            pl.BlockSpec((tile, width), lambda i: (i, 0)),
            pl.BlockSpec((tile // POOL, width), lambda i: (i, 0)),
        ],
        out_specs=pl.BlockSpec((tile, width), lambda i: (i, 0)),
        out_shape=jax.ShapeDtypeStruct((tok, width), fine_out.dtype),
    )(fine_out, lifted)


def pair_swap(value, axis, from_odd):
    count = lax.axis_size(axis)
    start = 1 if from_odd else 0
    step = -1 if from_odd else 1
    return lax.ppermute(value, axis, [(source, source + step) for source in range(start, count, 2)])


def coarse_kernel(qclip_ref, kc0_ref, kc1_ref, kc2_ref, kc3_ref, q_ref,
                  k0_ref, v0_ref, k1_ref, v1_ref, k2_ref, v2_ref, k3_ref, v3_ref,
                  out_ref, *, scale):
    tile = q_ref.shape[0]
    seg = k0_ref.shape[0]
    q = q_ref[...]
    qclip = qclip_ref[...]
    keys = (k0_ref, k1_ref, k2_ref, k3_ref)
    values = (v0_ref, v1_ref, v2_ref, v3_ref)
    clips = (kc0_ref, kc1_ref, kc2_ref, kc3_ref)
    qpos = pl.program_id(1) * tile + lax.broadcasted_iota(jnp.int32, (tile, seg), 0)
    kpos = lax.broadcasted_iota(jnp.int32, (tile, seg), 1)
    last = len(keys) - 1
    scores = []
    masks = []
    for j in range(len(keys)):
        allowed = clips[j][...] == qclip
        if j == last:
            allowed = allowed & (kpos <= qpos)
        s = lax.dot_general(q, keys[j][...], (((1,), (1,)), ((), ())),
                            preferred_element_type=jnp.float32) * scale
        scores.append(jnp.where(allowed, s, -1e30))
    top = jnp.max(scores[0], axis=1, keepdims=True)
    for j in range(1, len(keys)):
        top = jnp.maximum(top, jnp.max(scores[j], axis=1, keepdims=True))
    total = None
    summed = None
    for j in range(len(keys)):
        w = jnp.exp(scores[j] - top)
        part = jnp.sum(w, axis=1, keepdims=True)
        pv = jnp.dot(w.astype(jnp.bfloat16), values[j][...], preferred_element_type=jnp.float32)
        total = part if total is None else total + part
        summed = pv if summed is None else summed + pv
    out_ref[...] = (summed / total).astype(out_ref.dtype)


def coarse_attention(queries, windows, qclip, kclip, heads):
    rows, width = queries.shape
    head_dim = width // heads
    tile = min(FINE_TILE, rows)
    seg = windows[0].shape[1]
    kernel = functools.partial(coarse_kernel, scale=1.0 / math.sqrt(head_dim))
    clip_specs = [pl.BlockSpec((1, seg), functools.partial(lambda j, h, i: (0, j), j))
                  for j in range(len(windows))]
    kv_specs = []
    kv_args = []
    for window in windows:
        kv_specs.append(pl.BlockSpec((None, seg, head_dim), lambda h, i: (0, 0, h)))
        kv_specs.append(pl.BlockSpec((None, seg, head_dim), lambda h, i: (1, 0, h)))
        kv_args += [window, window]
    return pl.pallas_call(
        kernel,
        grid=(heads, rows // tile),
        in_specs=[pl.BlockSpec((tile, 1), lambda h, i: (i, 0))] + clip_specs
        + [pl.BlockSpec((tile, head_dim), lambda h, i: (i, h))] + kv_specs,
        out_specs=pl.BlockSpec((tile, head_dim), lambda h, i: (i, h)),
        out_shape=jax.ShapeDtypeStruct((rows, width), jnp.bfloat16),
    )(qclip, *([kclip] * len(windows)), queries, *kv_args)


def group_order(parts, quarter):
    ordered = jnp.stack([parts[0]] + parts[:0:-1], axis=0)
    return jnp.roll(ordered, quarter, axis=0)


def attend(queries, key_rows, value_rows, allowed, heads, head_groups):
    row_count = queries.shape[0]
    feat_width = queries.shape[1]
    head_dim = feat_width // heads
    per_group = heads // head_groups
    score_scale = 1.0 / math.sqrt(head_dim)

    def split_heads(source_rows):
        return source_rows.reshape(
            source_rows.shape[0], head_groups, per_group, head_dim
        ).transpose(1, 0, 2, 3)

    def one_group(operands):
        group_queries, group_keys, group_values = operands
        scores = (
            jnp.einsum(
                "rhd,khd->hrk", group_queries, group_keys, preferred_element_type=jnp.float32
            )
            * score_scale
        )
        masked = jnp.where(allowed[None], scores, -1e30)
        row_top = jnp.max(masked, axis=2, keepdims=True)
        weights = jnp.where(allowed[None], jnp.exp(masked - row_top), 0.0)
        row_total = jnp.sum(weights, axis=2)
        summed = jnp.einsum(
            "hrk,khd->rhd",
            weights.astype(jnp.bfloat16),
            group_values,
            preferred_element_type=jnp.float32,
        )
        return summed / jnp.transpose(row_total)[:, :, None]

    results = lax.map(
        one_group, (split_heads(queries), split_heads(key_rows), split_heads(value_rows))
    )
    return results.transpose(1, 0, 2, 3).reshape(row_count, feat_width).astype(jnp.bfloat16)


def body(fine_qkv, clip_ids, w_coarse, w_out):
    tok_count = fine_qkv.shape[0]
    feat_width = fine_qkv.shape[2]
    coarse_rows = tok_count // POOL
    group_rows = QUARTERS * coarse_rows
    position = lax.axis_index("seq")
    quarter = position % QUARTERS
    cycle_place = position // QUARTERS
    planes = jnp.transpose(fine_qkv, (1, 0, 2))
    own_pairs = planes[1:]
    prev0 = passed_along(own_pairs, "seq", 2)
    prev1a = pair_swap(own_pairs, "seq", False)
    prev1b = pair_swap(prev0, "seq", True)
    clip_front = jnp.concatenate([jnp.full((FREACH * coarse_rows,), -1, jnp.int32), clip_ids])
    key_clip = jnp.repeat(
        lax.dynamic_slice_in_dim(clip_front, position * coarse_rows, (FREACH + 1) * coarse_rows, 0),
        POOL,
    )
    own_clip = lax.dynamic_slice_in_dim(clip_ids, position * coarse_rows, coarse_rows, 0)
    query_clip = jnp.repeat(own_clip, POOL)
    fine_out, pooled = fine_attention(
        planes, prev0, prev1a, prev1b, query_clip.reshape(tok_count, 1),
        key_clip.reshape(1, (FREACH + 1) * tok_count), FHEADS,
    )
    quarter_width = w_coarse.shape[2] // QUARTERS
    wplanes = jnp.transpose(w_coarse, (1, 0, 2))
    projected = jnp.einsum(
        "rd,mdc->mrc", pooled, wplanes, preferred_element_type=jnp.float32
    ).astype(jnp.bfloat16)
    pieces = []
    for shift in range(QUARTERS):
        piece = lax.dynamic_slice_in_dim(
            projected, ((quarter + shift) % QUARTERS) * quarter_width, quarter_width, 2
        )
        pieces.append(piece if shift == 0 else within_group(piece, "seq", shift))
    grouped = group_order(pieces, quarter)
    grouped = jnp.transpose(grouped, (1, 0, 2, 3)).reshape(3, group_rows, quarter_width)
    coarse_queries = grouped[0]
    coarse_pairs = grouped[1:]
    one_back = passed_along(coarse_pairs, "seq", QUARTERS)
    two_back = passed_along(coarse_pairs, "seq", 2 * QUARTERS)
    three_back = passed_along(two_back, "seq", QUARTERS)
    earlier = [three_back, two_back, one_back]
    clip_back = jnp.concatenate([jnp.full((CREACH * group_rows,), -1, jnp.int32), clip_ids])
    coarse_key_clip = lax.dynamic_slice_in_dim(
        clip_back, cycle_place * group_rows, (CREACH + 1) * group_rows, 0
    )
    coarse_query_clip = lax.dynamic_slice_in_dim(clip_ids, cycle_place * group_rows, group_rows, 0)
    coarse_att = coarse_attention(
        coarse_queries, earlier + [coarse_pairs], coarse_query_clip.reshape(group_rows, 1),
        coarse_key_clip.reshape(1, (CREACH + 1) * group_rows), CHEADS // QUARTERS,
    )
    shares = []
    for shift in range(QUARTERS):
        share = lax.dynamic_slice_in_dim(
            coarse_att, ((quarter + shift) % QUARTERS) * coarse_rows, coarse_rows, 0
        )
        shares.append(share if shift == 0 else within_group(share, "seq", shift))
    att_rows = jnp.transpose(group_order(shares, quarter), (1, 0, 2)).reshape(
        coarse_rows, QUARTERS * quarter_width
    )
    coarse_up = jnp.dot(att_rows, w_out, preferred_element_type=jnp.float32).astype(jnp.bfloat16)
    carried = passed_along(coarse_up[-1:], "seq", 1)
    previous = jnp.concatenate([jnp.zeros_like(carried), coarse_up[:-1]], axis=0)
    clip_before = jnp.concatenate([jnp.full((1,), -1, jnp.int32), clip_ids])
    prev_clip = lax.dynamic_slice_in_dim(clip_before, position * coarse_rows, coarse_rows, 0)
    joined = prev_clip == own_clip
    lifted = jnp.where(joined[:, None], previous, jnp.zeros_like(previous))
    mixed = mix(fine_out, lifted)
    head_lift = jnp.where(joined[:1, None], carried, jnp.zeros_like(carried)).astype(jnp.float32)
    head_rows = (fine_out[:POOL].astype(jnp.float32) + head_lift).astype(mixed.dtype)
    return lax.dynamic_update_slice(mixed, head_rows, (0, 0))


def solution(mesh):
    return jax.shard_map(
        body,
        mesh=mesh,
        in_specs=(P(("groups", "seq"), None, None), P("groups"), P(), P()),
        out_specs=P(("groups", "seq"), None),
        check_vma=False,
    )
```

```python
import functools
import math

import jax
import jax.numpy as jnp
from jax import lax
from jax.experimental import pallas as pl
from jax.experimental.pallas import tpu as pltpu
from jax.sharding import PartitionSpec as P

FHEADS = 16
CHEADS = 8
POOL = 4
QUARTERS = 4
FREACH = 2
CREACH = 3
FINE_TILE = 256
HALVES = 2


def passed_along(value, axis, steps):
    count = lax.axis_size(axis)
    first, last = (max(0, -steps), min(count, count - steps))
    return lax.ppermute(value, axis, [(source, source + steps) for source in range(first, last)])


def within_group(value, axis, shift):
    count = lax.axis_size(axis)
    pairs = []
    for source in range(count):
        base = source - source % QUARTERS
        pairs.append((source, base + (source % QUARTERS + shift) % QUARTERS))
    return lax.ppermute(value, axis, pairs)


def fine_kernel(qclip_ref, kclip0_ref, kclip1_ref, kclip2_ref, q_ref,
                k0_ref, v0_ref, k1_ref, v1_ref, k1b_ref, v1b_ref, k2_ref, v2_ref,
                out_ref, pool_ref, bias_ref, *, scale):
    tile = q_ref.shape[0]
    width = q_ref.shape[1]
    half = width // 2
    seg = k0_ref.shape[0]
    tile_index = pl.program_id(0)

    @pl.when(pl.program_id(1) == 0)
    def _():
        qclip = qclip_ref[...]
        qpos = tile_index * tile + lax.broadcasted_iota(jnp.int32, (tile, seg), 0)
        kpos = lax.broadcasted_iota(jnp.int32, (tile, seg), 1)
        allowed = (
            kclip0_ref[...] == qclip,
            kclip1_ref[...] == qclip,
            (kclip2_ref[...] == qclip) & (kpos <= qpos),
        )
        for j in range(3):
            bias_ref[:, j * seg:(j + 1) * seg] = jnp.where(allowed[j], 0.0, -1e30)

    q = q_ref[...] * jnp.asarray(scale, q_ref.dtype)
    lane = lax.broadcasted_iota(jnp.int32, (1, width), 1)
    low = lane < half
    zero = jnp.zeros_like(q)
    head_q = (jnp.where(low, q, zero), jnp.where(low, zero, q))

    def run(step):
        own = (step + 1) * tile
        keys = (k0_ref[...], k1_ref[...] + k1b_ref[...], k2_ref[0:own, :])
        values = (v0_ref[...], v1_ref[...] + v1b_ref[...], v2_ref[0:own, :])
        spans = ((0, seg), (seg, seg), (2 * seg, own))
        results = []
        for h in range(2):
            scores = []
            for j in range(3):
                s = lax.dot_general(head_q[h], keys[j], (((1,), (1,)), ((), ())),
                                    preferred_element_type=jnp.float32)
                start, length = spans[j]
                scores.append(s + bias_ref[:, start:start + length])
            top = jnp.max(scores[0], axis=1, keepdims=True)
            for j in range(1, 3):
                top = jnp.maximum(top, jnp.max(scores[j], axis=1, keepdims=True))
            total = None
            summed = None
            for j in range(3):
                w = jnp.exp(scores[j] - top)
                part = jnp.sum(w, axis=1, keepdims=True)
                pv = jnp.dot(w.astype(jnp.bfloat16), values[j], preferred_element_type=jnp.float32)
                total = part if total is None else total + part
                summed = pv if summed is None else summed + pv
            results.append(summed / total)
        out = jnp.where(low, results[0], results[1]).astype(out_ref.dtype)
        out_ref[...] = out
        rows = tile // POOL
        pool_row = lax.broadcasted_iota(jnp.int32, (rows, tile), 0)
        pool_col = lax.broadcasted_iota(jnp.int32, (rows, tile), 1)
        pool_mat = jnp.where(pool_col // POOL == pool_row, 1.0 / POOL, 0.0).astype(jnp.bfloat16)
        pool_ref[...] = jnp.dot(pool_mat, out, preferred_element_type=jnp.float32).astype(
            pool_ref.dtype)

    for step in range(seg // tile):
        pl.when(tile_index == step)(functools.partial(run, step))


def fine_attention(planes, prev0, prev1a, prev1b, qclip, kclip, heads, first_pair):
    _, tok, width = planes.shape
    head_dim = width // heads
    pair = 2 * head_dim
    pairs = prev0.shape[2] // pair
    tile = min(FINE_TILE, tok)
    nq = tok // tile
    kernel = functools.partial(fine_kernel, scale=1.0 / math.sqrt(head_dim))

    def plane_spec(plane):
        return pl.BlockSpec((None, tok, pair), lambda i, h: (plane, 0, h))

    def own_spec(plane):
        return pl.BlockSpec((None, tok, pair), lambda i, h: (plane, 0, first_pair + h))

    return pl.pallas_call(
        kernel,
        grid=(nq, pairs),
        in_specs=[
            pl.BlockSpec((tile, 1), lambda i, h: (i, 0)),
            pl.BlockSpec((1, tok), lambda i, h: (0, 0)),
            pl.BlockSpec((1, tok), lambda i, h: (0, 1)),
            pl.BlockSpec((1, tok), lambda i, h: (0, 2)),
            pl.BlockSpec((None, tile, pair), lambda i, h: (0, i, first_pair + h)),
            plane_spec(0), plane_spec(1),
            plane_spec(0), plane_spec(1),
            plane_spec(0), plane_spec(1),
            own_spec(1), own_spec(2),
        ],
        out_specs=[
            pl.BlockSpec((tile, pair), lambda i, h: (i, h)),
            pl.BlockSpec((tile // POOL, pair), lambda i, h: (i, h)),
        ],
        out_shape=[
            jax.ShapeDtypeStruct((tok, pairs * pair), jnp.bfloat16),
            jax.ShapeDtypeStruct((tok // POOL, pairs * pair), jnp.bfloat16),
        ],
        scratch_shapes=[pltpu.VMEM((tile, 3 * tok), jnp.float32)],
    )(qclip, kclip, kclip, kclip, planes, prev0, prev0, prev1a, prev1a, prev1b, prev1b,
      planes, planes)


def mix_kernel(fine_ref, lift_ref, out_ref):
    tile = fine_ref.shape[0]
    rows = lift_ref.shape[0]
    spread_row = lax.broadcasted_iota(jnp.int32, (tile, rows), 0)
    spread_col = lax.broadcasted_iota(jnp.int32, (tile, rows), 1)
    spread = jnp.where(spread_row // POOL == spread_col, 1.0, 0.0).astype(jnp.bfloat16)
    lifted = jnp.dot(spread, lift_ref[...], preferred_element_type=jnp.float32)
    out_ref[...] = (fine_ref[...].astype(jnp.float32) + lifted).astype(out_ref.dtype)


def mix(fine_out, lifted):
    tok, width = fine_out.shape
    tile = min(FINE_TILE, tok)
    return pl.pallas_call(
        mix_kernel,
        grid=(tok // tile,),
        in_specs=[
            pl.BlockSpec((tile, width), lambda i: (i, 0)),
            pl.BlockSpec((tile // POOL, width), lambda i: (i, 0)),
        ],
        out_specs=pl.BlockSpec((tile, width), lambda i: (i, 0)),
        out_shape=jax.ShapeDtypeStruct((tok, width), fine_out.dtype),
    )(fine_out, lifted)


def pair_swap(value, axis, from_odd):
    count = lax.axis_size(axis)
    start = 1 if from_odd else 0
    step = -1 if from_odd else 1
    return lax.ppermute(value, axis, [(source, source + step) for source in range(start, count, 2)])


def coarse_kernel(qclip_ref, kc0_ref, kc1_ref, kc2_ref, kc3_ref, q_ref,
                  k0_ref, v0_ref, k1_ref, v1_ref, k2_ref, v2_ref, k3_ref, v3_ref,
                  out_ref, *, scale):
    tile = q_ref.shape[0]
    seg = k0_ref.shape[0]
    q = q_ref[...]
    qclip = qclip_ref[...]
    keys = (k0_ref, k1_ref, k2_ref, k3_ref)
    values = (v0_ref, v1_ref, v2_ref, v3_ref)
    clips = (kc0_ref, kc1_ref, kc2_ref, kc3_ref)
    qpos = pl.program_id(1) * tile + lax.broadcasted_iota(jnp.int32, (tile, seg), 0)
    kpos = lax.broadcasted_iota(jnp.int32, (tile, seg), 1)
    last = len(keys) - 1
    scores = []
    masks = []
    for j in range(len(keys)):
        allowed = clips[j][...] == qclip
        if j == last:
            allowed = allowed & (kpos <= qpos)
        s = lax.dot_general(q, keys[j][...], (((1,), (1,)), ((), ())),
                            preferred_element_type=jnp.float32) * scale
        scores.append(jnp.where(allowed, s, -1e30))
    top = jnp.max(scores[0], axis=1, keepdims=True)
    for j in range(1, len(keys)):
        top = jnp.maximum(top, jnp.max(scores[j], axis=1, keepdims=True))
    total = None
    summed = None
    for j in range(len(keys)):
        w = jnp.exp(scores[j] - top)
        part = jnp.sum(w, axis=1, keepdims=True)
        pv = jnp.dot(w.astype(jnp.bfloat16), values[j][...], preferred_element_type=jnp.float32)
        total = part if total is None else total + part
        summed = pv if summed is None else summed + pv
    out_ref[...] = (summed / total).astype(out_ref.dtype)


def coarse_attention(queries, windows, qclip, kclip, heads):
    rows, width = queries.shape
    head_dim = width // heads
    tile = min(FINE_TILE, rows)
    seg = windows[0].shape[1]
    kernel = functools.partial(coarse_kernel, scale=1.0 / math.sqrt(head_dim))
    clip_specs = [pl.BlockSpec((1, seg), functools.partial(lambda j, h, i: (0, j), j))
                  for j in range(len(windows))]
    kv_specs = []
    kv_args = []
    for window in windows:
        kv_specs.append(pl.BlockSpec((None, seg, head_dim), lambda h, i: (0, 0, h)))
        kv_specs.append(pl.BlockSpec((None, seg, head_dim), lambda h, i: (1, 0, h)))
        kv_args += [window, window]
    return pl.pallas_call(
        kernel,
        grid=(heads, rows // tile),
        in_specs=[pl.BlockSpec((tile, 1), lambda h, i: (i, 0))] + clip_specs
        + [pl.BlockSpec((tile, head_dim), lambda h, i: (i, h))] + kv_specs,
        out_specs=pl.BlockSpec((tile, head_dim), lambda h, i: (i, h)),
        out_shape=jax.ShapeDtypeStruct((rows, width), jnp.bfloat16),
    )(qclip, *([kclip] * len(windows)), queries, *kv_args)


def group_order(parts, quarter):
    ordered = jnp.stack([parts[0]] + parts[:0:-1], axis=0)
    return jnp.roll(ordered, quarter, axis=0)


def attend(queries, key_rows, value_rows, allowed, heads, head_groups):
    row_count = queries.shape[0]
    feat_width = queries.shape[1]
    head_dim = feat_width // heads
    per_group = heads // head_groups
    score_scale = 1.0 / math.sqrt(head_dim)

    def split_heads(source_rows):
        return source_rows.reshape(
            source_rows.shape[0], head_groups, per_group, head_dim
        ).transpose(1, 0, 2, 3)

    def one_group(operands):
        group_queries, group_keys, group_values = operands
        scores = (
            jnp.einsum(
                "rhd,khd->hrk", group_queries, group_keys, preferred_element_type=jnp.float32
            )
            * score_scale
        )
        masked = jnp.where(allowed[None], scores, -1e30)
        row_top = jnp.max(masked, axis=2, keepdims=True)
        weights = jnp.where(allowed[None], jnp.exp(masked - row_top), 0.0)
        row_total = jnp.sum(weights, axis=2)
        summed = jnp.einsum(
            "hrk,khd->rhd",
            weights.astype(jnp.bfloat16),
            group_values,
            preferred_element_type=jnp.float32,
        )
        return summed / jnp.transpose(row_total)[:, :, None]

    results = lax.map(
        one_group, (split_heads(queries), split_heads(key_rows), split_heads(value_rows))
    )
    return results.transpose(1, 0, 2, 3).reshape(row_count, feat_width).astype(jnp.bfloat16)


def body(fine_qkv, clip_ids, w_coarse, w_out):
    tok_count = fine_qkv.shape[0]
    feat_width = fine_qkv.shape[2]
    coarse_rows = tok_count // POOL
    group_rows = QUARTERS * coarse_rows
    position = lax.axis_index("seq")
    quarter = position % QUARTERS
    cycle_place = position // QUARTERS
    planes = jnp.transpose(fine_qkv, (1, 0, 2))
    clip_front = jnp.concatenate([jnp.full((FREACH * coarse_rows,), -1, jnp.int32), clip_ids])
    key_clip = jnp.repeat(
        lax.dynamic_slice_in_dim(clip_front, position * coarse_rows, (FREACH + 1) * coarse_rows, 0),
        POOL,
    )
    own_clip = lax.dynamic_slice_in_dim(clip_ids, position * coarse_rows, coarse_rows, 0)
    query_clip = jnp.repeat(own_clip, POOL)
    head_pair_width = 2 * feat_width // FHEADS
    part_width = feat_width // HALVES
    outs = []
    pools = []
    gate = None
    for part in range(HALVES):
        own_pairs = planes[1:, :, part * part_width:(part + 1) * part_width]
        if gate is not None:
            own_pairs, _ = lax.optimization_barrier((own_pairs, gate))
        prev0 = passed_along(own_pairs, "seq", 2)
        gate = prev0
        if outs:
            prev0, _ = lax.optimization_barrier((prev0, outs[-1]))
        prev1a = pair_swap(own_pairs, "seq", False)
        prev1b = pair_swap(prev0, "seq", True)
        part_out, part_pool = fine_attention(
            planes, prev0, prev1a, prev1b, query_clip.reshape(tok_count, 1),
            key_clip.reshape(1, (FREACH + 1) * tok_count), FHEADS,
            part * part_width // head_pair_width,
        )
        outs.append(part_out)
        pools.append(part_pool)
    fine_out = jnp.concatenate(outs, axis=1)
    pooled = jnp.concatenate(pools, axis=1)
    quarter_width = w_coarse.shape[2] // QUARTERS
    wplanes = jnp.transpose(w_coarse, (1, 0, 2))
    projected = jnp.einsum(
        "rd,mdc->mrc", pooled, wplanes, preferred_element_type=jnp.float32
    ).astype(jnp.bfloat16)
    pieces = []
    for shift in range(QUARTERS):
        piece = lax.dynamic_slice_in_dim(
            projected, ((quarter + shift) % QUARTERS) * quarter_width, quarter_width, 2
        )
        pieces.append(piece if shift == 0 else within_group(piece, "seq", shift))
    grouped = group_order(pieces, quarter)
    grouped = jnp.transpose(grouped, (1, 0, 2, 3)).reshape(3, group_rows, quarter_width)
    coarse_queries = grouped[0]
    coarse_pairs = grouped[1:]
    one_back = passed_along(coarse_pairs, "seq", QUARTERS)
    two_back = passed_along(coarse_pairs, "seq", 2 * QUARTERS)
    three_back = passed_along(two_back, "seq", QUARTERS)
    earlier = [three_back, two_back, one_back]
    clip_back = jnp.concatenate([jnp.full((CREACH * group_rows,), -1, jnp.int32), clip_ids])
    coarse_key_clip = lax.dynamic_slice_in_dim(
        clip_back, cycle_place * group_rows, (CREACH + 1) * group_rows, 0
    )
    coarse_query_clip = lax.dynamic_slice_in_dim(clip_ids, cycle_place * group_rows, group_rows, 0)
    coarse_att = coarse_attention(
        coarse_queries, earlier + [coarse_pairs], coarse_query_clip.reshape(group_rows, 1),
        coarse_key_clip.reshape(1, (CREACH + 1) * group_rows), CHEADS // QUARTERS,
    )
    shares = []
    for shift in range(QUARTERS):
        share = lax.dynamic_slice_in_dim(
            coarse_att, ((quarter + shift) % QUARTERS) * coarse_rows, coarse_rows, 0
        )
        shares.append(share if shift == 0 else within_group(share, "seq", shift))
    att_rows = jnp.transpose(group_order(shares, quarter), (1, 0, 2)).reshape(
        coarse_rows, QUARTERS * quarter_width
    )
    coarse_up = jnp.dot(att_rows, w_out, preferred_element_type=jnp.float32).astype(jnp.bfloat16)
    carried = passed_along(coarse_up[-1:], "seq", 1)
    previous = jnp.concatenate([jnp.zeros_like(carried), coarse_up[:-1]], axis=0)
    clip_before = jnp.concatenate([jnp.full((1,), -1, jnp.int32), clip_ids])
    prev_clip = lax.dynamic_slice_in_dim(clip_before, position * coarse_rows, coarse_rows, 0)
    joined = prev_clip == own_clip
    lifted = jnp.where(joined[:, None], previous, jnp.zeros_like(previous))
    mixed = mix(fine_out, lifted)
    head_lift = jnp.where(joined[:1, None], carried, jnp.zeros_like(carried)).astype(jnp.float32)
    head_rows = (fine_out[:POOL].astype(jnp.float32) + head_lift).astype(mixed.dtype)
    return lax.dynamic_update_slice(mixed, head_rows, (0, 0))


def solution(mesh):
    return jax.shard_map(
        body,
        mesh=mesh,
        in_specs=(P(("groups", "seq"), None, None), P("groups"), P(), P()),
        out_specs=P(("groups", "seq"), None),
        check_vma=False,
    )
```

```python
import functools
import math

import jax
import jax.numpy as jnp
from jax import lax
from jax.experimental import pallas as pl
from jax.experimental.pallas import tpu as pltpu
from jax.sharding import PartitionSpec as P

FHEADS = 16
CHEADS = 8
POOL = 4
QUARTERS = 4
FREACH = 2
CREACH = 3
FINE_TILE = 256
HALVES = 4


def passed_along(value, axis, steps):
    count = lax.axis_size(axis)
    first, last = (max(0, -steps), min(count, count - steps))
    return lax.ppermute(value, axis, [(source, source + steps) for source in range(first, last)])


def within_group(value, axis, shift):
    count = lax.axis_size(axis)
    pairs = []
    for source in range(count):
        base = source - source % QUARTERS
        pairs.append((source, base + (source % QUARTERS + shift) % QUARTERS))
    return lax.ppermute(value, axis, pairs)


def fine_kernel(qclip_ref, kclip0_ref, kclip1_ref, kclip2_ref, q_ref,
                k0_ref, v0_ref, k1_ref, v1_ref, k1b_ref, v1b_ref, k2_ref, v2_ref,
                out_ref, pool_ref, bias_ref, *, scale):
    tile = q_ref.shape[0]
    width = q_ref.shape[1]
    half = width // 2
    seg = k0_ref.shape[0]
    tile_index = pl.program_id(0)

    @pl.when(pl.program_id(1) == 0)
    def _():
        qclip = qclip_ref[...]
        qpos = tile_index * tile + lax.broadcasted_iota(jnp.int32, (tile, seg), 0)
        kpos = lax.broadcasted_iota(jnp.int32, (tile, seg), 1)
        allowed = (
            kclip0_ref[...] == qclip,
            kclip1_ref[...] == qclip,
            (kclip2_ref[...] == qclip) & (kpos <= qpos),
        )
        for j in range(3):
            bias_ref[:, j * seg:(j + 1) * seg] = jnp.where(allowed[j], 0.0, -1e30)

    q = q_ref[...] * jnp.asarray(scale, q_ref.dtype)
    lane = lax.broadcasted_iota(jnp.int32, (1, width), 1)
    low = lane < half
    zero = jnp.zeros_like(q)
    head_q = (jnp.where(low, q, zero), jnp.where(low, zero, q))

    def run(step):
        own = (step + 1) * tile
        keys = (k0_ref[...], k1_ref[...] + k1b_ref[...], k2_ref[0:own, :])
        values = (v0_ref[...], v1_ref[...] + v1b_ref[...], v2_ref[0:own, :])
        spans = ((0, seg), (seg, seg), (2 * seg, own))
        results = []
        for h in range(2):
            scores = []
            for j in range(3):
                s = lax.dot_general(head_q[h], keys[j], (((1,), (1,)), ((), ())),
                                    preferred_element_type=jnp.float32)
                start, length = spans[j]
                scores.append(s + bias_ref[:, start:start + length])
            top = jnp.max(scores[0], axis=1, keepdims=True)
            for j in range(1, 3):
                top = jnp.maximum(top, jnp.max(scores[j], axis=1, keepdims=True))
            total = None
            summed = None
            for j in range(3):
                w = jnp.exp(scores[j] - top)
                part = jnp.sum(w, axis=1, keepdims=True)
                pv = jnp.dot(w.astype(jnp.bfloat16), values[j], preferred_element_type=jnp.float32)
                total = part if total is None else total + part
                summed = pv if summed is None else summed + pv
            results.append(summed / total)
        out = jnp.where(low, results[0], results[1]).astype(out_ref.dtype)
        out_ref[...] = out
        rows = tile // POOL
        pool_row = lax.broadcasted_iota(jnp.int32, (rows, tile), 0)
        pool_col = lax.broadcasted_iota(jnp.int32, (rows, tile), 1)
        pool_mat = jnp.where(pool_col // POOL == pool_row, 1.0 / POOL, 0.0).astype(jnp.bfloat16)
        pool_ref[...] = jnp.dot(pool_mat, out, preferred_element_type=jnp.float32).astype(
            pool_ref.dtype)

    for step in range(seg // tile):
        pl.when(tile_index == step)(functools.partial(run, step))


def fine_attention(planes, prev0, prev1a, prev1b, qclip, kclip, heads, first_pair):
    _, tok, width = planes.shape
    head_dim = width // heads
    pair = 2 * head_dim
    pairs = prev0.shape[2] // pair
    tile = min(FINE_TILE, tok)
    nq = tok // tile
    kernel = functools.partial(fine_kernel, scale=1.0 / math.sqrt(head_dim))

    def plane_spec(plane):
        return pl.BlockSpec((None, tok, pair), lambda i, h: (plane, 0, h))

    def own_spec(plane):
        return pl.BlockSpec((None, tok, pair), lambda i, h: (plane, 0, first_pair + h))

    return pl.pallas_call(
        kernel,
        grid=(nq, pairs),
        in_specs=[
            pl.BlockSpec((tile, 1), lambda i, h: (i, 0)),
            pl.BlockSpec((1, tok), lambda i, h: (0, 0)),
            pl.BlockSpec((1, tok), lambda i, h: (0, 1)),
            pl.BlockSpec((1, tok), lambda i, h: (0, 2)),
            pl.BlockSpec((None, tile, pair), lambda i, h: (0, i, first_pair + h)),
            plane_spec(0), plane_spec(1),
            plane_spec(0), plane_spec(1),
            plane_spec(0), plane_spec(1),
            own_spec(1), own_spec(2),
        ],
        out_specs=[
            pl.BlockSpec((tile, pair), lambda i, h: (i, h)),
            pl.BlockSpec((tile // POOL, pair), lambda i, h: (i, h)),
        ],
        out_shape=[
            jax.ShapeDtypeStruct((tok, pairs * pair), jnp.bfloat16),
            jax.ShapeDtypeStruct((tok // POOL, pairs * pair), jnp.bfloat16),
        ],
        scratch_shapes=[pltpu.VMEM((tile, 3 * tok), jnp.float32)],
    )(qclip, kclip, kclip, kclip, planes, prev0, prev0, prev1a, prev1a, prev1b, prev1b,
      planes, planes)


def mix_kernel(fine_ref, lift_ref, out_ref):
    tile = fine_ref.shape[0]
    rows = lift_ref.shape[0]
    spread_row = lax.broadcasted_iota(jnp.int32, (tile, rows), 0)
    spread_col = lax.broadcasted_iota(jnp.int32, (tile, rows), 1)
    spread = jnp.where(spread_row // POOL == spread_col, 1.0, 0.0).astype(jnp.bfloat16)
    lifted = jnp.dot(spread, lift_ref[...], preferred_element_type=jnp.float32)
    out_ref[...] = (fine_ref[...].astype(jnp.float32) + lifted).astype(out_ref.dtype)


def mix(fine_out, lifted):
    tok, width = fine_out.shape
    tile = min(FINE_TILE, tok)
    return pl.pallas_call(
        mix_kernel,
        grid=(tok // tile,),
        in_specs=[
            pl.BlockSpec((tile, width), lambda i: (i, 0)),
            pl.BlockSpec((tile // POOL, width), lambda i: (i, 0)),
        ],
        out_specs=pl.BlockSpec((tile, width), lambda i: (i, 0)),
        out_shape=jax.ShapeDtypeStruct((tok, width), fine_out.dtype),
    )(fine_out, lifted)


def pair_swap(value, axis, from_odd):
    count = lax.axis_size(axis)
    start = 1 if from_odd else 0
    step = -1 if from_odd else 1
    return lax.ppermute(value, axis, [(source, source + step) for source in range(start, count, 2)])


def coarse_kernel(qclip_ref, kc0_ref, kc1_ref, kc2_ref, kc3_ref, q_ref,
                  k0_ref, v0_ref, k1_ref, v1_ref, k2_ref, v2_ref, k3_ref, v3_ref,
                  out_ref, *, scale):
    tile = q_ref.shape[0]
    seg = k0_ref.shape[0]
    q = q_ref[...]
    qclip = qclip_ref[...]
    keys = (k0_ref, k1_ref, k2_ref, k3_ref)
    values = (v0_ref, v1_ref, v2_ref, v3_ref)
    clips = (kc0_ref, kc1_ref, kc2_ref, kc3_ref)
    qpos = pl.program_id(1) * tile + lax.broadcasted_iota(jnp.int32, (tile, seg), 0)
    kpos = lax.broadcasted_iota(jnp.int32, (tile, seg), 1)
    last = len(keys) - 1
    scores = []
    masks = []
    for j in range(len(keys)):
        allowed = clips[j][...] == qclip
        if j == last:
            allowed = allowed & (kpos <= qpos)
        s = lax.dot_general(q, keys[j][...], (((1,), (1,)), ((), ())),
                            preferred_element_type=jnp.float32) * scale
        scores.append(jnp.where(allowed, s, -1e30))
    top = jnp.max(scores[0], axis=1, keepdims=True)
    for j in range(1, len(keys)):
        top = jnp.maximum(top, jnp.max(scores[j], axis=1, keepdims=True))
    total = None
    summed = None
    for j in range(len(keys)):
        w = jnp.exp(scores[j] - top)
        part = jnp.sum(w, axis=1, keepdims=True)
        pv = jnp.dot(w.astype(jnp.bfloat16), values[j][...], preferred_element_type=jnp.float32)
        total = part if total is None else total + part
        summed = pv if summed is None else summed + pv
    out_ref[...] = (summed / total).astype(out_ref.dtype)


def coarse_attention(queries, windows, qclip, kclip, heads):
    rows, width = queries.shape
    head_dim = width // heads
    tile = min(FINE_TILE, rows)
    seg = windows[0].shape[1]
    kernel = functools.partial(coarse_kernel, scale=1.0 / math.sqrt(head_dim))
    clip_specs = [pl.BlockSpec((1, seg), functools.partial(lambda j, h, i: (0, j), j))
                  for j in range(len(windows))]
    kv_specs = []
    kv_args = []
    for window in windows:
        kv_specs.append(pl.BlockSpec((None, seg, head_dim), lambda h, i: (0, 0, h)))
        kv_specs.append(pl.BlockSpec((None, seg, head_dim), lambda h, i: (1, 0, h)))
        kv_args += [window, window]
    return pl.pallas_call(
        kernel,
        grid=(heads, rows // tile),
        in_specs=[pl.BlockSpec((tile, 1), lambda h, i: (i, 0))] + clip_specs
        + [pl.BlockSpec((tile, head_dim), lambda h, i: (i, h))] + kv_specs,
        out_specs=pl.BlockSpec((tile, head_dim), lambda h, i: (i, h)),
        out_shape=jax.ShapeDtypeStruct((rows, width), jnp.bfloat16),
    )(qclip, *([kclip] * len(windows)), queries, *kv_args)


def group_order(parts, quarter):
    ordered = jnp.stack([parts[0]] + parts[:0:-1], axis=0)
    return jnp.roll(ordered, quarter, axis=0)


def attend(queries, key_rows, value_rows, allowed, heads, head_groups):
    row_count = queries.shape[0]
    feat_width = queries.shape[1]
    head_dim = feat_width // heads
    per_group = heads // head_groups
    score_scale = 1.0 / math.sqrt(head_dim)

    def split_heads(source_rows):
        return source_rows.reshape(
            source_rows.shape[0], head_groups, per_group, head_dim
        ).transpose(1, 0, 2, 3)

    def one_group(operands):
        group_queries, group_keys, group_values = operands
        scores = (
            jnp.einsum(
                "rhd,khd->hrk", group_queries, group_keys, preferred_element_type=jnp.float32
            )
            * score_scale
        )
        masked = jnp.where(allowed[None], scores, -1e30)
        row_top = jnp.max(masked, axis=2, keepdims=True)
        weights = jnp.where(allowed[None], jnp.exp(masked - row_top), 0.0)
        row_total = jnp.sum(weights, axis=2)
        summed = jnp.einsum(
            "hrk,khd->rhd",
            weights.astype(jnp.bfloat16),
            group_values,
            preferred_element_type=jnp.float32,
        )
        return summed / jnp.transpose(row_total)[:, :, None]

    results = lax.map(
        one_group, (split_heads(queries), split_heads(key_rows), split_heads(value_rows))
    )
    return results.transpose(1, 0, 2, 3).reshape(row_count, feat_width).astype(jnp.bfloat16)


def body(fine_qkv, clip_ids, w_coarse, w_out):
    tok_count = fine_qkv.shape[0]
    feat_width = fine_qkv.shape[2]
    coarse_rows = tok_count // POOL
    group_rows = QUARTERS * coarse_rows
    position = lax.axis_index("seq")
    quarter = position % QUARTERS
    cycle_place = position // QUARTERS
    planes = jnp.transpose(fine_qkv, (1, 0, 2))
    clip_front = jnp.concatenate([jnp.full((FREACH * coarse_rows,), -1, jnp.int32), clip_ids])
    key_clip = jnp.repeat(
        lax.dynamic_slice_in_dim(clip_front, position * coarse_rows, (FREACH + 1) * coarse_rows, 0),
        POOL,
    )
    own_clip = lax.dynamic_slice_in_dim(clip_ids, position * coarse_rows, coarse_rows, 0)
    query_clip = jnp.repeat(own_clip, POOL)
    head_pair_width = 2 * feat_width // FHEADS
    part_width = feat_width // HALVES
    outs = []
    pools = []
    gate = None
    for part in range(HALVES):
        own_pairs = planes[1:, :, part * part_width:(part + 1) * part_width]
        if gate is not None:
            own_pairs, _ = lax.optimization_barrier((own_pairs, gate))
        prev0 = passed_along(own_pairs, "seq", 2)
        gate = prev0
        if outs:
            prev0, _ = lax.optimization_barrier((prev0, outs[-1]))
        prev1a = pair_swap(own_pairs, "seq", False)
        prev1b = pair_swap(prev0, "seq", True)
        part_out, part_pool = fine_attention(
            planes, prev0, prev1a, prev1b, query_clip.reshape(tok_count, 1),
            key_clip.reshape(1, (FREACH + 1) * tok_count), FHEADS,
            part * part_width // head_pair_width,
        )
        outs.append(part_out)
        pools.append(part_pool)
    fine_out = jnp.concatenate(outs, axis=1)
    pooled = jnp.concatenate(pools, axis=1)
    quarter_width = w_coarse.shape[2] // QUARTERS
    wplanes = jnp.transpose(w_coarse, (1, 0, 2))
    projected = jnp.einsum(
        "rd,mdc->mrc", pooled, wplanes, preferred_element_type=jnp.float32
    ).astype(jnp.bfloat16)
    pieces = []
    for shift in range(QUARTERS):
        piece = lax.dynamic_slice_in_dim(
            projected, ((quarter + shift) % QUARTERS) * quarter_width, quarter_width, 2
        )
        pieces.append(piece if shift == 0 else within_group(piece, "seq", shift))
    grouped = group_order(pieces, quarter)
    grouped = jnp.transpose(grouped, (1, 0, 2, 3)).reshape(3, group_rows, quarter_width)
    coarse_queries = grouped[0]
    coarse_pairs = grouped[1:]
    one_back = passed_along(coarse_pairs, "seq", QUARTERS)
    two_back = passed_along(coarse_pairs, "seq", 2 * QUARTERS)
    three_back = passed_along(two_back, "seq", QUARTERS)
    earlier = [three_back, two_back, one_back]
    clip_back = jnp.concatenate([jnp.full((CREACH * group_rows,), -1, jnp.int32), clip_ids])
    coarse_key_clip = lax.dynamic_slice_in_dim(
        clip_back, cycle_place * group_rows, (CREACH + 1) * group_rows, 0
    )
    coarse_query_clip = lax.dynamic_slice_in_dim(clip_ids, cycle_place * group_rows, group_rows, 0)
    coarse_att = coarse_attention(
        coarse_queries, earlier + [coarse_pairs], coarse_query_clip.reshape(group_rows, 1),
        coarse_key_clip.reshape(1, (CREACH + 1) * group_rows), CHEADS // QUARTERS,
    )
    shares = []
    for shift in range(QUARTERS):
        share = lax.dynamic_slice_in_dim(
            coarse_att, ((quarter + shift) % QUARTERS) * coarse_rows, coarse_rows, 0
        )
        shares.append(share if shift == 0 else within_group(share, "seq", shift))
    att_rows = jnp.transpose(group_order(shares, quarter), (1, 0, 2)).reshape(
        coarse_rows, QUARTERS * quarter_width
    )
    coarse_up = jnp.dot(att_rows, w_out, preferred_element_type=jnp.float32).astype(jnp.bfloat16)
    carried = passed_along(coarse_up[-1:], "seq", 1)
    previous = jnp.concatenate([jnp.zeros_like(carried), coarse_up[:-1]], axis=0)
    clip_before = jnp.concatenate([jnp.full((1,), -1, jnp.int32), clip_ids])
    prev_clip = lax.dynamic_slice_in_dim(clip_before, position * coarse_rows, coarse_rows, 0)
    joined = prev_clip == own_clip
    lifted = jnp.where(joined[:, None], previous, jnp.zeros_like(previous))
    mixed = mix(fine_out, lifted)
    head_lift = jnp.where(joined[:1, None], carried, jnp.zeros_like(carried)).astype(jnp.float32)
    head_rows = (fine_out[:POOL].astype(jnp.float32) + head_lift).astype(mixed.dtype)
    return lax.dynamic_update_slice(mixed, head_rows, (0, 0))


def solution(mesh):
    return jax.shard_map(
        body,
        mesh=mesh,
        in_specs=(P(("groups", "seq"), None, None), P("groups"), P(), P()),
        out_specs=P(("groups", "seq"), None),
        check_vma=False,
    )
```

```python
import functools
import math

import jax
import jax.numpy as jnp
from jax import lax
from jax.experimental import pallas as pl
from jax.experimental.pallas import tpu as pltpu
from jax.sharding import PartitionSpec as P

FHEADS = 16
CHEADS = 8
POOL = 4
QUARTERS = 4
FREACH = 2
CREACH = 3
FINE_TILE = 256
HALVES = 2


def passed_along(value, axis, steps):
    count = lax.axis_size(axis)
    first, last = (max(0, -steps), min(count, count - steps))
    return lax.ppermute(value, axis, [(source, source + steps) for source in range(first, last)])


def within_group(value, axis, shift):
    count = lax.axis_size(axis)
    pairs = []
    for source in range(count):
        base = source - source % QUARTERS
        pairs.append((source, base + (source % QUARTERS + shift) % QUARTERS))
    return lax.ppermute(value, axis, pairs)


def fine_kernel(qclip_ref, kclip0_ref, kclip1_ref, kclip2_ref, q_ref,
                k0_ref, v0_ref, k1_ref, v1_ref, k1b_ref, v1b_ref, k2_ref, v2_ref,
                out_ref, pool_ref, bias_ref, *, scale):
    tile = q_ref.shape[0]
    width = q_ref.shape[1]
    half = width // 2
    seg = k0_ref.shape[0]
    tile_index = pl.program_id(0)

    @pl.when(pl.program_id(1) == 0)
    def _():
        qclip = qclip_ref[...]
        qpos = tile_index * tile + lax.broadcasted_iota(jnp.int32, (tile, seg), 0)
        kpos = lax.broadcasted_iota(jnp.int32, (tile, seg), 1)
        allowed = (
            kclip0_ref[...] == qclip,
            kclip1_ref[...] == qclip,
            (kclip2_ref[...] == qclip) & (kpos <= qpos),
        )
        for j in range(3):
            bias_ref[:, j * seg:(j + 1) * seg] = jnp.where(allowed[j], 0.0, -1e30)

    q = q_ref[...] * jnp.asarray(scale, q_ref.dtype)
    lane = lax.broadcasted_iota(jnp.int32, (1, width), 1)
    low = lane < half
    zero = jnp.zeros_like(q)
    head_q = (jnp.where(low, q, zero), jnp.where(low, zero, q))

    def run(step):
        own = (step + 1) * tile
        keys = (k0_ref[...], k1_ref[...] + k1b_ref[...], k2_ref[0:own, :])
        values = (v0_ref[...], v1_ref[...] + v1b_ref[...], v2_ref[0:own, :])
        spans = ((0, seg), (seg, seg), (2 * seg, own))
        results = []
        for h in range(2):
            scores = []
            for j in range(3):
                s = lax.dot_general(head_q[h], keys[j], (((1,), (1,)), ((), ())),
                                    preferred_element_type=jnp.float32)
                start, length = spans[j]
                scores.append(s + bias_ref[:, start:start + length])
            top = jnp.max(scores[0], axis=1, keepdims=True)
            for j in range(1, 3):
                top = jnp.maximum(top, jnp.max(scores[j], axis=1, keepdims=True))
            total = None
            summed = None
            for j in range(3):
                w = jnp.exp(scores[j] - top)
                part = jnp.sum(w, axis=1, keepdims=True)
                pv = jnp.dot(w.astype(jnp.bfloat16), values[j], preferred_element_type=jnp.float32)
                total = part if total is None else total + part
                summed = pv if summed is None else summed + pv
            results.append(summed / total)
        out = jnp.where(low, results[0], results[1]).astype(out_ref.dtype)
        out_ref[...] = out
        rows = tile // POOL
        pool_row = lax.broadcasted_iota(jnp.int32, (rows, tile), 0)
        pool_col = lax.broadcasted_iota(jnp.int32, (rows, tile), 1)
        pool_mat = jnp.where(pool_col // POOL == pool_row, 1.0 / POOL, 0.0).astype(jnp.bfloat16)
        pool_ref[...] = jnp.dot(pool_mat, out, preferred_element_type=jnp.float32).astype(
            pool_ref.dtype)

    for step in range(seg // tile):
        pl.when(tile_index == step)(functools.partial(run, step))


def fine_attention(planes, prev0, prev1a, prev1b, qclip, kclip, heads, first_pair):
    _, tok, width = planes.shape
    head_dim = width // heads
    pair = 2 * head_dim
    pairs = prev0.shape[2] // pair
    tile = min(FINE_TILE, tok)
    nq = tok // tile
    kernel = functools.partial(fine_kernel, scale=1.0 / math.sqrt(head_dim))

    def plane_spec(plane):
        return pl.BlockSpec((None, tok, pair), lambda i, h: (plane, 0, h))

    def own_spec(plane):
        return pl.BlockSpec((None, tok, pair), lambda i, h: (plane, 0, first_pair + h))

    return pl.pallas_call(
        kernel,
        grid=(nq, pairs),
        in_specs=[
            pl.BlockSpec((tile, 1), lambda i, h: (i, 0)),
            pl.BlockSpec((1, tok), lambda i, h: (0, 0)),
            pl.BlockSpec((1, tok), lambda i, h: (0, 1)),
            pl.BlockSpec((1, tok), lambda i, h: (0, 2)),
            pl.BlockSpec((None, tile, pair), lambda i, h: (0, i, first_pair + h)),
            plane_spec(0), plane_spec(1),
            plane_spec(0), plane_spec(1),
            plane_spec(0), plane_spec(1),
            own_spec(1), own_spec(2),
        ],
        out_specs=[
            pl.BlockSpec((tile, pair), lambda i, h: (i, h)),
            pl.BlockSpec((tile // POOL, pair), lambda i, h: (i, h)),
        ],
        out_shape=[
            jax.ShapeDtypeStruct((tok, pairs * pair), jnp.bfloat16),
            jax.ShapeDtypeStruct((tok // POOL, pairs * pair), jnp.bfloat16),
        ],
        scratch_shapes=[pltpu.VMEM((tile, 3 * tok), jnp.float32)],
    )(qclip, kclip, kclip, kclip, planes, prev0, prev0, prev1a, prev1a, prev1b, prev1b,
      planes, planes)


def mix_kernel(fine_ref, lift_ref, out_ref):
    tile = fine_ref.shape[0]
    rows = lift_ref.shape[0]
    spread_row = lax.broadcasted_iota(jnp.int32, (tile, rows), 0)
    spread_col = lax.broadcasted_iota(jnp.int32, (tile, rows), 1)
    spread = jnp.where(spread_row // POOL == spread_col, 1.0, 0.0).astype(jnp.bfloat16)
    lifted = jnp.dot(spread, lift_ref[...], preferred_element_type=jnp.float32)
    out_ref[...] = (fine_ref[...].astype(jnp.float32) + lifted).astype(out_ref.dtype)


def mix(fine_out, lifted):
    tok, width = fine_out.shape
    tile = min(FINE_TILE, tok)
    return pl.pallas_call(
        mix_kernel,
        grid=(tok // tile,),
        in_specs=[
            pl.BlockSpec((tile, width), lambda i: (i, 0)),
            pl.BlockSpec((tile // POOL, width), lambda i: (i, 0)),
        ],
        out_specs=pl.BlockSpec((tile, width), lambda i: (i, 0)),
        out_shape=jax.ShapeDtypeStruct((tok, width), fine_out.dtype),
    )(fine_out, lifted)


def pair_swap(value, axis, from_odd):
    count = lax.axis_size(axis)
    start = 1 if from_odd else 0
    step = -1 if from_odd else 1
    return lax.ppermute(value, axis, [(source, source + step) for source in range(start, count, 2)])


def coarse_kernel(qclip_ref, kc0_ref, kc1_ref, kc2_ref, kc3_ref, q_ref,
                  k0_ref, v0_ref, k1_ref, v1_ref, k2_ref, v2_ref, k3_ref, v3_ref,
                  out_ref, *, scale):
    tile = q_ref.shape[0]
    seg = k0_ref.shape[0]
    q = q_ref[...]
    qclip = qclip_ref[...]
    keys = (k0_ref, k1_ref, k2_ref, k3_ref)
    values = (v0_ref, v1_ref, v2_ref, v3_ref)
    clips = (kc0_ref, kc1_ref, kc2_ref, kc3_ref)
    qpos = pl.program_id(1) * tile + lax.broadcasted_iota(jnp.int32, (tile, seg), 0)
    kpos = lax.broadcasted_iota(jnp.int32, (tile, seg), 1)
    last = len(keys) - 1
    scores = []
    masks = []
    for j in range(len(keys)):
        allowed = clips[j][...] == qclip
        if j == last:
            allowed = allowed & (kpos <= qpos)
        s = lax.dot_general(q, keys[j][...], (((1,), (1,)), ((), ())),
                            preferred_element_type=jnp.float32) * scale
        scores.append(jnp.where(allowed, s, -1e30))
    top = jnp.max(scores[0], axis=1, keepdims=True)
    for j in range(1, len(keys)):
        top = jnp.maximum(top, jnp.max(scores[j], axis=1, keepdims=True))
    total = None
    summed = None
    for j in range(len(keys)):
        w = jnp.exp(scores[j] - top)
        part = jnp.sum(w, axis=1, keepdims=True)
        pv = jnp.dot(w.astype(jnp.bfloat16), values[j][...], preferred_element_type=jnp.float32)
        total = part if total is None else total + part
        summed = pv if summed is None else summed + pv
    out_ref[...] = (summed / total).astype(out_ref.dtype)


def coarse_attention(queries, windows, qclip, kclip, heads):
    rows, width = queries.shape
    head_dim = width // heads
    tile = min(FINE_TILE, rows)
    seg = windows[0].shape[1]
    kernel = functools.partial(coarse_kernel, scale=1.0 / math.sqrt(head_dim))
    clip_specs = [pl.BlockSpec((1, seg), functools.partial(lambda j, h, i: (0, j), j))
                  for j in range(len(windows))]
    kv_specs = []
    kv_args = []
    for window in windows:
        kv_specs.append(pl.BlockSpec((None, seg, head_dim), lambda h, i: (0, 0, h)))
        kv_specs.append(pl.BlockSpec((None, seg, head_dim), lambda h, i: (1, 0, h)))
        kv_args += [window, window]
    return pl.pallas_call(
        kernel,
        grid=(heads, rows // tile),
        in_specs=[pl.BlockSpec((tile, 1), lambda h, i: (i, 0))] + clip_specs
        + [pl.BlockSpec((tile, head_dim), lambda h, i: (i, h))] + kv_specs,
        out_specs=pl.BlockSpec((tile, head_dim), lambda h, i: (i, h)),
        out_shape=jax.ShapeDtypeStruct((rows, width), jnp.bfloat16),
    )(qclip, *([kclip] * len(windows)), queries, *kv_args)


def group_order(parts, quarter):
    ordered = jnp.stack([parts[0]] + parts[:0:-1], axis=0)
    return jnp.roll(ordered, quarter, axis=0)


def attend(queries, key_rows, value_rows, allowed, heads, head_groups):
    row_count = queries.shape[0]
    feat_width = queries.shape[1]
    head_dim = feat_width // heads
    per_group = heads // head_groups
    score_scale = 1.0 / math.sqrt(head_dim)

    def split_heads(source_rows):
        return source_rows.reshape(
            source_rows.shape[0], head_groups, per_group, head_dim
        ).transpose(1, 0, 2, 3)

    def one_group(operands):
        group_queries, group_keys, group_values = operands
        scores = (
            jnp.einsum(
                "rhd,khd->hrk", group_queries, group_keys, preferred_element_type=jnp.float32
            )
            * score_scale
        )
        masked = jnp.where(allowed[None], scores, -1e30)
        row_top = jnp.max(masked, axis=2, keepdims=True)
        weights = jnp.where(allowed[None], jnp.exp(masked - row_top), 0.0)
        row_total = jnp.sum(weights, axis=2)
        summed = jnp.einsum(
            "hrk,khd->rhd",
            weights.astype(jnp.bfloat16),
            group_values,
            preferred_element_type=jnp.float32,
        )
        return summed / jnp.transpose(row_total)[:, :, None]

    results = lax.map(
        one_group, (split_heads(queries), split_heads(key_rows), split_heads(value_rows))
    )
    return results.transpose(1, 0, 2, 3).reshape(row_count, feat_width).astype(jnp.bfloat16)


def body(fine_qkv, clip_ids, w_coarse, w_out):
    tok_count = fine_qkv.shape[0]
    feat_width = fine_qkv.shape[2]
    coarse_rows = tok_count // POOL
    group_rows = QUARTERS * coarse_rows
    position = lax.axis_index("seq")
    quarter = position % QUARTERS
    cycle_place = position // QUARTERS
    planes = jnp.transpose(fine_qkv, (1, 0, 2))
    clip_front = jnp.concatenate([jnp.full((FREACH * coarse_rows,), -1, jnp.int32), clip_ids])
    key_clip = jnp.repeat(
        lax.dynamic_slice_in_dim(clip_front, position * coarse_rows, (FREACH + 1) * coarse_rows, 0),
        POOL,
    )
    own_clip = lax.dynamic_slice_in_dim(clip_ids, position * coarse_rows, coarse_rows, 0)
    query_clip = jnp.repeat(own_clip, POOL)
    head_pair_width = 2 * feat_width // FHEADS
    part_width = feat_width // HALVES
    outs = []
    pools = []
    gate = None
    for part in range(HALVES):
        own_pairs = planes[1:, :, part * part_width:(part + 1) * part_width]
        if gate is not None:
            own_pairs, _ = lax.optimization_barrier((own_pairs, gate))
        prev0 = passed_along(own_pairs, "seq", 2)
        gate = prev0
        if outs:
            prev0, _ = lax.optimization_barrier((prev0, outs[-1]))
        local_pairs = own_pairs
        if outs:
            local_pairs, _ = lax.optimization_barrier((own_pairs, outs[-1]))
        prev1a = pair_swap(local_pairs, "seq", False)
        prev1b = pair_swap(prev0, "seq", True)
        part_out, part_pool = fine_attention(
            planes, prev0, prev1a, prev1b, query_clip.reshape(tok_count, 1),
            key_clip.reshape(1, (FREACH + 1) * tok_count), FHEADS,
            part * part_width // head_pair_width,
        )
        outs.append(part_out)
        pools.append(part_pool)
    fine_out = jnp.concatenate(outs, axis=1)
    pooled = jnp.concatenate(pools, axis=1)
    quarter_width = w_coarse.shape[2] // QUARTERS
    wplanes = jnp.transpose(w_coarse, (1, 0, 2))
    projected = jnp.einsum(
        "rd,mdc->mrc", pooled, wplanes, preferred_element_type=jnp.float32
    ).astype(jnp.bfloat16)
    pieces = []
    for shift in range(QUARTERS):
        piece = lax.dynamic_slice_in_dim(
            projected, ((quarter + shift) % QUARTERS) * quarter_width, quarter_width, 2
        )
        pieces.append(piece if shift == 0 else within_group(piece, "seq", shift))
    grouped = group_order(pieces, quarter)
    grouped = jnp.transpose(grouped, (1, 0, 2, 3)).reshape(3, group_rows, quarter_width)
    coarse_queries = grouped[0]
    coarse_pairs = grouped[1:]
    one_back = passed_along(coarse_pairs, "seq", QUARTERS)
    two_back = passed_along(coarse_pairs, "seq", 2 * QUARTERS)
    three_back = passed_along(two_back, "seq", QUARTERS)
    earlier = [three_back, two_back, one_back]
    clip_back = jnp.concatenate([jnp.full((CREACH * group_rows,), -1, jnp.int32), clip_ids])
    coarse_key_clip = lax.dynamic_slice_in_dim(
        clip_back, cycle_place * group_rows, (CREACH + 1) * group_rows, 0
    )
    coarse_query_clip = lax.dynamic_slice_in_dim(clip_ids, cycle_place * group_rows, group_rows, 0)
    coarse_att = coarse_attention(
        coarse_queries, earlier + [coarse_pairs], coarse_query_clip.reshape(group_rows, 1),
        coarse_key_clip.reshape(1, (CREACH + 1) * group_rows), CHEADS // QUARTERS,
    )
    shares = []
    for shift in range(QUARTERS):
        share = lax.dynamic_slice_in_dim(
            coarse_att, ((quarter + shift) % QUARTERS) * coarse_rows, coarse_rows, 0
        )
        shares.append(share if shift == 0 else within_group(share, "seq", shift))
    att_rows = jnp.transpose(group_order(shares, quarter), (1, 0, 2)).reshape(
        coarse_rows, QUARTERS * quarter_width
    )
    coarse_up = jnp.dot(att_rows, w_out, preferred_element_type=jnp.float32).astype(jnp.bfloat16)
    carried = passed_along(coarse_up[-1:], "seq", 1)
    previous = jnp.concatenate([jnp.zeros_like(carried), coarse_up[:-1]], axis=0)
    clip_before = jnp.concatenate([jnp.full((1,), -1, jnp.int32), clip_ids])
    prev_clip = lax.dynamic_slice_in_dim(clip_before, position * coarse_rows, coarse_rows, 0)
    joined = prev_clip == own_clip
    lifted = jnp.where(joined[:, None], previous, jnp.zeros_like(previous))
    mixed = mix(fine_out, lifted)
    head_lift = jnp.where(joined[:1, None], carried, jnp.zeros_like(carried)).astype(jnp.float32)
    head_rows = (fine_out[:POOL].astype(jnp.float32) + head_lift).astype(mixed.dtype)
    return lax.dynamic_update_slice(mixed, head_rows, (0, 0))


def solution(mesh):
    return jax.shard_map(
        body,
        mesh=mesh,
        in_specs=(P(("groups", "seq"), None, None), P("groups"), P(), P()),
        out_specs=P(("groups", "seq"), None),
        check_vma=False,
    )
```

```python
import functools
import math

import jax
import jax.numpy as jnp
from jax import lax
from jax.experimental import pallas as pl
from jax.experimental.pallas import tpu as pltpu
from jax.sharding import PartitionSpec as P

FHEADS = 16
CHEADS = 8
POOL = 4
QUARTERS = 4
FREACH = 2
CREACH = 3
FINE_TILE = 256
HALVES = 2


def passed_along(value, axis, steps):
    count = lax.axis_size(axis)
    first, last = (max(0, -steps), min(count, count - steps))
    return lax.ppermute(value, axis, [(source, source + steps) for source in range(first, last)])


def within_group(value, axis, shift):
    count = lax.axis_size(axis)
    pairs = []
    for source in range(count):
        base = source - source % QUARTERS
        pairs.append((source, base + (source % QUARTERS + shift) % QUARTERS))
    return lax.ppermute(value, axis, pairs)


def fine_kernel(qclip_ref, kclip0_ref, kclip1_ref, kclip2_ref, q_ref,
                k0_ref, v0_ref, k1_ref, v1_ref, k2_ref, v2_ref,
                out_ref, pool_ref, bias_ref, *, scale):
    tile = q_ref.shape[0]
    width = q_ref.shape[1]
    half = width // 2
    seg = k0_ref.shape[0]
    tile_index = pl.program_id(0)

    @pl.when(pl.program_id(1) == 0)
    def _():
        qclip = qclip_ref[...]
        qpos = tile_index * tile + lax.broadcasted_iota(jnp.int32, (tile, seg), 0)
        kpos = lax.broadcasted_iota(jnp.int32, (tile, seg), 1)
        allowed = (
            kclip0_ref[...] == qclip,
            kclip1_ref[...] == qclip,
            (kclip2_ref[...] == qclip) & (kpos <= qpos),
        )
        for j in range(3):
            bias_ref[:, j * seg:(j + 1) * seg] = jnp.where(allowed[j], 0.0, -1e30)

    q = q_ref[...] * jnp.asarray(scale, q_ref.dtype)
    lane = lax.broadcasted_iota(jnp.int32, (1, width), 1)
    low = lane < half
    zero = jnp.zeros_like(q)
    head_q = (jnp.where(low, q, zero), jnp.where(low, zero, q))

    def run(step):
        own = (step + 1) * tile
        keys = (k0_ref[...], k1_ref[...], k2_ref[0:own, :])
        values = (v0_ref[...], v1_ref[...], v2_ref[0:own, :])
        spans = ((0, seg), (seg, seg), (2 * seg, own))
        results = []
        for h in range(2):
            scores = []
            for j in range(3):
                s = lax.dot_general(head_q[h], keys[j], (((1,), (1,)), ((), ())),
                                    preferred_element_type=jnp.float32)
                start, length = spans[j]
                scores.append(s + bias_ref[:, start:start + length])
            top = jnp.max(scores[0], axis=1, keepdims=True)
            for j in range(1, 3):
                top = jnp.maximum(top, jnp.max(scores[j], axis=1, keepdims=True))
            total = None
            summed = None
            for j in range(3):
                w = jnp.exp(scores[j] - top)
                part = jnp.sum(w, axis=1, keepdims=True)
                pv = jnp.dot(w.astype(jnp.bfloat16), values[j], preferred_element_type=jnp.float32)
                total = part if total is None else total + part
                summed = pv if summed is None else summed + pv
            results.append(summed / total)
        out = jnp.where(low, results[0], results[1]).astype(out_ref.dtype)
        out_ref[...] = out
        rows = tile // POOL
        pool_row = lax.broadcasted_iota(jnp.int32, (rows, tile), 0)
        pool_col = lax.broadcasted_iota(jnp.int32, (rows, tile), 1)
        pool_mat = jnp.where(pool_col // POOL == pool_row, 1.0 / POOL, 0.0).astype(jnp.bfloat16)
        pool_ref[...] = jnp.dot(pool_mat, out, preferred_element_type=jnp.float32).astype(
            pool_ref.dtype)

    for step in range(seg // tile):
        pl.when(tile_index == step)(functools.partial(run, step))


def fine_attention(planes, prev0, prev1, qclip, kclip, heads, first_pair):
    _, tok, width = planes.shape
    head_dim = width // heads
    pair = 2 * head_dim
    pairs = prev0.shape[2] // pair
    tile = min(FINE_TILE, tok)
    nq = tok // tile
    kernel = functools.partial(fine_kernel, scale=1.0 / math.sqrt(head_dim))

    def plane_spec(plane):
        return pl.BlockSpec((None, tok, pair), lambda i, h: (plane, 0, h))

    def own_spec(plane):
        return pl.BlockSpec((None, tok, pair), lambda i, h: (plane, 0, first_pair + h))

    return pl.pallas_call(
        kernel,
        grid=(nq, pairs),
        in_specs=[
            pl.BlockSpec((tile, 1), lambda i, h: (i, 0)),
            pl.BlockSpec((1, tok), lambda i, h: (0, 0)),
            pl.BlockSpec((1, tok), lambda i, h: (0, 1)),
            pl.BlockSpec((1, tok), lambda i, h: (0, 2)),
            pl.BlockSpec((None, tile, pair), lambda i, h: (0, i, first_pair + h)),
            plane_spec(0), plane_spec(1),
            plane_spec(0), plane_spec(1),
            own_spec(1), own_spec(2),
        ],
        out_specs=[
            pl.BlockSpec((tile, pair), lambda i, h: (i, h)),
            pl.BlockSpec((tile // POOL, pair), lambda i, h: (i, h)),
        ],
        out_shape=[
            jax.ShapeDtypeStruct((tok, pairs * pair), jnp.bfloat16),
            jax.ShapeDtypeStruct((tok // POOL, pairs * pair), jnp.bfloat16),
        ],
        scratch_shapes=[pltpu.VMEM((tile, 3 * tok), jnp.float32)],
    )(qclip, kclip, kclip, kclip, planes, prev0, prev0, prev1, prev1, planes, planes)


def mix_kernel(fine_ref, lift_ref, out_ref):
    tile = fine_ref.shape[0]
    rows = lift_ref.shape[0]
    spread_row = lax.broadcasted_iota(jnp.int32, (tile, rows), 0)
    spread_col = lax.broadcasted_iota(jnp.int32, (tile, rows), 1)
    spread = jnp.where(spread_row // POOL == spread_col, 1.0, 0.0).astype(jnp.bfloat16)
    lifted = jnp.dot(spread, lift_ref[...], preferred_element_type=jnp.float32)
    out_ref[...] = (fine_ref[...].astype(jnp.float32) + lifted).astype(out_ref.dtype)


def mix(fine_out, lifted):
    tok, width = fine_out.shape
    tile = min(FINE_TILE, tok)
    return pl.pallas_call(
        mix_kernel,
        grid=(tok // tile,),
        in_specs=[
            pl.BlockSpec((tile, width), lambda i: (i, 0)),
            pl.BlockSpec((tile // POOL, width), lambda i: (i, 0)),
        ],
        out_specs=pl.BlockSpec((tile, width), lambda i: (i, 0)),
        out_shape=jax.ShapeDtypeStruct((tok, width), fine_out.dtype),
    )(fine_out, lifted)


def pair_swap(value, axis, from_odd):
    count = lax.axis_size(axis)
    start = 1 if from_odd else 0
    step = -1 if from_odd else 1
    return lax.ppermute(value, axis, [(source, source + step) for source in range(start, count, 2)])


def coarse_kernel(qclip_ref, kc0_ref, kc1_ref, kc2_ref, kc3_ref, q_ref,
                  k0_ref, v0_ref, k1_ref, v1_ref, k2_ref, v2_ref, k3_ref, v3_ref,
                  out_ref, *, scale):
    tile = q_ref.shape[0]
    seg = k0_ref.shape[0]
    q = q_ref[...]
    qclip = qclip_ref[...]
    keys = (k0_ref, k1_ref, k2_ref, k3_ref)
    values = (v0_ref, v1_ref, v2_ref, v3_ref)
    clips = (kc0_ref, kc1_ref, kc2_ref, kc3_ref)
    qpos = pl.program_id(1) * tile + lax.broadcasted_iota(jnp.int32, (tile, seg), 0)
    kpos = lax.broadcasted_iota(jnp.int32, (tile, seg), 1)
    last = len(keys) - 1
    scores = []
    masks = []
    for j in range(len(keys)):
        allowed = clips[j][...] == qclip
        if j == last:
            allowed = allowed & (kpos <= qpos)
        s = lax.dot_general(q, keys[j][...], (((1,), (1,)), ((), ())),
                            preferred_element_type=jnp.float32) * scale
        scores.append(jnp.where(allowed, s, -1e30))
    top = jnp.max(scores[0], axis=1, keepdims=True)
    for j in range(1, len(keys)):
        top = jnp.maximum(top, jnp.max(scores[j], axis=1, keepdims=True))
    total = None
    summed = None
    for j in range(len(keys)):
        w = jnp.exp(scores[j] - top)
        part = jnp.sum(w, axis=1, keepdims=True)
        pv = jnp.dot(w.astype(jnp.bfloat16), values[j][...], preferred_element_type=jnp.float32)
        total = part if total is None else total + part
        summed = pv if summed is None else summed + pv
    out_ref[...] = (summed / total).astype(out_ref.dtype)


def coarse_attention(queries, windows, qclip, kclip, heads):
    rows, width = queries.shape
    head_dim = width // heads
    tile = min(FINE_TILE, rows)
    seg = windows[0].shape[1]
    kernel = functools.partial(coarse_kernel, scale=1.0 / math.sqrt(head_dim))
    clip_specs = [pl.BlockSpec((1, seg), functools.partial(lambda j, h, i: (0, j), j))
                  for j in range(len(windows))]
    kv_specs = []
    kv_args = []
    for window in windows:
        kv_specs.append(pl.BlockSpec((None, seg, head_dim), lambda h, i: (0, 0, h)))
        kv_specs.append(pl.BlockSpec((None, seg, head_dim), lambda h, i: (1, 0, h)))
        kv_args += [window, window]
    return pl.pallas_call(
        kernel,
        grid=(heads, rows // tile),
        in_specs=[pl.BlockSpec((tile, 1), lambda h, i: (i, 0))] + clip_specs
        + [pl.BlockSpec((tile, head_dim), lambda h, i: (i, h))] + kv_specs,
        out_specs=pl.BlockSpec((tile, head_dim), lambda h, i: (i, h)),
        out_shape=jax.ShapeDtypeStruct((rows, width), jnp.bfloat16),
    )(qclip, *([kclip] * len(windows)), queries, *kv_args)


def group_order(parts, quarter):
    ordered = jnp.stack([parts[0]] + parts[:0:-1], axis=0)
    return jnp.roll(ordered, quarter, axis=0)


def attend(queries, key_rows, value_rows, allowed, heads, head_groups):
    row_count = queries.shape[0]
    feat_width = queries.shape[1]
    head_dim = feat_width // heads
    per_group = heads // head_groups
    score_scale = 1.0 / math.sqrt(head_dim)

    def split_heads(source_rows):
        return source_rows.reshape(
            source_rows.shape[0], head_groups, per_group, head_dim
        ).transpose(1, 0, 2, 3)

    def one_group(operands):
        group_queries, group_keys, group_values = operands
        scores = (
            jnp.einsum(
                "rhd,khd->hrk", group_queries, group_keys, preferred_element_type=jnp.float32
            )
            * score_scale
        )
        masked = jnp.where(allowed[None], scores, -1e30)
        row_top = jnp.max(masked, axis=2, keepdims=True)
        weights = jnp.where(allowed[None], jnp.exp(masked - row_top), 0.0)
        row_total = jnp.sum(weights, axis=2)
        summed = jnp.einsum(
            "hrk,khd->rhd",
            weights.astype(jnp.bfloat16),
            group_values,
            preferred_element_type=jnp.float32,
        )
        return summed / jnp.transpose(row_total)[:, :, None]

    results = lax.map(
        one_group, (split_heads(queries), split_heads(key_rows), split_heads(value_rows))
    )
    return results.transpose(1, 0, 2, 3).reshape(row_count, feat_width).astype(jnp.bfloat16)


def body(fine_qkv, clip_ids, w_coarse, w_out):
    tok_count = fine_qkv.shape[0]
    feat_width = fine_qkv.shape[2]
    coarse_rows = tok_count // POOL
    group_rows = QUARTERS * coarse_rows
    position = lax.axis_index("seq")
    quarter = position % QUARTERS
    cycle_place = position // QUARTERS
    planes = jnp.transpose(fine_qkv, (1, 0, 2))
    clip_front = jnp.concatenate([jnp.full((FREACH * coarse_rows,), -1, jnp.int32), clip_ids])
    key_clip = jnp.repeat(
        lax.dynamic_slice_in_dim(clip_front, position * coarse_rows, (FREACH + 1) * coarse_rows, 0),
        POOL,
    )
    own_clip = lax.dynamic_slice_in_dim(clip_ids, position * coarse_rows, coarse_rows, 0)
    query_clip = jnp.repeat(own_clip, POOL)
    head_pair_width = 2 * feat_width // FHEADS
    seq_count = lax.axis_size("seq")
    part_width = feat_width // HALVES
    outs = []
    pools = []
    gate = None
    for part in range(HALVES):
        own_pairs = planes[1:, :, part * part_width:(part + 1) * part_width]
        if gate is not None:
            own_pairs, _ = lax.optimization_barrier((own_pairs, gate))
        prev0 = passed_along(own_pairs, "seq", 2)
        gate = prev0
        if outs:
            prev0, _ = lax.optimization_barrier((prev0, outs[-1]))
        outgoing = jnp.where(position % 2 == 0, own_pairs, prev0)
        prev1 = lax.ppermute(outgoing, "seq", [(source, source ^ 1) for source in range(seq_count)])
        part_out, part_pool = fine_attention(
            planes, prev0, prev1, query_clip.reshape(tok_count, 1),
            key_clip.reshape(1, (FREACH + 1) * tok_count), FHEADS,
            part * part_width // head_pair_width,
        )
        outs.append(part_out)
        pools.append(part_pool)
    fine_out = jnp.concatenate(outs, axis=1)
    pooled = jnp.concatenate(pools, axis=1)
    quarter_width = w_coarse.shape[2] // QUARTERS
    wplanes = jnp.transpose(w_coarse, (1, 0, 2))
    projected = jnp.einsum(
        "rd,mdc->mrc", pooled, wplanes, preferred_element_type=jnp.float32
    ).astype(jnp.bfloat16)
    pieces = []
    for shift in range(QUARTERS):
        piece = lax.dynamic_slice_in_dim(
            projected, ((quarter + shift) % QUARTERS) * quarter_width, quarter_width, 2
        )
        pieces.append(piece if shift == 0 else within_group(piece, "seq", shift))
    grouped = group_order(pieces, quarter)
    grouped = jnp.transpose(grouped, (1, 0, 2, 3)).reshape(3, group_rows, quarter_width)
    coarse_queries = grouped[0]
    coarse_pairs = grouped[1:]
    one_back = passed_along(coarse_pairs, "seq", QUARTERS)
    two_back = passed_along(coarse_pairs, "seq", 2 * QUARTERS)
    three_back = passed_along(two_back, "seq", QUARTERS)
    earlier = [three_back, two_back, one_back]
    clip_back = jnp.concatenate([jnp.full((CREACH * group_rows,), -1, jnp.int32), clip_ids])
    coarse_key_clip = lax.dynamic_slice_in_dim(
        clip_back, cycle_place * group_rows, (CREACH + 1) * group_rows, 0
    )
    coarse_query_clip = lax.dynamic_slice_in_dim(clip_ids, cycle_place * group_rows, group_rows, 0)
    coarse_att = coarse_attention(
        coarse_queries, earlier + [coarse_pairs], coarse_query_clip.reshape(group_rows, 1),
        coarse_key_clip.reshape(1, (CREACH + 1) * group_rows), CHEADS // QUARTERS,
    )
    shares = []
    for shift in range(QUARTERS):
        share = lax.dynamic_slice_in_dim(
            coarse_att, ((quarter + shift) % QUARTERS) * coarse_rows, coarse_rows, 0
        )
        shares.append(share if shift == 0 else within_group(share, "seq", shift))
    att_rows = jnp.transpose(group_order(shares, quarter), (1, 0, 2)).reshape(
        coarse_rows, QUARTERS * quarter_width
    )
    coarse_up = jnp.dot(att_rows, w_out, preferred_element_type=jnp.float32).astype(jnp.bfloat16)
    carried = passed_along(coarse_up[-1:], "seq", 1)
    previous = jnp.concatenate([jnp.zeros_like(carried), coarse_up[:-1]], axis=0)
    clip_before = jnp.concatenate([jnp.full((1,), -1, jnp.int32), clip_ids])
    prev_clip = lax.dynamic_slice_in_dim(clip_before, position * coarse_rows, coarse_rows, 0)
    joined = prev_clip == own_clip
    lifted = jnp.where(joined[:, None], previous, jnp.zeros_like(previous))
    mixed = mix(fine_out, lifted)
    head_lift = jnp.where(joined[:1, None], carried, jnp.zeros_like(carried)).astype(jnp.float32)
    head_rows = (fine_out[:POOL].astype(jnp.float32) + head_lift).astype(mixed.dtype)
    return lax.dynamic_update_slice(mixed, head_rows, (0, 0))


def solution(mesh):
    return jax.shard_map(
        body,
        mesh=mesh,
        in_specs=(P(("groups", "seq"), None, None), P("groups"), P(), P()),
        out_specs=P(("groups", "seq"), None),
        check_vma=False,
    )
```

```python
import functools
import math

import jax
import jax.numpy as jnp
from jax import lax
from jax.experimental import pallas as pl
from jax.experimental.pallas import tpu as pltpu
from jax.sharding import PartitionSpec as P

FHEADS = 16
CHEADS = 8
POOL = 4
QUARTERS = 4
FREACH = 2
CREACH = 3
FINE_TILE = 256
HALVES = 2


def passed_along(value, axis, steps):
    count = lax.axis_size(axis)
    first, last = (max(0, -steps), min(count, count - steps))
    return lax.ppermute(value, axis, [(source, source + steps) for source in range(first, last)])


def within_group(value, axis, shift):
    count = lax.axis_size(axis)
    pairs = []
    for source in range(count):
        base = source - source % QUARTERS
        pairs.append((source, base + (source % QUARTERS + shift) % QUARTERS))
    return lax.ppermute(value, axis, pairs)


def fine_kernel(qclip_ref, kclip0_ref, kclip1_ref, kclip2_ref, q_ref,
                k0_ref, v0_ref, k1_ref, v1_ref, k1b_ref, v1b_ref, k2_ref, v2_ref,
                out_ref, pool_ref, bias_ref, *, scale):
    tile = q_ref.shape[0]
    width = q_ref.shape[1]
    half = width // 2
    seg = k0_ref.shape[0]
    tile_index = pl.program_id(0)

    @pl.when(pl.program_id(1) == 0)
    def _():
        qclip = qclip_ref[...]
        qpos = tile_index * tile + lax.broadcasted_iota(jnp.int32, (tile, seg), 0)
        kpos = lax.broadcasted_iota(jnp.int32, (tile, seg), 1)
        allowed = (
            kclip0_ref[...] == qclip,
            kclip1_ref[...] == qclip,
            (kclip2_ref[...] == qclip) & (kpos <= qpos),
        )
        for j in range(3):
            bias_ref[:, j * seg:(j + 1) * seg] = jnp.where(allowed[j], 0.0, -1e30)

    q = q_ref[...] * jnp.asarray(scale, q_ref.dtype)
    lane = lax.broadcasted_iota(jnp.int32, (1, width), 1)
    low = lane < half
    zero = jnp.zeros_like(q)
    head_q = (jnp.where(low, q, zero), jnp.where(low, zero, q))

    def run(step):
        own = (step + 1) * tile
        keys = (k0_ref[...], k1_ref[...] + k1b_ref[...], k2_ref[0:own, :])
        values = (v0_ref[...], v1_ref[...] + v1b_ref[...], v2_ref[0:own, :])
        spans = ((0, seg), (seg, seg), (2 * seg, own))
        results = []
        for h in range(2):
            scores = []
            for j in range(3):
                s = lax.dot_general(head_q[h], keys[j], (((1,), (1,)), ((), ())),
                                    preferred_element_type=jnp.float32)
                start, length = spans[j]
                scores.append(s + bias_ref[:, start:start + length])
            top = jnp.max(scores[0], axis=1, keepdims=True)
            for j in range(1, 3):
                top = jnp.maximum(top, jnp.max(scores[j], axis=1, keepdims=True))
            total = None
            summed = None
            for j in range(3):
                w = jnp.exp(scores[j] - top)
                part = jnp.sum(w, axis=1, keepdims=True)
                pv = jnp.dot(w.astype(jnp.bfloat16), values[j], preferred_element_type=jnp.float32)
                total = part if total is None else total + part
                summed = pv if summed is None else summed + pv
            results.append(summed / total)
        out = jnp.where(low, results[0], results[1]).astype(out_ref.dtype)
        out_ref[...] = out
        rows = tile // POOL
        pool_row = lax.broadcasted_iota(jnp.int32, (rows, tile), 0)
        pool_col = lax.broadcasted_iota(jnp.int32, (rows, tile), 1)
        pool_mat = jnp.where(pool_col // POOL == pool_row, 1.0 / POOL, 0.0).astype(jnp.bfloat16)
        pool_ref[...] = jnp.dot(pool_mat, out, preferred_element_type=jnp.float32).astype(
            pool_ref.dtype)

    for step in range(seg // tile):
        pl.when(tile_index == step)(functools.partial(run, step))


def fine_attention(planes, prev0, prev1a, prev1b, qclip, kclip, heads, first_pair):
    _, tok, width = planes.shape
    head_dim = width // heads
    pair = 2 * head_dim
    pairs = prev0.shape[2] // pair
    tile = min(FINE_TILE, tok)
    nq = tok // tile
    kernel = functools.partial(fine_kernel, scale=1.0 / math.sqrt(head_dim))

    def plane_spec(plane):
        return pl.BlockSpec((None, tok, pair), lambda i, h: (plane, 0, h))

    def own_spec(plane):
        return pl.BlockSpec((None, tok, pair), lambda i, h: (plane, 0, first_pair + h))

    return pl.pallas_call(
        kernel,
        grid=(nq, pairs),
        in_specs=[
            pl.BlockSpec((tile, 1), lambda i, h: (i, 0)),
            pl.BlockSpec((1, tok), lambda i, h: (0, 0)),
            pl.BlockSpec((1, tok), lambda i, h: (0, 1)),
            pl.BlockSpec((1, tok), lambda i, h: (0, 2)),
            pl.BlockSpec((None, tile, pair), lambda i, h: (0, i, first_pair + h)),
            plane_spec(0), plane_spec(1),
            plane_spec(0), plane_spec(1),
            plane_spec(0), plane_spec(1),
            own_spec(1), own_spec(2),
        ],
        out_specs=[
            pl.BlockSpec((tile, pair), lambda i, h: (i, h)),
            pl.BlockSpec((tile // POOL, pair), lambda i, h: (i, h)),
        ],
        out_shape=[
            jax.ShapeDtypeStruct((tok, pairs * pair), jnp.bfloat16),
            jax.ShapeDtypeStruct((tok // POOL, pairs * pair), jnp.bfloat16),
        ],
        scratch_shapes=[pltpu.VMEM((tile, 3 * tok), jnp.float32)],
    )(qclip, kclip, kclip, kclip, planes, prev0, prev0, prev1a, prev1a, prev1b, prev1b,
      planes, planes)


def mix_kernel(fine_ref, lift_ref, out_ref):
    tile = fine_ref.shape[0]
    rows = lift_ref.shape[0]
    spread_row = lax.broadcasted_iota(jnp.int32, (tile, rows), 0)
    spread_col = lax.broadcasted_iota(jnp.int32, (tile, rows), 1)
    spread = jnp.where(spread_row // POOL == spread_col, 1.0, 0.0).astype(jnp.bfloat16)
    lifted = jnp.dot(spread, lift_ref[...], preferred_element_type=jnp.float32)
    out_ref[...] = (fine_ref[...].astype(jnp.float32) + lifted).astype(out_ref.dtype)


def mix(fine_out, lifted):
    tok, width = fine_out.shape
    tile = min(FINE_TILE, tok)
    return pl.pallas_call(
        mix_kernel,
        grid=(tok // tile,),
        in_specs=[
            pl.BlockSpec((tile, width), lambda i: (i, 0)),
            pl.BlockSpec((tile // POOL, width), lambda i: (i, 0)),
        ],
        out_specs=pl.BlockSpec((tile, width), lambda i: (i, 0)),
        out_shape=jax.ShapeDtypeStruct((tok, width), fine_out.dtype),
    )(fine_out, lifted)


def pair_swap(value, axis, from_odd):
    count = lax.axis_size(axis)
    start = 1 if from_odd else 0
    step = -1 if from_odd else 1
    return lax.ppermute(value, axis, [(source, source + step) for source in range(start, count, 2)])


def coarse_kernel(qclip_ref, kc0_ref, kc1_ref, kc2_ref, kc3_ref, q_ref,
                  k0_ref, v0_ref, k1_ref, v1_ref, k2_ref, v2_ref, k3_ref, v3_ref,
                  out_ref, *, scale):
    tile = q_ref.shape[0]
    seg = k0_ref.shape[0]
    q = q_ref[...]
    qclip = qclip_ref[...]
    keys = (k0_ref, k1_ref, k2_ref, k3_ref)
    values = (v0_ref, v1_ref, v2_ref, v3_ref)
    clips = (kc0_ref, kc1_ref, kc2_ref, kc3_ref)
    qpos = pl.program_id(1) * tile + lax.broadcasted_iota(jnp.int32, (tile, seg), 0)
    kpos = lax.broadcasted_iota(jnp.int32, (tile, seg), 1)
    last = len(keys) - 1
    scores = []
    masks = []
    for j in range(len(keys)):
        allowed = clips[j][...] == qclip
        if j == last:
            allowed = allowed & (kpos <= qpos)
        s = lax.dot_general(q, keys[j][...], (((1,), (1,)), ((), ())),
                            preferred_element_type=jnp.float32) * scale
        scores.append(jnp.where(allowed, s, -1e30))
    top = jnp.max(scores[0], axis=1, keepdims=True)
    for j in range(1, len(keys)):
        top = jnp.maximum(top, jnp.max(scores[j], axis=1, keepdims=True))
    total = None
    summed = None
    for j in range(len(keys)):
        w = jnp.exp(scores[j] - top)
        part = jnp.sum(w, axis=1, keepdims=True)
        pv = jnp.dot(w.astype(jnp.bfloat16), values[j][...], preferred_element_type=jnp.float32)
        total = part if total is None else total + part
        summed = pv if summed is None else summed + pv
    out_ref[...] = (summed / total).astype(out_ref.dtype)


def coarse_attention(queries, windows, qclip, kclip, heads):
    rows, width = queries.shape
    head_dim = width // heads
    tile = min(FINE_TILE, rows)
    seg = windows[0].shape[1]
    kernel = functools.partial(coarse_kernel, scale=1.0 / math.sqrt(head_dim))
    clip_specs = [pl.BlockSpec((1, seg), functools.partial(lambda j, h, i: (0, j), j))
                  for j in range(len(windows))]
    kv_specs = []
    kv_args = []
    for window in windows:
        kv_specs.append(pl.BlockSpec((None, seg, head_dim), lambda h, i: (0, 0, h)))
        kv_specs.append(pl.BlockSpec((None, seg, head_dim), lambda h, i: (1, 0, h)))
        kv_args += [window, window]
    return pl.pallas_call(
        kernel,
        grid=(heads, rows // tile),
        in_specs=[pl.BlockSpec((tile, 1), lambda h, i: (i, 0))] + clip_specs
        + [pl.BlockSpec((tile, head_dim), lambda h, i: (i, h))] + kv_specs,
        out_specs=pl.BlockSpec((tile, head_dim), lambda h, i: (i, h)),
        out_shape=jax.ShapeDtypeStruct((rows, width), jnp.bfloat16),
    )(qclip, *([kclip] * len(windows)), queries, *kv_args)


def group_order(parts, quarter):
    ordered = jnp.stack([parts[0]] + parts[:0:-1], axis=0)
    return jnp.roll(ordered, quarter, axis=0)


def attend(queries, key_rows, value_rows, allowed, heads, head_groups):
    row_count = queries.shape[0]
    feat_width = queries.shape[1]
    head_dim = feat_width // heads
    per_group = heads // head_groups
    score_scale = 1.0 / math.sqrt(head_dim)

    def split_heads(source_rows):
        return source_rows.reshape(
            source_rows.shape[0], head_groups, per_group, head_dim
        ).transpose(1, 0, 2, 3)

    def one_group(operands):
        group_queries, group_keys, group_values = operands
        scores = (
            jnp.einsum(
                "rhd,khd->hrk", group_queries, group_keys, preferred_element_type=jnp.float32
            )
            * score_scale
        )
        masked = jnp.where(allowed[None], scores, -1e30)
        row_top = jnp.max(masked, axis=2, keepdims=True)
        weights = jnp.where(allowed[None], jnp.exp(masked - row_top), 0.0)
        row_total = jnp.sum(weights, axis=2)
        summed = jnp.einsum(
            "hrk,khd->rhd",
            weights.astype(jnp.bfloat16),
            group_values,
            preferred_element_type=jnp.float32,
        )
        return summed / jnp.transpose(row_total)[:, :, None]

    results = lax.map(
        one_group, (split_heads(queries), split_heads(key_rows), split_heads(value_rows))
    )
    return results.transpose(1, 0, 2, 3).reshape(row_count, feat_width).astype(jnp.bfloat16)


def body(fine_qkv, clip_ids, w_coarse, w_out):
    tok_count = fine_qkv.shape[0]
    feat_width = fine_qkv.shape[2]
    coarse_rows = tok_count // POOL
    group_rows = QUARTERS * coarse_rows
    position = lax.axis_index("seq")
    quarter = position % QUARTERS
    cycle_place = position // QUARTERS
    planes = jnp.transpose(fine_qkv, (1, 0, 2))
    clip_front = jnp.concatenate([jnp.full((FREACH * coarse_rows,), -1, jnp.int32), clip_ids])
    key_clip = jnp.repeat(
        lax.dynamic_slice_in_dim(clip_front, position * coarse_rows, (FREACH + 1) * coarse_rows, 0),
        POOL,
    )
    own_clip = lax.dynamic_slice_in_dim(clip_ids, position * coarse_rows, coarse_rows, 0)
    query_clip = jnp.repeat(own_clip, POOL)
    head_pair_width = 2 * feat_width // FHEADS
    part_width = feat_width // HALVES
    outs = []
    projected = None
    wplanes = jnp.transpose(w_coarse, (1, 0, 2))
    gate = None
    for part in range(HALVES):
        own_pairs = planes[1:, :, part * part_width:(part + 1) * part_width]
        if gate is not None:
            own_pairs, _ = lax.optimization_barrier((own_pairs, gate))
        prev0 = passed_along(own_pairs, "seq", 2)
        gate = prev0
        if outs:
            prev0, _ = lax.optimization_barrier((prev0, projected))
        prev1a = pair_swap(own_pairs, "seq", False)
        prev1b = pair_swap(prev0, "seq", True)
        part_out, part_pool = fine_attention(
            planes, prev0, prev1a, prev1b, query_clip.reshape(tok_count, 1),
            key_clip.reshape(1, (FREACH + 1) * tok_count), FHEADS,
            part * part_width // head_pair_width,
        )
        outs.append(part_out)
        part_weight = wplanes[:, part * part_width:(part + 1) * part_width, :]
        contribution = jnp.einsum(
            "rd,mdc->mrc", part_pool, part_weight, preferred_element_type=jnp.float32
        )
        projected = contribution if projected is None else projected + contribution
    fine_out = jnp.concatenate(outs, axis=1)
    quarter_width = w_coarse.shape[2] // QUARTERS
    projected = projected.astype(jnp.bfloat16)
    pieces = []
    for shift in range(QUARTERS):
        piece = lax.dynamic_slice_in_dim(
            projected, ((quarter + shift) % QUARTERS) * quarter_width, quarter_width, 2
        )
        pieces.append(piece if shift == 0 else within_group(piece, "seq", shift))
    grouped = group_order(pieces, quarter)
    grouped = jnp.transpose(grouped, (1, 0, 2, 3)).reshape(3, group_rows, quarter_width)
    coarse_queries = grouped[0]
    coarse_pairs = grouped[1:]
    one_back = passed_along(coarse_pairs, "seq", QUARTERS)
    two_back = passed_along(coarse_pairs, "seq", 2 * QUARTERS)
    three_back = passed_along(two_back, "seq", QUARTERS)
    earlier = [three_back, two_back, one_back]
    clip_back = jnp.concatenate([jnp.full((CREACH * group_rows,), -1, jnp.int32), clip_ids])
    coarse_key_clip = lax.dynamic_slice_in_dim(
        clip_back, cycle_place * group_rows, (CREACH + 1) * group_rows, 0
    )
    coarse_query_clip = lax.dynamic_slice_in_dim(clip_ids, cycle_place * group_rows, group_rows, 0)
    coarse_att = coarse_attention(
        coarse_queries, earlier + [coarse_pairs], coarse_query_clip.reshape(group_rows, 1),
        coarse_key_clip.reshape(1, (CREACH + 1) * group_rows), CHEADS // QUARTERS,
    )
    shares = []
    for shift in range(QUARTERS):
        share = lax.dynamic_slice_in_dim(
            coarse_att, ((quarter + shift) % QUARTERS) * coarse_rows, coarse_rows, 0
        )
        shares.append(share if shift == 0 else within_group(share, "seq", shift))
    att_rows = jnp.transpose(group_order(shares, quarter), (1, 0, 2)).reshape(
        coarse_rows, QUARTERS * quarter_width
    )
    coarse_up = jnp.dot(att_rows, w_out, preferred_element_type=jnp.float32).astype(jnp.bfloat16)
    carried = passed_along(coarse_up[-1:], "seq", 1)
    previous = jnp.concatenate([jnp.zeros_like(carried), coarse_up[:-1]], axis=0)
    clip_before = jnp.concatenate([jnp.full((1,), -1, jnp.int32), clip_ids])
    prev_clip = lax.dynamic_slice_in_dim(clip_before, position * coarse_rows, coarse_rows, 0)
    joined = prev_clip == own_clip
    lifted = jnp.where(joined[:, None], previous, jnp.zeros_like(previous))
    mixed = mix(fine_out, lifted)
    head_lift = jnp.where(joined[:1, None], carried, jnp.zeros_like(carried)).astype(jnp.float32)
    head_rows = (fine_out[:POOL].astype(jnp.float32) + head_lift).astype(mixed.dtype)
    return lax.dynamic_update_slice(mixed, head_rows, (0, 0))


def solution(mesh):
    return jax.shard_map(
        body,
        mesh=mesh,
        in_specs=(P(("groups", "seq"), None, None), P("groups"), P(), P()),
        out_specs=P(("groups", "seq"), None),
        check_vma=False,
    )
```

```python
import functools
import math

import jax
import jax.numpy as jnp
from jax import lax
from jax.experimental import pallas as pl
from jax.experimental.pallas import tpu as pltpu
from jax.sharding import PartitionSpec as P

FHEADS = 16
CHEADS = 8
POOL = 4
QUARTERS = 4
FREACH = 2
CREACH = 3
FINE_TILE = 256
HALVES = 2


def passed_along(value, axis, steps):
    count = lax.axis_size(axis)
    first, last = (max(0, -steps), min(count, count - steps))
    return lax.ppermute(value, axis, [(source, source + steps) for source in range(first, last)])


def within_group(value, axis, shift):
    count = lax.axis_size(axis)
    pairs = []
    for source in range(count):
        base = source - source % QUARTERS
        pairs.append((source, base + (source % QUARTERS + shift) % QUARTERS))
    return lax.ppermute(value, axis, pairs)


def fine_kernel(qclip_ref, kclip0_ref, kclip1_ref, kclip2_ref, q_ref,
                k0_ref, v0_ref, k1_ref, v1_ref, k1b_ref, v1b_ref, k2_ref, v2_ref,
                out_ref, pool_ref, bias_ref, *, scale):
    tile = q_ref.shape[0]
    width = q_ref.shape[1]
    half = width // 2
    seg = k0_ref.shape[0]
    tile_index = pl.program_id(0)

    @pl.when(pl.program_id(1) == 0)
    def _():
        qclip = qclip_ref[...]
        qpos = tile_index * tile + lax.broadcasted_iota(jnp.int32, (tile, seg), 0)
        kpos = lax.broadcasted_iota(jnp.int32, (tile, seg), 1)
        allowed = (
            kclip0_ref[...] == qclip,
            kclip1_ref[...] == qclip,
            (kclip2_ref[...] == qclip) & (kpos <= qpos),
        )
        for j in range(3):
            bias_ref[:, j * seg:(j + 1) * seg] = jnp.where(allowed[j], 0.0, -1e30)

    q = q_ref[...] * jnp.asarray(scale, q_ref.dtype)
    lane = lax.broadcasted_iota(jnp.int32, (1, width), 1)
    low = lane < half
    zero = jnp.zeros_like(q)
    head_q = (jnp.where(low, q, zero), jnp.where(low, zero, q))

    def run(step):
        own = (step + 1) * tile
        keys = (k0_ref[...], k1_ref[...] + k1b_ref[...], k2_ref[0:own, :])
        values = (v0_ref[...], v1_ref[...] + v1b_ref[...], v2_ref[0:own, :])
        spans = ((0, seg), (seg, seg), (2 * seg, own))
        results = []
        for h in range(2):
            scores = []
            for j in range(3):
                s = lax.dot_general(head_q[h], keys[j], (((1,), (1,)), ((), ())),
                                    preferred_element_type=jnp.float32)
                start, length = spans[j]
                scores.append(s + bias_ref[:, start:start + length])
            top = jnp.max(scores[0], axis=1, keepdims=True)
            for j in range(1, 3):
                top = jnp.maximum(top, jnp.max(scores[j], axis=1, keepdims=True))
            total = None
            summed = None
            for j in range(3):
                w = jnp.exp(scores[j] - top)
                part = jnp.sum(w, axis=1, keepdims=True)
                pv = jnp.dot(w.astype(jnp.bfloat16), values[j], preferred_element_type=jnp.float32)
                total = part if total is None else total + part
                summed = pv if summed is None else summed + pv
            results.append(summed / total)
        out = jnp.where(low, results[0], results[1]).astype(out_ref.dtype)
        out_ref[...] = out
        rows = tile // POOL
        pool_row = lax.broadcasted_iota(jnp.int32, (rows, tile), 0)
        pool_col = lax.broadcasted_iota(jnp.int32, (rows, tile), 1)
        pool_mat = jnp.where(pool_col // POOL == pool_row, 1.0 / POOL, 0.0).astype(jnp.bfloat16)
        pool_ref[...] = jnp.dot(pool_mat, out, preferred_element_type=jnp.float32).astype(
            pool_ref.dtype)

    for step in range(seg // tile):
        pl.when(tile_index == step)(functools.partial(run, step))


def fine_attention(planes, prev0, prev1a, prev1b, qclip, kclip, heads, first_pair):
    _, tok, width = planes.shape
    head_dim = width // heads
    pair = 2 * head_dim
    pairs = prev0.shape[2] // pair
    tile = min(FINE_TILE, tok)
    nq = tok // tile
    kernel = functools.partial(fine_kernel, scale=1.0 / math.sqrt(head_dim))

    def plane_spec(plane):
        return pl.BlockSpec((None, tok, pair), lambda i, h: (plane, 0, h))

    def own_spec(plane):
        return pl.BlockSpec((None, tok, pair), lambda i, h: (plane, 0, first_pair + h))

    return pl.pallas_call(
        kernel,
        grid=(nq, pairs),
        in_specs=[
            pl.BlockSpec((tile, 1), lambda i, h: (i, 0)),
            pl.BlockSpec((1, tok), lambda i, h: (0, 0)),
            pl.BlockSpec((1, tok), lambda i, h: (0, 1)),
            pl.BlockSpec((1, tok), lambda i, h: (0, 2)),
            pl.BlockSpec((None, tile, pair), lambda i, h: (0, i, first_pair + h)),
            plane_spec(0), plane_spec(1),
            plane_spec(0), plane_spec(1),
            plane_spec(0), plane_spec(1),
            own_spec(1), own_spec(2),
        ],
        out_specs=[
            pl.BlockSpec((tile, pair), lambda i, h: (i, h)),
            pl.BlockSpec((tile // POOL, pair), lambda i, h: (i, h)),
        ],
        out_shape=[
            jax.ShapeDtypeStruct((tok, pairs * pair), jnp.bfloat16),
            jax.ShapeDtypeStruct((tok // POOL, pairs * pair), jnp.bfloat16),
        ],
        scratch_shapes=[pltpu.VMEM((tile, 3 * tok), jnp.float32)],
    )(qclip, kclip, kclip, kclip, planes, prev0, prev0, prev1a, prev1a, prev1b, prev1b,
      planes, planes)


def mix_kernel(fine_ref, lift_ref, out_ref):
    tile = fine_ref.shape[0]
    rows = lift_ref.shape[0]
    spread_row = lax.broadcasted_iota(jnp.int32, (tile, rows), 0)
    spread_col = lax.broadcasted_iota(jnp.int32, (tile, rows), 1)
    spread = jnp.where(spread_row // POOL == spread_col, 1.0, 0.0).astype(jnp.bfloat16)
    lifted = jnp.dot(spread, lift_ref[...], preferred_element_type=jnp.float32)
    out_ref[...] = (fine_ref[...].astype(jnp.float32) + lifted).astype(out_ref.dtype)


def mix(fine_out, lifted):
    tok, width = fine_out.shape
    tile = min(FINE_TILE, tok)
    return pl.pallas_call(
        mix_kernel,
        grid=(tok // tile,),
        in_specs=[
            pl.BlockSpec((tile, width), lambda i: (i, 0)),
            pl.BlockSpec((tile // POOL, width), lambda i: (i, 0)),
        ],
        out_specs=pl.BlockSpec((tile, width), lambda i: (i, 0)),
        out_shape=jax.ShapeDtypeStruct((tok, width), fine_out.dtype),
    )(fine_out, lifted)


def pair_swap(value, axis, from_odd):
    count = lax.axis_size(axis)
    start = 1 if from_odd else 0
    step = -1 if from_odd else 1
    return lax.ppermute(value, axis, [(source, source + step) for source in range(start, count, 2)])


def coarse_kernel(qclip_ref, kc0_ref, kc1_ref, kc2_ref, kc3_ref, q_ref,
                  k0_ref, v0_ref, k1_ref, v1_ref, k2_ref, v2_ref, k3_ref, v3_ref,
                  out_ref, *, scale):
    tile = q_ref.shape[0]
    seg = k0_ref.shape[0]
    q = q_ref[...]
    qclip = qclip_ref[...]
    keys = (k0_ref, k1_ref, k2_ref, k3_ref)
    values = (v0_ref, v1_ref, v2_ref, v3_ref)
    clips = (kc0_ref, kc1_ref, kc2_ref, kc3_ref)
    qpos = pl.program_id(1) * tile + lax.broadcasted_iota(jnp.int32, (tile, seg), 0)
    kpos = lax.broadcasted_iota(jnp.int32, (tile, seg), 1)
    last = len(keys) - 1
    scores = []
    masks = []
    for j in range(len(keys)):
        allowed = clips[j][...] == qclip
        if j == last:
            allowed = allowed & (kpos <= qpos)
        s = lax.dot_general(q, keys[j][...], (((1,), (1,)), ((), ())),
                            preferred_element_type=jnp.float32) * scale
        scores.append(jnp.where(allowed, s, -1e30))
    top = jnp.max(scores[0], axis=1, keepdims=True)
    for j in range(1, len(keys)):
        top = jnp.maximum(top, jnp.max(scores[j], axis=1, keepdims=True))
    total = None
    summed = None
    for j in range(len(keys)):
        w = jnp.exp(scores[j] - top)
        part = jnp.sum(w, axis=1, keepdims=True)
        pv = jnp.dot(w.astype(jnp.bfloat16), values[j][...], preferred_element_type=jnp.float32)
        total = part if total is None else total + part
        summed = pv if summed is None else summed + pv
    out_ref[...] = (summed / total).astype(out_ref.dtype)


def coarse_attention(queries, windows, qclip, kclip, heads):
    rows, width = queries.shape
    head_dim = width // heads
    tile = min(FINE_TILE, rows)
    seg = windows[0].shape[1]
    kernel = functools.partial(coarse_kernel, scale=1.0 / math.sqrt(head_dim))
    clip_specs = [pl.BlockSpec((1, seg), functools.partial(lambda j, h, i: (0, j), j))
                  for j in range(len(windows))]
    kv_specs = []
    kv_args = []
    for window in windows:
        kv_specs.append(pl.BlockSpec((None, seg, head_dim), lambda h, i: (0, 0, h)))
        kv_specs.append(pl.BlockSpec((None, seg, head_dim), lambda h, i: (1, 0, h)))
        kv_args += [window, window]
    return pl.pallas_call(
        kernel,
        grid=(heads, rows // tile),
        in_specs=[pl.BlockSpec((tile, 1), lambda h, i: (i, 0))] + clip_specs
        + [pl.BlockSpec((tile, head_dim), lambda h, i: (i, h))] + kv_specs,
        out_specs=pl.BlockSpec((tile, head_dim), lambda h, i: (i, h)),
        out_shape=jax.ShapeDtypeStruct((rows, width), jnp.bfloat16),
    )(qclip, *([kclip] * len(windows)), queries, *kv_args)


def group_order(parts, quarter):
    ordered = jnp.stack([parts[0]] + parts[:0:-1], axis=0)
    return jnp.roll(ordered, quarter, axis=0)


def attend(queries, key_rows, value_rows, allowed, heads, head_groups):
    row_count = queries.shape[0]
    feat_width = queries.shape[1]
    head_dim = feat_width // heads
    per_group = heads // head_groups
    score_scale = 1.0 / math.sqrt(head_dim)

    def split_heads(source_rows):
        return source_rows.reshape(
            source_rows.shape[0], head_groups, per_group, head_dim
        ).transpose(1, 0, 2, 3)

    def one_group(operands):
        group_queries, group_keys, group_values = operands
        scores = (
            jnp.einsum(
                "rhd,khd->hrk", group_queries, group_keys, preferred_element_type=jnp.float32
            )
            * score_scale
        )
        masked = jnp.where(allowed[None], scores, -1e30)
        row_top = jnp.max(masked, axis=2, keepdims=True)
        weights = jnp.where(allowed[None], jnp.exp(masked - row_top), 0.0)
        row_total = jnp.sum(weights, axis=2)
        summed = jnp.einsum(
            "hrk,khd->rhd",
            weights.astype(jnp.bfloat16),
            group_values,
            preferred_element_type=jnp.float32,
        )
        return summed / jnp.transpose(row_total)[:, :, None]

    results = lax.map(
        one_group, (split_heads(queries), split_heads(key_rows), split_heads(value_rows))
    )
    return results.transpose(1, 0, 2, 3).reshape(row_count, feat_width).astype(jnp.bfloat16)


def body(fine_qkv, clip_ids, w_coarse, w_out):
    tok_count = fine_qkv.shape[0]
    feat_width = fine_qkv.shape[2]
    coarse_rows = tok_count // POOL
    group_rows = QUARTERS * coarse_rows
    position = lax.axis_index("seq")
    quarter = position % QUARTERS
    cycle_place = position // QUARTERS
    planes = jnp.transpose(fine_qkv, (1, 0, 2))
    clip_front = jnp.concatenate([jnp.full((FREACH * coarse_rows,), -1, jnp.int32), clip_ids])
    key_clip = jnp.repeat(
        lax.dynamic_slice_in_dim(clip_front, position * coarse_rows, (FREACH + 1) * coarse_rows, 0),
        POOL,
    )
    own_clip = lax.dynamic_slice_in_dim(clip_ids, position * coarse_rows, coarse_rows, 0)
    query_clip = jnp.repeat(own_clip, POOL)
    head_pair_width = 2 * feat_width // FHEADS
    part_width = feat_width // HALVES
    outs = []
    projected = None
    wplanes = jnp.transpose(w_coarse, (1, 0, 2))
    gate = None
    for part in range(HALVES):
        own_pairs = planes[1:, :, part * part_width:(part + 1) * part_width]
        if gate is not None:
            own_pairs, _ = lax.optimization_barrier((own_pairs, gate))
        prev0 = passed_along(own_pairs, "seq", 2)
        gate = prev0
        if outs:
            prev0, _ = lax.optimization_barrier((prev0, projected))
        prev1a = pair_swap(own_pairs, "seq", False)
        prev1b = pair_swap(prev0, "seq", True)
        part_out, part_pool = fine_attention(
            planes, prev0, prev1a, prev1b, query_clip.reshape(tok_count, 1),
            key_clip.reshape(1, (FREACH + 1) * tok_count), FHEADS,
            part * part_width // head_pair_width,
        )
        outs.append(part_out)
        part_weight = wplanes[:, part * part_width:(part + 1) * part_width, :]
        contribution = jnp.einsum(
            "rd,mdc->mrc", part_pool, part_weight, preferred_element_type=jnp.float32
        )
        projected = contribution if projected is None else projected + contribution
    fine_out = jnp.concatenate(outs, axis=1)
    quarter_width = w_coarse.shape[2] // QUARTERS
    projected = projected.astype(jnp.bfloat16)
    pieces = []
    for shift in range(QUARTERS):
        piece = lax.dynamic_slice_in_dim(
            projected, ((quarter + shift) % QUARTERS) * quarter_width, quarter_width, 2
        )
        pieces.append(piece if shift == 0 else within_group(piece, "seq", shift))
    grouped = group_order(pieces, quarter)
    grouped = jnp.transpose(grouped, (1, 0, 2, 3)).reshape(3, group_rows, quarter_width)
    coarse_queries = grouped[0]
    coarse_pairs = grouped[1:]
    one_back = passed_along(coarse_pairs, "seq", QUARTERS)
    two_back = passed_along(one_back, "seq", QUARTERS)
    three_back = passed_along(two_back, "seq", QUARTERS)
    earlier = [three_back, two_back, one_back]
    clip_back = jnp.concatenate([jnp.full((CREACH * group_rows,), -1, jnp.int32), clip_ids])
    coarse_key_clip = lax.dynamic_slice_in_dim(
        clip_back, cycle_place * group_rows, (CREACH + 1) * group_rows, 0
    )
    coarse_query_clip = lax.dynamic_slice_in_dim(clip_ids, cycle_place * group_rows, group_rows, 0)
    coarse_att = coarse_attention(
        coarse_queries, earlier + [coarse_pairs], coarse_query_clip.reshape(group_rows, 1),
        coarse_key_clip.reshape(1, (CREACH + 1) * group_rows), CHEADS // QUARTERS,
    )
    shares = []
    for shift in range(QUARTERS):
        share = lax.dynamic_slice_in_dim(
            coarse_att, ((quarter + shift) % QUARTERS) * coarse_rows, coarse_rows, 0
        )
        shares.append(share if shift == 0 else within_group(share, "seq", shift))
    att_rows = jnp.transpose(group_order(shares, quarter), (1, 0, 2)).reshape(
        coarse_rows, QUARTERS * quarter_width
    )
    coarse_up = jnp.dot(att_rows, w_out, preferred_element_type=jnp.float32).astype(jnp.bfloat16)
    carried = passed_along(coarse_up[-1:], "seq", 1)
    previous = jnp.concatenate([jnp.zeros_like(carried), coarse_up[:-1]], axis=0)
    clip_before = jnp.concatenate([jnp.full((1,), -1, jnp.int32), clip_ids])
    prev_clip = lax.dynamic_slice_in_dim(clip_before, position * coarse_rows, coarse_rows, 0)
    joined = prev_clip == own_clip
    lifted = jnp.where(joined[:, None], previous, jnp.zeros_like(previous))
    mixed = mix(fine_out, lifted)
    head_lift = jnp.where(joined[:1, None], carried, jnp.zeros_like(carried)).astype(jnp.float32)
    head_rows = (fine_out[:POOL].astype(jnp.float32) + head_lift).astype(mixed.dtype)
    return lax.dynamic_update_slice(mixed, head_rows, (0, 0))


def solution(mesh):
    return jax.shard_map(
        body,
        mesh=mesh,
        in_specs=(P(("groups", "seq"), None, None), P("groups"), P(), P()),
        out_specs=P(("groups", "seq"), None),
        check_vma=False,
    )
```

```python
import functools
import math

import jax
import jax.numpy as jnp
from jax import lax
from jax.experimental import pallas as pl
from jax.experimental.pallas import tpu as pltpu
from jax.sharding import PartitionSpec as P

FHEADS = 16
CHEADS = 8
POOL = 4
QUARTERS = 4
FREACH = 2
CREACH = 3
FINE_TILE = 256
HALVES = 2


def passed_along(value, axis, steps):
    count = lax.axis_size(axis)
    first, last = (max(0, -steps), min(count, count - steps))
    return lax.ppermute(value, axis, [(source, source + steps) for source in range(first, last)])


def within_group(value, axis, shift):
    count = lax.axis_size(axis)
    pairs = []
    for source in range(count):
        base = source - source % QUARTERS
        pairs.append((source, base + (source % QUARTERS + shift) % QUARTERS))
    return lax.ppermute(value, axis, pairs)


def fine_kernel(qclip_ref, kclip0_ref, kclip1_ref, kclip2_ref, q_ref,
                k0_ref, v0_ref, k1_ref, v1_ref, k1b_ref, v1b_ref, k2_ref, v2_ref,
                out_ref, pool_ref, bias_ref, *, scale):
    tile = q_ref.shape[0]
    width = q_ref.shape[1]
    half = width // 2
    seg = k0_ref.shape[0]
    tile_index = pl.program_id(0)

    @pl.when(pl.program_id(1) == 0)
    def _():
        qclip = qclip_ref[...]
        qpos = tile_index * tile + lax.broadcasted_iota(jnp.int32, (tile, seg), 0)
        kpos = lax.broadcasted_iota(jnp.int32, (tile, seg), 1)
        allowed = (
            kclip0_ref[...] == qclip,
            kclip1_ref[...] == qclip,
            (kclip2_ref[...] == qclip) & (kpos <= qpos),
        )
        for j in range(3):
            bias_ref[:, j * seg:(j + 1) * seg] = jnp.where(allowed[j], 0.0, -1e30)

    q = q_ref[...] * jnp.asarray(scale, q_ref.dtype)
    lane = lax.broadcasted_iota(jnp.int32, (1, width), 1)
    low = lane < half
    zero = jnp.zeros_like(q)
    head_q = (jnp.where(low, q, zero), jnp.where(low, zero, q))

    def run(step):
        own = (step + 1) * tile
        keys = (k0_ref[...], k1_ref[...] + k1b_ref[...], k2_ref[0:own, :])
        values = (v0_ref[...], v1_ref[...] + v1b_ref[...], v2_ref[0:own, :])
        spans = ((0, seg), (seg, seg), (2 * seg, own))
        results = []
        for h in range(2):
            scores = []
            for j in range(3):
                s = lax.dot_general(head_q[h], keys[j], (((1,), (1,)), ((), ())),
                                    preferred_element_type=jnp.float32)
                start, length = spans[j]
                scores.append(s + bias_ref[:, start:start + length])
            top = jnp.max(scores[0], axis=1, keepdims=True)
            for j in range(1, 3):
                top = jnp.maximum(top, jnp.max(scores[j], axis=1, keepdims=True))
            total = None
            summed = None
            for j in range(3):
                w = jnp.exp(scores[j] - top)
                part = jnp.sum(w, axis=1, keepdims=True)
                pv = jnp.dot(w.astype(jnp.bfloat16), values[j], preferred_element_type=jnp.float32)
                total = part if total is None else total + part
                summed = pv if summed is None else summed + pv
            results.append(summed / total)
        out = jnp.where(low, results[0], results[1]).astype(out_ref.dtype)
        out_ref[...] = out
        rows = tile // POOL
        pool_row = lax.broadcasted_iota(jnp.int32, (rows, tile), 0)
        pool_col = lax.broadcasted_iota(jnp.int32, (rows, tile), 1)
        pool_mat = jnp.where(pool_col // POOL == pool_row, 1.0 / POOL, 0.0).astype(jnp.bfloat16)
        pool_ref[...] = jnp.dot(pool_mat, out, preferred_element_type=jnp.float32).astype(
            pool_ref.dtype)

    for step in range(seg // tile):
        pl.when(tile_index == step)(functools.partial(run, step))


def fine_attention(planes, prev0, prev1a, prev1b, qclip, kclip, heads, first_pair):
    _, tok, width = planes.shape
    head_dim = width // heads
    pair = 2 * head_dim
    pairs = prev0.shape[2] // pair
    tile = min(FINE_TILE, tok)
    nq = tok // tile
    kernel = functools.partial(fine_kernel, scale=1.0 / math.sqrt(head_dim))

    def plane_spec(plane):
        return pl.BlockSpec((None, tok, pair), lambda i, h: (plane, 0, h))

    def own_spec(plane):
        return pl.BlockSpec((None, tok, pair), lambda i, h: (plane, 0, first_pair + h))

    return pl.pallas_call(
        kernel,
        grid=(nq, pairs),
        in_specs=[
            pl.BlockSpec((tile, 1), lambda i, h: (i, 0)),
            pl.BlockSpec((1, tok), lambda i, h: (0, 0)),
            pl.BlockSpec((1, tok), lambda i, h: (0, 1)),
            pl.BlockSpec((1, tok), lambda i, h: (0, 2)),
            pl.BlockSpec((None, tile, pair), lambda i, h: (0, i, first_pair + h)),
            plane_spec(0), plane_spec(1),
            plane_spec(0), plane_spec(1),
            plane_spec(0), plane_spec(1),
            own_spec(1), own_spec(2),
        ],
        out_specs=[
            pl.BlockSpec((tile, pair), lambda i, h: (i, h)),
            pl.BlockSpec((tile // POOL, pair), lambda i, h: (i, h)),
        ],
        out_shape=[
            jax.ShapeDtypeStruct((tok, pairs * pair), jnp.bfloat16),
            jax.ShapeDtypeStruct((tok // POOL, pairs * pair), jnp.bfloat16),
        ],
        scratch_shapes=[pltpu.VMEM((tile, 3 * tok), jnp.float32)],
    )(qclip, kclip, kclip, kclip, planes, prev0, prev0, prev1a, prev1a, prev1b, prev1b,
      planes, planes)


def mix_kernel(fine_ref, lift_ref, out_ref):
    tile = fine_ref.shape[0]
    rows = lift_ref.shape[0]
    spread_row = lax.broadcasted_iota(jnp.int32, (tile, rows), 0)
    spread_col = lax.broadcasted_iota(jnp.int32, (tile, rows), 1)
    spread = jnp.where(spread_row // POOL == spread_col, 1.0, 0.0).astype(jnp.bfloat16)
    lifted = jnp.dot(spread, lift_ref[...], preferred_element_type=jnp.float32)
    out_ref[...] = (fine_ref[...].astype(jnp.float32) + lifted).astype(out_ref.dtype)


def mix(fine_out, lifted):
    tok, width = fine_out.shape
    tile = min(FINE_TILE, tok)
    return pl.pallas_call(
        mix_kernel,
        grid=(tok // tile,),
        in_specs=[
            pl.BlockSpec((tile, width), lambda i: (i, 0)),
            pl.BlockSpec((tile // POOL, width), lambda i: (i, 0)),
        ],
        out_specs=pl.BlockSpec((tile, width), lambda i: (i, 0)),
        out_shape=jax.ShapeDtypeStruct((tok, width), fine_out.dtype),
    )(fine_out, lifted)


def pair_swap(value, axis, from_odd):
    count = lax.axis_size(axis)
    start = 1 if from_odd else 0
    step = -1 if from_odd else 1
    return lax.ppermute(value, axis, [(source, source + step) for source in range(start, count, 2)])


def coarse_kernel(qclip_ref, kc0_ref, kc1_ref, kc2_ref, kc3_ref, q_ref,
                  k0_ref, v0_ref, k1_ref, v1_ref, k2_ref, v2_ref, k3_ref, v3_ref,
                  out_ref, *, scale):
    tile = q_ref.shape[0]
    seg = k0_ref.shape[0]
    q = q_ref[...]
    qclip = qclip_ref[...]
    keys = (k0_ref, k1_ref, k2_ref, k3_ref)
    values = (v0_ref, v1_ref, v2_ref, v3_ref)
    clips = (kc0_ref, kc1_ref, kc2_ref, kc3_ref)
    qpos = pl.program_id(1) * tile + lax.broadcasted_iota(jnp.int32, (tile, seg), 0)
    kpos = lax.broadcasted_iota(jnp.int32, (tile, seg), 1)
    last = len(keys) - 1
    scores = []
    masks = []
    for j in range(len(keys)):
        allowed = clips[j][...] == qclip
        if j == last:
            allowed = allowed & (kpos <= qpos)
        s = lax.dot_general(q, keys[j][...], (((1,), (1,)), ((), ())),
                            preferred_element_type=jnp.float32) * scale
        scores.append(jnp.where(allowed, s, -1e30))
    top = jnp.max(scores[0], axis=1, keepdims=True)
    for j in range(1, len(keys)):
        top = jnp.maximum(top, jnp.max(scores[j], axis=1, keepdims=True))
    total = None
    summed = None
    for j in range(len(keys)):
        w = jnp.exp(scores[j] - top)
        part = jnp.sum(w, axis=1, keepdims=True)
        pv = jnp.dot(w.astype(jnp.bfloat16), values[j][...], preferred_element_type=jnp.float32)
        total = part if total is None else total + part
        summed = pv if summed is None else summed + pv
    out_ref[...] = (summed / total).astype(out_ref.dtype)


def coarse_attention(queries, windows, qclip, kclip, heads):
    rows, width = queries.shape
    head_dim = width // heads
    tile = min(FINE_TILE, rows)
    seg = windows[0].shape[1]
    kernel = functools.partial(coarse_kernel, scale=1.0 / math.sqrt(head_dim))
    clip_specs = [pl.BlockSpec((1, seg), functools.partial(lambda j, h, i: (0, j), j))
                  for j in range(len(windows))]
    kv_specs = []
    kv_args = []
    for window in windows:
        kv_specs.append(pl.BlockSpec((None, seg, head_dim), lambda h, i: (0, 0, h)))
        kv_specs.append(pl.BlockSpec((None, seg, head_dim), lambda h, i: (1, 0, h)))
        kv_args += [window, window]
    return pl.pallas_call(
        kernel,
        grid=(heads, rows // tile),
        in_specs=[pl.BlockSpec((tile, 1), lambda h, i: (i, 0))] + clip_specs
        + [pl.BlockSpec((tile, head_dim), lambda h, i: (i, h))] + kv_specs,
        out_specs=pl.BlockSpec((tile, head_dim), lambda h, i: (i, h)),
        out_shape=jax.ShapeDtypeStruct((rows, width), jnp.bfloat16),
    )(qclip, *([kclip] * len(windows)), queries, *kv_args)


def group_order(parts, quarter):
    ordered = jnp.stack([parts[0]] + parts[:0:-1], axis=0)
    return jnp.roll(ordered, quarter, axis=0)


def attend(queries, key_rows, value_rows, allowed, heads, head_groups):
    row_count = queries.shape[0]
    feat_width = queries.shape[1]
    head_dim = feat_width // heads
    per_group = heads // head_groups
    score_scale = 1.0 / math.sqrt(head_dim)

    def split_heads(source_rows):
        return source_rows.reshape(
            source_rows.shape[0], head_groups, per_group, head_dim
        ).transpose(1, 0, 2, 3)

    def one_group(operands):
        group_queries, group_keys, group_values = operands
        scores = (
            jnp.einsum(
                "rhd,khd->hrk", group_queries, group_keys, preferred_element_type=jnp.float32
            )
            * score_scale
        )
        masked = jnp.where(allowed[None], scores, -1e30)
        row_top = jnp.max(masked, axis=2, keepdims=True)
        weights = jnp.where(allowed[None], jnp.exp(masked - row_top), 0.0)
        row_total = jnp.sum(weights, axis=2)
        summed = jnp.einsum(
            "hrk,khd->rhd",
            weights.astype(jnp.bfloat16),
            group_values,
            preferred_element_type=jnp.float32,
        )
        return summed / jnp.transpose(row_total)[:, :, None]

    results = lax.map(
        one_group, (split_heads(queries), split_heads(key_rows), split_heads(value_rows))
    )
    return results.transpose(1, 0, 2, 3).reshape(row_count, feat_width).astype(jnp.bfloat16)


def body(fine_qkv, clip_ids, w_coarse, w_out):
    tok_count = fine_qkv.shape[0]
    feat_width = fine_qkv.shape[2]
    coarse_rows = tok_count // POOL
    group_rows = QUARTERS * coarse_rows
    position = lax.axis_index("seq")
    quarter = position % QUARTERS
    cycle_place = position // QUARTERS
    planes = jnp.transpose(fine_qkv, (1, 0, 2))
    clip_front = jnp.concatenate([jnp.full((FREACH * coarse_rows,), -1, jnp.int32), clip_ids])
    key_clip = jnp.repeat(
        lax.dynamic_slice_in_dim(clip_front, position * coarse_rows, (FREACH + 1) * coarse_rows, 0),
        POOL,
    )
    own_clip = lax.dynamic_slice_in_dim(clip_ids, position * coarse_rows, coarse_rows, 0)
    query_clip = jnp.repeat(own_clip, POOL)
    head_pair_width = 2 * feat_width // FHEADS
    part_width = feat_width // HALVES
    outs = []
    projected = None
    wplanes = jnp.transpose(w_coarse, (1, 0, 2))
    gate = None
    for part in range(HALVES):
        own_pairs = planes[1:, :, part * part_width:(part + 1) * part_width]
        if gate is not None:
            own_pairs, _ = lax.optimization_barrier((own_pairs, gate))
        prev0 = passed_along(own_pairs, "seq", 2)
        gate = prev0
        if outs:
            prev0, _ = lax.optimization_barrier((prev0, projected))
        prev1a = pair_swap(own_pairs, "seq", False)
        prev1b = pair_swap(prev0, "seq", True)
        part_out, part_pool = fine_attention(
            planes, prev0, prev1a, prev1b, query_clip.reshape(tok_count, 1),
            key_clip.reshape(1, (FREACH + 1) * tok_count), FHEADS,
            part * part_width // head_pair_width,
        )
        outs.append(part_out)
        part_weight = wplanes[:, part * part_width:(part + 1) * part_width, :]
        contribution = jnp.einsum(
            "rd,mdc->mrc", part_pool, part_weight, preferred_element_type=jnp.float32
        )
        projected = contribution if projected is None else projected + contribution
    fine_out = jnp.concatenate(outs, axis=1)
    quarter_width = w_coarse.shape[2] // QUARTERS
    projected = projected.astype(jnp.bfloat16)
    pieces = []
    pieces_kv = []
    for shift in range(QUARTERS):
        piece = lax.dynamic_slice_in_dim(
            projected, ((quarter + shift) % QUARTERS) * quarter_width, quarter_width, 2
        )
        pieces_kv.append(piece[1:])
        pieces.append(piece if shift == 0 else within_group(piece, "seq", shift))
    grouped = group_order(pieces, quarter)
    grouped = jnp.transpose(grouped, (1, 0, 2, 3)).reshape(3, group_rows, quarter_width)
    coarse_queries = grouped[0]
    coarse_pairs = grouped[1:]
    seq_count = lax.axis_size("seq")
    forward = []
    for shift in range(QUARTERS):
        pairs = [
            (source, source - source % QUARTERS + QUARTERS + (source + shift) % QUARTERS)
            for source in range(seq_count - QUARTERS)
        ]
        forward.append(lax.ppermute(pieces_kv[shift], "seq", pairs))
    one_back = jnp.transpose(group_order(forward, quarter), (1, 0, 2, 3)).reshape(
        2, group_rows, quarter_width
    )
    two_back = passed_along(one_back, "seq", QUARTERS)
    three_back = passed_along(two_back, "seq", QUARTERS)
    earlier = [three_back, two_back, one_back]
    clip_back = jnp.concatenate([jnp.full((CREACH * group_rows,), -1, jnp.int32), clip_ids])
    coarse_key_clip = lax.dynamic_slice_in_dim(
        clip_back, cycle_place * group_rows, (CREACH + 1) * group_rows, 0
    )
    coarse_query_clip = lax.dynamic_slice_in_dim(clip_ids, cycle_place * group_rows, group_rows, 0)
    coarse_att = coarse_attention(
        coarse_queries, earlier + [coarse_pairs], coarse_query_clip.reshape(group_rows, 1),
        coarse_key_clip.reshape(1, (CREACH + 1) * group_rows), CHEADS // QUARTERS,
    )
    shares = []
    for shift in range(QUARTERS):
        share = lax.dynamic_slice_in_dim(
            coarse_att, ((quarter + shift) % QUARTERS) * coarse_rows, coarse_rows, 0
        )
        shares.append(share if shift == 0 else within_group(share, "seq", shift))
    att_rows = jnp.transpose(group_order(shares, quarter), (1, 0, 2)).reshape(
        coarse_rows, QUARTERS * quarter_width
    )
    coarse_up = jnp.dot(att_rows, w_out, preferred_element_type=jnp.float32).astype(jnp.bfloat16)
    carried = passed_along(coarse_up[-1:], "seq", 1)
    previous = jnp.concatenate([jnp.zeros_like(carried), coarse_up[:-1]], axis=0)
    clip_before = jnp.concatenate([jnp.full((1,), -1, jnp.int32), clip_ids])
    prev_clip = lax.dynamic_slice_in_dim(clip_before, position * coarse_rows, coarse_rows, 0)
    joined = prev_clip == own_clip
    lifted = jnp.where(joined[:, None], previous, jnp.zeros_like(previous))
    mixed = mix(fine_out, lifted)
    head_lift = jnp.where(joined[:1, None], carried, jnp.zeros_like(carried)).astype(jnp.float32)
    head_rows = (fine_out[:POOL].astype(jnp.float32) + head_lift).astype(mixed.dtype)
    return lax.dynamic_update_slice(mixed, head_rows, (0, 0))


def solution(mesh):
    return jax.shard_map(
        body,
        mesh=mesh,
        in_specs=(P(("groups", "seq"), None, None), P("groups"), P(), P()),
        out_specs=P(("groups", "seq"), None),
        check_vma=False,
    )
```

```python
import functools
import math

import jax
import jax.numpy as jnp
from jax import lax
from jax.experimental import pallas as pl
from jax.experimental.pallas import tpu as pltpu
from jax.sharding import PartitionSpec as P

FHEADS = 16
CHEADS = 8
POOL = 4
QUARTERS = 4
FREACH = 2
CREACH = 3
FINE_TILE = 256
HALVES = 2


def passed_along(value, axis, steps):
    count = lax.axis_size(axis)
    first, last = (max(0, -steps), min(count, count - steps))
    return lax.ppermute(value, axis, [(source, source + steps) for source in range(first, last)])


def within_group(value, axis, shift):
    count = lax.axis_size(axis)
    pairs = []
    for source in range(count):
        base = source - source % QUARTERS
        pairs.append((source, base + (source % QUARTERS + shift) % QUARTERS))
    return lax.ppermute(value, axis, pairs)


def fine_kernel(qclip_ref, kclip0_ref, kclip1_ref, kclip2_ref, q_ref,
                k0_ref, v0_ref, k1_ref, v1_ref, k1b_ref, v1b_ref, k2_ref, v2_ref,
                out_ref, pool_ref, bias_ref, *, scale):
    tile = q_ref.shape[0]
    width = q_ref.shape[1]
    half = width // 2
    seg = k0_ref.shape[0]
    tile_index = pl.program_id(0)

    @pl.when(pl.program_id(1) == 0)
    def _():
        qclip = qclip_ref[...]
        qpos = tile_index * tile + lax.broadcasted_iota(jnp.int32, (tile, seg), 0)
        kpos = lax.broadcasted_iota(jnp.int32, (tile, seg), 1)
        allowed = (
            kclip0_ref[...] == qclip,
            kclip1_ref[...] == qclip,
            (kclip2_ref[...] == qclip) & (kpos <= qpos),
        )
        for j in range(3):
            bias_ref[:, j * seg:(j + 1) * seg] = jnp.where(allowed[j], 0.0, -1e30)

    q = q_ref[...] * jnp.asarray(scale, q_ref.dtype)
    lane = lax.broadcasted_iota(jnp.int32, (1, width), 1)
    low = lane < half
    zero = jnp.zeros_like(q)
    head_q = (jnp.where(low, q, zero), jnp.where(low, zero, q))

    def run(step):
        own = (step + 1) * tile
        keys = (k0_ref[...], k1_ref[...] + k1b_ref[...], k2_ref[0:own, :])
        values = (v0_ref[...], v1_ref[...] + v1b_ref[...], v2_ref[0:own, :])
        spans = ((0, seg), (seg, seg), (2 * seg, own))
        results = []
        for h in range(2):
            scores = []
            for j in range(3):
                s = lax.dot_general(head_q[h], keys[j], (((1,), (1,)), ((), ())),
                                    preferred_element_type=jnp.float32)
                start, length = spans[j]
                scores.append(s + bias_ref[:, start:start + length])
            top = jnp.max(scores[0], axis=1, keepdims=True)
            for j in range(1, 3):
                top = jnp.maximum(top, jnp.max(scores[j], axis=1, keepdims=True))
            total = None
            summed = None
            for j in range(3):
                w = jnp.exp(scores[j] - top)
                part = jnp.sum(w, axis=1, keepdims=True)
                pv = jnp.dot(w.astype(jnp.bfloat16), values[j], preferred_element_type=jnp.float32)
                total = part if total is None else total + part
                summed = pv if summed is None else summed + pv
            results.append(summed / total)
        out = jnp.where(low, results[0], results[1]).astype(out_ref.dtype)
        out_ref[...] = out
        rows = tile // POOL
        pool_row = lax.broadcasted_iota(jnp.int32, (rows, tile), 0)
        pool_col = lax.broadcasted_iota(jnp.int32, (rows, tile), 1)
        pool_mat = jnp.where(pool_col // POOL == pool_row, 1.0 / POOL, 0.0).astype(jnp.bfloat16)
        pool_ref[...] = jnp.dot(pool_mat, out, preferred_element_type=jnp.float32).astype(
            pool_ref.dtype)

    for step in range(seg // tile):
        pl.when(tile_index == step)(functools.partial(run, step))


def fine_attention(planes, prev0, prev1a, prev1b, qclip, kclip, heads, first_pair):
    _, tok, width = planes.shape
    head_dim = width // heads
    pair = 2 * head_dim
    pairs = prev0.shape[2] // pair
    tile = min(FINE_TILE, tok)
    nq = tok // tile
    kernel = functools.partial(fine_kernel, scale=1.0 / math.sqrt(head_dim))

    def plane_spec(plane):
        return pl.BlockSpec((None, tok, pair), lambda i, h: (plane, 0, h))

    def own_spec(plane):
        return pl.BlockSpec((None, tok, pair), lambda i, h: (plane, 0, first_pair + h))

    return pl.pallas_call(
        kernel,
        grid=(nq, pairs),
        in_specs=[
            pl.BlockSpec((tile, 1), lambda i, h: (i, 0)),
            pl.BlockSpec((1, tok), lambda i, h: (0, 0)),
            pl.BlockSpec((1, tok), lambda i, h: (0, 1)),
            pl.BlockSpec((1, tok), lambda i, h: (0, 2)),
            pl.BlockSpec((None, tile, pair), lambda i, h: (0, i, first_pair + h)),
            plane_spec(0), plane_spec(1),
            own_spec(1), own_spec(2),
            plane_spec(0), plane_spec(1),
            own_spec(1), own_spec(2),
        ],
        out_specs=[
            pl.BlockSpec((tile, pair), lambda i, h: (i, h)),
            pl.BlockSpec((tile // POOL, pair), lambda i, h: (i, h)),
        ],
        out_shape=[
            jax.ShapeDtypeStruct((tok, pairs * pair), jnp.bfloat16),
            jax.ShapeDtypeStruct((tok // POOL, pairs * pair), jnp.bfloat16),
        ],
        scratch_shapes=[pltpu.VMEM((tile, 3 * tok), jnp.float32)],
    )(qclip, kclip, kclip, kclip, planes, prev0, prev0, prev1a, prev1a, prev1b, prev1b,
      planes, planes)


def mix_kernel(fine_ref, lift_ref, out_ref):
    tile = fine_ref.shape[0]
    rows = lift_ref.shape[0]
    spread_row = lax.broadcasted_iota(jnp.int32, (tile, rows), 0)
    spread_col = lax.broadcasted_iota(jnp.int32, (tile, rows), 1)
    spread = jnp.where(spread_row // POOL == spread_col, 1.0, 0.0).astype(jnp.bfloat16)
    lifted = jnp.dot(spread, lift_ref[...], preferred_element_type=jnp.float32)
    out_ref[...] = (fine_ref[...].astype(jnp.float32) + lifted).astype(out_ref.dtype)


def mix(fine_out, lifted):
    tok, width = fine_out.shape
    tile = min(FINE_TILE, tok)
    return pl.pallas_call(
        mix_kernel,
        grid=(tok // tile,),
        in_specs=[
            pl.BlockSpec((tile, width), lambda i: (i, 0)),
            pl.BlockSpec((tile // POOL, width), lambda i: (i, 0)),
        ],
        out_specs=pl.BlockSpec((tile, width), lambda i: (i, 0)),
        out_shape=jax.ShapeDtypeStruct((tok, width), fine_out.dtype),
    )(fine_out, lifted)


def pair_swap(value, axis, from_odd):
    count = lax.axis_size(axis)
    start = 1 if from_odd else 0
    step = -1 if from_odd else 1
    return lax.ppermute(value, axis, [(source, source + step) for source in range(start, count, 2)])


def coarse_kernel(qclip_ref, kc0_ref, kc1_ref, kc2_ref, kc3_ref, q_ref,
                  k0_ref, v0_ref, k1_ref, v1_ref, k2_ref, v2_ref, k3_ref, v3_ref,
                  out_ref, *, scale):
    tile = q_ref.shape[0]
    seg = k0_ref.shape[0]
    q = q_ref[...]
    qclip = qclip_ref[...]
    keys = (k0_ref, k1_ref, k2_ref, k3_ref)
    values = (v0_ref, v1_ref, v2_ref, v3_ref)
    clips = (kc0_ref, kc1_ref, kc2_ref, kc3_ref)
    qpos = pl.program_id(1) * tile + lax.broadcasted_iota(jnp.int32, (tile, seg), 0)
    kpos = lax.broadcasted_iota(jnp.int32, (tile, seg), 1)
    last = len(keys) - 1
    scores = []
    masks = []
    for j in range(len(keys)):
        allowed = clips[j][...] == qclip
        if j == last:
            allowed = allowed & (kpos <= qpos)
        s = lax.dot_general(q, keys[j][...], (((1,), (1,)), ((), ())),
                            preferred_element_type=jnp.float32) * scale
        scores.append(jnp.where(allowed, s, -1e30))
    top = jnp.max(scores[0], axis=1, keepdims=True)
    for j in range(1, len(keys)):
        top = jnp.maximum(top, jnp.max(scores[j], axis=1, keepdims=True))
    total = None
    summed = None
    for j in range(len(keys)):
        w = jnp.exp(scores[j] - top)
        part = jnp.sum(w, axis=1, keepdims=True)
        pv = jnp.dot(w.astype(jnp.bfloat16), values[j][...], preferred_element_type=jnp.float32)
        total = part if total is None else total + part
        summed = pv if summed is None else summed + pv
    out_ref[...] = (summed / total).astype(out_ref.dtype)


def coarse_attention(queries, windows, qclip, kclip, heads):
    rows, width = queries.shape
    head_dim = width // heads
    tile = min(FINE_TILE, rows)
    seg = windows[0].shape[1]
    kernel = functools.partial(coarse_kernel, scale=1.0 / math.sqrt(head_dim))
    clip_specs = [pl.BlockSpec((1, seg), functools.partial(lambda j, h, i: (0, j), j))
                  for j in range(len(windows))]
    kv_specs = []
    kv_args = []
    for window in windows:
        kv_specs.append(pl.BlockSpec((None, seg, head_dim), lambda h, i: (0, 0, h)))
        kv_specs.append(pl.BlockSpec((None, seg, head_dim), lambda h, i: (1, 0, h)))
        kv_args += [window, window]
    return pl.pallas_call(
        kernel,
        grid=(heads, rows // tile),
        in_specs=[pl.BlockSpec((tile, 1), lambda h, i: (i, 0))] + clip_specs
        + [pl.BlockSpec((tile, head_dim), lambda h, i: (i, h))] + kv_specs,
        out_specs=pl.BlockSpec((tile, head_dim), lambda h, i: (i, h)),
        out_shape=jax.ShapeDtypeStruct((rows, width), jnp.bfloat16),
    )(qclip, *([kclip] * len(windows)), queries, *kv_args)


def group_order(parts, quarter):
    ordered = jnp.stack([parts[0]] + parts[:0:-1], axis=0)
    return jnp.roll(ordered, quarter, axis=0)


def attend(queries, key_rows, value_rows, allowed, heads, head_groups):
    row_count = queries.shape[0]
    feat_width = queries.shape[1]
    head_dim = feat_width // heads
    per_group = heads // head_groups
    score_scale = 1.0 / math.sqrt(head_dim)

    def split_heads(source_rows):
        return source_rows.reshape(
            source_rows.shape[0], head_groups, per_group, head_dim
        ).transpose(1, 0, 2, 3)

    def one_group(operands):
        group_queries, group_keys, group_values = operands
        scores = (
            jnp.einsum(
                "rhd,khd->hrk", group_queries, group_keys, preferred_element_type=jnp.float32
            )
            * score_scale
        )
        masked = jnp.where(allowed[None], scores, -1e30)
        row_top = jnp.max(masked, axis=2, keepdims=True)
        weights = jnp.where(allowed[None], jnp.exp(masked - row_top), 0.0)
        row_total = jnp.sum(weights, axis=2)
        summed = jnp.einsum(
            "hrk,khd->rhd",
            weights.astype(jnp.bfloat16),
            group_values,
            preferred_element_type=jnp.float32,
        )
        return summed / jnp.transpose(row_total)[:, :, None]

    results = lax.map(
        one_group, (split_heads(queries), split_heads(key_rows), split_heads(value_rows))
    )
    return results.transpose(1, 0, 2, 3).reshape(row_count, feat_width).astype(jnp.bfloat16)


def body(fine_qkv, clip_ids, w_coarse, w_out):
    tok_count = fine_qkv.shape[0]
    feat_width = fine_qkv.shape[2]
    coarse_rows = tok_count // POOL
    group_rows = QUARTERS * coarse_rows
    position = lax.axis_index("seq")
    quarter = position % QUARTERS
    cycle_place = position // QUARTERS
    planes = jnp.transpose(fine_qkv, (1, 0, 2))
    clip_front = jnp.concatenate([jnp.full((FREACH * coarse_rows,), -1, jnp.int32), clip_ids])
    key_clip = jnp.repeat(
        lax.dynamic_slice_in_dim(clip_front, position * coarse_rows, (FREACH + 1) * coarse_rows, 0),
        POOL,
    )
    own_clip = lax.dynamic_slice_in_dim(clip_ids, position * coarse_rows, coarse_rows, 0)
    query_clip = jnp.repeat(own_clip, POOL)
    head_pair_width = 2 * feat_width // FHEADS
    part_width = feat_width // HALVES
    outs = []
    projected = None
    wplanes = jnp.transpose(w_coarse, (1, 0, 2))
    gate = None
    prev1a = pair_swap(planes, "seq", False)
    for part in range(HALVES):
        own_pairs = planes[1:, :, part * part_width:(part + 1) * part_width]
        if gate is not None:
            own_pairs, _ = lax.optimization_barrier((own_pairs, gate))
        prev0 = passed_along(own_pairs, "seq", 2)
        gate = prev0
        if outs:
            prev0, _ = lax.optimization_barrier((prev0, projected))
        prev1b = pair_swap(prev0, "seq", True)
        part_out, part_pool = fine_attention(
            planes, prev0, prev1a, prev1b, query_clip.reshape(tok_count, 1),
            key_clip.reshape(1, (FREACH + 1) * tok_count), FHEADS,
            part * part_width // head_pair_width,
        )
        outs.append(part_out)
        part_weight = wplanes[:, part * part_width:(part + 1) * part_width, :]
        contribution = jnp.einsum(
            "rd,mdc->mrc", part_pool, part_weight, preferred_element_type=jnp.float32
        )
        projected = contribution if projected is None else projected + contribution
    fine_out = jnp.concatenate(outs, axis=1)
    quarter_width = w_coarse.shape[2] // QUARTERS
    projected = projected.astype(jnp.bfloat16)
    pieces = []
    for shift in range(QUARTERS):
        piece = lax.dynamic_slice_in_dim(
            projected, ((quarter + shift) % QUARTERS) * quarter_width, quarter_width, 2
        )
        pieces.append(piece if shift == 0 else within_group(piece, "seq", shift))
    grouped = group_order(pieces, quarter)
    grouped = jnp.transpose(grouped, (1, 0, 2, 3)).reshape(3, group_rows, quarter_width)
    coarse_queries = grouped[0]
    coarse_pairs = grouped[1:]
    one_back = passed_along(coarse_pairs, "seq", QUARTERS)
    two_back = passed_along(one_back, "seq", QUARTERS)
    three_back = passed_along(two_back, "seq", QUARTERS)
    earlier = [three_back, two_back, one_back]
    clip_back = jnp.concatenate([jnp.full((CREACH * group_rows,), -1, jnp.int32), clip_ids])
    coarse_key_clip = lax.dynamic_slice_in_dim(
        clip_back, cycle_place * group_rows, (CREACH + 1) * group_rows, 0
    )
    coarse_query_clip = lax.dynamic_slice_in_dim(clip_ids, cycle_place * group_rows, group_rows, 0)
    coarse_att = coarse_attention(
        coarse_queries, earlier + [coarse_pairs], coarse_query_clip.reshape(group_rows, 1),
        coarse_key_clip.reshape(1, (CREACH + 1) * group_rows), CHEADS // QUARTERS,
    )
    shares = []
    for shift in range(QUARTERS):
        share = lax.dynamic_slice_in_dim(
            coarse_att, ((quarter + shift) % QUARTERS) * coarse_rows, coarse_rows, 0
        )
        shares.append(share if shift == 0 else within_group(share, "seq", shift))
    att_rows = jnp.transpose(group_order(shares, quarter), (1, 0, 2)).reshape(
        coarse_rows, QUARTERS * quarter_width
    )
    coarse_up = jnp.dot(att_rows, w_out, preferred_element_type=jnp.float32).astype(jnp.bfloat16)
    carried = passed_along(coarse_up[-1:], "seq", 1)
    previous = jnp.concatenate([jnp.zeros_like(carried), coarse_up[:-1]], axis=0)
    clip_before = jnp.concatenate([jnp.full((1,), -1, jnp.int32), clip_ids])
    prev_clip = lax.dynamic_slice_in_dim(clip_before, position * coarse_rows, coarse_rows, 0)
    joined = prev_clip == own_clip
    lifted = jnp.where(joined[:, None], previous, jnp.zeros_like(previous))
    mixed = mix(fine_out, lifted)
    head_lift = jnp.where(joined[:1, None], carried, jnp.zeros_like(carried)).astype(jnp.float32)
    head_rows = (fine_out[:POOL].astype(jnp.float32) + head_lift).astype(mixed.dtype)
    return lax.dynamic_update_slice(mixed, head_rows, (0, 0))


def solution(mesh):
    return jax.shard_map(
        body,
        mesh=mesh,
        in_specs=(P(("groups", "seq"), None, None), P("groups"), P(), P()),
        out_specs=P(("groups", "seq"), None),
        check_vma=False,
    )
```

```python
import functools
import math

import jax
import jax.numpy as jnp
from jax import lax
from jax.experimental import pallas as pl
from jax.experimental.pallas import tpu as pltpu
from jax.sharding import PartitionSpec as P

FHEADS = 16
CHEADS = 8
POOL = 4
QUARTERS = 4
FREACH = 2
CREACH = 3
FINE_TILE = 256
HALVES = 2


def passed_along(value, axis, steps):
    count = lax.axis_size(axis)
    first, last = (max(0, -steps), min(count, count - steps))
    return lax.ppermute(value, axis, [(source, source + steps) for source in range(first, last)])


def within_group(value, axis, shift):
    count = lax.axis_size(axis)
    pairs = []
    for source in range(count):
        base = source - source % QUARTERS
        pairs.append((source, base + (source % QUARTERS + shift) % QUARTERS))
    return lax.ppermute(value, axis, pairs)


def fine_kernel(qclip_ref, kclip0_ref, kclip1_ref, kclip2_ref, q_ref,
                k0_ref, v0_ref, k1_ref, v1_ref, k1b_ref, v1b_ref, k2_ref, v2_ref,
                out_ref, pool_ref, bias_ref, *, scale):
    tile = q_ref.shape[0]
    width = q_ref.shape[1]
    half = width // 2
    seg = k0_ref.shape[0]
    tile_index = pl.program_id(0)

    @pl.when(pl.program_id(1) == 0)
    def _():
        qclip = qclip_ref[...]
        qpos = tile_index * tile + lax.broadcasted_iota(jnp.int32, (tile, seg), 0)
        kpos = lax.broadcasted_iota(jnp.int32, (tile, seg), 1)
        allowed = (
            kclip0_ref[...] == qclip,
            kclip1_ref[...] == qclip,
            (kclip2_ref[...] == qclip) & (kpos <= qpos),
        )
        for j in range(3):
            bias_ref[:, j * seg:(j + 1) * seg] = jnp.where(allowed[j], 0.0, -1e30)

    q = q_ref[...] * jnp.asarray(scale, q_ref.dtype)
    lane = lax.broadcasted_iota(jnp.int32, (1, width), 1)
    low = lane < half
    zero = jnp.zeros_like(q)
    head_q = (jnp.where(low, q, zero), jnp.where(low, zero, q))

    def run(step):
        own = (step + 1) * tile
        keys = (k0_ref[...], k1_ref[...] + k1b_ref[...], k2_ref[0:own, :])
        values = (v0_ref[...], v1_ref[...] + v1b_ref[...], v2_ref[0:own, :])
        spans = ((0, seg), (seg, seg), (2 * seg, own))
        results = []
        for h in range(2):
            scores = []
            for j in range(3):
                s = lax.dot_general(head_q[h], keys[j], (((1,), (1,)), ((), ())),
                                    preferred_element_type=jnp.float32)
                start, length = spans[j]
                scores.append(s + bias_ref[:, start:start + length])
            top = jnp.max(scores[0], axis=1, keepdims=True)
            for j in range(1, 3):
                top = jnp.maximum(top, jnp.max(scores[j], axis=1, keepdims=True))
            total = None
            summed = None
            for j in range(3):
                w = jnp.exp(scores[j] - top)
                part = jnp.sum(w, axis=1, keepdims=True)
                pv = jnp.dot(w.astype(jnp.bfloat16), values[j], preferred_element_type=jnp.float32)
                total = part if total is None else total + part
                summed = pv if summed is None else summed + pv
            results.append(summed / total)
        out = jnp.where(low, results[0], results[1]).astype(out_ref.dtype)
        out_ref[...] = out
        rows = tile // POOL
        pool_row = lax.broadcasted_iota(jnp.int32, (rows, tile), 0)
        pool_col = lax.broadcasted_iota(jnp.int32, (rows, tile), 1)
        pool_mat = jnp.where(pool_col // POOL == pool_row, 1.0 / POOL, 0.0).astype(jnp.bfloat16)
        pool_ref[...] = jnp.dot(pool_mat, out, preferred_element_type=jnp.float32).astype(
            pool_ref.dtype)

    for step in range(seg // tile):
        pl.when(tile_index == step)(functools.partial(run, step))


def fine_attention(planes, prev0, prev1a, prev1b, qclip, kclip, heads, first_pair):
    _, tok, width = planes.shape
    head_dim = width // heads
    pair = 2 * head_dim
    pairs = prev0.shape[2] // pair
    tile = min(FINE_TILE, tok)
    nq = tok // tile
    kernel = functools.partial(fine_kernel, scale=1.0 / math.sqrt(head_dim))

    def plane_spec(plane):
        return pl.BlockSpec((None, tok, pair), lambda i, h: (plane, 0, h))

    def own_spec(plane):
        return pl.BlockSpec((None, tok, pair), lambda i, h: (plane, 0, first_pair + h))

    return pl.pallas_call(
        kernel,
        grid=(nq, pairs),
        in_specs=[
            pl.BlockSpec((tile, 1), lambda i, h: (i, 0)),
            pl.BlockSpec((1, tok), lambda i, h: (0, 0)),
            pl.BlockSpec((1, tok), lambda i, h: (0, 1)),
            pl.BlockSpec((1, tok), lambda i, h: (0, 2)),
            pl.BlockSpec((None, tile, pair), lambda i, h: (0, i, first_pair + h)),
            plane_spec(0), plane_spec(1),
            own_spec(1), own_spec(2),
            plane_spec(0), plane_spec(1),
            own_spec(1), own_spec(2),
        ],
        out_specs=[
            pl.BlockSpec((tile, pair), lambda i, h: (i, h)),
            pl.BlockSpec((tile // POOL, pair), lambda i, h: (i, h)),
        ],
        out_shape=[
            jax.ShapeDtypeStruct((tok, pairs * pair), jnp.bfloat16),
            jax.ShapeDtypeStruct((tok // POOL, pairs * pair), jnp.bfloat16),
        ],
        scratch_shapes=[pltpu.VMEM((tile, 3 * tok), jnp.float32)],
    )(qclip, kclip, kclip, kclip, planes, prev0, prev0, prev1a, prev1a, prev1b, prev1b,
      planes, planes)


def mix_kernel(fine_ref, up_ref, join_ref, out_ref):
    tile = fine_ref.shape[0]
    rows = up_ref.shape[0]
    fine_row = pl.program_id(0) * tile + lax.broadcasted_iota(jnp.int32, (tile, rows), 0)
    spread_col = lax.broadcasted_iota(jnp.int32, (tile, rows), 1)
    hit = (spread_col == fine_row // POOL - 1) & (join_ref[...] != 0)
    spread = jnp.where(hit, 1.0, 0.0).astype(jnp.bfloat16)
    lifted = jnp.dot(spread, up_ref[...], preferred_element_type=jnp.float32)
    out_ref[...] = (fine_ref[...].astype(jnp.float32) + lifted).astype(out_ref.dtype)


def mix(fine_out, coarse_up, join_rows):
    tok, width = fine_out.shape
    tile = min(FINE_TILE, tok)
    return pl.pallas_call(
        mix_kernel,
        grid=(tok // tile,),
        in_specs=[
            pl.BlockSpec((tile, width), lambda i: (i, 0)),
            pl.BlockSpec(coarse_up.shape, lambda i: (0, 0)),
            pl.BlockSpec((tile, 1), lambda i: (i, 0)),
        ],
        out_specs=pl.BlockSpec((tile, width), lambda i: (i, 0)),
        out_shape=jax.ShapeDtypeStruct((tok, width), fine_out.dtype),
    )(fine_out, coarse_up, join_rows)


def patch_kernel(mixed_ref, fine_ref, lift_ref, out_ref):
    rows = out_ref.shape[0]
    row = lax.broadcasted_iota(jnp.int32, (rows, 1), 0)
    head = (fine_ref[...].astype(jnp.float32) + lift_ref[...].astype(jnp.float32)).astype(out_ref.dtype)
    out_ref[...] = jnp.where(row < POOL, head, mixed_ref[...])


def patch(mixed, fine_out, head_lift):
    width = mixed.shape[1]
    rows = 16
    return pl.pallas_call(
        patch_kernel,
        grid=(1,),
        in_specs=[
            pl.BlockSpec((rows, width), lambda i: (0, 0)),
            pl.BlockSpec((rows, width), lambda i: (0, 0)),
            pl.BlockSpec((1, width), lambda i: (0, 0)),
        ],
        out_specs=pl.BlockSpec((rows, width), lambda i: (0, 0)),
        out_shape=jax.ShapeDtypeStruct(mixed.shape, mixed.dtype),
        input_output_aliases={0: 0},
    )(mixed, fine_out, head_lift)


def pair_swap(value, axis, from_odd):
    count = lax.axis_size(axis)
    start = 1 if from_odd else 0
    step = -1 if from_odd else 1
    return lax.ppermute(value, axis, [(source, source + step) for source in range(start, count, 2)])


def coarse_kernel(qclip_ref, kc0_ref, kc1_ref, kc2_ref, kc3_ref, q_ref,
                  k0_ref, v0_ref, k1_ref, v1_ref, k2_ref, v2_ref, k3_ref, v3_ref,
                  out_ref, *, scale):
    tile = q_ref.shape[0]
    seg = k0_ref.shape[0]
    q = q_ref[...]
    qclip = qclip_ref[...]
    keys = (k0_ref, k1_ref, k2_ref, k3_ref)
    values = (v0_ref, v1_ref, v2_ref, v3_ref)
    clips = (kc0_ref, kc1_ref, kc2_ref, kc3_ref)
    qpos = pl.program_id(1) * tile + lax.broadcasted_iota(jnp.int32, (tile, seg), 0)
    kpos = lax.broadcasted_iota(jnp.int32, (tile, seg), 1)
    last = len(keys) - 1
    scores = []
    masks = []
    for j in range(len(keys)):
        allowed = clips[j][...] == qclip
        if j == last:
            allowed = allowed & (kpos <= qpos)
        s = lax.dot_general(q, keys[j][...], (((1,), (1,)), ((), ())),
                            preferred_element_type=jnp.float32) * scale
        scores.append(jnp.where(allowed, s, -1e30))
    top = jnp.max(scores[0], axis=1, keepdims=True)
    for j in range(1, len(keys)):
        top = jnp.maximum(top, jnp.max(scores[j], axis=1, keepdims=True))
    total = None
    summed = None
    for j in range(len(keys)):
        w = jnp.exp(scores[j] - top)
        part = jnp.sum(w, axis=1, keepdims=True)
        pv = jnp.dot(w.astype(jnp.bfloat16), values[j][...], preferred_element_type=jnp.float32)
        total = part if total is None else total + part
        summed = pv if summed is None else summed + pv
    out_ref[...] = (summed / total).astype(out_ref.dtype)


def coarse_attention(queries, windows, qclip, kclip, heads):
    rows, width = queries.shape
    head_dim = width // heads
    tile = min(FINE_TILE, rows)
    seg = windows[0].shape[1]
    kernel = functools.partial(coarse_kernel, scale=1.0 / math.sqrt(head_dim))
    clip_specs = [pl.BlockSpec((1, seg), functools.partial(lambda j, h, i: (0, j), j))
                  for j in range(len(windows))]
    kv_specs = []
    kv_args = []
    for window in windows:
        kv_specs.append(pl.BlockSpec((None, seg, head_dim), lambda h, i: (0, 0, h)))
        kv_specs.append(pl.BlockSpec((None, seg, head_dim), lambda h, i: (1, 0, h)))
        kv_args += [window, window]
    return pl.pallas_call(
        kernel,
        grid=(heads, rows // tile),
        in_specs=[pl.BlockSpec((tile, 1), lambda h, i: (i, 0))] + clip_specs
        + [pl.BlockSpec((tile, head_dim), lambda h, i: (i, h))] + kv_specs,
        out_specs=pl.BlockSpec((tile, head_dim), lambda h, i: (i, h)),
        out_shape=jax.ShapeDtypeStruct((rows, width), jnp.bfloat16),
    )(qclip, *([kclip] * len(windows)), queries, *kv_args)


def group_order(parts, quarter):
    ordered = jnp.stack([parts[0]] + parts[:0:-1], axis=0)
    return jnp.roll(ordered, quarter, axis=0)


def attend(queries, key_rows, value_rows, allowed, heads, head_groups):
    row_count = queries.shape[0]
    feat_width = queries.shape[1]
    head_dim = feat_width // heads
    per_group = heads // head_groups
    score_scale = 1.0 / math.sqrt(head_dim)

    def split_heads(source_rows):
        return source_rows.reshape(
            source_rows.shape[0], head_groups, per_group, head_dim
        ).transpose(1, 0, 2, 3)

    def one_group(operands):
        group_queries, group_keys, group_values = operands
        scores = (
            jnp.einsum(
                "rhd,khd->hrk", group_queries, group_keys, preferred_element_type=jnp.float32
            )
            * score_scale
        )
        masked = jnp.where(allowed[None], scores, -1e30)
        row_top = jnp.max(masked, axis=2, keepdims=True)
        weights = jnp.where(allowed[None], jnp.exp(masked - row_top), 0.0)
        row_total = jnp.sum(weights, axis=2)
        summed = jnp.einsum(
            "hrk,khd->rhd",
            weights.astype(jnp.bfloat16),
            group_values,
            preferred_element_type=jnp.float32,
        )
        return summed / jnp.transpose(row_total)[:, :, None]

    results = lax.map(
        one_group, (split_heads(queries), split_heads(key_rows), split_heads(value_rows))
    )
    return results.transpose(1, 0, 2, 3).reshape(row_count, feat_width).astype(jnp.bfloat16)


def body(fine_qkv, clip_ids, w_coarse, w_out):
    tok_count = fine_qkv.shape[0]
    feat_width = fine_qkv.shape[2]
    coarse_rows = tok_count // POOL
    group_rows = QUARTERS * coarse_rows
    position = lax.axis_index("seq")
    quarter = position % QUARTERS
    cycle_place = position // QUARTERS
    planes = jnp.transpose(fine_qkv, (1, 0, 2))
    clip_front = jnp.concatenate([jnp.full((FREACH * coarse_rows,), -1, jnp.int32), clip_ids])
    key_clip = jnp.repeat(
        lax.dynamic_slice_in_dim(clip_front, position * coarse_rows, (FREACH + 1) * coarse_rows, 0),
        POOL,
    )
    own_clip = lax.dynamic_slice_in_dim(clip_ids, position * coarse_rows, coarse_rows, 0)
    query_clip = jnp.repeat(own_clip, POOL)
    head_pair_width = 2 * feat_width // FHEADS
    part_width = feat_width // HALVES
    outs = []
    projected = None
    wplanes = jnp.transpose(w_coarse, (1, 0, 2))
    gate = None
    prev1a = pair_swap(planes, "seq", False)
    for part in range(HALVES):
        own_pairs = planes[1:, :, part * part_width:(part + 1) * part_width]
        if gate is not None:
            own_pairs, _ = lax.optimization_barrier((own_pairs, gate))
        prev0 = passed_along(own_pairs, "seq", 2)
        gate = prev0
        if outs:
            prev0, _ = lax.optimization_barrier((prev0, projected))
        prev1b = pair_swap(prev0, "seq", True)
        part_out, part_pool = fine_attention(
            planes, prev0, prev1a, prev1b, query_clip.reshape(tok_count, 1),
            key_clip.reshape(1, (FREACH + 1) * tok_count), FHEADS,
            part * part_width // head_pair_width,
        )
        outs.append(part_out)
        part_weight = wplanes[:, part * part_width:(part + 1) * part_width, :]
        contribution = jnp.einsum(
            "rd,mdc->mrc", part_pool, part_weight, preferred_element_type=jnp.float32
        )
        projected = contribution if projected is None else projected + contribution
    fine_out = jnp.concatenate(outs, axis=1)
    quarter_width = w_coarse.shape[2] // QUARTERS
    projected = projected.astype(jnp.bfloat16)
    pieces = []
    for shift in range(QUARTERS):
        piece = lax.dynamic_slice_in_dim(
            projected, ((quarter + shift) % QUARTERS) * quarter_width, quarter_width, 2
        )
        pieces.append(piece if shift == 0 else within_group(piece, "seq", shift))
    grouped = group_order(pieces, quarter)
    grouped = jnp.transpose(grouped, (1, 0, 2, 3)).reshape(3, group_rows, quarter_width)
    coarse_queries = grouped[0]
    coarse_pairs = grouped[1:]
    one_back = passed_along(coarse_pairs, "seq", QUARTERS)
    two_back = passed_along(one_back, "seq", QUARTERS)
    three_back = passed_along(two_back, "seq", QUARTERS)
    earlier = [three_back, two_back, one_back]
    clip_back = jnp.concatenate([jnp.full((CREACH * group_rows,), -1, jnp.int32), clip_ids])
    coarse_key_clip = lax.dynamic_slice_in_dim(
        clip_back, cycle_place * group_rows, (CREACH + 1) * group_rows, 0
    )
    coarse_query_clip = lax.dynamic_slice_in_dim(clip_ids, cycle_place * group_rows, group_rows, 0)
    coarse_att = coarse_attention(
        coarse_queries, earlier + [coarse_pairs], coarse_query_clip.reshape(group_rows, 1),
        coarse_key_clip.reshape(1, (CREACH + 1) * group_rows), CHEADS // QUARTERS,
    )
    shares = []
    for shift in range(QUARTERS):
        share = lax.dynamic_slice_in_dim(
            coarse_att, ((quarter + shift) % QUARTERS) * coarse_rows, coarse_rows, 0
        )
        shares.append(share if shift == 0 else within_group(share, "seq", shift))
    att_rows = jnp.transpose(group_order(shares, quarter), (1, 0, 2)).reshape(
        coarse_rows, QUARTERS * quarter_width
    )
    coarse_up = jnp.dot(att_rows, w_out, preferred_element_type=jnp.float32).astype(jnp.bfloat16)
    carried = passed_along(coarse_up[-1:], "seq", 1)
    clip_before = jnp.concatenate([jnp.full((1,), -1, jnp.int32), clip_ids])
    prev_clip = lax.dynamic_slice_in_dim(clip_before, position * coarse_rows, coarse_rows, 0)
    joined = prev_clip == own_clip
    join_rows = jnp.repeat(joined.astype(jnp.int32), POOL).reshape(tok_count, 1)
    mixed = mix(fine_out, coarse_up, join_rows)
    head_lift = jnp.where(joined[:1, None], carried, jnp.zeros_like(carried))
    return patch(mixed, fine_out, head_lift)


def solution(mesh):
    return jax.shard_map(
        body,
        mesh=mesh,
        in_specs=(P(("groups", "seq"), None, None), P("groups"), P(), P()),
        out_specs=P(("groups", "seq"), None),
        check_vma=False,
    )
```

```python
import functools
import math

import jax
import jax.numpy as jnp
from jax import lax
from jax.experimental import pallas as pl
from jax.experimental.pallas import tpu as pltpu
from jax.sharding import PartitionSpec as P

FHEADS = 16
CHEADS = 8
POOL = 4
QUARTERS = 4
FREACH = 2
CREACH = 3
FINE_TILE = 256
HALVES = 2


def passed_along(value, axis, steps):
    count = lax.axis_size(axis)
    first, last = (max(0, -steps), min(count, count - steps))
    return lax.ppermute(value, axis, [(source, source + steps) for source in range(first, last)])


def within_group(value, axis, shift):
    count = lax.axis_size(axis)
    pairs = []
    for source in range(count):
        base = source - source % QUARTERS
        pairs.append((source, base + (source % QUARTERS + shift) % QUARTERS))
    return lax.ppermute(value, axis, pairs)


def fine_kernel(qclip_ref, kclip0_ref, kclip1_ref, kclip2_ref, q_ref,
                k0_ref, v0_ref, k1_ref, v1_ref, k1b_ref, v1b_ref, k2_ref, v2_ref,
                out_ref, pool_ref, bias_ref, *, scale):
    tile = q_ref.shape[0]
    width = q_ref.shape[1]
    half = width // 2
    seg = k0_ref.shape[0]
    tile_index = pl.program_id(0)

    @pl.when(pl.program_id(1) == 0)
    def _():
        qclip = qclip_ref[...]
        qpos = tile_index * tile + lax.broadcasted_iota(jnp.int32, (tile, seg), 0)
        kpos = lax.broadcasted_iota(jnp.int32, (tile, seg), 1)
        allowed = (
            kclip0_ref[...] == qclip,
            kclip1_ref[...] == qclip,
            (kclip2_ref[...] == qclip) & (kpos <= qpos),
        )
        for j in range(3):
            bias_ref[:, j * seg:(j + 1) * seg] = jnp.where(allowed[j], 0.0, -1e30)

    q = q_ref[...] * jnp.asarray(scale, q_ref.dtype)
    lane = lax.broadcasted_iota(jnp.int32, (1, width), 1)
    low = lane < half
    zero = jnp.zeros_like(q)
    head_q = (jnp.where(low, q, zero), jnp.where(low, zero, q))

    def run(step):
        own = (step + 1) * tile
        keys = (k0_ref[...], k1_ref[...] + k1b_ref[...], k2_ref[0:own, :])
        values = (v0_ref[...], v1_ref[...] + v1b_ref[...], v2_ref[0:own, :])
        spans = ((0, seg), (seg, seg), (2 * seg, own))
        results = []
        for h in range(2):
            scores = []
            for j in range(3):
                s = lax.dot_general(head_q[h], keys[j], (((1,), (1,)), ((), ())),
                                    preferred_element_type=jnp.float32)
                start, length = spans[j]
                scores.append(s + bias_ref[:, start:start + length])
            top = jnp.max(scores[0], axis=1, keepdims=True)
            for j in range(1, 3):
                top = jnp.maximum(top, jnp.max(scores[j], axis=1, keepdims=True))
            total = None
            summed = None
            for j in range(3):
                w = jnp.exp(scores[j] - top)
                part = jnp.sum(w, axis=1, keepdims=True)
                pv = jnp.dot(w.astype(jnp.bfloat16), values[j], preferred_element_type=jnp.float32)
                total = part if total is None else total + part
                summed = pv if summed is None else summed + pv
            results.append(summed / total)
        out = jnp.where(low, results[0], results[1]).astype(out_ref.dtype)
        out_ref[...] = out
        rows = tile // POOL
        pool_row = lax.broadcasted_iota(jnp.int32, (rows, tile), 0)
        pool_col = lax.broadcasted_iota(jnp.int32, (rows, tile), 1)
        pool_mat = jnp.where(pool_col // POOL == pool_row, 1.0 / POOL, 0.0).astype(jnp.bfloat16)
        pool_ref[...] = jnp.dot(pool_mat, out, preferred_element_type=jnp.float32).astype(
            pool_ref.dtype)

    for step in range(seg // tile):
        pl.when(tile_index == step)(functools.partial(run, step))


def fine_attention(planes, prev0, prev1a, prev1b, qclip, kclip, heads, first_pair):
    _, tok, width = planes.shape
    head_dim = width // heads
    pair = 2 * head_dim
    pairs = prev0.shape[2] // pair
    tile = min(FINE_TILE, tok)
    nq = tok // tile
    kernel = functools.partial(fine_kernel, scale=1.0 / math.sqrt(head_dim))

    def plane_spec(plane):
        return pl.BlockSpec((None, tok, pair), lambda i, h: (plane, 0, h))

    def own_spec(plane):
        return pl.BlockSpec((None, tok, pair), lambda i, h: (plane, 0, first_pair + h))

    return pl.pallas_call(
        kernel,
        grid=(nq, pairs),
        in_specs=[
            pl.BlockSpec((tile, 1), lambda i, h: (i, 0)),
            pl.BlockSpec((1, tok), lambda i, h: (0, 0)),
            pl.BlockSpec((1, tok), lambda i, h: (0, 1)),
            pl.BlockSpec((1, tok), lambda i, h: (0, 2)),
            pl.BlockSpec((None, tile, pair), lambda i, h: (0, i, first_pair + h)),
            plane_spec(0), plane_spec(1),
            own_spec(1), own_spec(2),
            plane_spec(0), plane_spec(1),
            own_spec(1), own_spec(2),
        ],
        out_specs=[
            pl.BlockSpec((tile, pair), lambda i, h: (i, h)),
            pl.BlockSpec((tile // POOL, pair), lambda i, h: (i, h)),
        ],
        out_shape=[
            jax.ShapeDtypeStruct((tok, pairs * pair), jnp.bfloat16),
            jax.ShapeDtypeStruct((tok // POOL, pairs * pair), jnp.bfloat16),
        ],
        scratch_shapes=[pltpu.VMEM((tile, 3 * tok), jnp.float32)],
    )(qclip, kclip, kclip, kclip, planes, prev0, prev0, prev1a, prev1a, prev1b, prev1b,
      planes, planes)


def mix_kernel(fine_ref, lift_ref, out_ref):
    tile = fine_ref.shape[0]
    rows = lift_ref.shape[0]
    spread_row = lax.broadcasted_iota(jnp.int32, (tile, rows), 0)
    spread_col = lax.broadcasted_iota(jnp.int32, (tile, rows), 1)
    spread = jnp.where(spread_row // POOL == spread_col, 1.0, 0.0).astype(jnp.bfloat16)
    lifted = jnp.dot(spread, lift_ref[...], preferred_element_type=jnp.float32)
    out_ref[...] = (fine_ref[...].astype(jnp.float32) + lifted).astype(out_ref.dtype)


def mix(fine_out, lifted):
    tok, width = fine_out.shape
    tile = min(FINE_TILE, tok)
    return pl.pallas_call(
        mix_kernel,
        grid=(tok // tile,),
        in_specs=[
            pl.BlockSpec((tile, width), lambda i: (i, 0)),
            pl.BlockSpec((tile // POOL, width), lambda i: (i, 0)),
        ],
        out_specs=pl.BlockSpec((tile, width), lambda i: (i, 0)),
        out_shape=jax.ShapeDtypeStruct((tok, width), fine_out.dtype),
    )(fine_out, lifted)


def pair_swap(value, axis, from_odd):
    count = lax.axis_size(axis)
    start = 1 if from_odd else 0
    step = -1 if from_odd else 1
    return lax.ppermute(value, axis, [(source, source + step) for source in range(start, count, 2)])


def coarse_kernel(qclip_ref, kc0_ref, kc1_ref, kc2_ref, kc3_ref, q_ref,
                  k0_ref, v0_ref, k1_ref, v1_ref, k2_ref, v2_ref, k3_ref, v3_ref,
                  out_ref, *, scale):
    tile = q_ref.shape[0]
    seg = k0_ref.shape[0]
    q = q_ref[...]
    qclip = qclip_ref[...]
    keys = (k0_ref, k1_ref, k2_ref, k3_ref)
    values = (v0_ref, v1_ref, v2_ref, v3_ref)
    clips = (kc0_ref, kc1_ref, kc2_ref, kc3_ref)
    qpos = pl.program_id(1) * tile + lax.broadcasted_iota(jnp.int32, (tile, seg), 0)
    kpos = lax.broadcasted_iota(jnp.int32, (tile, seg), 1)
    last = len(keys) - 1
    scores = []
    masks = []
    for j in range(len(keys)):
        allowed = clips[j][...] == qclip
        if j == last:
            allowed = allowed & (kpos <= qpos)
        s = lax.dot_general(q, keys[j][...], (((1,), (1,)), ((), ())),
                            preferred_element_type=jnp.float32) * scale
        scores.append(jnp.where(allowed, s, -1e30))
    top = jnp.max(scores[0], axis=1, keepdims=True)
    for j in range(1, len(keys)):
        top = jnp.maximum(top, jnp.max(scores[j], axis=1, keepdims=True))
    total = None
    summed = None
    for j in range(len(keys)):
        w = jnp.exp(scores[j] - top)
        part = jnp.sum(w, axis=1, keepdims=True)
        pv = jnp.dot(w.astype(jnp.bfloat16), values[j][...], preferred_element_type=jnp.float32)
        total = part if total is None else total + part
        summed = pv if summed is None else summed + pv
    out_ref[...] = (summed / total).astype(out_ref.dtype)


def coarse_attention(queries, windows, qclip, kclip, heads):
    rows, width = queries.shape
    head_dim = width // heads
    tile = min(FINE_TILE, rows)
    seg = windows[0].shape[1]
    kernel = functools.partial(coarse_kernel, scale=1.0 / math.sqrt(head_dim))
    clip_specs = [pl.BlockSpec((1, seg), functools.partial(lambda j, h, i: (0, j), j))
                  for j in range(len(windows))]
    kv_specs = []
    kv_args = []
    for window in windows:
        kv_specs.append(pl.BlockSpec((None, seg, head_dim), lambda h, i: (0, 0, h)))
        kv_specs.append(pl.BlockSpec((None, seg, head_dim), lambda h, i: (1, 0, h)))
        kv_args += [window, window]
    return pl.pallas_call(
        kernel,
        grid=(heads, rows // tile),
        in_specs=[pl.BlockSpec((tile, 1), lambda h, i: (i, 0))] + clip_specs
        + [pl.BlockSpec((tile, head_dim), lambda h, i: (i, h))] + kv_specs,
        out_specs=pl.BlockSpec((tile, head_dim), lambda h, i: (i, h)),
        out_shape=jax.ShapeDtypeStruct((rows, width), jnp.bfloat16),
    )(qclip, *([kclip] * len(windows)), queries, *kv_args)


def group_order(parts, quarter):
    ordered = jnp.stack([parts[0]] + parts[:0:-1], axis=0)
    return jnp.roll(ordered, quarter, axis=0)


def attend(queries, key_rows, value_rows, allowed, heads, head_groups):
    row_count = queries.shape[0]
    feat_width = queries.shape[1]
    head_dim = feat_width // heads
    per_group = heads // head_groups
    score_scale = 1.0 / math.sqrt(head_dim)

    def split_heads(source_rows):
        return source_rows.reshape(
            source_rows.shape[0], head_groups, per_group, head_dim
        ).transpose(1, 0, 2, 3)

    def one_group(operands):
        group_queries, group_keys, group_values = operands
        scores = (
            jnp.einsum(
                "rhd,khd->hrk", group_queries, group_keys, preferred_element_type=jnp.float32
            )
            * score_scale
        )
        masked = jnp.where(allowed[None], scores, -1e30)
        row_top = jnp.max(masked, axis=2, keepdims=True)
        weights = jnp.where(allowed[None], jnp.exp(masked - row_top), 0.0)
        row_total = jnp.sum(weights, axis=2)
        summed = jnp.einsum(
            "hrk,khd->rhd",
            weights.astype(jnp.bfloat16),
            group_values,
            preferred_element_type=jnp.float32,
        )
        return summed / jnp.transpose(row_total)[:, :, None]

    results = lax.map(
        one_group, (split_heads(queries), split_heads(key_rows), split_heads(value_rows))
    )
    return results.transpose(1, 0, 2, 3).reshape(row_count, feat_width).astype(jnp.bfloat16)


def body(fine_qkv, clip_ids, w_coarse, w_out):
    tok_count = fine_qkv.shape[0]
    feat_width = fine_qkv.shape[2]
    coarse_rows = tok_count // POOL
    group_rows = QUARTERS * coarse_rows
    position = lax.axis_index("seq")
    quarter = position % QUARTERS
    cycle_place = position // QUARTERS
    planes = jnp.transpose(fine_qkv, (1, 0, 2))
    clip_front = jnp.concatenate([jnp.full((FREACH * coarse_rows,), -1, jnp.int32), clip_ids])
    key_clip = jnp.repeat(
        lax.dynamic_slice_in_dim(clip_front, position * coarse_rows, (FREACH + 1) * coarse_rows, 0),
        POOL,
    )
    own_clip = lax.dynamic_slice_in_dim(clip_ids, position * coarse_rows, coarse_rows, 0)
    query_clip = jnp.repeat(own_clip, POOL)
    head_pair_width = 2 * feat_width // FHEADS
    part_width = feat_width // HALVES
    outs = []
    projected = None
    wplanes = jnp.transpose(w_coarse, (1, 0, 2))
    gate = None
    prev1a = pair_swap(planes, "seq", False)
    for part in range(HALVES):
        own_pairs = planes[1:, :, part * part_width:(part + 1) * part_width]
        if gate is not None:
            own_pairs, _ = lax.optimization_barrier((own_pairs, gate))
        prev0 = passed_along(own_pairs, "seq", 2)
        gate = prev0
        if outs:
            prev0, _ = lax.optimization_barrier((prev0, outs[-1]))
        else:
            prev0, query_rows, key_row = lax.optimization_barrier(
                (prev0, query_clip.reshape(tok_count, 1),
                 key_clip.reshape(1, (FREACH + 1) * tok_count))
            )
        prev1b = pair_swap(prev0, "seq", True)
        if projected is not None:
            prev1b, _ = lax.optimization_barrier((prev1b, projected))
        part_out, part_pool = fine_attention(
            planes, prev0, prev1a, prev1b, query_rows, key_row, FHEADS,
            part * part_width // head_pair_width,
        )
        outs.append(part_out)
        part_weight = wplanes[:, part * part_width:(part + 1) * part_width, :]
        contribution = jnp.einsum(
            "rd,mdc->mrc", part_pool, part_weight, preferred_element_type=jnp.float32
        )
        projected = contribution if projected is None else projected + contribution
    fine_out = jnp.concatenate(outs, axis=1)
    quarter_width = w_coarse.shape[2] // QUARTERS
    projected = projected.astype(jnp.bfloat16)
    pieces = []
    for shift in range(QUARTERS):
        piece = lax.dynamic_slice_in_dim(
            projected, ((quarter + shift) % QUARTERS) * quarter_width, quarter_width, 2
        )
        pieces.append(piece if shift == 0 else within_group(piece, "seq", shift))
    grouped = group_order(pieces, quarter)
    grouped = jnp.transpose(grouped, (1, 0, 2, 3)).reshape(3, group_rows, quarter_width)
    coarse_queries = grouped[0]
    coarse_pairs = grouped[1:]
    one_back = passed_along(coarse_pairs, "seq", QUARTERS)
    two_back = passed_along(one_back, "seq", QUARTERS)
    three_back = passed_along(two_back, "seq", QUARTERS)
    earlier = [three_back, two_back, one_back]
    clip_back = jnp.concatenate([jnp.full((CREACH * group_rows,), -1, jnp.int32), clip_ids])
    coarse_key_clip = lax.dynamic_slice_in_dim(
        clip_back, cycle_place * group_rows, (CREACH + 1) * group_rows, 0
    )
    coarse_query_clip = lax.dynamic_slice_in_dim(clip_ids, cycle_place * group_rows, group_rows, 0)
    coarse_att = coarse_attention(
        coarse_queries, earlier + [coarse_pairs], coarse_query_clip.reshape(group_rows, 1),
        coarse_key_clip.reshape(1, (CREACH + 1) * group_rows), CHEADS // QUARTERS,
    )
    shares = []
    for shift in range(QUARTERS):
        share = lax.dynamic_slice_in_dim(
            coarse_att, ((quarter + shift) % QUARTERS) * coarse_rows, coarse_rows, 0
        )
        shares.append(share if shift == 0 else within_group(share, "seq", shift))
    att_rows = jnp.transpose(group_order(shares, quarter), (1, 0, 2)).reshape(
        coarse_rows, QUARTERS * quarter_width
    )
    coarse_up = jnp.dot(att_rows, w_out, preferred_element_type=jnp.float32).astype(jnp.bfloat16)
    carried = passed_along(coarse_up[-1:], "seq", 1)
    previous = jnp.concatenate([jnp.zeros_like(carried), coarse_up[:-1]], axis=0)
    clip_before = jnp.concatenate([jnp.full((1,), -1, jnp.int32), clip_ids])
    prev_clip = lax.dynamic_slice_in_dim(clip_before, position * coarse_rows, coarse_rows, 0)
    joined = prev_clip == own_clip
    lifted = jnp.where(joined[:, None], previous, jnp.zeros_like(previous))
    mixed = mix(fine_out, lifted)
    head_lift = jnp.where(joined[:1, None], carried, jnp.zeros_like(carried)).astype(jnp.float32)
    head_rows = (fine_out[:POOL].astype(jnp.float32) + head_lift).astype(mixed.dtype)
    return lax.dynamic_update_slice(mixed, head_rows, (0, 0))


def solution(mesh):
    return jax.shard_map(
        body,
        mesh=mesh,
        in_specs=(P(("groups", "seq"), None, None), P("groups"), P(), P()),
        out_specs=P(("groups", "seq"), None),
        check_vma=False,
    )
```

```python
import functools
import math

import jax
import jax.numpy as jnp
from jax import lax
from jax.experimental import pallas as pl
from jax.experimental.pallas import tpu as pltpu
from jax.sharding import PartitionSpec as P

FHEADS = 16
CHEADS = 8
POOL = 4
QUARTERS = 4
FREACH = 2
CREACH = 3
FINE_TILE = 256
HALVES = 2


def passed_along(value, axis, steps):
    count = lax.axis_size(axis)
    first, last = (max(0, -steps), min(count, count - steps))
    return lax.ppermute(value, axis, [(source, source + steps) for source in range(first, last)])


def within_group(value, axis, shift):
    count = lax.axis_size(axis)
    pairs = []
    for source in range(count):
        base = source - source % QUARTERS
        pairs.append((source, base + (source % QUARTERS + shift) % QUARTERS))
    return lax.ppermute(value, axis, pairs)


def fine_kernel(qclip_ref, kclip0_ref, kclip1_ref, kclip2_ref, q_ref,
                k0_ref, v0_ref, k1_ref, v1_ref, k1b_ref, v1b_ref, k2_ref, v2_ref,
                out_ref, pool_ref, bias_ref, *, scale):
    tile = q_ref.shape[0]
    width = q_ref.shape[1]
    half = width // 2
    seg = k0_ref.shape[0]
    tile_index = pl.program_id(0)

    @pl.when(pl.program_id(1) == 0)
    def _():
        qclip = qclip_ref[...]
        qpos = tile_index * tile + lax.broadcasted_iota(jnp.int32, (tile, seg), 0)
        kpos = lax.broadcasted_iota(jnp.int32, (tile, seg), 1)
        allowed = (
            kclip0_ref[...] == qclip,
            kclip1_ref[...] == qclip,
            (kclip2_ref[...] == qclip) & (kpos <= qpos),
        )
        for j in range(3):
            bias_ref[:, j * seg:(j + 1) * seg] = jnp.where(allowed[j], 0.0, -1e30)

    q = q_ref[...] * jnp.asarray(scale, q_ref.dtype)
    lane = lax.broadcasted_iota(jnp.int32, (1, width), 1)
    low = lane < half
    zero = jnp.zeros_like(q)
    head_q = (jnp.where(low, q, zero), jnp.where(low, zero, q))

    def run(step):
        own = (step + 1) * tile
        keys = (k0_ref[...], k1_ref[...] + k1b_ref[...], k2_ref[0:own, :])
        values = (v0_ref[...], v1_ref[...] + v1b_ref[...], v2_ref[0:own, :])
        spans = ((0, seg), (seg, seg), (2 * seg, own))
        results = []
        for h in range(2):
            scores = []
            for j in range(3):
                s = lax.dot_general(head_q[h], keys[j], (((1,), (1,)), ((), ())),
                                    preferred_element_type=jnp.float32)
                start, length = spans[j]
                scores.append(s + bias_ref[:, start:start + length])
            top = jnp.max(scores[0], axis=1, keepdims=True)
            for j in range(1, 3):
                top = jnp.maximum(top, jnp.max(scores[j], axis=1, keepdims=True))
            total = None
            summed = None
            for j in range(3):
                w = jnp.exp(scores[j] - top)
                part = jnp.sum(w, axis=1, keepdims=True)
                pv = jnp.dot(w.astype(jnp.bfloat16), values[j], preferred_element_type=jnp.float32)
                total = part if total is None else total + part
                summed = pv if summed is None else summed + pv
            results.append(summed / total)
        out = jnp.where(low, results[0], results[1]).astype(out_ref.dtype)
        out_ref[...] = out
        rows = tile // POOL
        pool_row = lax.broadcasted_iota(jnp.int32, (rows, tile), 0)
        pool_col = lax.broadcasted_iota(jnp.int32, (rows, tile), 1)
        pool_mat = jnp.where(pool_col // POOL == pool_row, 1.0 / POOL, 0.0).astype(jnp.bfloat16)
        pool_ref[...] = jnp.dot(pool_mat, out, preferred_element_type=jnp.float32).astype(
            pool_ref.dtype)

    for step in range(seg // tile):
        pl.when(tile_index == step)(functools.partial(run, step))


def fine_attention(planes, prev0, prev1a, prev1b, qclip, kclip, heads, first_pair):
    _, tok, width = planes.shape
    head_dim = width // heads
    pair = 2 * head_dim
    pairs = prev0.shape[2] // pair
    tile = min(FINE_TILE, tok)
    nq = tok // tile
    kernel = functools.partial(fine_kernel, scale=1.0 / math.sqrt(head_dim))

    def plane_spec(plane):
        return pl.BlockSpec((None, tok, pair), lambda i, h: (plane, 0, h))

    def own_spec(plane):
        return pl.BlockSpec((None, tok, pair), lambda i, h: (plane, 0, first_pair + h))

    return pl.pallas_call(
        kernel,
        grid=(nq, pairs),
        in_specs=[
            pl.BlockSpec((tile, 1), lambda i, h: (i, 0)),
            pl.BlockSpec((1, tok), lambda i, h: (0, 0)),
            pl.BlockSpec((1, tok), lambda i, h: (0, 1)),
            pl.BlockSpec((1, tok), lambda i, h: (0, 2)),
            pl.BlockSpec((None, tile, pair), lambda i, h: (0, i, first_pair + h)),
            plane_spec(0), plane_spec(1),
            own_spec(1), own_spec(2),
            plane_spec(0), plane_spec(1),
            own_spec(1), own_spec(2),
        ],
        out_specs=[
            pl.BlockSpec((tile, pair), lambda i, h: (i, h)),
            pl.BlockSpec((tile // POOL, pair), lambda i, h: (i, h)),
        ],
        out_shape=[
            jax.ShapeDtypeStruct((tok, pairs * pair), jnp.bfloat16),
            jax.ShapeDtypeStruct((tok // POOL, pairs * pair), jnp.bfloat16),
        ],
        scratch_shapes=[pltpu.VMEM((tile, 3 * tok), jnp.float32)],
    )(qclip, kclip, kclip, kclip, planes, prev0, prev0, prev1a, prev1a, prev1b, prev1b,
      planes, planes)


def mix_kernel(fine_ref, lift_ref, out_ref):
    tile = fine_ref.shape[0]
    rows = lift_ref.shape[0]
    spread_row = lax.broadcasted_iota(jnp.int32, (tile, rows), 0)
    spread_col = lax.broadcasted_iota(jnp.int32, (tile, rows), 1)
    spread = jnp.where(spread_row // POOL == spread_col, 1.0, 0.0).astype(jnp.bfloat16)
    lifted = jnp.dot(spread, lift_ref[...], preferred_element_type=jnp.float32)
    out_ref[...] = (fine_ref[...].astype(jnp.float32) + lifted).astype(out_ref.dtype)


def mix(fine_out, lifted):
    tok, width = fine_out.shape
    tile = min(FINE_TILE, tok)
    return pl.pallas_call(
        mix_kernel,
        grid=(tok // tile,),
        in_specs=[
            pl.BlockSpec((tile, width), lambda i: (i, 0)),
            pl.BlockSpec((tile // POOL, width), lambda i: (i, 0)),
        ],
        out_specs=pl.BlockSpec((tile, width), lambda i: (i, 0)),
        out_shape=jax.ShapeDtypeStruct((tok, width), fine_out.dtype),
    )(fine_out, lifted)


def pair_swap(value, axis, from_odd):
    count = lax.axis_size(axis)
    start = 1 if from_odd else 0
    step = -1 if from_odd else 1
    return lax.ppermute(value, axis, [(source, source + step) for source in range(start, count, 2)])


def coarse_kernel(qclip_ref, kc0_ref, kc1_ref, kc2_ref, kc3_ref, q_ref,
                  k0_ref, v0_ref, k1_ref, v1_ref, k2_ref, v2_ref, k3_ref, v3_ref,
                  out_ref, *, scale):
    tile = q_ref.shape[0]
    seg = k0_ref.shape[0]
    keys = (k0_ref, k1_ref, k2_ref, k3_ref)
    values = (v0_ref, v1_ref, v2_ref, v3_ref)
    clips = (kc0_ref, kc1_ref, kc2_ref, kc3_ref)
    last = len(keys) - 1

    def run(step):
        q = q_ref[...]
        qclip = qclip_ref[...]
        own = (step + 1) * tile
        scores = []
        for j in range(len(keys)):
            length = own if j == last else seg
            allowed = clips[j][:, 0:length] == qclip
            if j == last:
                qpos = step * tile + lax.broadcasted_iota(jnp.int32, (tile, length), 0)
                kpos = lax.broadcasted_iota(jnp.int32, (tile, length), 1)
                allowed = allowed & (kpos <= qpos)
            s = lax.dot_general(q, keys[j][0:length, :], (((1,), (1,)), ((), ())),
                                preferred_element_type=jnp.float32) * scale
            scores.append(jnp.where(allowed, s, -1e30))
        top = jnp.max(scores[0], axis=1, keepdims=True)
        for j in range(1, len(keys)):
            top = jnp.maximum(top, jnp.max(scores[j], axis=1, keepdims=True))
        total = None
        summed = None
        for j in range(len(keys)):
            length = own if j == last else seg
            w = jnp.exp(scores[j] - top)
            part = jnp.sum(w, axis=1, keepdims=True)
            pv = jnp.dot(w.astype(jnp.bfloat16), values[j][0:length, :],
                         preferred_element_type=jnp.float32)
            total = part if total is None else total + part
            summed = pv if summed is None else summed + pv
        out_ref[...] = (summed / total).astype(out_ref.dtype)

    for step in range(seg // tile):
        pl.when(pl.program_id(1) == step)(functools.partial(run, step))


def coarse_attention(queries, windows, qclip, kclip, heads):
    rows, width = queries.shape
    head_dim = width // heads
    tile = min(FINE_TILE, rows)
    seg = windows[0].shape[1]
    kernel = functools.partial(coarse_kernel, scale=1.0 / math.sqrt(head_dim))
    clip_specs = [pl.BlockSpec((1, seg), functools.partial(lambda j, h, i: (0, j), j))
                  for j in range(len(windows))]
    kv_specs = []
    kv_args = []
    for window in windows:
        kv_specs.append(pl.BlockSpec((None, seg, head_dim), lambda h, i: (0, 0, h)))
        kv_specs.append(pl.BlockSpec((None, seg, head_dim), lambda h, i: (1, 0, h)))
        kv_args += [window, window]
    return pl.pallas_call(
        kernel,
        grid=(heads, rows // tile),
        in_specs=[pl.BlockSpec((tile, 1), lambda h, i: (i, 0))] + clip_specs
        + [pl.BlockSpec((tile, head_dim), lambda h, i: (i, h))] + kv_specs,
        out_specs=pl.BlockSpec((tile, head_dim), lambda h, i: (i, h)),
        out_shape=jax.ShapeDtypeStruct((rows, width), jnp.bfloat16),
    )(qclip, *([kclip] * len(windows)), queries, *kv_args)


def group_order(parts, quarter):
    ordered = jnp.stack([parts[0]] + parts[:0:-1], axis=0)
    return jnp.roll(ordered, quarter, axis=0)


def attend(queries, key_rows, value_rows, allowed, heads, head_groups):
    row_count = queries.shape[0]
    feat_width = queries.shape[1]
    head_dim = feat_width // heads
    per_group = heads // head_groups
    score_scale = 1.0 / math.sqrt(head_dim)

    def split_heads(source_rows):
        return source_rows.reshape(
            source_rows.shape[0], head_groups, per_group, head_dim
        ).transpose(1, 0, 2, 3)

    def one_group(operands):
        group_queries, group_keys, group_values = operands
        scores = (
            jnp.einsum(
                "rhd,khd->hrk", group_queries, group_keys, preferred_element_type=jnp.float32
            )
            * score_scale
        )
        masked = jnp.where(allowed[None], scores, -1e30)
        row_top = jnp.max(masked, axis=2, keepdims=True)
        weights = jnp.where(allowed[None], jnp.exp(masked - row_top), 0.0)
        row_total = jnp.sum(weights, axis=2)
        summed = jnp.einsum(
            "hrk,khd->rhd",
            weights.astype(jnp.bfloat16),
            group_values,
            preferred_element_type=jnp.float32,
        )
        return summed / jnp.transpose(row_total)[:, :, None]

    results = lax.map(
        one_group, (split_heads(queries), split_heads(key_rows), split_heads(value_rows))
    )
    return results.transpose(1, 0, 2, 3).reshape(row_count, feat_width).astype(jnp.bfloat16)


def body(fine_qkv, clip_ids, w_coarse, w_out):
    tok_count = fine_qkv.shape[0]
    feat_width = fine_qkv.shape[2]
    coarse_rows = tok_count // POOL
    group_rows = QUARTERS * coarse_rows
    position = lax.axis_index("seq")
    quarter = position % QUARTERS
    cycle_place = position // QUARTERS
    planes = jnp.transpose(fine_qkv, (1, 0, 2))
    clip_front = jnp.concatenate([jnp.full((FREACH * coarse_rows,), -1, jnp.int32), clip_ids])
    key_clip = jnp.repeat(
        lax.dynamic_slice_in_dim(clip_front, position * coarse_rows, (FREACH + 1) * coarse_rows, 0),
        POOL,
    )
    own_clip = lax.dynamic_slice_in_dim(clip_ids, position * coarse_rows, coarse_rows, 0)
    query_clip = jnp.repeat(own_clip, POOL)
    head_pair_width = 2 * feat_width // FHEADS
    part_width = feat_width // HALVES
    outs = []
    projected = None
    wplanes = jnp.transpose(w_coarse, (1, 0, 2))
    gate = None
    prev1a = pair_swap(planes, "seq", False)
    for part in range(HALVES):
        own_pairs = planes[1:, :, part * part_width:(part + 1) * part_width]
        if gate is not None:
            own_pairs, _ = lax.optimization_barrier((own_pairs, gate))
        prev0 = passed_along(own_pairs, "seq", 2)
        gate = prev0
        if outs:
            prev0, _ = lax.optimization_barrier((prev0, projected))
        prev1b = pair_swap(prev0, "seq", True)
        part_out, part_pool = fine_attention(
            planes, prev0, prev1a, prev1b, query_clip.reshape(tok_count, 1),
            key_clip.reshape(1, (FREACH + 1) * tok_count), FHEADS,
            part * part_width // head_pair_width,
        )
        outs.append(part_out)
        part_weight = wplanes[:, part * part_width:(part + 1) * part_width, :]
        contribution = jnp.einsum(
            "rd,mdc->mrc", part_pool, part_weight, preferred_element_type=jnp.float32
        )
        projected = contribution if projected is None else projected + contribution
    fine_out = jnp.concatenate(outs, axis=1)
    quarter_width = w_coarse.shape[2] // QUARTERS
    projected = projected.astype(jnp.bfloat16)
    pieces = []
    for shift in range(QUARTERS):
        piece = lax.dynamic_slice_in_dim(
            projected, ((quarter + shift) % QUARTERS) * quarter_width, quarter_width, 2
        )
        pieces.append(piece if shift == 0 else within_group(piece, "seq", shift))
    grouped = group_order(pieces, quarter)
    grouped = jnp.transpose(grouped, (1, 0, 2, 3)).reshape(3, group_rows, quarter_width)
    coarse_queries = grouped[0]
    coarse_pairs = grouped[1:]
    one_back = passed_along(coarse_pairs, "seq", QUARTERS)
    two_back = passed_along(one_back, "seq", QUARTERS)
    three_back = passed_along(two_back, "seq", QUARTERS)
    earlier = [three_back, two_back, one_back]
    clip_back = jnp.concatenate([jnp.full((CREACH * group_rows,), -1, jnp.int32), clip_ids])
    coarse_key_clip = lax.dynamic_slice_in_dim(
        clip_back, cycle_place * group_rows, (CREACH + 1) * group_rows, 0
    )
    coarse_query_clip = lax.dynamic_slice_in_dim(clip_ids, cycle_place * group_rows, group_rows, 0)
    coarse_att = coarse_attention(
        coarse_queries, earlier + [coarse_pairs], coarse_query_clip.reshape(group_rows, 1),
        coarse_key_clip.reshape(1, (CREACH + 1) * group_rows), CHEADS // QUARTERS,
    )
    shares = []
    for shift in range(QUARTERS):
        share = lax.dynamic_slice_in_dim(
            coarse_att, ((quarter + shift) % QUARTERS) * coarse_rows, coarse_rows, 0
        )
        shares.append(share if shift == 0 else within_group(share, "seq", shift))
    att_rows = jnp.transpose(group_order(shares, quarter), (1, 0, 2)).reshape(
        coarse_rows, QUARTERS * quarter_width
    )
    coarse_up = jnp.dot(att_rows, w_out, preferred_element_type=jnp.float32).astype(jnp.bfloat16)
    carried = passed_along(coarse_up[-1:], "seq", 1)
    previous = jnp.concatenate([jnp.zeros_like(carried), coarse_up[:-1]], axis=0)
    clip_before = jnp.concatenate([jnp.full((1,), -1, jnp.int32), clip_ids])
    prev_clip = lax.dynamic_slice_in_dim(clip_before, position * coarse_rows, coarse_rows, 0)
    joined = prev_clip == own_clip
    lifted = jnp.where(joined[:, None], previous, jnp.zeros_like(previous))
    mixed = mix(fine_out, lifted)
    head_lift = jnp.where(joined[:1, None], carried, jnp.zeros_like(carried)).astype(jnp.float32)
    head_rows = (fine_out[:POOL].astype(jnp.float32) + head_lift).astype(mixed.dtype)
    return lax.dynamic_update_slice(mixed, head_rows, (0, 0))


def solution(mesh):
    return jax.shard_map(
        body,
        mesh=mesh,
        in_specs=(P(("groups", "seq"), None, None), P("groups"), P(), P()),
        out_specs=P(("groups", "seq"), None),
        check_vma=False,
    )
```

```python
import functools
import math

import jax
import jax.numpy as jnp
from jax import lax
from jax.experimental import pallas as pl
from jax.experimental.pallas import tpu as pltpu
from jax.sharding import PartitionSpec as P

FHEADS = 16
CHEADS = 8
POOL = 4
QUARTERS = 4
FREACH = 2
CREACH = 3
FINE_TILE = 256
HALVES = 2


def passed_along(value, axis, steps):
    count = lax.axis_size(axis)
    first, last = (max(0, -steps), min(count, count - steps))
    return lax.ppermute(value, axis, [(source, source + steps) for source in range(first, last)])


def within_group(value, axis, shift):
    count = lax.axis_size(axis)
    pairs = []
    for source in range(count):
        base = source - source % QUARTERS
        pairs.append((source, base + (source % QUARTERS + shift) % QUARTERS))
    return lax.ppermute(value, axis, pairs)


def fine_kernel(qclip_ref, kclip0_ref, kclip1_ref, kclip2_ref, q_ref,
                k0_ref, v0_ref, k1_ref, v1_ref, k1b_ref, v1b_ref, k2_ref, v2_ref,
                out_ref, pool_ref, bias_ref, *, scale):
    tile = q_ref.shape[0]
    width = q_ref.shape[1]
    half = width // 2
    seg = k0_ref.shape[0]
    tile_index = pl.program_id(0)

    @pl.when(pl.program_id(1) == 0)
    def _():
        qclip = qclip_ref[...]
        qpos = tile_index * tile + lax.broadcasted_iota(jnp.int32, (tile, seg), 0)
        kpos = lax.broadcasted_iota(jnp.int32, (tile, seg), 1)
        allowed = (
            kclip0_ref[...] == qclip,
            kclip1_ref[...] == qclip,
            (kclip2_ref[...] == qclip) & (kpos <= qpos),
        )
        for j in range(3):
            bias_ref[:, j * seg:(j + 1) * seg] = jnp.where(allowed[j], 0.0, -1e30)

    q = q_ref[...] * jnp.asarray(scale, q_ref.dtype)
    lane = lax.broadcasted_iota(jnp.int32, (1, width), 1)
    low = lane < half
    zero = jnp.zeros_like(q)
    head_q = (jnp.where(low, q, zero), jnp.where(low, zero, q))

    def run(step):
        own = (step + 1) * tile
        keys = (k0_ref[...], k1_ref[...] + k1b_ref[...], k2_ref[0:own, :])
        values = (v0_ref[...], v1_ref[...] + v1b_ref[...], v2_ref[0:own, :])
        spans = ((0, seg), (seg, seg), (2 * seg, own))
        results = []
        for h in range(2):
            scores = []
            for j in range(3):
                s = lax.dot_general(head_q[h], keys[j], (((1,), (1,)), ((), ())),
                                    preferred_element_type=jnp.float32)
                start, length = spans[j]
                scores.append(s + bias_ref[:, start:start + length])
            top = jnp.max(scores[0], axis=1, keepdims=True)
            for j in range(1, 3):
                top = jnp.maximum(top, jnp.max(scores[j], axis=1, keepdims=True))
            total = None
            summed = None
            for j in range(3):
                w = jnp.exp(scores[j] - top)
                part = jnp.sum(w, axis=1, keepdims=True)
                pv = jnp.dot(w.astype(jnp.bfloat16), values[j], preferred_element_type=jnp.float32)
                total = part if total is None else total + part
                summed = pv if summed is None else summed + pv
            results.append(summed / total)
        out = jnp.where(low, results[0], results[1]).astype(out_ref.dtype)
        out_ref[...] = out
        rows = tile // POOL
        pool_row = lax.broadcasted_iota(jnp.int32, (rows, tile), 0)
        pool_col = lax.broadcasted_iota(jnp.int32, (rows, tile), 1)
        pool_mat = jnp.where(pool_col // POOL == pool_row, 1.0 / POOL, 0.0).astype(jnp.bfloat16)
        pool_ref[...] = jnp.dot(pool_mat, out, preferred_element_type=jnp.float32).astype(
            pool_ref.dtype)

    for step in range(seg // tile):
        pl.when(tile_index == step)(functools.partial(run, step))


def fine_attention(planes, prev0, prev1a, prev1b, qclip, kclip, heads, first_pair):
    _, tok, width = planes.shape
    head_dim = width // heads
    pair = 2 * head_dim
    pairs = prev0.shape[2] // pair
    tile = min(FINE_TILE, tok)
    nq = tok // tile
    kernel = functools.partial(fine_kernel, scale=1.0 / math.sqrt(head_dim))

    def plane_spec(plane):
        return pl.BlockSpec((None, tok, pair), lambda i, h: (plane, 0, h))

    def own_spec(plane):
        return pl.BlockSpec((None, tok, pair), lambda i, h: (plane, 0, first_pair + h))

    return pl.pallas_call(
        kernel,
        grid=(nq, pairs),
        in_specs=[
            pl.BlockSpec((tile, 1), lambda i, h: (i, 0)),
            pl.BlockSpec((1, tok), lambda i, h: (0, 0)),
            pl.BlockSpec((1, tok), lambda i, h: (0, 1)),
            pl.BlockSpec((1, tok), lambda i, h: (0, 2)),
            pl.BlockSpec((None, tile, pair), lambda i, h: (0, i, first_pair + h)),
            plane_spec(0), plane_spec(1),
            own_spec(1), own_spec(2),
            plane_spec(0), plane_spec(1),
            own_spec(1), own_spec(2),
        ],
        out_specs=[
            pl.BlockSpec((tile, pair), lambda i, h: (i, h)),
            pl.BlockSpec((tile // POOL, pair), lambda i, h: (i, h)),
        ],
        out_shape=[
            jax.ShapeDtypeStruct((tok, pairs * pair), jnp.bfloat16),
            jax.ShapeDtypeStruct((tok // POOL, pairs * pair), jnp.bfloat16),
        ],
        scratch_shapes=[pltpu.VMEM((tile, 3 * tok), jnp.float32)],
    )(qclip, kclip, kclip, kclip, planes, prev0, prev0, prev1a, prev1a, prev1b, prev1b,
      planes, planes)


def mix_kernel(fine_ref, lift_ref, out_ref):
    tile = fine_ref.shape[0]
    rows = lift_ref.shape[0]
    spread_row = lax.broadcasted_iota(jnp.int32, (tile, rows), 0)
    spread_col = lax.broadcasted_iota(jnp.int32, (tile, rows), 1)
    spread = jnp.where(spread_row // POOL == spread_col, 1.0, 0.0).astype(jnp.bfloat16)
    lifted = jnp.dot(spread, lift_ref[...], preferred_element_type=jnp.float32)
    out_ref[...] = (fine_ref[...].astype(jnp.float32) + lifted).astype(out_ref.dtype)


def mix(fine_out, lifted):
    tok, width = fine_out.shape
    tile = min(FINE_TILE, tok)
    return pl.pallas_call(
        mix_kernel,
        grid=(tok // tile,),
        in_specs=[
            pl.BlockSpec((tile, width), lambda i: (i, 0)),
            pl.BlockSpec((tile // POOL, width), lambda i: (i, 0)),
        ],
        out_specs=pl.BlockSpec((tile, width), lambda i: (i, 0)),
        out_shape=jax.ShapeDtypeStruct((tok, width), fine_out.dtype),
    )(fine_out, lifted)


def pair_swap(value, axis, from_odd):
    count = lax.axis_size(axis)
    start = 1 if from_odd else 0
    step = -1 if from_odd else 1
    return lax.ppermute(value, axis, [(source, source + step) for source in range(start, count, 2)])


def coarse_kernel(qclip_ref, kc0_ref, kc1_ref, kc2_ref, kc3_ref, q_ref,
                  k0_ref, v0_ref, k1_ref, v1_ref, k2_ref, v2_ref, k3_ref, v3_ref,
                  out_ref, *, scale, heads):
    tile, width = q_ref.shape
    head_dim = width // heads
    seg = k0_ref.shape[0]
    keys = (k0_ref, k1_ref, k2_ref, k3_ref)
    values = (v0_ref, v1_ref, v2_ref, v3_ref)
    clips = (kc0_ref, kc1_ref, kc2_ref, kc3_ref)
    last = len(keys) - 1

    def run(step):
        q = q_ref[...]
        lane_head = lax.broadcasted_iota(jnp.int32, (1, width), 1) // head_dim
        zero = jnp.zeros_like(q)
        qclip = qclip_ref[...]
        own = (step + 1) * tile
        masks = []
        for j in range(len(keys)):
            length = own if j == last else seg
            allowed = clips[j][:, 0:length] == qclip
            if j == last:
                qpos = step * tile + lax.broadcasted_iota(jnp.int32, (tile, length), 0)
                kpos = lax.broadcasted_iota(jnp.int32, (tile, length), 1)
                allowed = allowed & (kpos <= qpos)
            masks.append(allowed)
        out = None
        for h in range(heads):
            head_q = jnp.where(lane_head == h, q, zero)
            scores = []
            for j in range(len(keys)):
                length = own if j == last else seg
                s = lax.dot_general(head_q, keys[j][0:length, :], (((1,), (1,)), ((), ())),
                                    preferred_element_type=jnp.float32) * scale
                scores.append(jnp.where(masks[j], s, -1e30))
            top = jnp.max(scores[0], axis=1, keepdims=True)
            for j in range(1, len(keys)):
                top = jnp.maximum(top, jnp.max(scores[j], axis=1, keepdims=True))
            total = None
            summed = None
            for j in range(len(keys)):
                length = own if j == last else seg
                w = jnp.exp(scores[j] - top)
                part = jnp.sum(w, axis=1, keepdims=True)
                pv = jnp.dot(w.astype(jnp.bfloat16), values[j][0:length, :],
                             preferred_element_type=jnp.float32)
                total = part if total is None else total + part
                summed = pv if summed is None else summed + pv
            result = summed / total
            out = result if out is None else jnp.where(lane_head == h, result, out)
        out_ref[...] = out.astype(out_ref.dtype)

    for step in range(seg // tile):
        pl.when(pl.program_id(1) == step)(functools.partial(run, step))


def coarse_attention(queries, windows, qclip, kclip, heads):
    rows, width = queries.shape
    head_dim = width // heads
    tile = min(FINE_TILE, rows)
    seg = windows[0].shape[1]
    kernel = functools.partial(coarse_kernel, scale=1.0 / math.sqrt(head_dim), heads=heads)
    clip_specs = [pl.BlockSpec((1, seg), functools.partial(lambda j, h, i: (0, j), j))
                  for j in range(len(windows))]
    kv_specs = []
    kv_args = []
    for window in windows:
        kv_specs.append(pl.BlockSpec((None, seg, width), lambda h, i: (0, 0, 0)))
        kv_specs.append(pl.BlockSpec((None, seg, width), lambda h, i: (1, 0, 0)))
        kv_args += [window, window]
    return pl.pallas_call(
        kernel,
        grid=(1, rows // tile),
        in_specs=[pl.BlockSpec((tile, 1), lambda h, i: (i, 0))] + clip_specs
        + [pl.BlockSpec((tile, width), lambda h, i: (i, 0))] + kv_specs,
        out_specs=pl.BlockSpec((tile, width), lambda h, i: (i, 0)),
        out_shape=jax.ShapeDtypeStruct((rows, width), jnp.bfloat16),
    )(qclip, *([kclip] * len(windows)), queries, *kv_args)


def group_order(parts, quarter):
    ordered = jnp.stack([parts[0]] + parts[:0:-1], axis=0)
    return jnp.roll(ordered, quarter, axis=0)


def attend(queries, key_rows, value_rows, allowed, heads, head_groups):
    row_count = queries.shape[0]
    feat_width = queries.shape[1]
    head_dim = feat_width // heads
    per_group = heads // head_groups
    score_scale = 1.0 / math.sqrt(head_dim)

    def split_heads(source_rows):
        return source_rows.reshape(
            source_rows.shape[0], head_groups, per_group, head_dim
        ).transpose(1, 0, 2, 3)

    def one_group(operands):
        group_queries, group_keys, group_values = operands
        scores = (
            jnp.einsum(
                "rhd,khd->hrk", group_queries, group_keys, preferred_element_type=jnp.float32
            )
            * score_scale
        )
        masked = jnp.where(allowed[None], scores, -1e30)
        row_top = jnp.max(masked, axis=2, keepdims=True)
        weights = jnp.where(allowed[None], jnp.exp(masked - row_top), 0.0)
        row_total = jnp.sum(weights, axis=2)
        summed = jnp.einsum(
            "hrk,khd->rhd",
            weights.astype(jnp.bfloat16),
            group_values,
            preferred_element_type=jnp.float32,
        )
        return summed / jnp.transpose(row_total)[:, :, None]

    results = lax.map(
        one_group, (split_heads(queries), split_heads(key_rows), split_heads(value_rows))
    )
    return results.transpose(1, 0, 2, 3).reshape(row_count, feat_width).astype(jnp.bfloat16)


def body(fine_qkv, clip_ids, w_coarse, w_out):
    tok_count = fine_qkv.shape[0]
    feat_width = fine_qkv.shape[2]
    coarse_rows = tok_count // POOL
    group_rows = QUARTERS * coarse_rows
    position = lax.axis_index("seq")
    quarter = position % QUARTERS
    cycle_place = position // QUARTERS
    planes = jnp.transpose(fine_qkv, (1, 0, 2))
    clip_front = jnp.concatenate([jnp.full((FREACH * coarse_rows,), -1, jnp.int32), clip_ids])
    key_clip = jnp.repeat(
        lax.dynamic_slice_in_dim(clip_front, position * coarse_rows, (FREACH + 1) * coarse_rows, 0),
        POOL,
    )
    own_clip = lax.dynamic_slice_in_dim(clip_ids, position * coarse_rows, coarse_rows, 0)
    query_clip = jnp.repeat(own_clip, POOL)
    head_pair_width = 2 * feat_width // FHEADS
    part_width = feat_width // HALVES
    outs = []
    projected = None
    wplanes = jnp.transpose(w_coarse, (1, 0, 2))
    gate = None
    prev1a = pair_swap(planes, "seq", False)
    for part in range(HALVES):
        own_pairs = planes[1:, :, part * part_width:(part + 1) * part_width]
        if gate is not None:
            own_pairs, _ = lax.optimization_barrier((own_pairs, gate))
        prev0 = passed_along(own_pairs, "seq", 2)
        gate = prev0
        if outs:
            prev0, _ = lax.optimization_barrier((prev0, projected))
        prev1b = pair_swap(prev0, "seq", True)
        part_out, part_pool = fine_attention(
            planes, prev0, prev1a, prev1b, query_clip.reshape(tok_count, 1),
            key_clip.reshape(1, (FREACH + 1) * tok_count), FHEADS,
            part * part_width // head_pair_width,
        )
        outs.append(part_out)
        part_weight = wplanes[:, part * part_width:(part + 1) * part_width, :]
        contribution = jnp.einsum(
            "rd,mdc->mrc", part_pool, part_weight, preferred_element_type=jnp.float32
        )
        projected = contribution if projected is None else projected + contribution
    fine_out = jnp.concatenate(outs, axis=1)
    quarter_width = w_coarse.shape[2] // QUARTERS
    projected = projected.astype(jnp.bfloat16)
    pieces = []
    for shift in range(QUARTERS):
        piece = lax.dynamic_slice_in_dim(
            projected, ((quarter + shift) % QUARTERS) * quarter_width, quarter_width, 2
        )
        pieces.append(piece if shift == 0 else within_group(piece, "seq", shift))
    grouped = group_order(pieces, quarter)
    grouped = jnp.transpose(grouped, (1, 0, 2, 3)).reshape(3, group_rows, quarter_width)
    coarse_queries = grouped[0]
    coarse_pairs = grouped[1:]
    one_back = passed_along(coarse_pairs, "seq", QUARTERS)
    two_back = passed_along(one_back, "seq", QUARTERS)
    three_back = passed_along(two_back, "seq", QUARTERS)
    earlier = [three_back, two_back, one_back]
    clip_back = jnp.concatenate([jnp.full((CREACH * group_rows,), -1, jnp.int32), clip_ids])
    coarse_key_clip = lax.dynamic_slice_in_dim(
        clip_back, cycle_place * group_rows, (CREACH + 1) * group_rows, 0
    )
    coarse_query_clip = lax.dynamic_slice_in_dim(clip_ids, cycle_place * group_rows, group_rows, 0)
    coarse_att = coarse_attention(
        coarse_queries, earlier + [coarse_pairs], coarse_query_clip.reshape(group_rows, 1),
        coarse_key_clip.reshape(1, (CREACH + 1) * group_rows), CHEADS // QUARTERS,
    )
    shares = []
    for shift in range(QUARTERS):
        share = lax.dynamic_slice_in_dim(
            coarse_att, ((quarter + shift) % QUARTERS) * coarse_rows, coarse_rows, 0
        )
        shares.append(share if shift == 0 else within_group(share, "seq", shift))
    att_rows = jnp.transpose(group_order(shares, quarter), (1, 0, 2)).reshape(
        coarse_rows, QUARTERS * quarter_width
    )
    coarse_up = jnp.dot(att_rows, w_out, preferred_element_type=jnp.float32).astype(jnp.bfloat16)
    carried = passed_along(coarse_up[-1:], "seq", 1)
    previous = jnp.concatenate([jnp.zeros_like(carried), coarse_up[:-1]], axis=0)
    clip_before = jnp.concatenate([jnp.full((1,), -1, jnp.int32), clip_ids])
    prev_clip = lax.dynamic_slice_in_dim(clip_before, position * coarse_rows, coarse_rows, 0)
    joined = prev_clip == own_clip
    lifted = jnp.where(joined[:, None], previous, jnp.zeros_like(previous))
    mixed = mix(fine_out, lifted)
    head_lift = jnp.where(joined[:1, None], carried, jnp.zeros_like(carried)).astype(jnp.float32)
    head_rows = (fine_out[:POOL].astype(jnp.float32) + head_lift).astype(mixed.dtype)
    return lax.dynamic_update_slice(mixed, head_rows, (0, 0))


def solution(mesh):
    return jax.shard_map(
        body,
        mesh=mesh,
        in_specs=(P(("groups", "seq"), None, None), P("groups"), P(), P()),
        out_specs=P(("groups", "seq"), None),
        check_vma=False,
    )
```

```python
import functools
import math

import jax
import jax.numpy as jnp
from jax import lax
from jax.experimental import pallas as pl
from jax.experimental.pallas import tpu as pltpu
from jax.sharding import PartitionSpec as P

FHEADS = 16
CHEADS = 8
POOL = 4
QUARTERS = 4
FREACH = 2
CREACH = 3
FINE_TILE = 256
HALVES = 2


def passed_along(value, axis, steps):
    count = lax.axis_size(axis)
    first, last = (max(0, -steps), min(count, count - steps))
    return lax.ppermute(value, axis, [(source, source + steps) for source in range(first, last)])


def within_group(value, axis, shift):
    count = lax.axis_size(axis)
    pairs = []
    for source in range(count):
        base = source - source % QUARTERS
        pairs.append((source, base + (source % QUARTERS + shift) % QUARTERS))
    return lax.ppermute(value, axis, pairs)


def fine_kernel(qclip_ref, kclip0_ref, kclip1_ref, kclip2_ref, q_ref,
                k0_ref, v0_ref, k1_ref, v1_ref, k1b_ref, v1b_ref, k2_ref, v2_ref,
                out_ref, pool_ref, bias_ref, *, scale):
    tile = q_ref.shape[0]
    width = q_ref.shape[1]
    half = width // 2
    seg = k0_ref.shape[0]
    tile_index = pl.program_id(0)

    @pl.when(pl.program_id(1) == 0)
    def _():
        qclip = qclip_ref[...]
        qpos = tile_index * tile + lax.broadcasted_iota(jnp.int32, (tile, seg), 0)
        kpos = lax.broadcasted_iota(jnp.int32, (tile, seg), 1)
        allowed = (
            kclip0_ref[...] == qclip,
            kclip1_ref[...] == qclip,
            (kclip2_ref[...] == qclip) & (kpos <= qpos),
        )
        for j in range(3):
            bias_ref[:, j * seg:(j + 1) * seg] = jnp.where(allowed[j], 0.0, -1e30)

    q = q_ref[...] * jnp.asarray(scale, q_ref.dtype)
    lane = lax.broadcasted_iota(jnp.int32, (1, width), 1)
    low = lane < half
    zero = jnp.zeros_like(q)
    head_q = (jnp.where(low, q, zero), jnp.where(low, zero, q))

    def run(step):
        own = (step + 1) * tile
        keys = (k0_ref[...], k1_ref[...] + k1b_ref[...], k2_ref[0:own, :])
        values = (v0_ref[...], v1_ref[...] + v1b_ref[...], v2_ref[0:own, :])
        spans = ((0, seg), (seg, seg), (2 * seg, own))
        results = []
        for h in range(2):
            scores = []
            for j in range(3):
                s = lax.dot_general(head_q[h], keys[j], (((1,), (1,)), ((), ())),
                                    preferred_element_type=jnp.float32)
                start, length = spans[j]
                scores.append(s + bias_ref[:, start:start + length])
            top = jnp.max(scores[0], axis=1, keepdims=True)
            for j in range(1, 3):
                top = jnp.maximum(top, jnp.max(scores[j], axis=1, keepdims=True))
            total = None
            summed = None
            for j in range(3):
                w = jnp.exp(scores[j] - top)
                part = jnp.sum(w, axis=1, keepdims=True)
                pv = jnp.dot(w.astype(jnp.bfloat16), values[j], preferred_element_type=jnp.float32)
                total = part if total is None else total + part
                summed = pv if summed is None else summed + pv
            results.append(summed / total)
        out = jnp.where(low, results[0], results[1]).astype(out_ref.dtype)
        out_ref[...] = out
        rows = tile // POOL
        pool_row = lax.broadcasted_iota(jnp.int32, (rows, tile), 0)
        pool_col = lax.broadcasted_iota(jnp.int32, (rows, tile), 1)
        pool_mat = jnp.where(pool_col // POOL == pool_row, 1.0 / POOL, 0.0).astype(jnp.bfloat16)
        pool_ref[...] = jnp.dot(pool_mat, out, preferred_element_type=jnp.float32).astype(
            pool_ref.dtype)

    for step in range(seg // tile):
        pl.when(tile_index == step)(functools.partial(run, step))


def fine_attention(planes, prev0, prev1a, prev1b, qclip, kclip, heads, first_pair):
    _, tok, width = planes.shape
    head_dim = width // heads
    pair = 2 * head_dim
    pairs = prev0.shape[2] // pair
    tile = min(FINE_TILE, tok)
    nq = tok // tile
    kernel = functools.partial(fine_kernel, scale=1.0 / math.sqrt(head_dim))

    def plane_spec(plane):
        return pl.BlockSpec((None, tok, pair), lambda i, h: (plane, 0, h))

    def own_spec(plane):
        return pl.BlockSpec((None, tok, pair), lambda i, h: (plane, 0, first_pair + h))

    return pl.pallas_call(
        kernel,
        grid=(nq, pairs),
        in_specs=[
            pl.BlockSpec((tile, 1), lambda i, h: (i, 0)),
            pl.BlockSpec((1, tok), lambda i, h: (0, 0)),
            pl.BlockSpec((1, tok), lambda i, h: (0, 1)),
            pl.BlockSpec((1, tok), lambda i, h: (0, 2)),
            pl.BlockSpec((None, tile, pair), lambda i, h: (0, i, first_pair + h)),
            plane_spec(0), plane_spec(1),
            own_spec(1), own_spec(2),
            plane_spec(0), plane_spec(1),
            own_spec(1), own_spec(2),
        ],
        out_specs=[
            pl.BlockSpec((tile, pair), lambda i, h: (i, h)),
            pl.BlockSpec((tile // POOL, pair), lambda i, h: (i, h)),
        ],
        out_shape=[
            jax.ShapeDtypeStruct((tok, pairs * pair), jnp.bfloat16),
            jax.ShapeDtypeStruct((tok // POOL, pairs * pair), jnp.bfloat16),
        ],
        scratch_shapes=[pltpu.VMEM((tile, 3 * tok), jnp.float32)],
    )(qclip, kclip, kclip, kclip, planes, prev0, prev0, prev1a, prev1a, prev1b, prev1b,
      planes, planes)


def mix_kernel(fine_ref, lift_ref, out_ref):
    tile = fine_ref.shape[0]
    rows = lift_ref.shape[0]
    spread_row = lax.broadcasted_iota(jnp.int32, (tile, rows), 0)
    spread_col = lax.broadcasted_iota(jnp.int32, (tile, rows), 1)
    spread = jnp.where(spread_row // POOL == spread_col, 1.0, 0.0).astype(jnp.bfloat16)
    lifted = jnp.dot(spread, lift_ref[...], preferred_element_type=jnp.float32)
    out_ref[...] = (fine_ref[...].astype(jnp.float32) + lifted).astype(out_ref.dtype)


def mix(fine_out, lifted):
    tok, width = fine_out.shape
    tile = min(FINE_TILE, tok)
    return pl.pallas_call(
        mix_kernel,
        grid=(tok // tile,),
        in_specs=[
            pl.BlockSpec((tile, width), lambda i: (i, 0)),
            pl.BlockSpec((tile // POOL, width), lambda i: (i, 0)),
        ],
        out_specs=pl.BlockSpec((tile, width), lambda i: (i, 0)),
        out_shape=jax.ShapeDtypeStruct((tok, width), fine_out.dtype),
    )(fine_out, lifted)


def pair_swap(value, axis, from_odd):
    count = lax.axis_size(axis)
    start = 1 if from_odd else 0
    step = -1 if from_odd else 1
    return lax.ppermute(value, axis, [(source, source + step) for source in range(start, count, 2)])


def coarse_kernel(qclip_ref, kc0_ref, kc1_ref, kc2_ref, kc3_ref, q_ref,
                  k0_ref, v0_ref, k1_ref, v1_ref, k2_ref, v2_ref, k3_ref, v3_ref,
                  out_ref, *, scale):
    tile = q_ref.shape[0]
    seg = k0_ref.shape[0]
    keys = (k0_ref, k1_ref, k2_ref, k3_ref)
    values = (v0_ref, v1_ref, v2_ref, v3_ref)
    clips = (kc0_ref, kc1_ref, kc2_ref, kc3_ref)
    last = len(keys) - 1

    def run(step):
        q = q_ref[...]
        qclip = qclip_ref[...]
        own = (step + 1) * tile
        scores = []
        for j in range(len(keys)):
            length = own if j == last else seg
            allowed = clips[j][:, 0:length] == qclip
            if j == last:
                qpos = step * tile + lax.broadcasted_iota(jnp.int32, (tile, length), 0)
                kpos = lax.broadcasted_iota(jnp.int32, (tile, length), 1)
                allowed = allowed & (kpos <= qpos)
            s = lax.dot_general(q, keys[j][0:length, :], (((1,), (1,)), ((), ())),
                                preferred_element_type=jnp.float32) * scale
            scores.append(jnp.where(allowed, s, -1e30))
        top = jnp.max(scores[0], axis=1, keepdims=True)
        for j in range(1, len(keys)):
            top = jnp.maximum(top, jnp.max(scores[j], axis=1, keepdims=True))
        total = None
        summed = None
        for j in range(len(keys)):
            length = own if j == last else seg
            w = jnp.exp(scores[j] - top)
            part = jnp.sum(w, axis=1, keepdims=True)
            pv = jnp.dot(w.astype(jnp.bfloat16), values[j][0:length, :],
                         preferred_element_type=jnp.float32)
            total = part if total is None else total + part
            summed = pv if summed is None else summed + pv
        out_ref[...] = (summed / total).astype(out_ref.dtype)

    for step in range(seg // tile):
        pl.when(pl.program_id(1) == step)(functools.partial(run, step))


def coarse_attention(queries, windows, qclip, kclip, heads):
    rows, width = queries.shape
    head_dim = width // heads
    tile = min(FINE_TILE // 2, rows)
    seg = windows[0].shape[1]
    kernel = functools.partial(coarse_kernel, scale=1.0 / math.sqrt(head_dim))
    clip_specs = [pl.BlockSpec((1, seg), functools.partial(lambda j, h, i: (0, j), j))
                  for j in range(len(windows))]
    kv_specs = []
    kv_args = []
    for window in windows:
        kv_specs.append(pl.BlockSpec((None, seg, head_dim), lambda h, i: (0, 0, h)))
        kv_specs.append(pl.BlockSpec((None, seg, head_dim), lambda h, i: (1, 0, h)))
        kv_args += [window, window]
    return pl.pallas_call(
        kernel,
        grid=(heads, rows // tile),
        in_specs=[pl.BlockSpec((tile, 1), lambda h, i: (i, 0))] + clip_specs
        + [pl.BlockSpec((tile, head_dim), lambda h, i: (i, h))] + kv_specs,
        out_specs=pl.BlockSpec((tile, head_dim), lambda h, i: (i, h)),
        out_shape=jax.ShapeDtypeStruct((rows, width), jnp.bfloat16),
    )(qclip, *([kclip] * len(windows)), queries, *kv_args)


def group_order(parts, quarter):
    ordered = jnp.stack([parts[0]] + parts[:0:-1], axis=0)
    return jnp.roll(ordered, quarter, axis=0)


def attend(queries, key_rows, value_rows, allowed, heads, head_groups):
    row_count = queries.shape[0]
    feat_width = queries.shape[1]
    head_dim = feat_width // heads
    per_group = heads // head_groups
    score_scale = 1.0 / math.sqrt(head_dim)

    def split_heads(source_rows):
        return source_rows.reshape(
            source_rows.shape[0], head_groups, per_group, head_dim
        ).transpose(1, 0, 2, 3)

    def one_group(operands):
        group_queries, group_keys, group_values = operands
        scores = (
            jnp.einsum(
                "rhd,khd->hrk", group_queries, group_keys, preferred_element_type=jnp.float32
            )
            * score_scale
        )
        masked = jnp.where(allowed[None], scores, -1e30)
        row_top = jnp.max(masked, axis=2, keepdims=True)
        weights = jnp.where(allowed[None], jnp.exp(masked - row_top), 0.0)
        row_total = jnp.sum(weights, axis=2)
        summed = jnp.einsum(
            "hrk,khd->rhd",
            weights.astype(jnp.bfloat16),
            group_values,
            preferred_element_type=jnp.float32,
        )
        return summed / jnp.transpose(row_total)[:, :, None]

    results = lax.map(
        one_group, (split_heads(queries), split_heads(key_rows), split_heads(value_rows))
    )
    return results.transpose(1, 0, 2, 3).reshape(row_count, feat_width).astype(jnp.bfloat16)


def body(fine_qkv, clip_ids, w_coarse, w_out):
    tok_count = fine_qkv.shape[0]
    feat_width = fine_qkv.shape[2]
    coarse_rows = tok_count // POOL
    group_rows = QUARTERS * coarse_rows
    position = lax.axis_index("seq")
    quarter = position % QUARTERS
    cycle_place = position // QUARTERS
    planes = jnp.transpose(fine_qkv, (1, 0, 2))
    clip_front = jnp.concatenate([jnp.full((FREACH * coarse_rows,), -1, jnp.int32), clip_ids])
    key_clip = jnp.repeat(
        lax.dynamic_slice_in_dim(clip_front, position * coarse_rows, (FREACH + 1) * coarse_rows, 0),
        POOL,
    )
    own_clip = lax.dynamic_slice_in_dim(clip_ids, position * coarse_rows, coarse_rows, 0)
    query_clip = jnp.repeat(own_clip, POOL)
    head_pair_width = 2 * feat_width // FHEADS
    part_width = feat_width // HALVES
    outs = []
    projected = None
    wplanes = jnp.transpose(w_coarse, (1, 0, 2))
    gate = None
    prev1a = pair_swap(planes, "seq", False)
    for part in range(HALVES):
        own_pairs = planes[1:, :, part * part_width:(part + 1) * part_width]
        if gate is not None:
            own_pairs, _ = lax.optimization_barrier((own_pairs, gate))
        prev0 = passed_along(own_pairs, "seq", 2)
        gate = prev0
        if outs:
            prev0, _ = lax.optimization_barrier((prev0, projected))
        prev1b = pair_swap(prev0, "seq", True)
        part_out, part_pool = fine_attention(
            planes, prev0, prev1a, prev1b, query_clip.reshape(tok_count, 1),
            key_clip.reshape(1, (FREACH + 1) * tok_count), FHEADS,
            part * part_width // head_pair_width,
        )
        outs.append(part_out)
        part_weight = wplanes[:, part * part_width:(part + 1) * part_width, :]
        contribution = jnp.einsum(
            "rd,mdc->mrc", part_pool, part_weight, preferred_element_type=jnp.float32
        )
        projected = contribution if projected is None else projected + contribution
    fine_out = jnp.concatenate(outs, axis=1)
    quarter_width = w_coarse.shape[2] // QUARTERS
    projected = projected.astype(jnp.bfloat16)
    pieces = []
    for shift in range(QUARTERS):
        piece = lax.dynamic_slice_in_dim(
            projected, ((quarter + shift) % QUARTERS) * quarter_width, quarter_width, 2
        )
        pieces.append(piece if shift == 0 else within_group(piece, "seq", shift))
    grouped = group_order(pieces, quarter)
    grouped = jnp.transpose(grouped, (1, 0, 2, 3)).reshape(3, group_rows, quarter_width)
    coarse_queries = grouped[0]
    coarse_pairs = grouped[1:]
    one_back = passed_along(coarse_pairs, "seq", QUARTERS)
    two_back = passed_along(one_back, "seq", QUARTERS)
    three_back = passed_along(two_back, "seq", QUARTERS)
    earlier = [three_back, two_back, one_back]
    clip_back = jnp.concatenate([jnp.full((CREACH * group_rows,), -1, jnp.int32), clip_ids])
    coarse_key_clip = lax.dynamic_slice_in_dim(
        clip_back, cycle_place * group_rows, (CREACH + 1) * group_rows, 0
    )
    coarse_query_clip = lax.dynamic_slice_in_dim(clip_ids, cycle_place * group_rows, group_rows, 0)
    coarse_att = coarse_attention(
        coarse_queries, earlier + [coarse_pairs], coarse_query_clip.reshape(group_rows, 1),
        coarse_key_clip.reshape(1, (CREACH + 1) * group_rows), CHEADS // QUARTERS,
    )
    shares = []
    for shift in range(QUARTERS):
        share = lax.dynamic_slice_in_dim(
            coarse_att, ((quarter + shift) % QUARTERS) * coarse_rows, coarse_rows, 0
        )
        shares.append(share if shift == 0 else within_group(share, "seq", shift))
    att_rows = jnp.transpose(group_order(shares, quarter), (1, 0, 2)).reshape(
        coarse_rows, QUARTERS * quarter_width
    )
    coarse_up = jnp.dot(att_rows, w_out, preferred_element_type=jnp.float32).astype(jnp.bfloat16)
    carried = passed_along(coarse_up[-1:], "seq", 1)
    previous = jnp.concatenate([jnp.zeros_like(carried), coarse_up[:-1]], axis=0)
    clip_before = jnp.concatenate([jnp.full((1,), -1, jnp.int32), clip_ids])
    prev_clip = lax.dynamic_slice_in_dim(clip_before, position * coarse_rows, coarse_rows, 0)
    joined = prev_clip == own_clip
    lifted = jnp.where(joined[:, None], previous, jnp.zeros_like(previous))
    mixed = mix(fine_out, lifted)
    head_lift = jnp.where(joined[:1, None], carried, jnp.zeros_like(carried)).astype(jnp.float32)
    head_rows = (fine_out[:POOL].astype(jnp.float32) + head_lift).astype(mixed.dtype)
    return lax.dynamic_update_slice(mixed, head_rows, (0, 0))


def solution(mesh):
    return jax.shard_map(
        body,
        mesh=mesh,
        in_specs=(P(("groups", "seq"), None, None), P("groups"), P(), P()),
        out_specs=P(("groups", "seq"), None),
        check_vma=False,
    )
```

```python
import functools
import math

import jax
import jax.numpy as jnp
from jax import lax
from jax.experimental import pallas as pl
from jax.experimental.pallas import tpu as pltpu
from jax.sharding import PartitionSpec as P

FHEADS = 16
CHEADS = 8
POOL = 4
QUARTERS = 4
FREACH = 2
CREACH = 3
FINE_TILE = 256
HALVES = 2


def passed_along(value, axis, steps):
    count = lax.axis_size(axis)
    first, last = (max(0, -steps), min(count, count - steps))
    return lax.ppermute(value, axis, [(source, source + steps) for source in range(first, last)])


def within_group(value, axis, shift):
    count = lax.axis_size(axis)
    pairs = []
    for source in range(count):
        base = source - source % QUARTERS
        pairs.append((source, base + (source % QUARTERS + shift) % QUARTERS))
    return lax.ppermute(value, axis, pairs)


def fine_kernel(qclip_ref, kclip0_ref, kclip1_ref, kclip2_ref, q_ref,
                k0_ref, v0_ref, k1_ref, v1_ref, k1b_ref, v1b_ref, k2_ref, v2_ref,
                out_ref, pool_ref, bias_ref, *, scale):
    tile = q_ref.shape[0]
    width = q_ref.shape[1]
    half = width // 2
    seg = k0_ref.shape[0]
    tile_index = pl.program_id(0)

    @pl.when(pl.program_id(1) == 0)
    def _():
        qclip = qclip_ref[...]
        qpos = tile_index * tile + lax.broadcasted_iota(jnp.int32, (tile, seg), 0)
        kpos = lax.broadcasted_iota(jnp.int32, (tile, seg), 1)
        allowed = (
            kclip0_ref[...] == qclip,
            kclip1_ref[...] == qclip,
            (kclip2_ref[...] == qclip) & (kpos <= qpos),
        )
        for j in range(3):
            bias_ref[:, j * seg:(j + 1) * seg] = jnp.where(allowed[j], 0.0, -1e30)

    q = q_ref[...] * jnp.asarray(scale, q_ref.dtype)
    lane = lax.broadcasted_iota(jnp.int32, (1, width), 1)
    low = lane < half
    zero = jnp.zeros_like(q)
    head_q = (jnp.where(low, q, zero), jnp.where(low, zero, q))

    def run(step):
        own = (step + 1) * tile
        keys = (k0_ref[...], k1_ref[...] + k1b_ref[...], k2_ref[0:own, :])
        values = (v0_ref[...], v1_ref[...] + v1b_ref[...], v2_ref[0:own, :])
        spans = ((0, seg), (seg, seg), (2 * seg, own))
        results = []
        for h in range(2):
            scores = []
            for j in range(3):
                s = lax.dot_general(head_q[h], keys[j], (((1,), (1,)), ((), ())),
                                    preferred_element_type=jnp.float32)
                start, length = spans[j]
                scores.append(s + bias_ref[:, start:start + length])
            top = jnp.max(scores[0], axis=1, keepdims=True)
            for j in range(1, 3):
                top = jnp.maximum(top, jnp.max(scores[j], axis=1, keepdims=True))
            total = None
            summed = None
            for j in range(3):
                w = jnp.exp(scores[j] - top)
                part = jnp.sum(w, axis=1, keepdims=True)
                pv = jnp.dot(w.astype(jnp.bfloat16), values[j], preferred_element_type=jnp.float32)
                total = part if total is None else total + part
                summed = pv if summed is None else summed + pv
            results.append(summed / total)
        out = jnp.where(low, results[0], results[1]).astype(out_ref.dtype)
        out_ref[...] = out
        rows = tile // POOL
        pool_row = lax.broadcasted_iota(jnp.int32, (rows, tile), 0)
        pool_col = lax.broadcasted_iota(jnp.int32, (rows, tile), 1)
        pool_mat = jnp.where(pool_col // POOL == pool_row, 1.0 / POOL, 0.0).astype(jnp.bfloat16)
        pool_ref[...] = jnp.dot(pool_mat, out, preferred_element_type=jnp.float32).astype(
            pool_ref.dtype)

    for step in range(seg // tile):
        pl.when(tile_index == step)(functools.partial(run, step))


def fine_attention(planes, prev0, prev1a, prev1b, qclip, kclip, heads, first_pair):
    _, tok, width = planes.shape
    head_dim = width // heads
    pair = 2 * head_dim
    pairs = prev0.shape[2] // pair
    tile = min(FINE_TILE, tok)
    nq = tok // tile
    kernel = functools.partial(fine_kernel, scale=1.0 / math.sqrt(head_dim))

    def plane_spec(plane):
        return pl.BlockSpec((None, tok, pair), lambda i, h: (plane, 0, h))

    def own_spec(plane):
        return pl.BlockSpec((None, tok, pair), lambda i, h: (plane, 0, first_pair + h))

    return pl.pallas_call(
        kernel,
        grid=(nq, pairs),
        in_specs=[
            pl.BlockSpec((tile, 1), lambda i, h: (i, 0)),
            pl.BlockSpec((1, tok), lambda i, h: (0, 0)),
            pl.BlockSpec((1, tok), lambda i, h: (0, 1)),
            pl.BlockSpec((1, tok), lambda i, h: (0, 2)),
            pl.BlockSpec((None, tile, pair), lambda i, h: (0, i, first_pair + h)),
            plane_spec(0), plane_spec(1),
            own_spec(1), own_spec(2),
            plane_spec(0), plane_spec(1),
            own_spec(1), own_spec(2),
        ],
        out_specs=[
            pl.BlockSpec((tile, pair), lambda i, h: (i, h)),
            pl.BlockSpec((tile // POOL, pair), lambda i, h: (i, h)),
        ],
        out_shape=[
            jax.ShapeDtypeStruct((tok, pairs * pair), jnp.bfloat16),
            jax.ShapeDtypeStruct((tok // POOL, pairs * pair), jnp.bfloat16),
        ],
        scratch_shapes=[pltpu.VMEM((tile, 3 * tok), jnp.float32)],
    )(qclip, kclip, kclip, kclip, planes, prev0, prev0, prev1a, prev1a, prev1b, prev1b,
      planes, planes)


def mix_kernel(fine_ref, lift_ref, out_ref):
    tile = fine_ref.shape[0]
    rows = lift_ref.shape[0]
    spread_row = lax.broadcasted_iota(jnp.int32, (tile, rows), 0)
    spread_col = lax.broadcasted_iota(jnp.int32, (tile, rows), 1)
    spread = jnp.where(spread_row // POOL == spread_col, 1.0, 0.0).astype(jnp.bfloat16)
    lifted = jnp.dot(spread, lift_ref[...], preferred_element_type=jnp.float32)
    out_ref[...] = (fine_ref[...].astype(jnp.float32) + lifted).astype(out_ref.dtype)


def mix(fine_out, lifted):
    tok, width = fine_out.shape
    tile = min(FINE_TILE // 2, tok)
    return pl.pallas_call(
        mix_kernel,
        grid=(tok // tile,),
        in_specs=[
            pl.BlockSpec((tile, width), lambda i: (i, 0)),
            pl.BlockSpec((tile // POOL, width), lambda i: (i, 0)),
        ],
        out_specs=pl.BlockSpec((tile, width), lambda i: (i, 0)),
        out_shape=jax.ShapeDtypeStruct((tok, width), fine_out.dtype),
    )(fine_out, lifted)


def pair_swap(value, axis, from_odd):
    count = lax.axis_size(axis)
    start = 1 if from_odd else 0
    step = -1 if from_odd else 1
    return lax.ppermute(value, axis, [(source, source + step) for source in range(start, count, 2)])


def coarse_kernel(qclip_ref, kc0_ref, kc1_ref, kc2_ref, kc3_ref, q_ref,
                  k0_ref, v0_ref, k1_ref, v1_ref, k2_ref, v2_ref, k3_ref, v3_ref,
                  out_ref, *, scale):
    tile = q_ref.shape[0]
    seg = k0_ref.shape[0]
    keys = (k0_ref, k1_ref, k2_ref, k3_ref)
    values = (v0_ref, v1_ref, v2_ref, v3_ref)
    clips = (kc0_ref, kc1_ref, kc2_ref, kc3_ref)
    last = len(keys) - 1

    def run(step):
        q = q_ref[...]
        qclip = qclip_ref[...]
        own = (step + 1) * tile
        scores = []
        for j in range(len(keys)):
            length = own if j == last else seg
            allowed = clips[j][:, 0:length] == qclip
            if j == last:
                qpos = step * tile + lax.broadcasted_iota(jnp.int32, (tile, length), 0)
                kpos = lax.broadcasted_iota(jnp.int32, (tile, length), 1)
                allowed = allowed & (kpos <= qpos)
            s = lax.dot_general(q, keys[j][0:length, :], (((1,), (1,)), ((), ())),
                                preferred_element_type=jnp.float32) * scale
            scores.append(jnp.where(allowed, s, -1e30))
        top = jnp.max(scores[0], axis=1, keepdims=True)
        for j in range(1, len(keys)):
            top = jnp.maximum(top, jnp.max(scores[j], axis=1, keepdims=True))
        total = None
        summed = None
        for j in range(len(keys)):
            length = own if j == last else seg
            w = jnp.exp(scores[j] - top)
            part = jnp.sum(w, axis=1, keepdims=True)
            pv = jnp.dot(w.astype(jnp.bfloat16), values[j][0:length, :],
                         preferred_element_type=jnp.float32)
            total = part if total is None else total + part
            summed = pv if summed is None else summed + pv
        out_ref[...] = (summed / total).astype(out_ref.dtype)

    for step in range(seg // tile):
        pl.when(pl.program_id(1) == step)(functools.partial(run, step))


def coarse_attention(queries, windows, qclip, kclip, heads):
    rows, width = queries.shape
    head_dim = width // heads
    tile = min(FINE_TILE, rows)
    seg = windows[0].shape[1]
    kernel = functools.partial(coarse_kernel, scale=1.0 / math.sqrt(head_dim))
    clip_specs = [pl.BlockSpec((1, seg), functools.partial(lambda j, h, i: (0, j), j))
                  for j in range(len(windows))]
    kv_specs = []
    kv_args = []
    for window in windows:
        kv_specs.append(pl.BlockSpec((None, seg, head_dim), lambda h, i: (0, 0, h)))
        kv_specs.append(pl.BlockSpec((None, seg, head_dim), lambda h, i: (1, 0, h)))
        kv_args += [window, window]
    return pl.pallas_call(
        kernel,
        grid=(heads, rows // tile),
        in_specs=[pl.BlockSpec((tile, 1), lambda h, i: (i, 0))] + clip_specs
        + [pl.BlockSpec((tile, head_dim), lambda h, i: (i, h))] + kv_specs,
        out_specs=pl.BlockSpec((tile, head_dim), lambda h, i: (i, h)),
        out_shape=jax.ShapeDtypeStruct((rows, width), jnp.bfloat16),
    )(qclip, *([kclip] * len(windows)), queries, *kv_args)


def group_order(parts, quarter):
    ordered = jnp.stack([parts[0]] + parts[:0:-1], axis=0)
    return jnp.roll(ordered, quarter, axis=0)


def attend(queries, key_rows, value_rows, allowed, heads, head_groups):
    row_count = queries.shape[0]
    feat_width = queries.shape[1]
    head_dim = feat_width // heads
    per_group = heads // head_groups
    score_scale = 1.0 / math.sqrt(head_dim)

    def split_heads(source_rows):
        return source_rows.reshape(
            source_rows.shape[0], head_groups, per_group, head_dim
        ).transpose(1, 0, 2, 3)

    def one_group(operands):
        group_queries, group_keys, group_values = operands
        scores = (
            jnp.einsum(
                "rhd,khd->hrk", group_queries, group_keys, preferred_element_type=jnp.float32
            )
            * score_scale
        )
        masked = jnp.where(allowed[None], scores, -1e30)
        row_top = jnp.max(masked, axis=2, keepdims=True)
        weights = jnp.where(allowed[None], jnp.exp(masked - row_top), 0.0)
        row_total = jnp.sum(weights, axis=2)
        summed = jnp.einsum(
            "hrk,khd->rhd",
            weights.astype(jnp.bfloat16),
            group_values,
            preferred_element_type=jnp.float32,
        )
        return summed / jnp.transpose(row_total)[:, :, None]

    results = lax.map(
        one_group, (split_heads(queries), split_heads(key_rows), split_heads(value_rows))
    )
    return results.transpose(1, 0, 2, 3).reshape(row_count, feat_width).astype(jnp.bfloat16)


def body(fine_qkv, clip_ids, w_coarse, w_out):
    tok_count = fine_qkv.shape[0]
    feat_width = fine_qkv.shape[2]
    coarse_rows = tok_count // POOL
    group_rows = QUARTERS * coarse_rows
    position = lax.axis_index("seq")
    quarter = position % QUARTERS
    cycle_place = position // QUARTERS
    planes = jnp.transpose(fine_qkv, (1, 0, 2))
    clip_front = jnp.concatenate([jnp.full((FREACH * coarse_rows,), -1, jnp.int32), clip_ids])
    key_clip = jnp.repeat(
        lax.dynamic_slice_in_dim(clip_front, position * coarse_rows, (FREACH + 1) * coarse_rows, 0),
        POOL,
    )
    own_clip = lax.dynamic_slice_in_dim(clip_ids, position * coarse_rows, coarse_rows, 0)
    query_clip = jnp.repeat(own_clip, POOL)
    head_pair_width = 2 * feat_width // FHEADS
    part_width = feat_width // HALVES
    outs = []
    projected = None
    wplanes = jnp.transpose(w_coarse, (1, 0, 2))
    gate = None
    prev1a = pair_swap(planes, "seq", False)
    for part in range(HALVES):
        own_pairs = planes[1:, :, part * part_width:(part + 1) * part_width]
        if gate is not None:
            own_pairs, _ = lax.optimization_barrier((own_pairs, gate))
        prev0 = passed_along(own_pairs, "seq", 2)
        gate = prev0
        if outs:
            prev0, _ = lax.optimization_barrier((prev0, projected))
        prev1b = pair_swap(prev0, "seq", True)
        part_out, part_pool = fine_attention(
            planes, prev0, prev1a, prev1b, query_clip.reshape(tok_count, 1),
            key_clip.reshape(1, (FREACH + 1) * tok_count), FHEADS,
            part * part_width // head_pair_width,
        )
        outs.append(part_out)
        part_weight = wplanes[:, part * part_width:(part + 1) * part_width, :]
        contribution = jnp.einsum(
            "rd,mdc->mrc", part_pool, part_weight, preferred_element_type=jnp.float32
        )
        projected = contribution if projected is None else projected + contribution
    fine_out = jnp.concatenate(outs, axis=1)
    quarter_width = w_coarse.shape[2] // QUARTERS
    projected = projected.astype(jnp.bfloat16)
    pieces = []
    for shift in range(QUARTERS):
        piece = lax.dynamic_slice_in_dim(
            projected, ((quarter + shift) % QUARTERS) * quarter_width, quarter_width, 2
        )
        pieces.append(piece if shift == 0 else within_group(piece, "seq", shift))
    grouped = group_order(pieces, quarter)
    grouped = jnp.transpose(grouped, (1, 0, 2, 3)).reshape(3, group_rows, quarter_width)
    coarse_queries = grouped[0]
    coarse_pairs = grouped[1:]
    one_back = passed_along(coarse_pairs, "seq", QUARTERS)
    two_back = passed_along(one_back, "seq", QUARTERS)
    three_back = passed_along(two_back, "seq", QUARTERS)
    earlier = [three_back, two_back, one_back]
    clip_back = jnp.concatenate([jnp.full((CREACH * group_rows,), -1, jnp.int32), clip_ids])
    coarse_key_clip = lax.dynamic_slice_in_dim(
        clip_back, cycle_place * group_rows, (CREACH + 1) * group_rows, 0
    )
    coarse_query_clip = lax.dynamic_slice_in_dim(clip_ids, cycle_place * group_rows, group_rows, 0)
    coarse_att = coarse_attention(
        coarse_queries, earlier + [coarse_pairs], coarse_query_clip.reshape(group_rows, 1),
        coarse_key_clip.reshape(1, (CREACH + 1) * group_rows), CHEADS // QUARTERS,
    )
    shares = []
    for shift in range(QUARTERS):
        share = lax.dynamic_slice_in_dim(
            coarse_att, ((quarter + shift) % QUARTERS) * coarse_rows, coarse_rows, 0
        )
        shares.append(share if shift == 0 else within_group(share, "seq", shift))
    att_rows = jnp.transpose(group_order(shares, quarter), (1, 0, 2)).reshape(
        coarse_rows, QUARTERS * quarter_width
    )
    coarse_up = jnp.dot(att_rows, w_out, preferred_element_type=jnp.float32).astype(jnp.bfloat16)
    carried = passed_along(coarse_up[-1:], "seq", 1)
    previous = jnp.concatenate([jnp.zeros_like(carried), coarse_up[:-1]], axis=0)
    clip_before = jnp.concatenate([jnp.full((1,), -1, jnp.int32), clip_ids])
    prev_clip = lax.dynamic_slice_in_dim(clip_before, position * coarse_rows, coarse_rows, 0)
    joined = prev_clip == own_clip
    lifted = jnp.where(joined[:, None], previous, jnp.zeros_like(previous))
    mixed = mix(fine_out, lifted)
    head_lift = jnp.where(joined[:1, None], carried, jnp.zeros_like(carried)).astype(jnp.float32)
    head_rows = (fine_out[:POOL].astype(jnp.float32) + head_lift).astype(mixed.dtype)
    return lax.dynamic_update_slice(mixed, head_rows, (0, 0))


def solution(mesh):
    return jax.shard_map(
        body,
        mesh=mesh,
        in_specs=(P(("groups", "seq"), None, None), P("groups"), P(), P()),
        out_specs=P(("groups", "seq"), None),
        check_vma=False,
    )
```

```python
import functools
import math

import jax
import jax.numpy as jnp
from jax import lax
from jax.experimental import pallas as pl
from jax.experimental.pallas import tpu as pltpu
from jax.sharding import PartitionSpec as P

FHEADS = 16
CHEADS = 8
POOL = 4
QUARTERS = 4
FREACH = 2
CREACH = 3
FINE_TILE = 256
HALVES = 2


def passed_along(value, axis, steps):
    count = lax.axis_size(axis)
    first, last = (max(0, -steps), min(count, count - steps))
    return lax.ppermute(value, axis, [(source, source + steps) for source in range(first, last)])


def within_group(value, axis, shift):
    count = lax.axis_size(axis)
    pairs = []
    for source in range(count):
        base = source - source % QUARTERS
        pairs.append((source, base + (source % QUARTERS + shift) % QUARTERS))
    return lax.ppermute(value, axis, pairs)


def fine_kernel(qclip_ref, kclip0_ref, kclip1_ref, kclip2_ref, q_ref,
                k0_ref, v0_ref, k1_ref, v1_ref, k1b_ref, v1b_ref, k2_ref, v2_ref,
                out_ref, pool_ref, bias_ref, *, scale):
    tile = q_ref.shape[0]
    width = q_ref.shape[1]
    half = width // 2
    seg = k0_ref.shape[0]
    tile_index = pl.program_id(0)

    @pl.when(pl.program_id(1) == 0)
    def _():
        qclip = qclip_ref[...]
        qpos = tile_index * tile + lax.broadcasted_iota(jnp.int32, (tile, seg), 0)
        kpos = lax.broadcasted_iota(jnp.int32, (tile, seg), 1)
        allowed = (
            kclip0_ref[...] == qclip,
            kclip1_ref[...] == qclip,
            (kclip2_ref[...] == qclip) & (kpos <= qpos),
        )
        for j in range(3):
            bias_ref[:, j * seg:(j + 1) * seg] = jnp.where(allowed[j], 0.0, -1e30)

    q = q_ref[...] * jnp.asarray(scale, q_ref.dtype)
    lane = lax.broadcasted_iota(jnp.int32, (1, width), 1)
    low = lane < half
    zero = jnp.zeros_like(q)
    head_q = (jnp.where(low, q, zero), jnp.where(low, zero, q))

    def run(step):
        own = (step + 1) * tile
        keys = (k0_ref[...], k1_ref[...] + k1b_ref[...], k2_ref[0:own, :])
        values = (v0_ref[...], v1_ref[...] + v1b_ref[...], v2_ref[0:own, :])
        spans = ((0, seg), (seg, seg), (2 * seg, own))
        results = []
        for h in range(2):
            scores = []
            for j in range(3):
                s = lax.dot_general(head_q[h], keys[j], (((1,), (1,)), ((), ())),
                                    preferred_element_type=jnp.float32)
                start, length = spans[j]
                scores.append(s + bias_ref[:, start:start + length])
            top = jnp.max(scores[0], axis=1, keepdims=True)
            for j in range(1, 3):
                top = jnp.maximum(top, jnp.max(scores[j], axis=1, keepdims=True))
            total = None
            summed = None
            for j in range(3):
                w = jnp.exp(scores[j] - top)
                part = jnp.sum(w, axis=1, keepdims=True)
                pv = jnp.dot(w.astype(jnp.bfloat16), values[j], preferred_element_type=jnp.float32)
                total = part if total is None else total + part
                summed = pv if summed is None else summed + pv
            results.append(summed / total)
        out = jnp.where(low, results[0], results[1]).astype(out_ref.dtype)
        out_ref[...] = out
        rows = tile // POOL
        pool_row = lax.broadcasted_iota(jnp.int32, (rows, tile), 0)
        pool_col = lax.broadcasted_iota(jnp.int32, (rows, tile), 1)
        pool_mat = jnp.where(pool_col // POOL == pool_row, 1.0 / POOL, 0.0).astype(jnp.bfloat16)
        pool_ref[...] = jnp.dot(pool_mat, out, preferred_element_type=jnp.float32).astype(
            pool_ref.dtype)

    for step in range(seg // tile):
        pl.when(tile_index == step)(functools.partial(run, step))


def fine_attention(planes, prev0, prev1a, prev1b, qclip, kclip, heads, first_pair):
    _, tok, width = planes.shape
    head_dim = width // heads
    pair = 2 * head_dim
    pairs = prev0.shape[2] // pair
    tile = min(FINE_TILE, tok)
    nq = tok // tile
    kernel = functools.partial(fine_kernel, scale=1.0 / math.sqrt(head_dim))

    def plane_spec(plane):
        return pl.BlockSpec((None, tok, pair), lambda i, h: (plane, 0, h))

    def own_spec(plane):
        return pl.BlockSpec((None, tok, pair), lambda i, h: (plane, 0, first_pair + h))

    return pl.pallas_call(
        kernel,
        grid=(nq, pairs),
        in_specs=[
            pl.BlockSpec((tile, 1), lambda i, h: (i, 0)),
            pl.BlockSpec((1, tok), lambda i, h: (0, 0)),
            pl.BlockSpec((1, tok), lambda i, h: (0, 1)),
            pl.BlockSpec((1, tok), lambda i, h: (0, 2)),
            pl.BlockSpec((None, tile, pair), lambda i, h: (0, i, first_pair + h)),
            plane_spec(0), plane_spec(1),
            own_spec(1), own_spec(2),
            plane_spec(0), plane_spec(1),
            own_spec(1), own_spec(2),
        ],
        out_specs=[
            pl.BlockSpec((tile, pair), lambda i, h: (i, h)),
            pl.BlockSpec((tile // POOL, pair), lambda i, h: (i, h)),
        ],
        out_shape=[
            jax.ShapeDtypeStruct((tok, pairs * pair), jnp.bfloat16),
            jax.ShapeDtypeStruct((tok // POOL, pairs * pair), jnp.bfloat16),
        ],
        scratch_shapes=[pltpu.VMEM((tile, 3 * tok), jnp.float32)],
    )(qclip, kclip, kclip, kclip, planes, prev0, prev0, prev1a, prev1a, prev1b, prev1b,
      planes, planes)


def mix_kernel(fine_ref, lift_ref, out_ref):
    tile = fine_ref.shape[0]
    rows = lift_ref.shape[0]
    spread_row = lax.broadcasted_iota(jnp.int32, (tile, rows), 0)
    spread_col = lax.broadcasted_iota(jnp.int32, (tile, rows), 1)
    spread = jnp.where(spread_row // POOL == spread_col, 1.0, 0.0).astype(jnp.bfloat16)
    lifted = jnp.dot(spread, lift_ref[...], preferred_element_type=jnp.float32)
    out_ref[...] = (fine_ref[...].astype(jnp.float32) + lifted).astype(out_ref.dtype)


def mix(fine_out, lifted):
    tok, width = fine_out.shape
    tile = min(2 * FINE_TILE, tok)
    return pl.pallas_call(
        mix_kernel,
        grid=(tok // tile,),
        in_specs=[
            pl.BlockSpec((tile, width), lambda i: (i, 0)),
            pl.BlockSpec((tile // POOL, width), lambda i: (i, 0)),
        ],
        out_specs=pl.BlockSpec((tile, width), lambda i: (i, 0)),
        out_shape=jax.ShapeDtypeStruct((tok, width), fine_out.dtype),
    )(fine_out, lifted)


def pair_swap(value, axis, from_odd):
    count = lax.axis_size(axis)
    start = 1 if from_odd else 0
    step = -1 if from_odd else 1
    return lax.ppermute(value, axis, [(source, source + step) for source in range(start, count, 2)])


def coarse_kernel(qclip_ref, kc0_ref, kc1_ref, kc2_ref, kc3_ref, q_ref,
                  k0_ref, v0_ref, k1_ref, v1_ref, k2_ref, v2_ref, k3_ref, v3_ref,
                  out_ref, *, scale):
    tile = q_ref.shape[0]
    seg = k0_ref.shape[0]
    keys = (k0_ref, k1_ref, k2_ref, k3_ref)
    values = (v0_ref, v1_ref, v2_ref, v3_ref)
    clips = (kc0_ref, kc1_ref, kc2_ref, kc3_ref)
    last = len(keys) - 1

    def run(step):
        q = q_ref[...]
        qclip = qclip_ref[...]
        own = (step + 1) * tile
        scores = []
        for j in range(len(keys)):
            length = own if j == last else seg
            allowed = clips[j][:, 0:length] == qclip
            if j == last:
                qpos = step * tile + lax.broadcasted_iota(jnp.int32, (tile, length), 0)
                kpos = lax.broadcasted_iota(jnp.int32, (tile, length), 1)
                allowed = allowed & (kpos <= qpos)
            s = lax.dot_general(q, keys[j][0:length, :], (((1,), (1,)), ((), ())),
                                preferred_element_type=jnp.float32) * scale
            scores.append(jnp.where(allowed, s, -1e30))
        top = jnp.max(scores[0], axis=1, keepdims=True)
        for j in range(1, len(keys)):
            top = jnp.maximum(top, jnp.max(scores[j], axis=1, keepdims=True))
        total = None
        summed = None
        for j in range(len(keys)):
            length = own if j == last else seg
            w = jnp.exp(scores[j] - top)
            part = jnp.sum(w, axis=1, keepdims=True)
            pv = jnp.dot(w.astype(jnp.bfloat16), values[j][0:length, :],
                         preferred_element_type=jnp.float32)
            total = part if total is None else total + part
            summed = pv if summed is None else summed + pv
        out_ref[...] = (summed / total).astype(out_ref.dtype)

    for step in range(seg // tile):
        pl.when(pl.program_id(1) == step)(functools.partial(run, step))


def coarse_attention(queries, windows, qclip, kclip, heads):
    rows, width = queries.shape
    head_dim = width // heads
    tile = min(FINE_TILE, rows)
    seg = windows[0].shape[1]
    kernel = functools.partial(coarse_kernel, scale=1.0 / math.sqrt(head_dim))
    clip_specs = [pl.BlockSpec((1, seg), functools.partial(lambda j, h, i: (0, j), j))
                  for j in range(len(windows))]
    kv_specs = []
    kv_args = []
    for window in windows:
        kv_specs.append(pl.BlockSpec((None, seg, head_dim), lambda h, i: (0, 0, h)))
        kv_specs.append(pl.BlockSpec((None, seg, head_dim), lambda h, i: (1, 0, h)))
        kv_args += [window, window]
    return pl.pallas_call(
        kernel,
        grid=(heads, rows // tile),
        in_specs=[pl.BlockSpec((tile, 1), lambda h, i: (i, 0))] + clip_specs
        + [pl.BlockSpec((tile, head_dim), lambda h, i: (i, h))] + kv_specs,
        out_specs=pl.BlockSpec((tile, head_dim), lambda h, i: (i, h)),
        out_shape=jax.ShapeDtypeStruct((rows, width), jnp.bfloat16),
    )(qclip, *([kclip] * len(windows)), queries, *kv_args)


def group_order(parts, quarter):
    ordered = jnp.stack([parts[0]] + parts[:0:-1], axis=0)
    return jnp.roll(ordered, quarter, axis=0)


def attend(queries, key_rows, value_rows, allowed, heads, head_groups):
    row_count = queries.shape[0]
    feat_width = queries.shape[1]
    head_dim = feat_width // heads
    per_group = heads // head_groups
    score_scale = 1.0 / math.sqrt(head_dim)

    def split_heads(source_rows):
        return source_rows.reshape(
            source_rows.shape[0], head_groups, per_group, head_dim
        ).transpose(1, 0, 2, 3)

    def one_group(operands):
        group_queries, group_keys, group_values = operands
        scores = (
            jnp.einsum(
                "rhd,khd->hrk", group_queries, group_keys, preferred_element_type=jnp.float32
            )
            * score_scale
        )
        masked = jnp.where(allowed[None], scores, -1e30)
        row_top = jnp.max(masked, axis=2, keepdims=True)
        weights = jnp.where(allowed[None], jnp.exp(masked - row_top), 0.0)
        row_total = jnp.sum(weights, axis=2)
        summed = jnp.einsum(
            "hrk,khd->rhd",
            weights.astype(jnp.bfloat16),
            group_values,
            preferred_element_type=jnp.float32,
        )
        return summed / jnp.transpose(row_total)[:, :, None]

    results = lax.map(
        one_group, (split_heads(queries), split_heads(key_rows), split_heads(value_rows))
    )
    return results.transpose(1, 0, 2, 3).reshape(row_count, feat_width).astype(jnp.bfloat16)


def body(fine_qkv, clip_ids, w_coarse, w_out):
    tok_count = fine_qkv.shape[0]
    feat_width = fine_qkv.shape[2]
    coarse_rows = tok_count // POOL
    group_rows = QUARTERS * coarse_rows
    position = lax.axis_index("seq")
    quarter = position % QUARTERS
    cycle_place = position // QUARTERS
    planes = jnp.transpose(fine_qkv, (1, 0, 2))
    clip_front = jnp.concatenate([jnp.full((FREACH * coarse_rows,), -1, jnp.int32), clip_ids])
    key_clip = jnp.repeat(
        lax.dynamic_slice_in_dim(clip_front, position * coarse_rows, (FREACH + 1) * coarse_rows, 0),
        POOL,
    )
    own_clip = lax.dynamic_slice_in_dim(clip_ids, position * coarse_rows, coarse_rows, 0)
    query_clip = jnp.repeat(own_clip, POOL)
    head_pair_width = 2 * feat_width // FHEADS
    part_width = feat_width // HALVES
    outs = []
    projected = None
    wplanes = jnp.transpose(w_coarse, (1, 0, 2))
    gate = None
    prev1a = pair_swap(planes, "seq", False)
    for part in range(HALVES):
        own_pairs = planes[1:, :, part * part_width:(part + 1) * part_width]
        if gate is not None:
            own_pairs, _ = lax.optimization_barrier((own_pairs, gate))
        prev0 = passed_along(own_pairs, "seq", 2)
        gate = prev0
        if outs:
            prev0, _ = lax.optimization_barrier((prev0, projected))
        prev1b = pair_swap(prev0, "seq", True)
        part_out, part_pool = fine_attention(
            planes, prev0, prev1a, prev1b, query_clip.reshape(tok_count, 1),
            key_clip.reshape(1, (FREACH + 1) * tok_count), FHEADS,
            part * part_width // head_pair_width,
        )
        outs.append(part_out)
        part_weight = wplanes[:, part * part_width:(part + 1) * part_width, :]
        contribution = jnp.einsum(
            "rd,mdc->mrc", part_pool, part_weight, preferred_element_type=jnp.float32
        )
        projected = contribution if projected is None else projected + contribution
    fine_out = jnp.concatenate(outs, axis=1)
    quarter_width = w_coarse.shape[2] // QUARTERS
    projected = projected.astype(jnp.bfloat16)
    pieces = []
    for shift in range(QUARTERS):
        piece = lax.dynamic_slice_in_dim(
            projected, ((quarter + shift) % QUARTERS) * quarter_width, quarter_width, 2
        )
        pieces.append(piece if shift == 0 else within_group(piece, "seq", shift))
    grouped = group_order(pieces, quarter)
    grouped = jnp.transpose(grouped, (1, 0, 2, 3)).reshape(3, group_rows, quarter_width)
    coarse_queries = grouped[0]
    coarse_pairs = grouped[1:]
    one_back = passed_along(coarse_pairs, "seq", QUARTERS)
    two_back = passed_along(one_back, "seq", QUARTERS)
    three_back = passed_along(two_back, "seq", QUARTERS)
    earlier = [three_back, two_back, one_back]
    clip_back = jnp.concatenate([jnp.full((CREACH * group_rows,), -1, jnp.int32), clip_ids])
    coarse_key_clip = lax.dynamic_slice_in_dim(
        clip_back, cycle_place * group_rows, (CREACH + 1) * group_rows, 0
    )
    coarse_query_clip = lax.dynamic_slice_in_dim(clip_ids, cycle_place * group_rows, group_rows, 0)
    coarse_att = coarse_attention(
        coarse_queries, earlier + [coarse_pairs], coarse_query_clip.reshape(group_rows, 1),
        coarse_key_clip.reshape(1, (CREACH + 1) * group_rows), CHEADS // QUARTERS,
    )
    shares = []
    for shift in range(QUARTERS):
        share = lax.dynamic_slice_in_dim(
            coarse_att, ((quarter + shift) % QUARTERS) * coarse_rows, coarse_rows, 0
        )
        shares.append(share if shift == 0 else within_group(share, "seq", shift))
    att_rows = jnp.transpose(group_order(shares, quarter), (1, 0, 2)).reshape(
        coarse_rows, QUARTERS * quarter_width
    )
    coarse_up = jnp.dot(att_rows, w_out, preferred_element_type=jnp.float32).astype(jnp.bfloat16)
    carried = passed_along(coarse_up[-1:], "seq", 1)
    previous = jnp.concatenate([jnp.zeros_like(carried), coarse_up[:-1]], axis=0)
    clip_before = jnp.concatenate([jnp.full((1,), -1, jnp.int32), clip_ids])
    prev_clip = lax.dynamic_slice_in_dim(clip_before, position * coarse_rows, coarse_rows, 0)
    joined = prev_clip == own_clip
    lifted = jnp.where(joined[:, None], previous, jnp.zeros_like(previous))
    mixed = mix(fine_out, lifted)
    head_lift = jnp.where(joined[:1, None], carried, jnp.zeros_like(carried)).astype(jnp.float32)
    head_rows = (fine_out[:POOL].astype(jnp.float32) + head_lift).astype(mixed.dtype)
    return lax.dynamic_update_slice(mixed, head_rows, (0, 0))


def solution(mesh):
    return jax.shard_map(
        body,
        mesh=mesh,
        in_specs=(P(("groups", "seq"), None, None), P("groups"), P(), P()),
        out_specs=P(("groups", "seq"), None),
        check_vma=False,
    )
```
